32 devices in a mesh: fsdp: 8 (over z, x), tensor: 4 (over y, core).
Axes of the slice: x: 2, y: 2, z: 4, core: 2. Of those that a mesh axis runs over, the one named last changes fastest.
Arguments:
- hidden: bfloat16 [16384, 1024], P(('fsdp', 'tensor')), may hold values from -6 to 6
- out_grad: bfloat16 [16384, 1024], P(('fsdp', 'tensor')), may hold values from -6 to 6
- lengths: int32 [4, 3], replicated, may hold values from 0 to 4096, as said below
- q_weight: float32 [1024, 2048], P('fsdp', 'tensor'), may hold values from -0.1875 to 0.1875
- key_matrix: float32 [1024, 1024], P('fsdp', 'tensor'), may hold values from -0.1875 to 0.1875
- value_matrix: float32 [1024, 1024], P('fsdp', 'tensor'), may hold values from -0.1875 to 0.1875
- o_weight: float32 [2048, 1024], P('tensor', 'fsdp'), may hold values from -0.375 to 0.375
- gate_weight: float32 [1024, 3072], P('fsdp', 'tensor'), may hold values from -0.1875 to 0.1875
- up_weight: float32 [1024, 3072], P('fsdp', 'tensor'), may hold values from -0.1875 to 0.1875
- down_weight: float32 [3072, 1024], P('tensor', 'fsdp'), may hold values from -0.109375 to 0.109375
- input_gain: float32 [1024], P('fsdp'), may hold values from 0.1 to 1.9
- q_gain: float32 [128], P('fsdp'), may hold values from 1.2 to 1.8
- k_gain: float32 [128], P('fsdp'), may hold values from 1.2 to 1.8
- post_gain: float32 [1024], P('fsdp'), may hold values from 0.1 to 1.9
Outputs:
- output: bfloat16 [16384, 1024], P(('fsdp', 'tensor'))
- input_grad: bfloat16 [16384, 1024], P(('fsdp', 'tensor'))
- q_weight_grad: float32 [1024, 2048], P('fsdp', 'tensor')
- k_weight_grad: float32 [1024, 1024], P('fsdp', 'tensor')
- v_weight_grad: float32 [1024, 1024], P('fsdp', 'tensor')
- o_weight_grad: float32 [2048, 1024], P('tensor', 'fsdp')
- gate_weight_grad: float32 [1024, 3072], P('fsdp', 'tensor')
- up_weight_grad: float32 [1024, 3072], P('fsdp', 'tensor')
- down_weight_grad: float32 [3072, 1024], P('tensor', 'fsdp')
- input_gain_grad: float32 [1024], P('fsdp')
- q_gain_grad: float32 [128], P('fsdp')
- k_gain_grad: float32 [128], P('fsdp')
- post_gain_grad: float32 [1024], P('fsdp')
The draws below stay inside these ranges and needn't reach their ends.
Inputs may be any that keep to these rules, and one draw needn't show every extreme that they name: `lengths`: row s lists the sequences packed from the start of slot s: its first one to 3 entries are 1024 or more, the rest are zero; a row sums to more than half of 4096 and at most 4096; row 0 holds one sequence of 4096.
All inputs are finite; a program needn't handle non-finite values.
Results may differ from the reference program's by a relative error of at most 0.022.
The reference program's roundings to bfloat16 on the way count: a program that leaves them out, or rounds other values in their place, can miss the bound.
Values may be sent and summed in bfloat16 or wider, within the bound.
No kernel may reach another device: no remote copies, remote signals or barrier semaphores. Data moves between devices by JAX's collectives and lax.ppermute only.
A program may use at most 192 MiB of HBM per device.

```python
import jax
import jax.numpy as jnp
from jax import lax

MODEL_WIDTH = 1024
QUERY_HEADS = 16
KEY_VALUE_HEADS = 8
HEAD_SIZE = 128
FF = 3072
SLOT_TOKENS = 4096
MINLEN = 1024
DOCS = 3
SLOT_COUNT = 4
TOKENS = 16384


def draw_lengths(key, part):
    count_key, fill_key, weight_key = jax.random.split(key, 3)
    most = min(DOCS, SLOT_TOKENS // MINLEN)
    first = jnp.arange(SLOT_COUNT) == 0
    count = jax.random.randint(count_key, (SLOT_COUNT,), 1, most + 1).astype(jnp.int32)
    count = jnp.where(first, 1, count)
    floor_fill = jnp.maximum(count * MINLEN, SLOT_TOKENS // 2 + 1)
    spread = jax.random.randint(fill_key, (SLOT_COUNT,), 0, SLOT_TOKENS + 1).astype(jnp.int32)
    fill = floor_fill + spread % (SLOT_TOKENS + 1 - floor_fill)
    fill = jnp.where(first, SLOT_TOKENS, fill)
    column = jnp.arange(DOCS)[None, :]
    used = column < count[:, None]
    weights = jnp.where(used, jax.random.randint(weight_key, (SLOT_COUNT, DOCS), 1, 9), 0)
    extra = fill - count * MINLEN
    shares = extra[:, None] * weights // jnp.sum(weights, axis=1, keepdims=True)
    remain = extra - jnp.sum(shares, axis=1)
    lengths = jnp.where(used, MINLEN + shares, 0) + jnp.where(column == 0, remain[:, None], 0)
    return lengths.astype(jnp.int32)


def levels(key, dims, cuts, smallest, largest):
    level = 1.0
    for axis_at, blocks in cuts:
        heights = jax.random.uniform(jax.random.fold_in(jax.random.fold_in(key, 6), axis_at), (blocks,), jnp.float32, smallest / len(cuts), largest / len(cuts))
        level = level * jnp.repeat(jnp.exp(heights), dims[axis_at] // blocks).reshape((-1,) + (1,) * (len(dims) - 1 - axis_at))
    return level


def gaussian(rng, shape, deviation, bound, shards=(), kind=jnp.bfloat16):
    loudness = levels(rng, shape, shards, -0.22, 0.18) if shards else 1.0
    drawn = jax.random.normal(rng, shape, jnp.float32) * deviation * loudness
    return jnp.minimum(jnp.maximum(drawn, -bound), bound).astype(kind)


def setup_inputs(seed: int = 0) -> dict:
    seeds = jax.random.split(jax.random.key(seed), 15)
    return {
        "hidden": gaussian(seeds[0], (TOKENS, MODEL_WIDTH), 1.0, 6.0, ((0, 32),)),
        "out_grad": gaussian(seeds[1], (TOKENS, MODEL_WIDTH), 1.0, 6.0, ((0, 32),)),
        "lengths": draw_lengths(jax.random.fold_in(seeds[14], 71), 0),
        "q_weight": gaussian(seeds[3], (MODEL_WIDTH, QUERY_HEADS * HEAD_SIZE), MODEL_WIDTH ** -0.5, 0.1875, ((0, 8), (1, 4)), jnp.float32),
        "key_matrix": gaussian(seeds[4], (MODEL_WIDTH, KEY_VALUE_HEADS * HEAD_SIZE), MODEL_WIDTH ** -0.5, 0.1875, ((0, 8), (1, 4)), jnp.float32),
        "value_matrix": gaussian(seeds[5], (MODEL_WIDTH, KEY_VALUE_HEADS * HEAD_SIZE), MODEL_WIDTH ** -0.5, 0.1875, ((0, 8), (1, 4)), jnp.float32),
        "o_weight": gaussian(seeds[6], (QUERY_HEADS * HEAD_SIZE, MODEL_WIDTH), (QUERY_HEADS * HEAD_SIZE // 8) ** -0.5, 0.375, ((0, 4), (1, 8)), jnp.float32),
        "gate_weight": gaussian(seeds[7], (MODEL_WIDTH, FF), MODEL_WIDTH ** -0.5, 0.1875, ((0, 8), (1, 4)), jnp.float32),
        "up_weight": gaussian(seeds[8], (MODEL_WIDTH, FF), MODEL_WIDTH ** -0.5, 0.1875, ((0, 8), (1, 4)), jnp.float32),
        "down_weight": gaussian(seeds[9], (FF, MODEL_WIDTH), FF ** -0.5, 0.109375, ((0, 4), (1, 8)), jnp.float32),
        "input_gain": jnp.clip(1.0 + 0.18 * jax.random.normal(seeds[10], (MODEL_WIDTH,), jnp.float32), 0.1, 1.9),
        "q_gain": jnp.clip(1.2 + 0.5999999 * jax.random.uniform(seeds[11], (HEAD_SIZE,), jnp.float32) ** levels(seeds[11], (HEAD_SIZE,), ((0, 8),), -0.2, 0.2), 1.2, 1.8),
        "k_gain": jnp.clip(1.2 + 0.5999999 * jax.random.uniform(seeds[12], (HEAD_SIZE,), jnp.float32) ** levels(seeds[12], (HEAD_SIZE,), ((0, 8),), -0.2, 0.2), 1.2, 1.8),
        "post_gain": jnp.clip(1.0 + 0.18 * jax.random.normal(seeds[13], (MODEL_WIDTH,), jnp.float32), 0.1, 1.9),
    }


@jax.custom_vjp
def low(v):
    return lax.optimization_barrier(v.astype(jnp.bfloat16)).astype(jnp.float32)

@jax.custom_vjp
def low_back(v):
    return v

def low_keep(v):
    return (low(v), None)

def low_pass(kept, grad):
    return (grad,)

def back_keep(v):
    return (v, None)

def back_low(kept, grad):
    return (low(grad),)
low.defvjp(low_keep, low_pass)
low_back.defvjp(back_keep, back_low)
EPSILON = 1e-06
THETA = 1000000.0
HIGHEST = lax.Precision.HIGHEST

def rms_scale(values, gain):
    inverse = lax.rsqrt(lax.optimization_barrier(jnp.mean(values * values, axis=-1, keepdims=True)) + EPSILON)
    return values * inverse * gain

def rotary(values, start_offset):
    half = values.shape[-1] // 2
    frequency = THETA ** (-(jnp.arange(half, dtype=jnp.float32) * 2.0 / values.shape[-1]))
    angle = start_offset.astype(jnp.float32)[:, None] * frequency[None, :]
    cosine = jnp.cos(angle)[:, None, :]
    sine = jnp.sin(angle)[:, None, :]
    first = values[..., :half]
    second = values[..., half:]
    return jnp.concatenate([first * cosine - second * sine, second * cosine + first * sine], axis=-1)

def prepare_inputs(projected, gain, start_offset, head_groups):
    shaped = projected.reshape(projected.shape[0], head_groups, -1)
    return rotary(rms_scale(shaped, gain), start_offset)

def slot_tables(lengths_row):
    ends = jnp.cumsum(lengths_row).astype(jnp.int32)
    place = jnp.arange(SLOT_TOKENS, dtype=jnp.int32)
    passed = place[:, None] >= ends[None, :]
    segment_ids = lax.optimization_barrier(jnp.sum(passed.astype(jnp.int32), axis=1)).astype(jnp.int32)
    start = lax.optimization_barrier(jnp.sum(jnp.where(passed, lengths_row[None, :], 0), axis=1)).astype(jnp.int32)
    return (segment_ids, place - start, place < ends[-1])

def reorder_blocks(values, order):
    shaped = values.reshape(SLOT_COUNT, 4, SLOT_TOKENS // 4, values.shape[-1])
    picked = jnp.concatenate([shaped[:, index:index + 1] for index in order], axis=1)
    return picked.reshape(values.shape)

def attention_per_slot(query_rows, key_rows, values, segment_ids):
    group = query_rows.shape[1] // key_rows.shape[1]
    keys_wide = jnp.repeat(key_rows, group, axis=1)
    values_wide = jnp.repeat(values, group, axis=1)
    place = jnp.arange(SLOT_TOKENS, dtype=jnp.int32)
    size = min(512, SLOT_TOKENS)
    scale = HEAD_SIZE ** (-0.5)

    def block(start):
        query_block = lax.dynamic_slice_in_dim(query_rows, start, size, 0)
        query_place = lax.dynamic_slice_in_dim(place, start, size, 0)
        query_segment = lax.dynamic_slice_in_dim(segment_ids, start, size, 0)
        scores = low_back(jnp.einsum('qhd,khd->hqk', query_block, keys_wide, precision=HIGHEST) * scale)
        allowed = (query_segment[:, None] == segment_ids[None, :]) & (place[None, :] <= query_place[:, None])
        weights = jnp.where(allowed[None], jnp.exp(scores), 0.0)
        total = lax.optimization_barrier(jnp.sum(weights, axis=-1))
        summed = low_back(jnp.einsum('hqk,khd->qhd', low(weights), values_wide, precision=HIGHEST))
        return summed / jnp.transpose(total)[:, :, None]
    starts = jnp.arange(SLOT_TOKENS // size, dtype=jnp.int32) * size
    result = lax.map(jax.checkpoint(block), starts)
    return result.reshape(SLOT_TOKENS, query_rows.shape[1], query_rows.shape[2])

def layer(x_float, segment_ids, start_offset, q_weight, key_matrix, value_matrix, o_weight, gate_weight, up_weight, down_weight, input_gain, q_gain, k_gain, post_gain):
    w_query = low(q_weight)
    w_key = low(key_matrix)
    w_value = low(value_matrix)
    w_out = low(o_weight)
    w_gate = low(gate_weight)
    w_up = low(up_weight)
    w_down = low(down_weight)
    gain_query = low(q_gain)
    gain_keys = low(k_gain)
    first_normed = low(rms_scale(x_float, low(input_gain)))
    query_projected = low_back(jnp.dot(first_normed, w_query, precision=HIGHEST))
    key_projected = low_back(jnp.dot(first_normed, w_key, precision=HIGHEST))
    value_projected = low_back(low(jnp.dot(first_normed, w_value, precision=HIGHEST)))

    def one_slot(carry, input_rows):
        query_slot, slot_keys, slot_values, segment_of_slot, offset_of_slot = input_rows
        query_rows = low(prepare_inputs(query_slot, gain_query, offset_of_slot, QUERY_HEADS))
        key_rows = low(prepare_inputs(slot_keys, gain_keys, offset_of_slot, KEY_VALUE_HEADS))
        head_groups = attention_per_slot(query_rows, key_rows, slot_values.reshape(SLOT_TOKENS, KEY_VALUE_HEADS, HEAD_SIZE), segment_of_slot)
        return (carry, head_groups)
    input_rows = (query_projected.reshape(SLOT_COUNT, SLOT_TOKENS, QUERY_HEADS * HEAD_SIZE), key_projected.reshape(SLOT_COUNT, SLOT_TOKENS, KEY_VALUE_HEADS * HEAD_SIZE), value_projected.reshape(SLOT_COUNT, SLOT_TOKENS, KEY_VALUE_HEADS * HEAD_SIZE), segment_ids, start_offset)
    unused, head_groups = lax.scan(one_slot, jnp.zeros((), jnp.float32), input_rows)
    heads_flat = low_back(low(head_groups.reshape(TOKENS, QUERY_HEADS * HEAD_SIZE)))
    after_attn = x_float + low_back(jnp.dot(heads_flat, w_out, precision=HIGHEST))
    second_normed = low(rms_scale(after_attn, low(post_gain)))
    gate_out = low_back(jnp.dot(second_normed, w_gate, precision=HIGHEST))
    up_out = low_back(jnp.dot(second_normed, w_up, precision=HIGHEST))
    activated = low(jax.nn.silu(gate_out) * up_out)
    return after_attn + low_back(jnp.dot(activated, w_down, precision=HIGHEST))

def reference(hidden, out_grad, lengths, q_weight, key_matrix, value_matrix, o_weight, gate_weight, up_weight, down_weight, input_gain, q_gain, k_gain, post_gain):
    to_places = (0, 2, 3, 1)
    to_rows = (0, 3, 1, 2)
    segment_ids, start_offset, valid = jax.vmap(slot_tables)(lengths)
    x_float = reorder_blocks(hidden.astype(jnp.float32), to_places)

    def forward(x_in, w_query, w_key, w_value, w_out, w_gate, w_up, w_down, gain_in, gain_query, gain_keys, gain_post):
        return layer(x_in, segment_ids, start_offset, w_query, w_key, w_value, w_out, w_gate, w_up, w_down, gain_in, gain_query, gain_keys, gain_post)
    result, pull = jax.vjp(forward, x_float, q_weight, key_matrix, value_matrix, o_weight, gate_weight, up_weight, down_weight, input_gain, q_gain, k_gain, post_gain)
    cotangent = reorder_blocks(out_grad.astype(jnp.float32), to_places) * valid.reshape(TOKENS, 1).astype(jnp.float32)
    grads = pull(cotangent)
    output = reorder_blocks(result, to_rows).astype(jnp.bfloat16)
    input_grad = reorder_blocks(grads[0], to_rows).astype(jnp.bfloat16)
    return (output, input_grad, grads[1], grads[2], grads[3], grads[4], grads[5], grads[6], grads[7], grads[8], grads[9], grads[10], grads[11])
```

```python
import functools

import numpy as np
import jax
import jax.numpy as jnp
from jax import lax
from jax.experimental import pallas as pl
from jax.experimental.pallas import tpu as pltpu
from jax.sharding import PartitionSpec as P

HEAD_SIZE = 128
TRANS_B = (((1,), (1,)), ((), ()))
TRANS_A = (((0,), (0,)), ((), ()))


def _own_place(p, quarter, r):
    return (p * quarter + r) if r < quarter else ((3 - p) * quarter + r - quarter)


def _far_place(p, quarter, r):
    return ((1 - p) * quarter + r) if r < quarter else ((2 + p) * quarter + r - quarter)


def _pair_tables(p, quarter, block, by_key):
    rows = 2 * quarter
    count = rows // block
    kmap = {}
    for src, fn in ((0, _own_place), (1, _far_place)):
        for j in range(count):
            kmap[fn(p, quarter, j * block) // block] = (src, j)
    pairs = []
    for j in range(count):
        qpb = _own_place(p, quarter, j * block) // block
        for kpb in range(qpb + 1):
            pairs.append((j, qpb, kpb))
    if by_key:
        pairs.sort(key=lambda t: (t[2], t[0]))
    group = [t[2] if by_key else t[0] for t in pairs]
    first = [1 if n == 0 or group[n - 1] != group[n] else 0 for n in range(len(pairs))]
    last = [1 if n == len(pairs) - 1 or group[n + 1] != group[n] else 0 for n in range(len(pairs))]
    table = np.array(
        [
            [t[0] for t in pairs],
            [t[1] for t in pairs],
            [t[2] for t in pairs],
            [kmap[t[2]][0] for t in pairs],
            [kmap[t[2]][1] for t in pairs],
            first,
            last,
        ],
        np.int32,
    )
    return table


def pair_tables(piece, quarter, block, by_key):
    t0 = _pair_tables(0, quarter, block, by_key)
    t1 = _pair_tables(1, quarter, block, by_key)
    assert t0.shape == t1.shape
    return jnp.where(piece == 0, jnp.asarray(t0), jnp.asarray(t1))


def _mask(qpb, kpb, qs, block):
    qp = qpb * block + lax.broadcasted_iota(jnp.int32, (block, block), 0)
    kp = kpb * block + lax.broadcasted_iota(jnp.int32, (block, block), 1)
    start = jnp.tile(qs, (1, block // 128))
    return (kp >= start) & (kp <= qp)


def _fwd_kernel(tab_ref, q_ref, qs_ref, k_ref, v_ref, o_ref, l_ref, acc_ref, sum_ref, *, scale, block):
    n = pl.program_id(1)
    share = q_ref.shape[1]

    @pl.when(tab_ref[5, n] == 1)
    def _():
        acc_ref[...] = jnp.zeros(acc_ref.shape, acc_ref.dtype)
        sum_ref[...] = jnp.zeros(sum_ref.shape, sum_ref.dtype)

    q = q_ref[0].reshape(share * block, HEAD_SIZE)
    k = k_ref[0, 0]
    v = v_ref[0, 0]
    s = lax.dot_general(q, k, TRANS_B, preferred_element_type=jnp.float32) * scale
    allowed = _mask(tab_ref[1, n], tab_ref[2, n], qs_ref[...], block)
    e = jnp.where(allowed[None], jnp.exp(s.reshape(share, block, block)), 0.0)
    sum_ref[...] += jnp.sum(e, axis=-1, keepdims=True)
    acc_ref[...] += jnp.dot(
        e.reshape(share * block, block).astype(jnp.bfloat16), v, preferred_element_type=jnp.float32
    )

    @pl.when(tab_ref[6, n] == 1)
    def _():
        total = sum_ref[...]
        o_ref[0] = acc_ref[...].reshape(share, block, HEAD_SIZE) / total
        l_ref[0] = jnp.broadcast_to(total, (share, block, 128))


def attention_forward(q, qs, k_all, v_all, piece, quarter, block=512):
    kvh, share, rows, _ = q.shape
    tab = pair_tables(piece, quarter, block, False)
    npairs = tab.shape[1]
    scale = HEAD_SIZE ** (-0.5)
    grid_spec = pltpu.PrefetchScalarGridSpec(
        num_scalar_prefetch=1,
        grid=(kvh, npairs),
        in_specs=[
            pl.BlockSpec((1, share, block, HEAD_SIZE), lambda h, n, t: (h, 0, t[0, n], 0)),
            pl.BlockSpec((block, 128), lambda h, n, t: (t[0, n], 0)),
            pl.BlockSpec((1, 1, block, HEAD_SIZE), lambda h, n, t: (t[3, n], h, t[4, n], 0)),
            pl.BlockSpec((1, 1, block, HEAD_SIZE), lambda h, n, t: (t[3, n], h, t[4, n], 0)),
        ],
        out_specs=[
            pl.BlockSpec((1, share, block, HEAD_SIZE), lambda h, n, t: (h, 0, t[0, n], 0)),
            pl.BlockSpec((1, share, block, 128), lambda h, n, t: (h, 0, t[0, n], 0)),
        ],
        scratch_shapes=[
            pltpu.VMEM((share * block, HEAD_SIZE), jnp.float32),
            pltpu.VMEM((share, block, 1), jnp.float32),
        ],
    )
    flops = 4 * kvh * npairs * share * block * block * HEAD_SIZE
    return pl.pallas_call(
        functools.partial(_fwd_kernel, scale=scale, block=block),
        grid_spec=grid_spec,
        out_shape=[
            jax.ShapeDtypeStruct((kvh, share, rows, HEAD_SIZE), jnp.float32),
            jax.ShapeDtypeStruct((kvh, share, rows, 128), jnp.float32),
        ],
        compiler_params=pltpu.CompilerParams(
            dimension_semantics=("arbitrary", "arbitrary"), vmem_limit_bytes=48 * 1024 * 1024
        ),
        cost_estimate=pl.CostEstimate(
            flops=flops, transcendentals=kvh * npairs * share * block * block,
            bytes_accessed=kvh * npairs * (4 * block * HEAD_SIZE * 2),
        ),
        name="attn_fwd",
    )(tab, q, qs, k_all, v_all)


def _bwd_kernel(tab_ref, q_ref, h_ref, dl_ref, qs_ref, k_ref, v_ref, dq_ref, dk_ref, dv_ref, dk_acc, dv_acc, *, scale, block):
    n = pl.program_id(1)
    share = q_ref.shape[1]

    @pl.when(n == 0)
    def _():
        dq_ref[...] = jnp.zeros(dq_ref.shape, dq_ref.dtype)

    @pl.when(tab_ref[5, n] == 1)
    def _():
        dk_acc[...] = jnp.zeros(dk_acc.shape, dk_acc.dtype)
        dv_acc[...] = jnp.zeros(dv_acc.shape, dv_acc.dtype)

    q = q_ref[0].reshape(share * block, HEAD_SIZE)
    hh = h_ref[0].reshape(share * block, HEAD_SIZE)
    k = k_ref[0, 0]
    v = v_ref[0, 0]
    s = lax.dot_general(q, k, TRANS_B, preferred_element_type=jnp.float32) * scale
    allowed = _mask(tab_ref[1, n], tab_ref[2, n], qs_ref[...], block)
    e = jnp.where(allowed[None], jnp.exp(s.reshape(share, block, block)), 0.0)
    dp = lax.dot_general(hh, v, TRANS_B, preferred_element_type=jnp.float32).reshape(share, block, block)
    delta = jnp.tile(dl_ref[0], (1, 1, block // 128))
    ds = (e * (dp - delta)).reshape(share * block, block).astype(jnp.bfloat16)
    rows = pl.ds(pl.multiple_of(tab_ref[0, n] * block, block), block)
    dq_ref[0, :, rows, :] += jnp.dot(ds, k, preferred_element_type=jnp.float32).reshape(share, block, HEAD_SIZE)
    dk_acc[...] += lax.dot_general(ds, q, TRANS_A, preferred_element_type=jnp.float32)
    dv_acc[...] += lax.dot_general(
        e.reshape(share * block, block).astype(jnp.bfloat16), hh, TRANS_A, preferred_element_type=jnp.float32
    )

    @pl.when(tab_ref[6, n] == 1)
    def _():
        dk_ref[0, 0] = dk_acc[...] * scale
        dv_ref[0, 0] = dv_acc[...]


def attention_backward(q, hgrad, delta, qs, k_all, v_all, piece, quarter, block=512):
    kvh, share, rows, _ = q.shape
    tab = pair_tables(piece, quarter, block, True)
    npairs = tab.shape[1]
    scale = HEAD_SIZE ** (-0.5)
    grid_spec = pltpu.PrefetchScalarGridSpec(
        num_scalar_prefetch=1,
        grid=(kvh, npairs),
        in_specs=[
            pl.BlockSpec((1, share, block, HEAD_SIZE), lambda h, n, t: (h, 0, t[0, n], 0)),
            pl.BlockSpec((1, share, block, HEAD_SIZE), lambda h, n, t: (h, 0, t[0, n], 0)),
            pl.BlockSpec((1, share, block, 128), lambda h, n, t: (h, 0, t[0, n], 0)),
            pl.BlockSpec((block, 128), lambda h, n, t: (t[0, n], 0)),
            pl.BlockSpec((1, 1, block, HEAD_SIZE), lambda h, n, t: (t[3, n], h, t[4, n], 0)),
            pl.BlockSpec((1, 1, block, HEAD_SIZE), lambda h, n, t: (t[3, n], h, t[4, n], 0)),
        ],
        out_specs=[
            pl.BlockSpec((1, share, rows, HEAD_SIZE), lambda h, n, t: (h, 0, 0, 0)),
            pl.BlockSpec((1, 1, block, HEAD_SIZE), lambda h, n, t: (t[3, n], h, t[4, n], 0)),
            pl.BlockSpec((1, 1, block, HEAD_SIZE), lambda h, n, t: (t[3, n], h, t[4, n], 0)),
        ],
        scratch_shapes=[
            pltpu.VMEM((block, HEAD_SIZE), jnp.float32),
            pltpu.VMEM((block, HEAD_SIZE), jnp.float32),
        ],
    )
    flops = 10 * kvh * npairs * share * block * block * HEAD_SIZE
    return pl.pallas_call(
        functools.partial(_bwd_kernel, scale=scale, block=block),
        grid_spec=grid_spec,
        out_shape=[
            jax.ShapeDtypeStruct((kvh, share, rows, HEAD_SIZE), jnp.float32),
            jax.ShapeDtypeStruct(k_all.shape, jnp.float32),
            jax.ShapeDtypeStruct(v_all.shape, jnp.float32),
        ],
        compiler_params=pltpu.CompilerParams(
            dimension_semantics=("arbitrary", "arbitrary"), vmem_limit_bytes=56 * 1024 * 1024
        ),
        cost_estimate=pl.CostEstimate(
            flops=flops, transcendentals=kvh * npairs * share * block * block,
            bytes_accessed=kvh * npairs * (8 * block * HEAD_SIZE * 2),
        ),
        name="attn_bwd",
    )(tab, q, hgrad, delta, qs, k_all, v_all)

SLOT_TOKENS = 4096
PIECES = 2


EPSILON = 1e-06
THETA = 1000000.0


def swapped(shard, axis, distance):
    return lax.ppermute(shard, axis, [(i, i ^ 1 << distance) for i in range(lax.axis_size(axis))])


def rms_scale(values, gain):
    inverse = lax.rsqrt(jnp.mean(values * values, axis=-1, keepdims=True) + EPSILON)
    return values * inverse * gain


def rotary(values, start_offset):
    half = values.shape[-1] // 2
    frequency = THETA ** (-(jnp.arange(half, dtype=jnp.float32) * 2.0 / values.shape[-1]))
    angle = start_offset.astype(jnp.float32)[:, None] * frequency[None, :]
    cosine = jnp.cos(angle)[:, None, :]
    sine = jnp.sin(angle)[:, None, :]
    first = values[..., :half]
    second = values[..., half:]
    return jnp.concatenate(
        [first * cosine - second * sine, second * cosine + first * sine], axis=-1
    )


def prepare_inputs(projected, gain, start_offset, head_groups):
    shaped = projected.reshape(projected.shape[0], head_groups, -1)
    return rotary(rms_scale(shaped, gain), start_offset)


def slot_tables(lengths_row, slot_length):
    ends = jnp.cumsum(lengths_row)
    place = jnp.arange(slot_length, dtype=jnp.int32)
    passed = place[:, None] >= ends[None, :]
    segment_ids = jnp.sum(passed.astype(jnp.int32), axis=1)
    start = jnp.sum(jnp.where(passed, lengths_row[None, :], 0), axis=1)
    return (segment_ids, place - start, place < ends[-1])


def piece_places(which, group_rows):
    quarter = group_rows // 2
    local = jnp.arange(group_rows, dtype=jnp.int32)
    chosen = jnp.where(local < quarter, which, 3 - which)
    return chosen * quarter + local % quarter


def contract_rows(left, right):
    return lax.dot_general(
        left, right, (((0,), (0,)), ((), ())), preferred_element_type=jnp.float32
    )


def contract_last(left, right):
    return lax.dot_general(
        left, right, (((1,), (1,)), ((), ())), preferred_element_type=jnp.float32
    )


def token_gather(values):
    return lax.all_gather(values, "tensor", axis=0, tiled=True)


def token_sum(term, rows):
    return lax.psum_scatter(
        term(jnp.int32(0), rows * lax.axis_size("tensor")).astype(jnp.bfloat16),
        "tensor",
        scatter_dimension=0,
        tiled=True,
    ).astype(jnp.float32)


def shards(
    hidden,
    out_grad,
    lengths,
    q_weight,
    key_matrix,
    value_matrix,
    o_weight,
    gate_weight,
    up_weight,
    down_weight,
    input_gain,
    q_gain,
    k_gain,
    post_gain,
):
    split = lax.axis_size("tensor")
    rows = hidden.shape[0]
    group_rows = rows * split
    q_heads = q_weight.shape[1] // HEAD_SIZE
    kv_heads = key_matrix.shape[1] // HEAD_SIZE
    share = q_heads // kv_heads
    scale = HEAD_SIZE ** (-0.5)
    size = min(512, group_rows)
    blocks = group_rows // size
    member = lax.axis_index("fsdp")
    slot = member // PIECES
    piece = member % PIECES
    segment_ids, start_offset, valid = slot_tables(
        lax.dynamic_index_in_dim(lengths, slot, 0, keepdims=False), SLOT_TOKENS
    )
    group_place = piece_places(piece, group_rows)
    group_segment = jnp.take(segment_ids, group_place)
    group_offset = jnp.take(start_offset, group_place)
    local_valid = lax.dynamic_slice_in_dim(
        jnp.take(valid, group_place), lax.axis_index("tensor") * rows, rows, 0
    )
    attn_gathered = (
        lax.all_gather(q_weight.astype(jnp.bfloat16), "fsdp", axis=0, tiled=True),
        lax.all_gather(key_matrix.astype(jnp.bfloat16), "fsdp", axis=0, tiled=True),
        lax.all_gather(value_matrix.astype(jnp.bfloat16), "fsdp", axis=0, tiled=True),
        lax.all_gather(jnp.transpose(o_weight).astype(jnp.bfloat16), "fsdp", axis=0, tiled=True),
        lax.all_gather(input_gain.astype(jnp.bfloat16), "fsdp", axis=0, tiled=True),
        lax.all_gather(q_gain.astype(jnp.bfloat16), "fsdp", axis=0, tiled=True),
        lax.all_gather(k_gain.astype(jnp.bfloat16), "fsdp", axis=0, tiled=True),
    )
    w_query, w_key, w_value, w_out, gain_in, gain_query, gain_keys = attn_gathered
    x_float = hidden.astype(jnp.float32)
    gain_first = gain_in.astype(jnp.float32)
    first_all = token_gather(rms_scale(x_float, gain_first).astype(jnp.bfloat16))
    query_projected = jnp.dot(first_all, w_query, preferred_element_type=jnp.float32)
    key_projected = jnp.dot(first_all, w_key, preferred_element_type=jnp.float32)
    value_rows = (
        jnp.dot(first_all, w_value, preferred_element_type=jnp.float32)
        .astype(jnp.bfloat16)
        .reshape(group_rows, kv_heads, HEAD_SIZE)
    )
    gain_q = gain_query.astype(jnp.float32)
    gain_k = gain_keys.astype(jnp.float32)
    query_rope = (
        prepare_inputs(query_projected, gain_q, group_offset, q_heads)
        .astype(jnp.bfloat16)
        .reshape(group_rows, kv_heads, share, HEAD_SIZE)
    )
    key_rope = prepare_inputs(key_projected, gain_k, group_offset, kv_heads).astype(jnp.bfloat16)
    moved = swapped(jnp.stack([key_rope, value_rows]), "fsdp", 0)
    quarter = group_rows // 2
    query_start = jnp.broadcast_to((group_place - group_offset)[:, None], (group_rows, 128))
    query_t = jnp.transpose(query_rope, (1, 2, 0, 3))
    keys_all = jnp.stack([jnp.transpose(key_rope, (1, 0, 2)), jnp.transpose(moved[0], (1, 0, 2))])
    values_all = jnp.stack([jnp.transpose(value_rows, (1, 0, 2)), jnp.transpose(moved[1], (1, 0, 2))])
    heads_t, totals_t = attention_forward(query_t, query_start, keys_all, values_all, piece, quarter)
    heads_out = jnp.transpose(heads_t, (2, 0, 1, 3))
    row_totals = jnp.transpose(totals_t[..., 0], (2, 0, 1))
    out_rows = heads_out.reshape(group_rows, q_heads * HEAD_SIZE).astype(jnp.bfloat16)

    def out_term(start, count):
        return contract_last(out_rows, w_out)

    after_attn = x_float + token_sum(out_term, rows)
    mlp_gathered = (
        lax.all_gather(gate_weight.astype(jnp.bfloat16), "fsdp", axis=0, tiled=True),
        lax.all_gather(up_weight.astype(jnp.bfloat16), "fsdp", axis=0, tiled=True),
        lax.all_gather(jnp.transpose(down_weight).astype(jnp.bfloat16), "fsdp", axis=0, tiled=True),
        lax.all_gather(post_gain.astype(jnp.bfloat16), "fsdp", axis=0, tiled=True),
    )
    w_gate, w_up, w_down_t, gain_post = mlp_gathered
    gain_second = gain_post.astype(jnp.float32)
    second_all = token_gather(rms_scale(after_attn, gain_second).astype(jnp.bfloat16))
    gate_out = jnp.dot(second_all, w_gate, preferred_element_type=jnp.float32)
    up_out = jnp.dot(second_all, w_up, preferred_element_type=jnp.float32)
    activated = (jax.nn.silu(gate_out) * up_out).astype(jnp.bfloat16)

    def down_term(start, count):
        return contract_last(activated, w_down_t)

    output = (after_attn + token_sum(down_term, rows)).astype(jnp.bfloat16)
    cotangent = out_grad.astype(jnp.float32) * local_valid[:, None].astype(jnp.float32)
    mlp_grad_all = token_gather(cotangent.astype(jnp.bfloat16))
    w_gate, w_up, w_down_t = (
        lax.all_gather(gate_weight.astype(jnp.bfloat16), "fsdp", axis=0, tiled=True),
        lax.all_gather(up_weight.astype(jnp.bfloat16), "fsdp", axis=0, tiled=True),
        lax.all_gather(jnp.transpose(down_weight).astype(jnp.bfloat16), "fsdp", axis=0, tiled=True),
    )
    grad_act = jnp.dot(mlp_grad_all, w_down_t, preferred_element_type=jnp.float32)
    unused, pull_gate = jax.vjp(
        lambda gate_in, up_in: jax.nn.silu(gate_in) * up_in, gate_out, up_out
    )
    grad_gate, grad_up = pull_gate(grad_act)
    grad_gate = grad_gate.astype(jnp.bfloat16)
    grad_up = grad_up.astype(jnp.bfloat16)
    down_grad_t = contract_rows(mlp_grad_all, activated)
    gate_grad = contract_rows(second_all, grad_gate)
    up_grad = contract_rows(second_all, grad_up)

    def second_term(start, count):
        return contract_last(grad_gate, w_gate) + contract_last(grad_up, w_up)

    second_back = token_sum(second_term, rows)
    unused, pull_second = jax.vjp(rms_scale, after_attn, gain_second)
    norm_second_grad, post_gain_part = pull_second(second_back)
    residual_grad = cotangent + norm_second_grad
    mlp_shards = (
        lax.psum_scatter(gate_grad, "fsdp", scatter_dimension=0, tiled=True),
        lax.psum_scatter(up_grad, "fsdp", scatter_dimension=0, tiled=True),
        lax.psum_scatter(down_grad_t, "fsdp", scatter_dimension=0, tiled=True),
    )
    w_query, w_key, w_value, w_out = (
        lax.all_gather(q_weight.astype(jnp.bfloat16), "fsdp", axis=0, tiled=True),
        lax.all_gather(key_matrix.astype(jnp.bfloat16), "fsdp", axis=0, tiled=True),
        lax.all_gather(value_matrix.astype(jnp.bfloat16), "fsdp", axis=0, tiled=True),
        lax.all_gather(jnp.transpose(o_weight).astype(jnp.bfloat16), "fsdp", axis=0, tiled=True),
    )
    attn_grad_all = token_gather(residual_grad.astype(jnp.bfloat16))
    out_weight_grad_t = contract_rows(attn_grad_all, out_rows)
    head_grad = jnp.dot(attn_grad_all, w_out, preferred_element_type=jnp.float32).astype(
        jnp.bfloat16
    )
    head_float = head_grad.astype(jnp.float32).reshape(group_rows, kv_heads, share, HEAD_SIZE)
    scaled_grad = (head_float / row_totals[..., None]).astype(jnp.bfloat16)
    delta = jnp.sum(head_float * heads_out, axis=-1) / row_totals

    dq_raw, dk_all, dv_all = attention_backward(
        query_t,
        jnp.transpose(scaled_grad, (1, 2, 0, 3)),
        jnp.broadcast_to(jnp.transpose(delta, (1, 2, 0))[..., None], (kv_heads, share, group_rows, 128)),
        query_start, keys_all, values_all, piece, quarter,
    )
    unseen = (piece == 1) & (jnp.arange(group_rows) >= quarter)
    far_grads = jnp.where(unseen[None, None, :, None], 0.0, jnp.stack([dk_all[1], dv_all[1]]))
    returned = swapped(far_grads.astype(jnp.bfloat16), "fsdp", 0).astype(jnp.float32)
    grad_keys_total = jnp.transpose(dk_all[0] + returned[0], (1, 0, 2))
    grad_values_total = jnp.transpose(dv_all[0] + returned[1], (1, 0, 2))
    query_grads = jnp.transpose(dq_raw, (2, 0, 1, 3)) * scale
    query_grads = query_grads.reshape(group_rows, q_heads, HEAD_SIZE)
    unused, pull_query = jax.vjp(
        lambda projected, gain: prepare_inputs(projected, gain, group_offset, q_heads),
        query_projected,
        gain_q,
    )
    query_proj_grad, q_gain_part = pull_query(query_grads)
    unused, pull_key = jax.vjp(
        lambda projected, gain: prepare_inputs(projected, gain, group_offset, kv_heads),
        key_projected,
        gain_k,
    )
    key_proj_grad, k_gain_part = pull_key(grad_keys_total)
    query_low = query_proj_grad.astype(jnp.bfloat16)
    key_low = key_proj_grad.astype(jnp.bfloat16)
    value_low = grad_values_total.reshape(group_rows, kv_heads * HEAD_SIZE).astype(jnp.bfloat16)
    query_weight_grad = contract_rows(first_all, query_low)
    key_weight_grad = contract_rows(first_all, key_low)
    value_weight_grad = contract_rows(first_all, value_low)

    def first_term(start, count):
        return (
            contract_last(query_low, w_query)
            + contract_last(key_low, w_key)
            + contract_last(value_low, w_value)
        )

    first_back = token_sum(first_term, rows)
    unused, pull_first = jax.vjp(rms_scale, x_float, gain_first)
    norm_first_grad, input_gain_part = pull_first(first_back)
    input_grad = (residual_grad + norm_first_grad).astype(jnp.bfloat16)
    gain_totals = lax.psum((input_gain_part, q_gain_part, k_gain_part, post_gain_part), "tensor")
    attn_shards = (
        lax.psum_scatter(query_weight_grad, "fsdp", scatter_dimension=0, tiled=True),
        lax.psum_scatter(key_weight_grad, "fsdp", scatter_dimension=0, tiled=True),
        lax.psum_scatter(value_weight_grad, "fsdp", scatter_dimension=0, tiled=True),
        lax.psum_scatter(out_weight_grad_t, "fsdp", scatter_dimension=0, tiled=True),
        lax.psum_scatter(gain_totals[0], "fsdp", scatter_dimension=0, tiled=True),
        lax.psum_scatter(gain_totals[1], "fsdp", scatter_dimension=0, tiled=True),
        lax.psum_scatter(gain_totals[2], "fsdp", scatter_dimension=0, tiled=True),
        lax.psum_scatter(gain_totals[3], "fsdp", scatter_dimension=0, tiled=True),
    )
    gate_shard, up_shard, down_shard_t = mlp_shards
    (
        query_shard,
        key_shard,
        value_shard,
        out_shard_t,
        input_gain_shard,
        q_gain_shard,
        k_gain_shard,
        post_gain_shard,
    ) = attn_shards
    return (
        output,
        input_grad,
        query_shard,
        key_shard,
        value_shard,
        jnp.transpose(out_shard_t),
        gate_shard,
        up_shard,
        jnp.transpose(down_shard_t),
        input_gain_shard,
        q_gain_shard,
        k_gain_shard,
        post_gain_shard,
    )


def solution(mesh):
    placed = (
        P(("fsdp", "tensor"), None),
        P(("fsdp", "tensor"), None),
        P(),
        P("fsdp", "tensor"),
        P("fsdp", "tensor"),
        P("fsdp", "tensor"),
        P("tensor", "fsdp"),
        P("fsdp", "tensor"),
        P("fsdp", "tensor"),
        P("tensor", "fsdp"),
        P("fsdp"),
        P("fsdp"),
        P("fsdp"),
        P("fsdp"),
    )
    return jax.shard_map(
        shards,
        mesh=mesh,
        in_specs=placed,
        out_specs=(
            P(("fsdp", "tensor"), None),
            P(("fsdp", "tensor"), None),
            P("fsdp", "tensor"),
            P("fsdp", "tensor"),
            P("fsdp", "tensor"),
            P("tensor", "fsdp"),
            P("fsdp", "tensor"),
            P("fsdp", "tensor"),
            P("tensor", "fsdp"),
            P("fsdp"),
            P("fsdp"),
            P("fsdp"),
            P("fsdp"),
        ),
        check_vma=False,
    )
```

```python
import functools

import numpy as np
import jax
import jax.numpy as jnp
from jax import lax
from jax.experimental import pallas as pl
from jax.experimental.pallas import tpu as pltpu
from jax.sharding import PartitionSpec as P

HEAD_SIZE = 128
TRANS_B = (((1,), (1,)), ((), ()))
TRANS_A = (((0,), (0,)), ((), ()))


def _own_place(p, quarter, r):
    return (p * quarter + r) if r < quarter else ((3 - p) * quarter + r - quarter)


def _far_place(p, quarter, r):
    return ((1 - p) * quarter + r) if r < quarter else ((2 + p) * quarter + r - quarter)


def _pair_tables(p, quarter, block, by_key):
    rows = 2 * quarter
    count = rows // block
    kmap = {}
    for src, fn in ((0, _own_place), (1, _far_place)):
        for j in range(count):
            kmap[fn(p, quarter, j * block) // block] = (src, j)
    pairs = []
    for j in range(count):
        qpb = _own_place(p, quarter, j * block) // block
        for kpb in range(qpb + 1):
            pairs.append((j, qpb, kpb))
    if by_key:
        pairs.sort(key=lambda t: (t[2], t[0]))
    group = [t[2] if by_key else t[0] for t in pairs]
    first = [1 if n == 0 or group[n - 1] != group[n] else 0 for n in range(len(pairs))]
    last = [1 if n == len(pairs) - 1 or group[n + 1] != group[n] else 0 for n in range(len(pairs))]
    table = np.array(
        [
            [t[0] for t in pairs],
            [t[1] for t in pairs],
            [t[2] for t in pairs],
            [kmap[t[2]][0] for t in pairs],
            [kmap[t[2]][1] for t in pairs],
            first,
            last,
        ],
        np.int32,
    )
    return table


def pair_tables(piece, quarter, block, by_key):
    t0 = _pair_tables(0, quarter, block, by_key)
    t1 = _pair_tables(1, quarter, block, by_key)
    assert t0.shape == t1.shape
    return jnp.where(piece == 0, jnp.asarray(t0), jnp.asarray(t1))


def _mask(qpb, kpb, qs, block):
    qp = qpb * block + lax.broadcasted_iota(jnp.int32, (block, block), 0)
    kp = kpb * block + lax.broadcasted_iota(jnp.int32, (block, block), 1)
    start = jnp.tile(qs, (1, block // 128))
    return (kp >= start) & (kp <= qp)


def _fwd_kernel(tab_ref, q_ref, qs_ref, k_ref, v_ref, o_ref, l_ref, acc_ref, sum_ref, *, scale, block):
    n = pl.program_id(1)
    share = q_ref.shape[1]

    @pl.when(tab_ref[5, n] == 1)
    def _():
        acc_ref[...] = jnp.zeros(acc_ref.shape, acc_ref.dtype)
        sum_ref[...] = jnp.zeros(sum_ref.shape, sum_ref.dtype)

    q = q_ref[0].reshape(share * block, HEAD_SIZE)
    k = k_ref[0, 0]
    v = v_ref[0, 0]
    s = lax.dot_general(q, k, TRANS_B, preferred_element_type=jnp.float32) * scale
    allowed = _mask(tab_ref[1, n], tab_ref[2, n], qs_ref[...], block)
    e = jnp.where(allowed[None], jnp.exp(s.reshape(share, block, block)), 0.0)
    sum_ref[...] += jnp.sum(e, axis=-1, keepdims=True)
    acc_ref[...] += jnp.dot(
        e.reshape(share * block, block).astype(jnp.bfloat16), v, preferred_element_type=jnp.float32
    )

    @pl.when(tab_ref[6, n] == 1)
    def _():
        total = sum_ref[...]
        o_ref[0] = acc_ref[...].reshape(share, block, HEAD_SIZE) / total
        l_ref[0] = jnp.broadcast_to(total, (share, block, 128))


def attention_forward(q, qs, k_all, v_all, piece, quarter, block=512):
    kvh, share, rows, _ = q.shape
    tab = pair_tables(piece, quarter, block, False)
    npairs = tab.shape[1]
    scale = HEAD_SIZE ** (-0.5)
    grid_spec = pltpu.PrefetchScalarGridSpec(
        num_scalar_prefetch=1,
        grid=(kvh, npairs),
        in_specs=[
            pl.BlockSpec((1, share, block, HEAD_SIZE), lambda h, n, t: (h, 0, t[0, n], 0)),
            pl.BlockSpec((block, 128), lambda h, n, t: (t[0, n], 0)),
            pl.BlockSpec((1, 1, block, HEAD_SIZE), lambda h, n, t: (t[3, n], h, t[4, n], 0)),
            pl.BlockSpec((1, 1, block, HEAD_SIZE), lambda h, n, t: (t[3, n], h, t[4, n], 0)),
        ],
        out_specs=[
            pl.BlockSpec((1, share, block, HEAD_SIZE), lambda h, n, t: (h, 0, t[0, n], 0)),
            pl.BlockSpec((1, share, block, 128), lambda h, n, t: (h, 0, t[0, n], 0)),
        ],
        scratch_shapes=[
            pltpu.VMEM((share * block, HEAD_SIZE), jnp.float32),
            pltpu.VMEM((share, block, 1), jnp.float32),
        ],
    )
    flops = 4 * kvh * npairs * share * block * block * HEAD_SIZE
    return pl.pallas_call(
        functools.partial(_fwd_kernel, scale=scale, block=block),
        grid_spec=grid_spec,
        out_shape=[
            jax.ShapeDtypeStruct((kvh, share, rows, HEAD_SIZE), jnp.float32),
            jax.ShapeDtypeStruct((kvh, share, rows, 128), jnp.float32),
        ],
        compiler_params=pltpu.CompilerParams(
            dimension_semantics=("arbitrary", "arbitrary"), vmem_limit_bytes=48 * 1024 * 1024
        ),
        cost_estimate=pl.CostEstimate(
            flops=flops, transcendentals=kvh * npairs * share * block * block,
            bytes_accessed=kvh * npairs * (4 * block * HEAD_SIZE * 2),
        ),
        name="attn_fwd",
    )(tab, q, qs, k_all, v_all)


def _bwd_kernel(tab_ref, q_ref, h_ref, dl_ref, qs_ref, k_ref, v_ref, dq_ref, dk_ref, dv_ref, dk_acc, dv_acc, *, scale, block):
    n = pl.program_id(1)
    share = q_ref.shape[1]

    @pl.when(n == 0)
    def _():
        dq_ref[...] = jnp.zeros(dq_ref.shape, dq_ref.dtype)

    @pl.when(tab_ref[5, n] == 1)
    def _():
        dk_acc[...] = jnp.zeros(dk_acc.shape, dk_acc.dtype)
        dv_acc[...] = jnp.zeros(dv_acc.shape, dv_acc.dtype)

    q = q_ref[0].reshape(share * block, HEAD_SIZE)
    hh = h_ref[0].reshape(share * block, HEAD_SIZE)
    k = k_ref[0, 0]
    v = v_ref[0, 0]
    s = lax.dot_general(q, k, TRANS_B, preferred_element_type=jnp.float32) * scale
    allowed = _mask(tab_ref[1, n], tab_ref[2, n], qs_ref[...], block)
    e = jnp.where(allowed[None], jnp.exp(s.reshape(share, block, block)), 0.0)
    dp = lax.dot_general(hh, v, TRANS_B, preferred_element_type=jnp.float32).reshape(share, block, block)
    delta = jnp.tile(dl_ref[0], (1, 1, block // 128))
    ds = (e * (dp - delta)).reshape(share * block, block).astype(jnp.bfloat16)
    rows = pl.ds(pl.multiple_of(tab_ref[0, n] * block, block), block)
    dq_ref[0, :, rows, :] += jnp.dot(ds, k, preferred_element_type=jnp.float32).reshape(share, block, HEAD_SIZE)
    dk_acc[...] += lax.dot_general(ds, q, TRANS_A, preferred_element_type=jnp.float32)
    dv_acc[...] += lax.dot_general(
        e.reshape(share * block, block).astype(jnp.bfloat16), hh, TRANS_A, preferred_element_type=jnp.float32
    )

    @pl.when(tab_ref[6, n] == 1)
    def _():
        dk_ref[0, 0] = dk_acc[...] * scale
        dv_ref[0, 0] = dv_acc[...]


def attention_backward(q, hgrad, delta, qs, k_all, v_all, piece, quarter, block=512):
    kvh, share, rows, _ = q.shape
    tab = pair_tables(piece, quarter, block, True)
    npairs = tab.shape[1]
    scale = HEAD_SIZE ** (-0.5)
    grid_spec = pltpu.PrefetchScalarGridSpec(
        num_scalar_prefetch=1,
        grid=(kvh, npairs),
        in_specs=[
            pl.BlockSpec((1, share, block, HEAD_SIZE), lambda h, n, t: (h, 0, t[0, n], 0)),
            pl.BlockSpec((1, share, block, HEAD_SIZE), lambda h, n, t: (h, 0, t[0, n], 0)),
            pl.BlockSpec((1, share, block, 128), lambda h, n, t: (h, 0, t[0, n], 0)),
            pl.BlockSpec((block, 128), lambda h, n, t: (t[0, n], 0)),
            pl.BlockSpec((1, 1, block, HEAD_SIZE), lambda h, n, t: (t[3, n], h, t[4, n], 0)),
            pl.BlockSpec((1, 1, block, HEAD_SIZE), lambda h, n, t: (t[3, n], h, t[4, n], 0)),
        ],
        out_specs=[
            pl.BlockSpec((1, share, rows, HEAD_SIZE), lambda h, n, t: (h, 0, 0, 0)),
            pl.BlockSpec((1, 1, block, HEAD_SIZE), lambda h, n, t: (t[3, n], h, t[4, n], 0)),
            pl.BlockSpec((1, 1, block, HEAD_SIZE), lambda h, n, t: (t[3, n], h, t[4, n], 0)),
        ],
        scratch_shapes=[
            pltpu.VMEM((block, HEAD_SIZE), jnp.float32),
            pltpu.VMEM((block, HEAD_SIZE), jnp.float32),
        ],
    )
    flops = 10 * kvh * npairs * share * block * block * HEAD_SIZE
    return pl.pallas_call(
        functools.partial(_bwd_kernel, scale=scale, block=block),
        grid_spec=grid_spec,
        out_shape=[
            jax.ShapeDtypeStruct((kvh, share, rows, HEAD_SIZE), jnp.float32),
            jax.ShapeDtypeStruct(k_all.shape, jnp.float32),
            jax.ShapeDtypeStruct(v_all.shape, jnp.float32),
        ],
        compiler_params=pltpu.CompilerParams(
            dimension_semantics=("arbitrary", "arbitrary"), vmem_limit_bytes=56 * 1024 * 1024
        ),
        cost_estimate=pl.CostEstimate(
            flops=flops, transcendentals=kvh * npairs * share * block * block,
            bytes_accessed=kvh * npairs * (8 * block * HEAD_SIZE * 2),
        ),
        name="attn_bwd",
    )(tab, q, hgrad, delta, qs, k_all, v_all)

SLOT_TOKENS = 4096
PIECES = 2


EPSILON = 1e-06
THETA = 1000000.0


def swapped(shard, axis, distance):
    return lax.ppermute(shard, axis, [(i, i ^ 1 << distance) for i in range(lax.axis_size(axis))])


def rms_scale(values, gain):
    inverse = lax.rsqrt(jnp.mean(values * values, axis=-1, keepdims=True) + EPSILON)
    return values * inverse * gain


def rotary(values, start_offset):
    half = values.shape[-1] // 2
    frequency = THETA ** (-(jnp.arange(half, dtype=jnp.float32) * 2.0 / values.shape[-1]))
    angle = start_offset.astype(jnp.float32)[:, None] * frequency[None, :]
    cosine = jnp.cos(angle)[:, None, :]
    sine = jnp.sin(angle)[:, None, :]
    first = values[..., :half]
    second = values[..., half:]
    return jnp.concatenate(
        [first * cosine - second * sine, second * cosine + first * sine], axis=-1
    )


def prepare_inputs(projected, gain, start_offset, head_groups):
    shaped = projected.reshape(projected.shape[0], head_groups, -1)
    return rotary(rms_scale(shaped, gain), start_offset)


def slot_tables(lengths_row, slot_length):
    ends = jnp.cumsum(lengths_row)
    place = jnp.arange(slot_length, dtype=jnp.int32)
    passed = place[:, None] >= ends[None, :]
    segment_ids = jnp.sum(passed.astype(jnp.int32), axis=1)
    start = jnp.sum(jnp.where(passed, lengths_row[None, :], 0), axis=1)
    return (segment_ids, place - start, place < ends[-1])


def piece_places(which, group_rows):
    quarter = group_rows // 2
    local = jnp.arange(group_rows, dtype=jnp.int32)
    chosen = jnp.where(local < quarter, which, 3 - which)
    return chosen * quarter + local % quarter


def contract_rows(left, right):
    return lax.dot_general(
        left, right, (((0,), (0,)), ((), ())), preferred_element_type=jnp.float32
    )


def contract_last(left, right):
    return lax.dot_general(
        left, right, (((1,), (1,)), ((), ())), preferred_element_type=jnp.float32
    )


def gain_column(values, rows_f):
    column = values.astype(jnp.bfloat16)
    return jnp.pad(column, (0, rows_f - column.shape[0]))[:, None]


def gain_rows(column, fs, rows_f, own):
    return column.reshape(fs, rows_f)[:, :own].reshape(fs * own)


def split_columns(full, widths):
    parts = []
    at = 0
    for width in widths:
        parts.append(full[:, at : at + width])
        at += width
    return parts


def grad_scatter(grads):
    packed = jnp.concatenate([g.astype(jnp.bfloat16) for g in grads], axis=1)
    shard = lax.psum_scatter(packed, "fsdp", scatter_dimension=0, tiled=True)
    return [part.astype(jnp.float32) for part in split_columns(shard, [g.shape[1] for g in grads])]


def all_sum(values):
    for axis in ("tensor", "fsdp"):
        distance = 1
        while distance < lax.axis_size(axis):
            values = values + lax.ppermute(
                values, axis, [(i, i ^ distance) for i in range(lax.axis_size(axis))]
            )
            distance *= 2
    return values


def token_gather(values):
    return lax.all_gather(values, "tensor", axis=0, tiled=True)


def token_sum(term, rows):
    return lax.psum_scatter(
        term(jnp.int32(0), rows * lax.axis_size("tensor")).astype(jnp.bfloat16),
        "tensor",
        scatter_dimension=0,
        tiled=True,
    ).astype(jnp.float32)


def shards(
    hidden,
    out_grad,
    lengths,
    q_weight,
    key_matrix,
    value_matrix,
    o_weight,
    gate_weight,
    up_weight,
    down_weight,
    input_gain,
    q_gain,
    k_gain,
    post_gain,
):
    split = lax.axis_size("tensor")
    rows = hidden.shape[0]
    group_rows = rows * split
    q_heads = q_weight.shape[1] // HEAD_SIZE
    kv_heads = key_matrix.shape[1] // HEAD_SIZE
    share = q_heads // kv_heads
    scale = HEAD_SIZE ** (-0.5)
    size = min(512, group_rows)
    blocks = group_rows // size
    member = lax.axis_index("fsdp")
    slot = member // PIECES
    piece = member % PIECES
    segment_ids, start_offset, valid = slot_tables(
        lax.dynamic_index_in_dim(lengths, slot, 0, keepdims=False), SLOT_TOKENS
    )
    group_place = piece_places(piece, group_rows)
    group_segment = jnp.take(segment_ids, group_place)
    group_offset = jnp.take(start_offset, group_place)
    local_valid = lax.dynamic_slice_in_dim(
        jnp.take(valid, group_place), lax.axis_index("tensor") * rows, rows, 0
    )
    fs = lax.axis_size("fsdp")
    rows_f = q_weight.shape[0]
    attn_full = lax.all_gather(
        jnp.concatenate(
            [
                q_weight.astype(jnp.bfloat16),
                key_matrix.astype(jnp.bfloat16),
                value_matrix.astype(jnp.bfloat16),
                jnp.transpose(o_weight).astype(jnp.bfloat16),
                gain_column(input_gain, rows_f),
                gain_column(q_gain, rows_f),
                gain_column(k_gain, rows_f),
                gain_column(post_gain, rows_f),
            ],
            axis=1,
        ),
        "fsdp",
        axis=0,
        tiled=True,
    )
    widths = (q_weight.shape[1], key_matrix.shape[1], value_matrix.shape[1], o_weight.shape[0])
    w_query, w_key, w_value, w_out = split_columns(attn_full, widths)
    gains_at = sum(widths)
    gain_in = attn_full[:, gains_at]
    gain_query = gain_rows(attn_full[:, gains_at + 1], fs, rows_f, q_gain.shape[0])
    gain_keys = gain_rows(attn_full[:, gains_at + 2], fs, rows_f, k_gain.shape[0])
    gain_post = attn_full[:, gains_at + 3]
    x_float = hidden.astype(jnp.float32)
    gain_first = gain_in.astype(jnp.float32)
    first_all = token_gather(rms_scale(x_float, gain_first).astype(jnp.bfloat16))
    query_projected = jnp.dot(first_all, w_query, preferred_element_type=jnp.float32)
    key_projected = jnp.dot(first_all, w_key, preferred_element_type=jnp.float32)
    value_rows = (
        jnp.dot(first_all, w_value, preferred_element_type=jnp.float32)
        .astype(jnp.bfloat16)
        .reshape(group_rows, kv_heads, HEAD_SIZE)
    )
    gain_q = gain_query.astype(jnp.float32)
    gain_k = gain_keys.astype(jnp.float32)
    query_rope = (
        prepare_inputs(query_projected, gain_q, group_offset, q_heads)
        .astype(jnp.bfloat16)
        .reshape(group_rows, kv_heads, share, HEAD_SIZE)
    )
    key_rope = prepare_inputs(key_projected, gain_k, group_offset, kv_heads).astype(jnp.bfloat16)
    moved = swapped(jnp.stack([key_rope, value_rows]), "fsdp", 0)
    quarter = group_rows // 2
    query_start = jnp.broadcast_to((group_place - group_offset)[:, None], (group_rows, 128))
    query_t = jnp.transpose(query_rope, (1, 2, 0, 3))
    keys_all = jnp.stack([jnp.transpose(key_rope, (1, 0, 2)), jnp.transpose(moved[0], (1, 0, 2))])
    values_all = jnp.stack([jnp.transpose(value_rows, (1, 0, 2)), jnp.transpose(moved[1], (1, 0, 2))])
    heads_t, totals_t = attention_forward(query_t, query_start, keys_all, values_all, piece, quarter)
    heads_out = jnp.transpose(heads_t, (2, 0, 1, 3))
    row_totals = jnp.transpose(totals_t[..., 0], (2, 0, 1))
    out_rows = heads_out.reshape(group_rows, q_heads * HEAD_SIZE).astype(jnp.bfloat16)

    def out_term(start, count):
        return contract_last(out_rows, w_out)

    after_attn = x_float + token_sum(out_term, rows)
    mlp_full = lax.all_gather(
        jnp.concatenate(
            [
                gate_weight.astype(jnp.bfloat16),
                up_weight.astype(jnp.bfloat16),
                jnp.transpose(down_weight).astype(jnp.bfloat16),
            ],
            axis=1,
        ),
        "fsdp",
        axis=0,
        tiled=True,
    )
    w_gate, w_up, w_down_t = split_columns(
        mlp_full, (gate_weight.shape[1], up_weight.shape[1], down_weight.shape[0])
    )
    gain_second = gain_post.astype(jnp.float32)
    second_all = token_gather(rms_scale(after_attn, gain_second).astype(jnp.bfloat16))
    gate_out = jnp.dot(second_all, w_gate, preferred_element_type=jnp.float32)
    up_out = jnp.dot(second_all, w_up, preferred_element_type=jnp.float32)
    activated = (jax.nn.silu(gate_out) * up_out).astype(jnp.bfloat16)

    def down_term(start, count):
        return contract_last(activated, w_down_t)

    output = (after_attn + token_sum(down_term, rows)).astype(jnp.bfloat16)
    cotangent = out_grad.astype(jnp.float32) * local_valid[:, None].astype(jnp.float32)
    mlp_grad_all = token_gather(cotangent.astype(jnp.bfloat16))
    grad_act = jnp.dot(mlp_grad_all, w_down_t, preferred_element_type=jnp.float32)
    unused, pull_gate = jax.vjp(
        lambda gate_in, up_in: jax.nn.silu(gate_in) * up_in, gate_out, up_out
    )
    grad_gate, grad_up = pull_gate(grad_act)
    grad_gate = grad_gate.astype(jnp.bfloat16)
    grad_up = grad_up.astype(jnp.bfloat16)
    down_grad_t = contract_rows(mlp_grad_all, activated)
    gate_grad = contract_rows(second_all, grad_gate)
    up_grad = contract_rows(second_all, grad_up)

    def second_term(start, count):
        return contract_last(grad_gate, w_gate) + contract_last(grad_up, w_up)

    second_back = token_sum(second_term, rows)
    unused, pull_second = jax.vjp(rms_scale, after_attn, gain_second)
    norm_second_grad, post_gain_part = pull_second(second_back)
    residual_grad = cotangent + norm_second_grad
    attn_grad_all = token_gather(residual_grad.astype(jnp.bfloat16))
    out_weight_grad_t = contract_rows(attn_grad_all, out_rows)
    mlp_shards = grad_scatter(
        (gate_grad, up_grad, down_grad_t, out_weight_grad_t)
    )
    head_grad = jnp.dot(attn_grad_all, w_out, preferred_element_type=jnp.float32).astype(
        jnp.bfloat16
    )
    head_float = head_grad.astype(jnp.float32).reshape(group_rows, kv_heads, share, HEAD_SIZE)
    scaled_grad = (head_float / row_totals[..., None]).astype(jnp.bfloat16)
    delta = jnp.sum(head_float * heads_out, axis=-1) / row_totals

    dq_raw, dk_all, dv_all = attention_backward(
        query_t,
        jnp.transpose(scaled_grad, (1, 2, 0, 3)),
        jnp.broadcast_to(jnp.transpose(delta, (1, 2, 0))[..., None], (kv_heads, share, group_rows, 128)),
        query_start, keys_all, values_all, piece, quarter,
    )
    unseen = (piece == 1) & (jnp.arange(group_rows) >= quarter)
    far_grads = jnp.where(unseen[None, None, :, None], 0.0, jnp.stack([dk_all[1], dv_all[1]]))
    returned = swapped(far_grads.astype(jnp.bfloat16), "fsdp", 0).astype(jnp.float32)
    grad_keys_total = jnp.transpose(dk_all[0] + returned[0], (1, 0, 2))
    grad_values_total = jnp.transpose(dv_all[0] + returned[1], (1, 0, 2))
    query_grads = jnp.transpose(dq_raw, (2, 0, 1, 3)) * scale
    query_grads = query_grads.reshape(group_rows, q_heads, HEAD_SIZE)
    unused, pull_query = jax.vjp(
        lambda projected, gain: prepare_inputs(projected, gain, group_offset, q_heads),
        query_projected,
        gain_q,
    )
    query_proj_grad, q_gain_part = pull_query(query_grads)
    unused, pull_key = jax.vjp(
        lambda projected, gain: prepare_inputs(projected, gain, group_offset, kv_heads),
        key_projected,
        gain_k,
    )
    key_proj_grad, k_gain_part = pull_key(grad_keys_total)
    query_low = query_proj_grad.astype(jnp.bfloat16)
    key_low = key_proj_grad.astype(jnp.bfloat16)
    value_low = grad_values_total.reshape(group_rows, kv_heads * HEAD_SIZE).astype(jnp.bfloat16)
    query_weight_grad = contract_rows(first_all, query_low)
    key_weight_grad = contract_rows(first_all, key_low)
    value_weight_grad = contract_rows(first_all, value_low)

    def first_term(start, count):
        return (
            contract_last(query_low, w_query)
            + contract_last(key_low, w_key)
            + contract_last(value_low, w_value)
        )

    first_back = token_sum(first_term, rows)
    unused, pull_first = jax.vjp(rms_scale, x_float, gain_first)
    norm_first_grad, input_gain_part = pull_first(first_back)
    input_grad = (residual_grad + norm_first_grad).astype(jnp.bfloat16)
    query_shard, key_shard, value_shard = grad_scatter(
        (query_weight_grad, key_weight_grad, value_weight_grad)
    )
    gain_totals = all_sum(
        jnp.concatenate([input_gain_part, q_gain_part, k_gain_part, post_gain_part])
    )
    member_f = lax.axis_index("fsdp")
    sizes = (input_gain.shape[0], q_gain.shape[0], k_gain.shape[0], post_gain.shape[0])
    gain_shards = []
    at = 0
    for own in sizes:
        whole = own * fs
        gain_shards.append(lax.dynamic_slice_in_dim(gain_totals, at + member_f * own, own, 0))
        at += whole
    input_gain_shard, q_gain_shard, k_gain_shard, post_gain_shard = gain_shards
    gate_shard, up_shard, down_shard_t, out_shard_t = mlp_shards
    return (
        output,
        input_grad,
        query_shard,
        key_shard,
        value_shard,
        jnp.transpose(out_shard_t),
        gate_shard,
        up_shard,
        jnp.transpose(down_shard_t),
        input_gain_shard,
        q_gain_shard,
        k_gain_shard,
        post_gain_shard,
    )


def solution(mesh):
    placed = (
        P(("fsdp", "tensor"), None),
        P(("fsdp", "tensor"), None),
        P(),
        P("fsdp", "tensor"),
        P("fsdp", "tensor"),
        P("fsdp", "tensor"),
        P("tensor", "fsdp"),
        P("fsdp", "tensor"),
        P("fsdp", "tensor"),
        P("tensor", "fsdp"),
        P("fsdp"),
        P("fsdp"),
        P("fsdp"),
        P("fsdp"),
    )
    return jax.shard_map(
        shards,
        mesh=mesh,
        in_specs=placed,
        out_specs=(
            P(("fsdp", "tensor"), None),
            P(("fsdp", "tensor"), None),
            P("fsdp", "tensor"),
            P("fsdp", "tensor"),
            P("fsdp", "tensor"),
            P("tensor", "fsdp"),
            P("fsdp", "tensor"),
            P("fsdp", "tensor"),
            P("tensor", "fsdp"),
            P("fsdp"),
            P("fsdp"),
            P("fsdp"),
            P("fsdp"),
        ),
        check_vma=False,
    )
```

```python
import functools

import numpy as np
import jax
import jax.numpy as jnp
from jax import lax
from jax.experimental import pallas as pl
from jax.experimental.pallas import tpu as pltpu
from jax.sharding import PartitionSpec as P


HEAD_SIZE = 128
TRANS_B = (((1,), (1,)), ((), ()))
TRANS_A = (((0,), (0,)), ((), ()))


def _own_place(p, quarter, r):
    return (p * quarter + r) if r < quarter else ((3 - p) * quarter + r - quarter)


def _far_place(p, quarter, r):
    return ((1 - p) * quarter + r) if r < quarter else ((2 + p) * quarter + r - quarter)


def _pair_tables(p, quarter, block, by_key):
    rows = 2 * quarter
    count = rows // block
    kmap = {}
    for src, fn in ((0, _own_place), (1, _far_place)):
        for j in range(count):
            kmap[fn(p, quarter, j * block) // block] = (src, j)
    pairs = []
    for j in range(count):
        qpb = _own_place(p, quarter, j * block) // block
        for kpb in range(qpb + 1):
            pairs.append((j, qpb, kpb))
    if by_key:
        pairs.sort(key=lambda t: (t[2], t[0]))
    group = [t[2] if by_key else t[0] for t in pairs]
    first = [1 if n == 0 or group[n - 1] != group[n] else 0 for n in range(len(pairs))]
    last = [1 if n == len(pairs) - 1 or group[n + 1] != group[n] else 0 for n in range(len(pairs))]
    table = np.array(
        [
            [t[0] for t in pairs],
            [t[1] for t in pairs],
            [t[2] for t in pairs],
            [kmap[t[2]][0] for t in pairs],
            [kmap[t[2]][1] for t in pairs],
            first,
            last,
        ],
        np.int32,
    )
    return table


def pair_tables(piece, quarter, block, by_key):
    t0 = _pair_tables(0, quarter, block, by_key)
    t1 = _pair_tables(1, quarter, block, by_key)
    assert t0.shape == t1.shape
    return jnp.where(piece == 0, jnp.asarray(t0), jnp.asarray(t1))


def _mask(qpb, kpb, qs, block):
    qp = qpb * block + lax.broadcasted_iota(jnp.int32, (block, block), 0)
    kp = kpb * block + lax.broadcasted_iota(jnp.int32, (block, block), 1)
    start = jnp.tile(qs, (1, block // 128))
    return (kp >= start) & (kp <= qp)


def _fwd_kernel(tab_ref, q_ref, qs_ref, k_ref, v_ref, o_ref, l_ref, acc_ref, sum_ref, *, scale, block):
    n = pl.program_id(1)
    share = q_ref.shape[1]

    @pl.when(tab_ref[5, n] == 1)
    def _():
        acc_ref[...] = jnp.zeros(acc_ref.shape, acc_ref.dtype)
        sum_ref[...] = jnp.zeros(sum_ref.shape, sum_ref.dtype)

    q = q_ref[0].reshape(share * block, HEAD_SIZE)
    k = k_ref[0, 0]
    v = v_ref[0, 0]
    s = lax.dot_general(q, k, TRANS_B, preferred_element_type=jnp.float32) * scale
    allowed = _mask(tab_ref[1, n], tab_ref[2, n], qs_ref[...], block)
    e = jnp.where(allowed[None], jnp.exp(s.reshape(share, block, block)), 0.0)
    sum_ref[...] += jnp.sum(e, axis=-1, keepdims=True)
    acc_ref[...] += jnp.dot(
        e.reshape(share * block, block).astype(jnp.bfloat16), v, preferred_element_type=jnp.float32
    )

    @pl.when(tab_ref[6, n] == 1)
    def _():
        total = sum_ref[...]
        o_ref[0] = acc_ref[...].reshape(share, block, HEAD_SIZE) / total
        l_ref[0] = jnp.broadcast_to(total, (share, block, 128))


def attention_forward(q, qs, k_all, v_all, piece, quarter, block=512):
    kvh, share, rows, _ = q.shape
    tab = pair_tables(piece, quarter, block, False)
    npairs = tab.shape[1]
    scale = HEAD_SIZE ** (-0.5)
    grid_spec = pltpu.PrefetchScalarGridSpec(
        num_scalar_prefetch=1,
        grid=(kvh, npairs),
        in_specs=[
            pl.BlockSpec((1, share, block, HEAD_SIZE), lambda h, n, t: (h, 0, t[0, n], 0)),
            pl.BlockSpec((block, 128), lambda h, n, t: (t[0, n], 0)),
            pl.BlockSpec((1, 1, block, HEAD_SIZE), lambda h, n, t: (t[3, n], h, t[4, n], 0)),
            pl.BlockSpec((1, 1, block, HEAD_SIZE), lambda h, n, t: (t[3, n], h, t[4, n], 0)),
        ],
        out_specs=[
            pl.BlockSpec((1, share, block, HEAD_SIZE), lambda h, n, t: (h, 0, t[0, n], 0)),
            pl.BlockSpec((1, share, block, 128), lambda h, n, t: (h, 0, t[0, n], 0)),
        ],
        scratch_shapes=[
            pltpu.VMEM((share * block, HEAD_SIZE), jnp.float32),
            pltpu.VMEM((share, block, 1), jnp.float32),
        ],
    )
    flops = 4 * kvh * npairs * share * block * block * HEAD_SIZE
    return pl.pallas_call(
        functools.partial(_fwd_kernel, scale=scale, block=block),
        grid_spec=grid_spec,
        out_shape=[
            jax.ShapeDtypeStruct((kvh, share, rows, HEAD_SIZE), jnp.float32),
            jax.ShapeDtypeStruct((kvh, share, rows, 128), jnp.float32),
        ],
        compiler_params=pltpu.CompilerParams(
            dimension_semantics=("arbitrary", "arbitrary"), vmem_limit_bytes=48 * 1024 * 1024
        ),
        cost_estimate=pl.CostEstimate(
            flops=flops, transcendentals=kvh * npairs * share * block * block,
            bytes_accessed=kvh * npairs * (4 * block * HEAD_SIZE * 2),
        ),
        name="attn_fwd",
    )(tab, q, qs, k_all, v_all)


def _bwd_kernel(tab_ref, q_ref, h_ref, dl_ref, qs_ref, k_ref, v_ref, dq_ref, dk_ref, dv_ref, dk_acc, dv_acc, *, scale, block):
    n = pl.program_id(1)
    share = q_ref.shape[1]

    @pl.when(n == 0)
    def _():
        dq_ref[...] = jnp.zeros(dq_ref.shape, dq_ref.dtype)

    @pl.when(tab_ref[5, n] == 1)
    def _():
        dk_acc[...] = jnp.zeros(dk_acc.shape, dk_acc.dtype)
        dv_acc[...] = jnp.zeros(dv_acc.shape, dv_acc.dtype)

    q = q_ref[0].reshape(share * block, HEAD_SIZE)
    hh = h_ref[0].reshape(share * block, HEAD_SIZE)
    k = k_ref[0, 0]
    v = v_ref[0, 0]
    s = lax.dot_general(q, k, TRANS_B, preferred_element_type=jnp.float32) * scale
    allowed = _mask(tab_ref[1, n], tab_ref[2, n], qs_ref[...], block)
    e = jnp.where(allowed[None], jnp.exp(s.reshape(share, block, block)), 0.0)
    dp = lax.dot_general(hh, v, TRANS_B, preferred_element_type=jnp.float32).reshape(share, block, block)
    delta = jnp.tile(dl_ref[0], (1, 1, block // 128))
    ds = (e * (dp - delta)).reshape(share * block, block).astype(jnp.bfloat16)
    rows = pl.ds(pl.multiple_of(tab_ref[0, n] * block, block), block)
    dq_ref[0, :, rows, :] += jnp.dot(ds, k, preferred_element_type=jnp.float32).reshape(share, block, HEAD_SIZE)
    dk_acc[...] += lax.dot_general(ds, q, TRANS_A, preferred_element_type=jnp.float32)
    dv_acc[...] += lax.dot_general(
        e.reshape(share * block, block).astype(jnp.bfloat16), hh, TRANS_A, preferred_element_type=jnp.float32
    )

    @pl.when(tab_ref[6, n] == 1)
    def _():
        dk_ref[0, 0] = dk_acc[...] * scale
        dv_ref[0, 0] = dv_acc[...]


def attention_backward(q, hgrad, delta, qs, k_all, v_all, piece, quarter, block=512):
    kvh, share, rows, _ = q.shape
    tab = pair_tables(piece, quarter, block, True)
    npairs = tab.shape[1]
    scale = HEAD_SIZE ** (-0.5)
    grid_spec = pltpu.PrefetchScalarGridSpec(
        num_scalar_prefetch=1,
        grid=(kvh, npairs),
        in_specs=[
            pl.BlockSpec((1, share, block, HEAD_SIZE), lambda h, n, t: (h, 0, t[0, n], 0)),
            pl.BlockSpec((1, share, block, HEAD_SIZE), lambda h, n, t: (h, 0, t[0, n], 0)),
            pl.BlockSpec((1, share, block, 128), lambda h, n, t: (h, 0, t[0, n], 0)),
            pl.BlockSpec((block, 128), lambda h, n, t: (t[0, n], 0)),
            pl.BlockSpec((1, 1, block, HEAD_SIZE), lambda h, n, t: (t[3, n], h, t[4, n], 0)),
            pl.BlockSpec((1, 1, block, HEAD_SIZE), lambda h, n, t: (t[3, n], h, t[4, n], 0)),
        ],
        out_specs=[
            pl.BlockSpec((1, share, rows, HEAD_SIZE), lambda h, n, t: (h, 0, 0, 0)),
            pl.BlockSpec((1, 1, block, HEAD_SIZE), lambda h, n, t: (t[3, n], h, t[4, n], 0)),
            pl.BlockSpec((1, 1, block, HEAD_SIZE), lambda h, n, t: (t[3, n], h, t[4, n], 0)),
        ],
        scratch_shapes=[
            pltpu.VMEM((block, HEAD_SIZE), jnp.float32),
            pltpu.VMEM((block, HEAD_SIZE), jnp.float32),
        ],
    )
    flops = 10 * kvh * npairs * share * block * block * HEAD_SIZE
    return pl.pallas_call(
        functools.partial(_bwd_kernel, scale=scale, block=block),
        grid_spec=grid_spec,
        out_shape=[
            jax.ShapeDtypeStruct((kvh, share, rows, HEAD_SIZE), jnp.float32),
            jax.ShapeDtypeStruct(k_all.shape, jnp.float32),
            jax.ShapeDtypeStruct(v_all.shape, jnp.float32),
        ],
        compiler_params=pltpu.CompilerParams(
            dimension_semantics=("arbitrary", "arbitrary"), vmem_limit_bytes=56 * 1024 * 1024
        ),
        cost_estimate=pl.CostEstimate(
            flops=flops, transcendentals=kvh * npairs * share * block * block,
            bytes_accessed=kvh * npairs * (8 * block * HEAD_SIZE * 2),
        ),
        name="attn_bwd",
    )(tab, q, hgrad, delta, qs, k_all, v_all)


SLOT_TOKENS = 4096
PIECES = 2


EPSILON = 1e-06
THETA = 1000000.0


def swapped(shard, axis, distance):
    return lax.ppermute(shard, axis, [(i, i ^ 1 << distance) for i in range(lax.axis_size(axis))])


def rms_scale(values, gain):
    inverse = lax.rsqrt(jnp.mean(values * values, axis=-1, keepdims=True) + EPSILON)
    return values * inverse * gain


def rotary(values, start_offset):
    half = values.shape[-1] // 2
    frequency = THETA ** (-(jnp.arange(half, dtype=jnp.float32) * 2.0 / values.shape[-1]))
    angle = start_offset.astype(jnp.float32)[:, None] * frequency[None, :]
    cosine = jnp.cos(angle)[:, None, :]
    sine = jnp.sin(angle)[:, None, :]
    first = values[..., :half]
    second = values[..., half:]
    return jnp.concatenate(
        [first * cosine - second * sine, second * cosine + first * sine], axis=-1
    )


def prepare_inputs(projected, gain, start_offset, head_groups):
    shaped = projected.reshape(projected.shape[0], head_groups, -1)
    return rotary(rms_scale(shaped, gain), start_offset)


def slot_tables(lengths_row, slot_length):
    ends = jnp.cumsum(lengths_row)
    place = jnp.arange(slot_length, dtype=jnp.int32)
    passed = place[:, None] >= ends[None, :]
    segment_ids = jnp.sum(passed.astype(jnp.int32), axis=1)
    start = jnp.sum(jnp.where(passed, lengths_row[None, :], 0), axis=1)
    return (segment_ids, place - start, place < ends[-1])


def piece_places(which, group_rows):
    quarter = group_rows // 2
    local = jnp.arange(group_rows, dtype=jnp.int32)
    chosen = jnp.where(local < quarter, which, 3 - which)
    return chosen * quarter + local % quarter


def contract_rows(left, right):
    return lax.dot_general(
        left, right, (((0,), (0,)), ((), ())), preferred_element_type=jnp.float32
    )


def contract_last(left, right):
    return lax.dot_general(
        left, right, (((1,), (1,)), ((), ())), preferred_element_type=jnp.float32
    )


def gain_column(values, rows_f):
    column = values.astype(jnp.bfloat16)
    return jnp.pad(column, (0, rows_f - column.shape[0]))[:, None]


def gain_rows(column, fs, rows_f, own):
    return column.reshape(fs, rows_f)[:, :own].reshape(fs * own)


def split_columns(full, widths):
    parts = []
    at = 0
    for width in widths:
        parts.append(full[:, at : at + width])
        at += width
    return parts


def halving_scatter(grads):
    widths = [g.shape[1] for g in grads]
    packed = jnp.concatenate(grads, axis=1)
    count = lax.axis_size("fsdp")
    me = lax.axis_index("fsdp")
    rows_f = packed.shape[0] // count
    bits = count.bit_length() - 1
    buf = packed.reshape((2,) * bits + (rows_f, packed.shape[1]))
    for bit in range(bits):
        axis = bits - 1 - bit
        mine = (me >> bit) & 1
        keep = lax.dynamic_index_in_dim(buf, mine, axis, keepdims=False)
        send = lax.dynamic_index_in_dim(buf, 1 - mine, axis, keepdims=False)
        got = lax.ppermute(
            send.astype(jnp.bfloat16), "fsdp", [(i, i ^ (1 << bit)) for i in range(count)]
        )
        buf = keep + got.astype(jnp.float32)
    return split_columns(buf, widths)


def all_sum(values):
    for axis in ("tensor", "fsdp"):
        distance = 1
        while distance < lax.axis_size(axis):
            values = values + lax.ppermute(
                values, axis, [(i, i ^ distance) for i in range(lax.axis_size(axis))]
            )
            distance *= 2
    return values


def exchange(values, distance):
    count = lax.axis_size("tensor")
    return lax.ppermute(values, "tensor", [(i, i ^ distance) for i in range(count)])


def token_gather(values):
    rows = values.shape[0]
    me = lax.axis_index("tensor")
    across = exchange(values, 2)
    pair = jnp.stack([values, across])
    beside = exchange(pair, 1)
    full = jnp.zeros((4 * rows,) + values.shape[1:], values.dtype)
    for part, place in ((values, me), (across, me ^ 2), (beside[0], me ^ 1), (beside[1], me ^ 3)):
        full = lax.dynamic_update_slice_in_dim(full, part, place * rows, 0)
    return full


def token_sum(term, rows):
    partial = term(jnp.int32(0), rows * lax.axis_size("tensor"))
    me = lax.axis_index("tensor")

    def block(place):
        return lax.dynamic_slice_in_dim(partial, place * rows, rows, 0)

    sent = jnp.stack([block(me ^ 1), block(me ^ 3)]).astype(jnp.bfloat16)
    got = exchange(sent, 1).astype(jnp.float32)
    mine = block(me) + got[0]
    other = (block(me ^ 2) + got[1]).astype(jnp.bfloat16)
    return mine + exchange(other, 2).astype(jnp.float32)


def shards(
    hidden,
    out_grad,
    lengths,
    q_weight,
    key_matrix,
    value_matrix,
    o_weight,
    gate_weight,
    up_weight,
    down_weight,
    input_gain,
    q_gain,
    k_gain,
    post_gain,
):
    split = lax.axis_size("tensor")
    rows = hidden.shape[0]
    group_rows = rows * split
    q_heads = q_weight.shape[1] // HEAD_SIZE
    kv_heads = key_matrix.shape[1] // HEAD_SIZE
    share = q_heads // kv_heads
    scale = HEAD_SIZE ** (-0.5)
    member = lax.axis_index("fsdp")
    slot = member // PIECES
    piece = member % PIECES
    segment_ids, start_offset, valid = slot_tables(
        lax.dynamic_index_in_dim(lengths, slot, 0, keepdims=False), SLOT_TOKENS
    )
    group_place = piece_places(piece, group_rows)
    group_segment = jnp.take(segment_ids, group_place)
    group_offset = jnp.take(start_offset, group_place)
    local_valid = lax.dynamic_slice_in_dim(
        jnp.take(valid, group_place), lax.axis_index("tensor") * rows, rows, 0
    )
    fs = lax.axis_size("fsdp")
    rows_f = q_weight.shape[0]
    attn_full = lax.all_gather(
        jnp.concatenate(
            [
                q_weight.astype(jnp.bfloat16),
                key_matrix.astype(jnp.bfloat16),
                value_matrix.astype(jnp.bfloat16),
                jnp.transpose(o_weight).astype(jnp.bfloat16),
                gain_column(input_gain, rows_f),
                gain_column(q_gain, rows_f),
                gain_column(k_gain, rows_f),
                gain_column(post_gain, rows_f),
            ],
            axis=1,
        ),
        "fsdp",
        axis=0,
        tiled=True,
    )
    widths = (q_weight.shape[1], key_matrix.shape[1], value_matrix.shape[1], o_weight.shape[0])
    w_query, w_key, w_value, w_out = split_columns(attn_full, widths)
    gains_at = sum(widths)
    gain_in = attn_full[:, gains_at]
    gain_query = gain_rows(attn_full[:, gains_at + 1], fs, rows_f, q_gain.shape[0])
    gain_keys = gain_rows(attn_full[:, gains_at + 2], fs, rows_f, k_gain.shape[0])
    gain_post = attn_full[:, gains_at + 3]
    x_float = hidden.astype(jnp.float32)
    gain_first = gain_in.astype(jnp.float32)
    first_all = token_gather(rms_scale(x_float, gain_first).astype(jnp.bfloat16))
    query_projected = jnp.dot(first_all, w_query, preferred_element_type=jnp.float32)
    key_projected = jnp.dot(first_all, w_key, preferred_element_type=jnp.float32)
    value_rows = (
        jnp.dot(first_all, w_value, preferred_element_type=jnp.float32)
        .astype(jnp.bfloat16)
        .reshape(group_rows, kv_heads, HEAD_SIZE)
    )
    gain_q = gain_query.astype(jnp.float32)
    gain_k = gain_keys.astype(jnp.float32)
    query_rope = (
        prepare_inputs(query_projected, gain_q, group_offset, q_heads)
        .astype(jnp.bfloat16)
        .reshape(group_rows, kv_heads, share, HEAD_SIZE)
    )
    key_rope = prepare_inputs(key_projected, gain_k, group_offset, kv_heads).astype(jnp.bfloat16)
    moved = swapped(jnp.stack([key_rope, value_rows]), "fsdp", 0)
    quarter = group_rows // 2
    query_start = jnp.broadcast_to((group_place - group_offset)[:, None], (group_rows, 128))
    query_t = jnp.transpose(query_rope, (1, 2, 0, 3))
    keys_all = jnp.stack([jnp.transpose(key_rope, (1, 0, 2)), jnp.transpose(moved[0], (1, 0, 2))])
    values_all = jnp.stack([jnp.transpose(value_rows, (1, 0, 2)), jnp.transpose(moved[1], (1, 0, 2))])
    heads_t, totals_t = attention_forward(query_t, query_start, keys_all, values_all, piece, quarter)
    heads_out = jnp.transpose(heads_t, (2, 0, 1, 3))
    row_totals = jnp.transpose(totals_t[..., 0], (2, 0, 1))
    out_rows = heads_out.reshape(group_rows, q_heads * HEAD_SIZE).astype(jnp.bfloat16)

    def out_term(start, count):
        return contract_last(out_rows, w_out)

    after_attn = x_float + token_sum(out_term, rows)
    mlp_full = lax.all_gather(
        jnp.concatenate(
            [
                gate_weight.astype(jnp.bfloat16),
                up_weight.astype(jnp.bfloat16),
                jnp.transpose(down_weight).astype(jnp.bfloat16),
            ],
            axis=1,
        ),
        "fsdp",
        axis=0,
        tiled=True,
    )
    w_gate, w_up, w_down_t = split_columns(
        mlp_full, (gate_weight.shape[1], up_weight.shape[1], down_weight.shape[0])
    )
    gain_second = gain_post.astype(jnp.float32)
    second_all = token_gather(rms_scale(after_attn, gain_second).astype(jnp.bfloat16))
    gate_out = jnp.dot(second_all, w_gate, preferred_element_type=jnp.float32)
    up_out = jnp.dot(second_all, w_up, preferred_element_type=jnp.float32)
    activated = (jax.nn.silu(gate_out) * up_out).astype(jnp.bfloat16)

    def down_term(start, count):
        return contract_last(activated, w_down_t)

    output = (after_attn + token_sum(down_term, rows)).astype(jnp.bfloat16)
    cotangent = out_grad.astype(jnp.float32) * local_valid[:, None].astype(jnp.float32)
    mlp_grad_all = token_gather(cotangent.astype(jnp.bfloat16))
    grad_act = jnp.dot(mlp_grad_all, w_down_t, preferred_element_type=jnp.float32)
    unused, pull_gate = jax.vjp(
        lambda gate_in, up_in: jax.nn.silu(gate_in) * up_in, gate_out, up_out
    )
    grad_gate, grad_up = pull_gate(grad_act)
    grad_gate = grad_gate.astype(jnp.bfloat16)
    grad_up = grad_up.astype(jnp.bfloat16)
    down_grad_t = contract_rows(mlp_grad_all, activated)
    gate_grad = contract_rows(second_all, grad_gate)
    up_grad = contract_rows(second_all, grad_up)

    def second_term(start, count):
        return contract_last(grad_gate, w_gate) + contract_last(grad_up, w_up)

    second_back = token_sum(second_term, rows)
    unused, pull_second = jax.vjp(rms_scale, after_attn, gain_second)
    norm_second_grad, post_gain_part = pull_second(second_back)
    residual_grad = cotangent + norm_second_grad
    attn_grad_all = token_gather(residual_grad.astype(jnp.bfloat16))
    out_weight_grad_t = contract_rows(attn_grad_all, out_rows)
    mlp_packed = jnp.concatenate(
        [g.astype(jnp.bfloat16) for g in (gate_grad, up_grad, down_grad_t, out_weight_grad_t)],
        axis=1,
    )
    head_grad = jnp.dot(attn_grad_all, w_out, preferred_element_type=jnp.float32).astype(
        jnp.bfloat16
    )
    head_float = head_grad.astype(jnp.float32).reshape(group_rows, kv_heads, share, HEAD_SIZE)
    scaled_grad = (head_float / row_totals[..., None]).astype(jnp.bfloat16)
    delta = jnp.sum(head_float * heads_out, axis=-1) / row_totals

    grad_t = jnp.transpose(scaled_grad, (1, 2, 0, 3))
    delta_t = jnp.broadcast_to(
        jnp.transpose(delta, (1, 2, 0))[..., None], (kv_heads, share, group_rows, 128)
    )
    mlp_packed, grad_t, delta_t = lax.optimization_barrier((mlp_packed, grad_t, delta_t))
    mlp_shards = split_columns(
        lax.psum_scatter(mlp_packed, "fsdp", scatter_dimension=0, tiled=True),
        [g.shape[1] for g in (gate_grad, up_grad, down_grad_t, out_weight_grad_t)],
    )
    mlp_shards = [part.astype(jnp.float32) for part in mlp_shards]
    dq_raw, dk_all, dv_all = attention_backward(
        query_t, grad_t, delta_t, query_start, keys_all, values_all, piece, quarter
    )
    mlp_shards, dq_raw = lax.optimization_barrier((mlp_shards, dq_raw))
    unseen = (piece == 1) & (jnp.arange(group_rows) >= quarter)
    far_grads = jnp.where(unseen[None, None, :, None], 0.0, jnp.stack([dk_all[1], dv_all[1]]))
    returned = swapped(far_grads.astype(jnp.bfloat16), "fsdp", 0).astype(jnp.float32)
    grad_keys_total = jnp.transpose(dk_all[0] + returned[0], (1, 0, 2))
    grad_values_total = jnp.transpose(dv_all[0] + returned[1], (1, 0, 2))
    query_grads = jnp.transpose(dq_raw, (2, 0, 1, 3)) * scale
    query_grads = query_grads.reshape(group_rows, q_heads, HEAD_SIZE)
    unused, pull_query = jax.vjp(
        lambda projected, gain: prepare_inputs(projected, gain, group_offset, q_heads),
        query_projected,
        gain_q,
    )
    query_proj_grad, q_gain_part = pull_query(query_grads)
    unused, pull_key = jax.vjp(
        lambda projected, gain: prepare_inputs(projected, gain, group_offset, kv_heads),
        key_projected,
        gain_k,
    )
    key_proj_grad, k_gain_part = pull_key(grad_keys_total)
    query_low = query_proj_grad.astype(jnp.bfloat16)
    key_low = key_proj_grad.astype(jnp.bfloat16)
    value_low = grad_values_total.reshape(group_rows, kv_heads * HEAD_SIZE).astype(jnp.bfloat16)
    query_weight_grad = contract_rows(first_all, query_low)
    key_weight_grad = contract_rows(first_all, key_low)
    value_weight_grad = contract_rows(first_all, value_low)

    def first_term(start, count):
        return (
            contract_last(query_low, w_query)
            + contract_last(key_low, w_key)
            + contract_last(value_low, w_value)
        )

    first_back = token_sum(first_term, rows)
    unused, pull_first = jax.vjp(rms_scale, x_float, gain_first)
    norm_first_grad, input_gain_part = pull_first(first_back)
    input_grad = (residual_grad + norm_first_grad).astype(jnp.bfloat16)
    query_shard, key_shard, value_shard = halving_scatter(
        (query_weight_grad, key_weight_grad, value_weight_grad)
    )
    gain_totals = all_sum(
        jnp.concatenate([input_gain_part, q_gain_part, k_gain_part, post_gain_part])
    )
    member_f = lax.axis_index("fsdp")
    sizes = (input_gain.shape[0], q_gain.shape[0], k_gain.shape[0], post_gain.shape[0])
    gain_shards = []
    at = 0
    for own in sizes:
        whole = own * fs
        gain_shards.append(lax.dynamic_slice_in_dim(gain_totals, at + member_f * own, own, 0))
        at += whole
    input_gain_shard, q_gain_shard, k_gain_shard, post_gain_shard = gain_shards
    gate_shard, up_shard, down_shard_t, out_shard_t = mlp_shards
    return (
        output,
        input_grad,
        query_shard,
        key_shard,
        value_shard,
        jnp.transpose(out_shard_t),
        gate_shard,
        up_shard,
        jnp.transpose(down_shard_t),
        input_gain_shard,
        q_gain_shard,
        k_gain_shard,
        post_gain_shard,
    )


def solution(mesh):
    return layer_program(mesh)


def layer_program(mesh):
    placed = (
        P(("fsdp", "tensor"), None),
        P(("fsdp", "tensor"), None),
        P(),
        P("fsdp", "tensor"),
        P("fsdp", "tensor"),
        P("fsdp", "tensor"),
        P("tensor", "fsdp"),
        P("fsdp", "tensor"),
        P("fsdp", "tensor"),
        P("tensor", "fsdp"),
        P("fsdp"),
        P("fsdp"),
        P("fsdp"),
        P("fsdp"),
    )
    return jax.shard_map(
        shards,
        mesh=mesh,
        in_specs=placed,
        out_specs=(
            P(("fsdp", "tensor"), None),
            P(("fsdp", "tensor"), None),
            P("fsdp", "tensor"),
            P("fsdp", "tensor"),
            P("fsdp", "tensor"),
            P("tensor", "fsdp"),
            P("fsdp", "tensor"),
            P("fsdp", "tensor"),
            P("tensor", "fsdp"),
            P("fsdp"),
            P("fsdp"),
            P("fsdp"),
            P("fsdp"),
        ),
        check_vma=False,
    )
```

```python
import functools

import numpy as np
import jax
import jax.numpy as jnp
from jax import lax
from jax.experimental import pallas as pl
from jax.experimental.pallas import tpu as pltpu
from jax.sharding import PartitionSpec as P


HEAD_SIZE = 128
TRANS_B = (((1,), (1,)), ((), ()))
TRANS_A = (((0,), (0,)), ((), ()))


def _own_place(p, quarter, r):
    return (p * quarter + r) if r < quarter else ((3 - p) * quarter + r - quarter)


def _far_place(p, quarter, r):
    return ((1 - p) * quarter + r) if r < quarter else ((2 + p) * quarter + r - quarter)


def _pair_tables(p, quarter, block, by_key, source):
    rows = 2 * quarter
    count = rows // block
    kmap = {}
    for src, fn in ((0, _own_place), (1, _far_place)):
        for j in range(count):
            kmap[fn(p, quarter, j * block) // block] = (src, j)
    pairs = []
    for j in range(count):
        qpb = _own_place(p, quarter, j * block) // block
        for kpb in range(qpb + 1):
            if kmap[kpb][0] == source:
                pairs.append((j, qpb, kpb))
    if by_key:
        pairs.sort(key=lambda t: (t[2], t[0]))
    group = [t[2] if by_key else t[0] for t in pairs]
    size = len(pairs)
    first = [1 if n == 0 or group[n - 1] != group[n] else 0 for n in range(size)]
    last = [1 if n == size - 1 or group[n + 1] != group[n] else 0 for n in range(size)]
    return np.array(
        [
            [t[0] for t in pairs],
            [t[1] for t in pairs],
            [t[2] for t in pairs],
            [kmap[t[2]][0] for t in pairs],
            [kmap[t[2]][1] for t in pairs],
            first,
            last,
        ],
        np.int32,
    )


def pair_tables(piece, quarter, block, by_key, source):
    t0 = _pair_tables(0, quarter, block, by_key, source)
    t1 = _pair_tables(1, quarter, block, by_key, source)
    assert t0.shape == t1.shape
    return jnp.where(piece == 0, jnp.asarray(t0), jnp.asarray(t1))


def _mask(qpb, kpb, qs, block):
    qp = qpb * block + lax.broadcasted_iota(jnp.int32, (block, block), 0)
    kp = kpb * block + lax.broadcasted_iota(jnp.int32, (block, block), 1)
    start = jnp.tile(qs, (1, block // 128))
    return (kp >= start) & (kp <= qp)


def _fwd_kernel(tab_ref, q_ref, qs_ref, k_ref, v_ref, a_in_ref, l_in_ref, a_ref, l_ref, acc_ref, sum_ref, *, scale, block):
    n = pl.program_id(1)
    share = q_ref.shape[1]

    @pl.when(tab_ref[5, n] == 1)
    def _():
        acc_ref[...] = a_in_ref[0].reshape(share * block, HEAD_SIZE)
        sum_ref[...] = l_in_ref[0][:, :, :1]

    q = q_ref[0].reshape(share * block, HEAD_SIZE)
    k = k_ref[0]
    v = v_ref[0]
    s = lax.dot_general(q, k, TRANS_B, preferred_element_type=jnp.float32) * scale
    allowed = _mask(tab_ref[1, n], tab_ref[2, n], qs_ref[...], block)
    e = jnp.where(allowed[None], jnp.exp(s.reshape(share, block, block)), 0.0)
    sum_ref[...] += jnp.sum(e, axis=-1, keepdims=True)
    acc_ref[...] += jnp.dot(
        e.reshape(share * block, block).astype(jnp.bfloat16), v, preferred_element_type=jnp.float32
    )

    @pl.when(tab_ref[6, n] == 1)
    def _():
        a_ref[0] = acc_ref[...].reshape(share, block, HEAD_SIZE)
        l_ref[0] = jnp.broadcast_to(sum_ref[...], (share, block, 128))


def attention_forward(q, qs, keys, values, a_in, l_in, piece, quarter, source, block=512):
    kvh, share, _, _ = q.shape
    tab = pair_tables(piece, quarter, block, False, source)
    npairs = tab.shape[1]
    scale = HEAD_SIZE ** (-0.5)
    row_spec = pl.BlockSpec((1, share, block, HEAD_SIZE), lambda h, n, t: (h, 0, t[0, n], 0))
    lane_spec = pl.BlockSpec((1, share, block, 128), lambda h, n, t: (h, 0, t[0, n], 0))
    key_spec = pl.BlockSpec((1, block, HEAD_SIZE), lambda h, n, t: (h, t[4, n], 0))
    grid_spec = pltpu.PrefetchScalarGridSpec(
        num_scalar_prefetch=1,
        grid=(kvh, npairs),
        in_specs=[
            row_spec,
            pl.BlockSpec((block, 128), lambda h, n, t: (t[0, n], 0)),
            key_spec,
            key_spec,
            row_spec,
            lane_spec,
        ],
        out_specs=[row_spec, lane_spec],
        scratch_shapes=[
            pltpu.VMEM((share * block, HEAD_SIZE), jnp.float32),
            pltpu.VMEM((share, block, 1), jnp.float32),
        ],
    )
    flops = 4 * kvh * npairs * share * block * block * HEAD_SIZE
    return pl.pallas_call(
        functools.partial(_fwd_kernel, scale=scale, block=block),
        grid_spec=grid_spec,
        out_shape=[
            jax.ShapeDtypeStruct(a_in.shape, jnp.float32),
            jax.ShapeDtypeStruct(l_in.shape, jnp.float32),
        ],
        input_output_aliases={5: 0, 6: 1},
        compiler_params=pltpu.CompilerParams(
            dimension_semantics=("arbitrary", "arbitrary"), vmem_limit_bytes=48 * 1024 * 1024
        ),
        cost_estimate=pl.CostEstimate(
            flops=flops,
            transcendentals=kvh * npairs * share * block * block,
            bytes_accessed=kvh * npairs * (8 * block * HEAD_SIZE * 2),
        ),
        name="attn_fwd",
    )(tab, q, qs, keys, values, a_in, l_in)


def _bwd_kernel(tab_ref, q_ref, h_ref, dl_ref, qs_ref, k_ref, v_ref, dq_in_ref, dq_ref, dk_ref, dv_ref, dk_acc, dv_acc, *, scale, block):
    n = pl.program_id(1)
    share = q_ref.shape[1]

    @pl.when(n == 0)
    def _():
        dq_ref[...] = dq_in_ref[...]

    @pl.when(tab_ref[5, n] == 1)
    def _():
        dk_acc[...] = jnp.zeros(dk_acc.shape, dk_acc.dtype)
        dv_acc[...] = jnp.zeros(dv_acc.shape, dv_acc.dtype)

    q = q_ref[0].reshape(share * block, HEAD_SIZE)
    hh = h_ref[0].reshape(share * block, HEAD_SIZE)
    k = k_ref[0]
    v = v_ref[0]
    s = lax.dot_general(q, k, TRANS_B, preferred_element_type=jnp.float32) * scale
    allowed = _mask(tab_ref[1, n], tab_ref[2, n], qs_ref[...], block)
    e = jnp.where(allowed[None], jnp.exp(s.reshape(share, block, block)), 0.0)
    dp = lax.dot_general(hh, v, TRANS_B, preferred_element_type=jnp.float32).reshape(share, block, block)
    delta = jnp.tile(dl_ref[0], (1, 1, block // 128))
    ds = (e * (dp - delta)).reshape(share * block, block).astype(jnp.bfloat16)
    rows = pl.ds(pl.multiple_of(tab_ref[0, n] * block, block), block)
    dq_ref[0, :, rows, :] += jnp.dot(ds, k, preferred_element_type=jnp.float32).reshape(share, block, HEAD_SIZE)
    dk_acc[...] += lax.dot_general(ds, q, TRANS_A, preferred_element_type=jnp.float32)
    dv_acc[...] += lax.dot_general(
        e.reshape(share * block, block).astype(jnp.bfloat16), hh, TRANS_A, preferred_element_type=jnp.float32
    )

    @pl.when(tab_ref[6, n] == 1)
    def _():
        dk_ref[0] = dk_acc[...] * scale
        dv_ref[0] = dv_acc[...]


def attention_backward(q, hgrad, delta, qs, keys, values, dq_in, piece, quarter, source, block=512):
    kvh, share, rows, _ = q.shape
    tab = pair_tables(piece, quarter, block, True, source)
    npairs = tab.shape[1]
    scale = HEAD_SIZE ** (-0.5)
    row_spec = pl.BlockSpec((1, share, block, HEAD_SIZE), lambda h, n, t: (h, 0, t[0, n], 0))
    key_spec = pl.BlockSpec((1, block, HEAD_SIZE), lambda h, n, t: (h, t[4, n], 0))
    full_spec = pl.BlockSpec((1, share, rows, HEAD_SIZE), lambda h, n, t: (h, 0, 0, 0))
    grid_spec = pltpu.PrefetchScalarGridSpec(
        num_scalar_prefetch=1,
        grid=(kvh, npairs),
        in_specs=[
            row_spec,
            row_spec,
            pl.BlockSpec((1, share, block, 128), lambda h, n, t: (h, 0, t[0, n], 0)),
            pl.BlockSpec((block, 128), lambda h, n, t: (t[0, n], 0)),
            key_spec,
            key_spec,
            full_spec,
        ],
        out_specs=[full_spec, key_spec, key_spec],
        scratch_shapes=[
            pltpu.VMEM((block, HEAD_SIZE), jnp.float32),
            pltpu.VMEM((block, HEAD_SIZE), jnp.float32),
        ],
    )
    flops = 10 * kvh * npairs * share * block * block * HEAD_SIZE
    return pl.pallas_call(
        functools.partial(_bwd_kernel, scale=scale, block=block),
        grid_spec=grid_spec,
        out_shape=[
            jax.ShapeDtypeStruct(dq_in.shape, jnp.float32),
            jax.ShapeDtypeStruct(keys.shape, jnp.float32),
            jax.ShapeDtypeStruct(values.shape, jnp.float32),
        ],
        input_output_aliases={7: 0},
        compiler_params=pltpu.CompilerParams(
            dimension_semantics=("arbitrary", "arbitrary"), vmem_limit_bytes=56 * 1024 * 1024
        ),
        cost_estimate=pl.CostEstimate(
            flops=flops,
            transcendentals=kvh * npairs * share * block * block,
            bytes_accessed=kvh * npairs * (10 * block * HEAD_SIZE * 2),
        ),
        name="attn_bwd",
    )(tab, q, hgrad, delta, qs, keys, values, dq_in)


PIECES = 2


EPSILON = 1e-06
THETA = 1000000.0


def swapped(shard, axis, distance):
    return lax.ppermute(shard, axis, [(i, i ^ 1 << distance) for i in range(lax.axis_size(axis))])


def rms_scale(values, gain):
    inverse = lax.rsqrt(jnp.mean(values * values, axis=-1, keepdims=True) + EPSILON)
    return values * inverse * gain


def rotary(values, start_offset):
    half = values.shape[-1] // 2
    frequency = THETA ** (-(jnp.arange(half, dtype=jnp.float32) * 2.0 / values.shape[-1]))
    angle = start_offset.astype(jnp.float32)[:, None] * frequency[None, :]
    cosine = jnp.cos(angle)[:, None, :]
    sine = jnp.sin(angle)[:, None, :]
    first = values[..., :half]
    second = values[..., half:]
    return jnp.concatenate(
        [first * cosine - second * sine, second * cosine + first * sine], axis=-1
    )


def prepare_inputs(projected, gain, start_offset, head_groups):
    shaped = projected.reshape(projected.shape[0], head_groups, -1)
    return rotary(rms_scale(shaped, gain), start_offset)


def piece_places(which, group_rows):
    quarter = group_rows // 2
    local = jnp.arange(group_rows, dtype=jnp.int32)
    chosen = jnp.where(local < quarter, which, 3 - which)
    return chosen * quarter + local % quarter


def contract_rows(left, right):
    return lax.dot_general(
        left, right, (((0,), (0,)), ((), ())), preferred_element_type=jnp.float32
    )


def contract_last(left, right):
    return lax.dot_general(
        left, right, (((1,), (1,)), ((), ())), preferred_element_type=jnp.float32
    )


def split_columns(full, widths):
    parts = []
    at = 0
    for width in widths:
        parts.append(full[:, at : at + width])
        at += width
    return parts


def halving_scatter(grads):
    widths = [g.shape[1] for g in grads]
    packed = jnp.concatenate(grads, axis=1)
    count = lax.axis_size("fsdp")
    me = lax.axis_index("fsdp")
    rows_f = packed.shape[0] // count
    bits = count.bit_length() - 1
    buf = packed.reshape((2,) * bits + (rows_f, packed.shape[1]))
    for bit in range(bits):
        axis = bits - 1 - bit
        mine = (me >> bit) & 1
        keep = lax.dynamic_index_in_dim(buf, mine, axis, keepdims=False)
        send = lax.dynamic_index_in_dim(buf, 1 - mine, axis, keepdims=False)
        got = lax.ppermute(
            send.astype(jnp.bfloat16), "fsdp", [(i, i ^ (1 << bit)) for i in range(count)]
        )
        buf = keep + got.astype(jnp.float32)
    return split_columns(buf, widths)


def fsdp_gather(values):
    count = lax.axis_size("fsdp")
    me = lax.axis_index("fsdp")
    distance = 1
    while distance < count:
        got = lax.ppermute(values, "fsdp", [(i, i ^ distance) for i in range(count)])
        low = (me & distance) == 0
        values = jnp.concatenate(
            [jnp.where(low, values, got), jnp.where(low, got, values)]
        )
        distance *= 2
    return values


def all_sum(values):
    for axis in ("tensor", "fsdp"):
        distance = 1
        while distance < lax.axis_size(axis):
            values = values + lax.ppermute(
                values, axis, [(i, i ^ distance) for i in range(lax.axis_size(axis))]
            )
            distance *= 2
    return values


def exchange(values, distance):
    count = lax.axis_size("tensor")
    return lax.ppermute(values, "tensor", [(i, i ^ distance) for i in range(count)])


def token_gather(values):
    rows = values.shape[0]
    me = lax.axis_index("tensor")
    across = exchange(values, 2)
    pair = jnp.stack([values, across])
    beside = exchange(pair, 1)
    full = jnp.zeros((4 * rows,) + values.shape[1:], values.dtype)
    for part, place in ((values, me), (across, me ^ 2), (beside[0], me ^ 1), (beside[1], me ^ 3)):
        full = lax.dynamic_update_slice_in_dim(full, part, place * rows, 0)
    return full


def token_sum(term, rows):
    partial = term(jnp.int32(0), rows * lax.axis_size("tensor"))
    me = lax.axis_index("tensor")

    def block(place):
        return lax.dynamic_slice_in_dim(partial, place * rows, rows, 0)

    sent = jnp.stack([block(me ^ 1), block(me ^ 3)]).astype(jnp.bfloat16)
    got = exchange(sent, 1).astype(jnp.float32)
    mine = block(me) + got[0]
    other = (block(me ^ 2) + got[1]).astype(jnp.bfloat16)
    return mine + exchange(other, 2).astype(jnp.float32)


def shards(
    hidden,
    out_grad,
    lengths,
    q_weight,
    key_matrix,
    value_matrix,
    o_weight,
    gate_weight,
    up_weight,
    down_weight,
    input_gain,
    q_gain,
    k_gain,
    post_gain,
):
    split = lax.axis_size("tensor")
    rows = hidden.shape[0]
    group_rows = rows * split
    q_heads = q_weight.shape[1] // HEAD_SIZE
    kv_heads = key_matrix.shape[1] // HEAD_SIZE
    share = q_heads // kv_heads
    scale = HEAD_SIZE ** (-0.5)
    member = lax.axis_index("fsdp")
    slot = member // PIECES
    piece = member % PIECES
    lengths_row = lax.dynamic_index_in_dim(lengths, slot, 0, keepdims=False)
    ends = jnp.cumsum(lengths_row)
    group_place = piece_places(piece, group_rows)
    passed = group_place[:, None] >= ends[None, :]
    group_start = jnp.sum(jnp.where(passed, lengths_row[None, :], 0), axis=1)
    group_offset = group_place - group_start
    local_valid = lax.dynamic_slice_in_dim(
        group_place < ends[-1], lax.axis_index("tensor") * rows, rows, 0
    )
    fs = lax.axis_size("fsdp")
    gain_sizes = (input_gain.shape[0], q_gain.shape[0], k_gain.shape[0], post_gain.shape[0])
    gains_all = fsdp_gather(
        jnp.concatenate([input_gain, q_gain, k_gain, post_gain]).astype(jnp.bfloat16)
    ).reshape(fs, sum(gain_sizes))
    gain_in, gain_query, gain_keys, gain_post = [
        part.reshape(-1) for part in split_columns(gains_all, gain_sizes)
    ]
    attn_full = lax.all_gather(
        jnp.concatenate(
            [
                q_weight.astype(jnp.bfloat16),
                key_matrix.astype(jnp.bfloat16),
                value_matrix.astype(jnp.bfloat16),
            ],
            axis=1,
        ),
        "fsdp",
        axis=0,
        tiled=True,
    )
    widths = (q_weight.shape[1], key_matrix.shape[1], value_matrix.shape[1])
    w_query, w_key, w_value = split_columns(attn_full, widths)
    x_float = hidden.astype(jnp.float32)
    gain_first = gain_in.astype(jnp.float32)
    first_all = token_gather(rms_scale(x_float, gain_first).astype(jnp.bfloat16))
    query_projected = jnp.dot(first_all, w_query, preferred_element_type=jnp.float32)
    key_projected = jnp.dot(first_all, w_key, preferred_element_type=jnp.float32)
    value_rows = (
        jnp.dot(first_all, w_value, preferred_element_type=jnp.float32)
        .astype(jnp.bfloat16)
        .reshape(group_rows, kv_heads, HEAD_SIZE)
    )
    gain_q = gain_query.astype(jnp.float32)
    gain_k = gain_keys.astype(jnp.float32)
    query_rope = (
        prepare_inputs(query_projected, gain_q, group_offset, q_heads)
        .astype(jnp.bfloat16)
        .reshape(group_rows, kv_heads, share, HEAD_SIZE)
    )
    key_rope = prepare_inputs(key_projected, gain_k, group_offset, kv_heads).astype(jnp.bfloat16)
    quarter = group_rows // 2
    query_start = jnp.broadcast_to(group_start[:, None], (group_rows, 128))
    query_t = jnp.transpose(query_rope, (1, 2, 0, 3))
    own_keys = jnp.transpose(key_rope, (1, 0, 2))
    own_values = jnp.transpose(value_rows, (1, 0, 2))
    moved = swapped(jnp.stack([own_keys, own_values]), "fsdp", 0)
    sums = jnp.zeros(query_t.shape, jnp.float32)
    totals = jnp.zeros(query_t.shape[:3] + (128,), jnp.float32)
    sums, totals = attention_forward(
        query_t, query_start, own_keys, own_values, sums, totals, piece, quarter, 0
    )
    sums, totals_t = attention_forward(
        query_t, query_start, moved[0], moved[1], sums, totals, piece, quarter, 1
    )
    heads_t = sums / totals_t[..., :1]
    heads_out = jnp.transpose(heads_t, (2, 0, 1, 3))
    row_totals = jnp.transpose(totals_t[..., 0], (2, 0, 1))
    out_rows = heads_out.reshape(group_rows, q_heads * HEAD_SIZE).astype(jnp.bfloat16)

    mlp_full = lax.all_gather(
        jnp.concatenate(
            [
                gate_weight.astype(jnp.bfloat16),
                up_weight.astype(jnp.bfloat16),
                jnp.transpose(down_weight).astype(jnp.bfloat16),
                jnp.transpose(o_weight).astype(jnp.bfloat16),
            ],
            axis=1,
        ),
        "fsdp",
        axis=0,
        tiled=True,
    )
    w_gate, w_up, w_down_t, w_out = split_columns(
        mlp_full, (gate_weight.shape[1], up_weight.shape[1], down_weight.shape[0], o_weight.shape[0])
    )

    def out_term(start, count):
        return contract_last(out_rows, w_out)

    after_attn = x_float + token_sum(out_term, rows)
    gain_second = gain_post.astype(jnp.float32)
    second_all = token_gather(rms_scale(after_attn, gain_second).astype(jnp.bfloat16))
    gate_out = jnp.dot(second_all, w_gate, preferred_element_type=jnp.float32)
    up_out = jnp.dot(second_all, w_up, preferred_element_type=jnp.float32)
    activated = (jax.nn.silu(gate_out) * up_out).astype(jnp.bfloat16)

    def down_term(start, count):
        return contract_last(activated, w_down_t)

    output = (after_attn + token_sum(down_term, rows)).astype(jnp.bfloat16)
    cotangent = out_grad.astype(jnp.float32) * local_valid[:, None].astype(jnp.float32)
    mlp_grad_all = token_gather(cotangent.astype(jnp.bfloat16))
    grad_act = jnp.dot(mlp_grad_all, w_down_t, preferred_element_type=jnp.float32)
    unused, pull_gate = jax.vjp(
        lambda gate_in, up_in: jax.nn.silu(gate_in) * up_in, gate_out, up_out
    )
    grad_gate, grad_up = pull_gate(grad_act)
    grad_gate = grad_gate.astype(jnp.bfloat16)
    grad_up = grad_up.astype(jnp.bfloat16)
    down_grad_t = contract_rows(mlp_grad_all, activated)
    gate_grad = contract_rows(second_all, grad_gate)
    up_grad = contract_rows(second_all, grad_up)

    def second_term(start, count):
        return contract_last(grad_gate, w_gate) + contract_last(grad_up, w_up)

    second_back = token_sum(second_term, rows)
    unused, pull_second = jax.vjp(rms_scale, after_attn, gain_second)
    norm_second_grad, post_gain_part = pull_second(second_back)
    residual_grad = cotangent + norm_second_grad
    attn_grad_all = token_gather(residual_grad.astype(jnp.bfloat16))
    out_weight_grad_t = contract_rows(attn_grad_all, out_rows)
    mlp_packed = jnp.concatenate(
        [g.astype(jnp.bfloat16) for g in (gate_grad, up_grad, down_grad_t, out_weight_grad_t)],
        axis=1,
    )
    head_grad = jnp.dot(attn_grad_all, w_out, preferred_element_type=jnp.float32).astype(
        jnp.bfloat16
    )
    head_float = head_grad.astype(jnp.float32).reshape(group_rows, kv_heads, share, HEAD_SIZE)
    scaled_grad = (head_float / row_totals[..., None]).astype(jnp.bfloat16)
    delta = jnp.sum(head_float * heads_out, axis=-1) / row_totals

    grad_t = jnp.transpose(scaled_grad, (1, 2, 0, 3))
    delta_t = jnp.broadcast_to(
        jnp.transpose(delta, (1, 2, 0))[..., None], (kv_heads, share, group_rows, 128)
    )
    mlp_packed, grad_t, delta_t = lax.optimization_barrier((mlp_packed, grad_t, delta_t))
    mlp_shards = split_columns(
        lax.psum_scatter(mlp_packed, "fsdp", scatter_dimension=0, tiled=True),
        [g.shape[1] for g in (gate_grad, up_grad, down_grad_t, out_weight_grad_t)],
    )
    mlp_shards = [part.astype(jnp.float32) for part in mlp_shards]
    dq_raw, dk_far, dv_far = attention_backward(
        query_t, grad_t, delta_t, query_start, moved[0], moved[1],
        jnp.zeros(query_t.shape, jnp.float32), piece, quarter, 1,
    )
    unseen = (piece == 1) & (jnp.arange(group_rows) >= quarter)
    far_grads = jnp.where(unseen[None, None, :, None], 0.0, jnp.stack([dk_far, dv_far]))
    returned = swapped(far_grads.astype(jnp.bfloat16), "fsdp", 0)
    dq_raw, dk_own, dv_own = attention_backward(
        query_t, grad_t, delta_t, query_start, own_keys, own_values,
        dq_raw, piece, quarter, 0,
    )
    mlp_shards, dq_raw = lax.optimization_barrier((mlp_shards, dq_raw))
    grad_keys_total = jnp.transpose(dk_own + returned[0].astype(jnp.float32), (1, 0, 2))
    grad_values_total = jnp.transpose(dv_own + returned[1].astype(jnp.float32), (1, 0, 2))
    query_grads = jnp.transpose(dq_raw, (2, 0, 1, 3)) * scale
    query_grads = query_grads.reshape(group_rows, q_heads, HEAD_SIZE)
    unused, pull_query = jax.vjp(
        lambda projected, gain: prepare_inputs(projected, gain, group_offset, q_heads),
        query_projected,
        gain_q,
    )
    query_proj_grad, q_gain_part = pull_query(query_grads)
    unused, pull_key = jax.vjp(
        lambda projected, gain: prepare_inputs(projected, gain, group_offset, kv_heads),
        key_projected,
        gain_k,
    )
    key_proj_grad, k_gain_part = pull_key(grad_keys_total)
    query_low = query_proj_grad.astype(jnp.bfloat16)
    key_low = key_proj_grad.astype(jnp.bfloat16)
    value_low = grad_values_total.reshape(group_rows, kv_heads * HEAD_SIZE).astype(jnp.bfloat16)
    query_weight_grad = contract_rows(first_all, query_low)
    key_weight_grad = contract_rows(first_all, key_low)
    value_weight_grad = contract_rows(first_all, value_low)

    def first_term(start, count):
        return (
            contract_last(query_low, w_query)
            + contract_last(key_low, w_key)
            + contract_last(value_low, w_value)
        )

    first_back = token_sum(first_term, rows)
    unused, pull_first = jax.vjp(rms_scale, x_float, gain_first)
    norm_first_grad, input_gain_part = pull_first(first_back)
    input_grad = (residual_grad + norm_first_grad).astype(jnp.bfloat16)
    query_shard, key_shard, value_shard = halving_scatter(
        (query_weight_grad, key_weight_grad, value_weight_grad)
    )
    gain_totals = all_sum(
        jnp.concatenate([input_gain_part, q_gain_part, k_gain_part, post_gain_part])
    )
    member_f = lax.axis_index("fsdp")
    sizes = (input_gain.shape[0], q_gain.shape[0], k_gain.shape[0], post_gain.shape[0])
    gain_shards = []
    at = 0
    for own in sizes:
        whole = own * fs
        gain_shards.append(lax.dynamic_slice_in_dim(gain_totals, at + member_f * own, own, 0))
        at += whole
    input_gain_shard, q_gain_shard, k_gain_shard, post_gain_shard = gain_shards
    gate_shard, up_shard, down_shard_t, out_shard_t = mlp_shards
    return (
        output,
        input_grad,
        query_shard,
        key_shard,
        value_shard,
        jnp.transpose(out_shard_t),
        gate_shard,
        up_shard,
        jnp.transpose(down_shard_t),
        input_gain_shard,
        q_gain_shard,
        k_gain_shard,
        post_gain_shard,
    )


def solution(mesh):
    return layer_program(mesh)


def layer_program(mesh):
    placed = (
        P(("fsdp", "tensor"), None),
        P(("fsdp", "tensor"), None),
        P(),
        P("fsdp", "tensor"),
        P("fsdp", "tensor"),
        P("fsdp", "tensor"),
        P("tensor", "fsdp"),
        P("fsdp", "tensor"),
        P("fsdp", "tensor"),
        P("tensor", "fsdp"),
        P("fsdp"),
        P("fsdp"),
        P("fsdp"),
        P("fsdp"),
    )
    return jax.shard_map(
        shards,
        mesh=mesh,
        in_specs=placed,
        out_specs=(
            P(("fsdp", "tensor"), None),
            P(("fsdp", "tensor"), None),
            P("fsdp", "tensor"),
            P("fsdp", "tensor"),
            P("fsdp", "tensor"),
            P("tensor", "fsdp"),
            P("fsdp", "tensor"),
            P("fsdp", "tensor"),
            P("tensor", "fsdp"),
            P("fsdp"),
            P("fsdp"),
            P("fsdp"),
            P("fsdp"),
        ),
        check_vma=False,
    )
```

```python
import functools

import numpy as np
import jax
import jax.numpy as jnp
from jax import lax
from jax.experimental import pallas as pl
from jax.experimental.pallas import tpu as pltpu
from jax.sharding import PartitionSpec as P


HEAD_SIZE = 128
TRANS_B = (((1,), (1,)), ((), ()))
TRANS_A = (((0,), (0,)), ((), ()))


def _own_place(p, quarter, r):
    return (p * quarter + r) if r < quarter else ((3 - p) * quarter + r - quarter)


def _far_place(p, quarter, r):
    return ((1 - p) * quarter + r) if r < quarter else ((2 + p) * quarter + r - quarter)


def _pair_tables(p, quarter, block, by_key, source):
    rows = 2 * quarter
    count = rows // block
    kmap = {}
    for src, fn in ((0, _own_place), (1, _far_place)):
        for j in range(count):
            kmap[fn(p, quarter, j * block) // block] = (src, j)
    pairs = []
    for j in range(count):
        qpb = _own_place(p, quarter, j * block) // block
        for kpb in range(qpb + 1):
            if kmap[kpb][0] == source:
                pairs.append((j, qpb, kpb))
    if by_key:
        pairs.sort(key=lambda t: (t[2], t[0]))
    group = [t[2] if by_key else t[0] for t in pairs]
    size = len(pairs)
    first = [1 if n == 0 or group[n - 1] != group[n] else 0 for n in range(size)]
    last = [1 if n == size - 1 or group[n + 1] != group[n] else 0 for n in range(size)]
    return np.array(
        [
            [t[0] for t in pairs],
            [t[1] for t in pairs],
            [t[2] for t in pairs],
            [kmap[t[2]][0] for t in pairs],
            [kmap[t[2]][1] for t in pairs],
            first,
            last,
        ],
        np.int32,
    )


def pair_tables(piece, quarter, block, by_key, source):
    t0 = _pair_tables(0, quarter, block, by_key, source)
    t1 = _pair_tables(1, quarter, block, by_key, source)
    assert t0.shape == t1.shape
    return jnp.where(piece == 0, jnp.asarray(t0), jnp.asarray(t1))


def _mask(qpb, kpb, qs, block):
    qp = qpb * block + lax.broadcasted_iota(jnp.int32, (block, block), 0)
    kp = kpb * block + lax.broadcasted_iota(jnp.int32, (block, block), 1)
    start = jnp.tile(qs, (1, block // 128))
    return (kp >= start) & (kp <= qp)


def _fwd_kernel(tab_ref, q_ref, qs_ref, k_ref, v_ref, a_in_ref, l_in_ref, a_ref, l_ref, acc_ref, sum_ref, *, scale, block):
    n = pl.program_id(1)
    share = q_ref.shape[1]

    @pl.when(tab_ref[5, n] == 1)
    def _():
        acc_ref[...] = a_in_ref[0].reshape(share * block, HEAD_SIZE)
        sum_ref[...] = l_in_ref[0][:, :, :1]

    q = q_ref[0].reshape(share * block, HEAD_SIZE)
    k = k_ref[0]
    v = v_ref[0]
    s = lax.dot_general(q, k, TRANS_B, preferred_element_type=jnp.float32) * scale
    allowed = _mask(tab_ref[1, n], tab_ref[2, n], qs_ref[...], block)
    e = jnp.where(allowed[None], jnp.exp(s.reshape(share, block, block)), 0.0)
    sum_ref[...] += jnp.sum(e, axis=-1, keepdims=True)
    acc_ref[...] += jnp.dot(
        e.reshape(share * block, block).astype(jnp.bfloat16), v, preferred_element_type=jnp.float32
    )

    @pl.when(tab_ref[6, n] == 1)
    def _():
        a_ref[0] = acc_ref[...].reshape(share, block, HEAD_SIZE)
        l_ref[0] = jnp.broadcast_to(sum_ref[...], (share, block, 128))


def attention_forward(q, qs, keys, values, a_in, l_in, piece, quarter, source, block=512):
    kvh, share, _, _ = q.shape
    tab = pair_tables(piece, quarter, block, False, source)
    npairs = tab.shape[1]
    scale = HEAD_SIZE ** (-0.5)
    row_spec = pl.BlockSpec((1, share, block, HEAD_SIZE), lambda h, n, t: (h, 0, t[0, n], 0))
    lane_spec = pl.BlockSpec((1, share, block, 128), lambda h, n, t: (h, 0, t[0, n], 0))
    key_spec = pl.BlockSpec((1, block, HEAD_SIZE), lambda h, n, t: (h, t[4, n], 0))
    grid_spec = pltpu.PrefetchScalarGridSpec(
        num_scalar_prefetch=1,
        grid=(kvh, npairs),
        in_specs=[
            row_spec,
            pl.BlockSpec((block, 128), lambda h, n, t: (t[0, n], 0)),
            key_spec,
            key_spec,
            row_spec,
            lane_spec,
        ],
        out_specs=[row_spec, lane_spec],
        scratch_shapes=[
            pltpu.VMEM((share * block, HEAD_SIZE), jnp.float32),
            pltpu.VMEM((share, block, 1), jnp.float32),
        ],
    )
    flops = 4 * kvh * npairs * share * block * block * HEAD_SIZE
    return pl.pallas_call(
        functools.partial(_fwd_kernel, scale=scale, block=block),
        grid_spec=grid_spec,
        out_shape=[
            jax.ShapeDtypeStruct(a_in.shape, jnp.float32),
            jax.ShapeDtypeStruct(l_in.shape, jnp.float32),
        ],
        input_output_aliases={5: 0, 6: 1},
        compiler_params=pltpu.CompilerParams(
            dimension_semantics=("arbitrary", "arbitrary"), vmem_limit_bytes=48 * 1024 * 1024
        ),
        cost_estimate=pl.CostEstimate(
            flops=flops,
            transcendentals=kvh * npairs * share * block * block,
            bytes_accessed=kvh * npairs * (8 * block * HEAD_SIZE * 2),
        ),
        name="attn_fwd",
    )(tab, q, qs, keys, values, a_in, l_in)


def _bwd_kernel(tab_ref, q_ref, h_ref, dl_ref, qs_ref, k_ref, v_ref, dq_in_ref, dq_ref, dk_ref, dv_ref, dk_acc, dv_acc, *, scale, block):
    n = pl.program_id(1)
    share = q_ref.shape[1]

    @pl.when(n == 0)
    def _():
        dq_ref[...] = dq_in_ref[...]

    @pl.when(tab_ref[5, n] == 1)
    def _():
        dk_acc[...] = jnp.zeros(dk_acc.shape, dk_acc.dtype)
        dv_acc[...] = jnp.zeros(dv_acc.shape, dv_acc.dtype)

    q = q_ref[0].reshape(share * block, HEAD_SIZE)
    hh = h_ref[0].reshape(share * block, HEAD_SIZE)
    k = k_ref[0]
    v = v_ref[0]
    s = lax.dot_general(q, k, TRANS_B, preferred_element_type=jnp.float32) * scale
    allowed = _mask(tab_ref[1, n], tab_ref[2, n], qs_ref[...], block)
    e = jnp.where(allowed[None], jnp.exp(s.reshape(share, block, block)), 0.0)
    dp = lax.dot_general(hh, v, TRANS_B, preferred_element_type=jnp.float32).reshape(share, block, block)
    delta = jnp.tile(dl_ref[0], (1, 1, block // 128))
    ds = (e * (dp - delta)).reshape(share * block, block).astype(jnp.bfloat16)
    rows = pl.ds(pl.multiple_of(tab_ref[0, n] * block, block), block)
    dq_ref[0, :, rows, :] += jnp.dot(ds, k, preferred_element_type=jnp.float32).reshape(share, block, HEAD_SIZE)
    dk_acc[...] += lax.dot_general(ds, q, TRANS_A, preferred_element_type=jnp.float32)
    dv_acc[...] += lax.dot_general(
        e.reshape(share * block, block).astype(jnp.bfloat16), hh, TRANS_A, preferred_element_type=jnp.float32
    )

    @pl.when(tab_ref[6, n] == 1)
    def _():
        dk_ref[0] = dk_acc[...] * scale
        dv_ref[0] = dv_acc[...]


def attention_backward(q, hgrad, delta, qs, keys, values, dq_in, piece, quarter, source, block=512):
    kvh, share, rows, _ = q.shape
    tab = pair_tables(piece, quarter, block, True, source)
    npairs = tab.shape[1]
    scale = HEAD_SIZE ** (-0.5)
    row_spec = pl.BlockSpec((1, share, block, HEAD_SIZE), lambda h, n, t: (h, 0, t[0, n], 0))
    key_spec = pl.BlockSpec((1, block, HEAD_SIZE), lambda h, n, t: (h, t[4, n], 0))
    full_spec = pl.BlockSpec((1, share, rows, HEAD_SIZE), lambda h, n, t: (h, 0, 0, 0))
    grid_spec = pltpu.PrefetchScalarGridSpec(
        num_scalar_prefetch=1,
        grid=(kvh, npairs),
        in_specs=[
            row_spec,
            row_spec,
            pl.BlockSpec((1, share, block, 128), lambda h, n, t: (h, 0, t[0, n], 0)),
            pl.BlockSpec((block, 128), lambda h, n, t: (t[0, n], 0)),
            key_spec,
            key_spec,
            full_spec,
        ],
        out_specs=[full_spec, key_spec, key_spec],
        scratch_shapes=[
            pltpu.VMEM((block, HEAD_SIZE), jnp.float32),
            pltpu.VMEM((block, HEAD_SIZE), jnp.float32),
        ],
    )
    flops = 10 * kvh * npairs * share * block * block * HEAD_SIZE
    return pl.pallas_call(
        functools.partial(_bwd_kernel, scale=scale, block=block),
        grid_spec=grid_spec,
        out_shape=[
            jax.ShapeDtypeStruct(dq_in.shape, jnp.float32),
            jax.ShapeDtypeStruct(keys.shape, jnp.float32),
            jax.ShapeDtypeStruct(values.shape, jnp.float32),
        ],
        input_output_aliases={7: 0},
        compiler_params=pltpu.CompilerParams(
            dimension_semantics=("arbitrary", "arbitrary"), vmem_limit_bytes=56 * 1024 * 1024
        ),
        cost_estimate=pl.CostEstimate(
            flops=flops,
            transcendentals=kvh * npairs * share * block * block,
            bytes_accessed=kvh * npairs * (10 * block * HEAD_SIZE * 2),
        ),
        name="attn_bwd",
    )(tab, q, hgrad, delta, qs, keys, values, dq_in)


PIECES = 2


EPSILON = 1e-06
THETA = 1000000.0


def swapped(shard, axis, distance):
    return lax.ppermute(shard, axis, [(i, i ^ 1 << distance) for i in range(lax.axis_size(axis))])


def rms_scale(values, gain):
    inverse = lax.rsqrt(jnp.mean(values * values, axis=-1, keepdims=True) + EPSILON)
    return values * inverse * gain


def rotary(values, start_offset):
    half = values.shape[-1] // 2
    frequency = THETA ** (-(jnp.arange(half, dtype=jnp.float32) * 2.0 / values.shape[-1]))
    angle = start_offset.astype(jnp.float32)[:, None] * frequency[None, :]
    cosine = jnp.cos(angle)
    sine = jnp.sin(angle)
    cos_full = jnp.concatenate([cosine, cosine], axis=-1)[:, None, :]
    sin_signed = jnp.concatenate([-sine, sine], axis=-1)[:, None, :]
    return values * cos_full + jnp.roll(values, half, axis=-1) * sin_signed


def prepare_inputs(projected, gain, start_offset, head_groups):
    shaped = projected.reshape(projected.shape[0], head_groups, -1)
    return rotary(rms_scale(shaped, gain), start_offset)


def piece_places(which, group_rows):
    quarter = group_rows // 2
    local = jnp.arange(group_rows, dtype=jnp.int32)
    chosen = jnp.where(local < quarter, which, 3 - which)
    return chosen * quarter + local % quarter


def contract_rows(left, right):
    return lax.dot_general(
        left, right, (((0,), (0,)), ((), ())), preferred_element_type=jnp.float32
    )


def contract_last(left, right):
    return lax.dot_general(
        left, right, (((1,), (1,)), ((), ())), preferred_element_type=jnp.float32
    )


def split_columns(full, widths):
    parts = []
    at = 0
    for width in widths:
        parts.append(full[:, at : at + width])
        at += width
    return parts


def halving_scatter(grads):
    widths = [g.shape[1] for g in grads]
    buf = jnp.concatenate(grads, axis=1)
    count = lax.axis_size("fsdp")
    me = lax.axis_index("fsdp")
    bit = count // 2
    while bit >= 1:
        half = buf.shape[0] // 2
        mine = (me & bit) // bit
        keep = lax.dynamic_slice_in_dim(buf, mine * half, half, 0)
        send = lax.dynamic_slice_in_dim(buf, (1 - mine) * half, half, 0)
        got = lax.ppermute(
            send.astype(jnp.bfloat16), "fsdp", [(i, i ^ bit) for i in range(count)]
        )
        buf = keep + got.astype(jnp.float32)
        bit //= 2
    return split_columns(buf, widths)


def fsdp_gather(values):
    count = lax.axis_size("fsdp")
    me = lax.axis_index("fsdp")
    distance = 1
    while distance < count:
        got = lax.ppermute(values, "fsdp", [(i, i ^ distance) for i in range(count)])
        low = (me & distance) == 0
        values = jnp.concatenate(
            [jnp.where(low, values, got), jnp.where(low, got, values)]
        )
        distance *= 2
    return values


def all_sum(values):
    for axis in ("tensor", "fsdp"):
        distance = 1
        while distance < lax.axis_size(axis):
            values = values + lax.ppermute(
                values, axis, [(i, i ^ distance) for i in range(lax.axis_size(axis))]
            )
            distance *= 2
    return values


def exchange(values, distance):
    count = lax.axis_size("tensor")
    return lax.ppermute(values, "tensor", [(i, i ^ distance) for i in range(count)])


def token_gather(values):
    rows = values.shape[0]
    me = lax.axis_index("tensor")
    across = exchange(values, 2)
    pair = jnp.stack([values, across])
    beside = exchange(pair, 1)
    full = jnp.zeros((4 * rows,) + values.shape[1:], values.dtype)
    for part, place in ((values, me), (across, me ^ 2), (beside[0], me ^ 1), (beside[1], me ^ 3)):
        full = lax.dynamic_update_slice_in_dim(full, part, place * rows, 0)
    return full


def token_sum(term, rows):
    partial = term(jnp.int32(0), rows * lax.axis_size("tensor"))
    me = lax.axis_index("tensor")

    def block(place):
        return lax.dynamic_slice_in_dim(partial, place * rows, rows, 0)

    sent = jnp.stack([block(me ^ 1), block(me ^ 3)]).astype(jnp.bfloat16)
    got = exchange(sent, 1).astype(jnp.float32)
    mine = block(me) + got[0]
    other = (block(me ^ 2) + got[1]).astype(jnp.bfloat16)
    return mine + exchange(other, 2).astype(jnp.float32)


def shards(
    hidden,
    out_grad,
    lengths,
    q_weight,
    key_matrix,
    value_matrix,
    o_weight,
    gate_weight,
    up_weight,
    down_weight,
    input_gain,
    q_gain,
    k_gain,
    post_gain,
):
    split = lax.axis_size("tensor")
    rows = hidden.shape[0]
    group_rows = rows * split
    q_heads = q_weight.shape[1] // HEAD_SIZE
    kv_heads = key_matrix.shape[1] // HEAD_SIZE
    share = q_heads // kv_heads
    scale = HEAD_SIZE ** (-0.5)
    member = lax.axis_index("fsdp")
    slot = member // PIECES
    piece = member % PIECES
    lengths_row = lax.dynamic_index_in_dim(lengths, slot, 0, keepdims=False)
    ends = jnp.cumsum(lengths_row)
    group_place = piece_places(piece, group_rows)
    passed = group_place[:, None] >= ends[None, :]
    group_start = jnp.sum(jnp.where(passed, lengths_row[None, :], 0), axis=1)
    group_offset = group_place - group_start
    local_valid = lax.dynamic_slice_in_dim(
        group_place < ends[-1], lax.axis_index("tensor") * rows, rows, 0
    )
    fs = lax.axis_size("fsdp")
    gain_sizes = (input_gain.shape[0], q_gain.shape[0], k_gain.shape[0], post_gain.shape[0])
    gains_all = fsdp_gather(
        jnp.concatenate([input_gain, q_gain, k_gain, post_gain]).astype(jnp.bfloat16)
    ).reshape(fs, sum(gain_sizes))
    gain_in, gain_query, gain_keys, gain_post = [
        part.reshape(-1) for part in split_columns(gains_all, gain_sizes)
    ]
    attn_full = lax.all_gather(
        jnp.concatenate(
            [
                q_weight.astype(jnp.bfloat16),
                key_matrix.astype(jnp.bfloat16),
                value_matrix.astype(jnp.bfloat16),
            ],
            axis=1,
        ),
        "fsdp",
        axis=0,
        tiled=True,
    )
    widths = (q_weight.shape[1], key_matrix.shape[1], value_matrix.shape[1])
    w_query, w_key, w_value = split_columns(attn_full, widths)
    x_float = hidden.astype(jnp.float32)
    gain_first = gain_in.astype(jnp.float32)
    first_all = token_gather(rms_scale(x_float, gain_first).astype(jnp.bfloat16))
    cotangent = out_grad.astype(jnp.float32) * local_valid[:, None].astype(jnp.float32)
    mlp_grad_all = token_gather(cotangent.astype(jnp.bfloat16))
    first_all, mlp_grad_all = lax.optimization_barrier((first_all, mlp_grad_all))
    query_projected = jnp.dot(first_all, w_query, preferred_element_type=jnp.float32)
    key_projected = jnp.dot(first_all, w_key, preferred_element_type=jnp.float32)
    value_rows = (
        jnp.dot(first_all, w_value, preferred_element_type=jnp.float32)
        .astype(jnp.bfloat16)
        .reshape(group_rows, kv_heads, HEAD_SIZE)
    )
    gain_q = gain_query.astype(jnp.float32)
    gain_k = gain_keys.astype(jnp.float32)
    query_rope = (
        prepare_inputs(query_projected, gain_q, group_offset, q_heads)
        .astype(jnp.bfloat16)
        .reshape(group_rows, kv_heads, share, HEAD_SIZE)
    )
    key_rope = prepare_inputs(key_projected, gain_k, group_offset, kv_heads).astype(jnp.bfloat16)
    quarter = group_rows // 2
    query_start = jnp.broadcast_to(group_start[:, None], (group_rows, 128))
    query_t = jnp.transpose(query_rope, (1, 2, 0, 3))
    own_keys = jnp.transpose(key_rope, (1, 0, 2))
    own_values = jnp.transpose(value_rows, (1, 0, 2))
    moved = swapped(jnp.stack([own_keys, own_values]), "fsdp", 0)
    sums = jnp.zeros(query_t.shape, jnp.float32)
    totals = jnp.zeros(query_t.shape[:3] + (128,), jnp.float32)
    sums, totals = attention_forward(
        query_t, query_start, own_keys, own_values, sums, totals, piece, quarter, 0
    )
    sums, totals_t = attention_forward(
        query_t, query_start, moved[0], moved[1], sums, totals, piece, quarter, 1
    )
    heads_t = sums / totals_t[..., :1]
    heads_out = jnp.transpose(heads_t, (2, 0, 1, 3))
    row_totals = jnp.transpose(totals_t[..., 0], (2, 0, 1))
    out_rows = heads_out.reshape(group_rows, q_heads * HEAD_SIZE).astype(jnp.bfloat16)

    mlp_full = lax.all_gather(
        jnp.concatenate(
            [
                gate_weight.astype(jnp.bfloat16),
                up_weight.astype(jnp.bfloat16),
                jnp.transpose(down_weight).astype(jnp.bfloat16),
                jnp.transpose(o_weight).astype(jnp.bfloat16),
            ],
            axis=1,
        ),
        "fsdp",
        axis=0,
        tiled=True,
    )
    w_gate, w_up, w_down_t, w_out = split_columns(
        mlp_full, (gate_weight.shape[1], up_weight.shape[1], down_weight.shape[0], o_weight.shape[0])
    )

    def out_term(start, count):
        return contract_last(out_rows, w_out)

    after_attn = x_float + token_sum(out_term, rows)
    gain_second = gain_post.astype(jnp.float32)
    second_all = token_gather(rms_scale(after_attn, gain_second).astype(jnp.bfloat16))
    gate_out = jnp.dot(second_all, w_gate, preferred_element_type=jnp.float32)
    up_out = jnp.dot(second_all, w_up, preferred_element_type=jnp.float32)
    activated = (jax.nn.silu(gate_out) * up_out).astype(jnp.bfloat16)

    def down_term(start, count):
        return contract_last(activated, w_down_t)

    output = (after_attn + token_sum(down_term, rows)).astype(jnp.bfloat16)
    grad_act = jnp.dot(mlp_grad_all, w_down_t, preferred_element_type=jnp.float32)
    unused, pull_gate = jax.vjp(
        lambda gate_in, up_in: jax.nn.silu(gate_in) * up_in, gate_out, up_out
    )
    grad_gate, grad_up = pull_gate(grad_act)
    grad_gate = grad_gate.astype(jnp.bfloat16)
    grad_up = grad_up.astype(jnp.bfloat16)
    down_grad_t = contract_rows(mlp_grad_all, activated)
    gate_grad = contract_rows(second_all, grad_gate)
    up_grad = contract_rows(second_all, grad_up)

    def second_term(start, count):
        return contract_last(grad_gate, w_gate) + contract_last(grad_up, w_up)

    second_back = token_sum(second_term, rows)
    unused, pull_second = jax.vjp(rms_scale, after_attn, gain_second)
    norm_second_grad, post_gain_part = pull_second(second_back)
    residual_grad = cotangent + norm_second_grad
    attn_grad_all = token_gather(residual_grad.astype(jnp.bfloat16))
    out_weight_grad_t = contract_rows(attn_grad_all, out_rows)
    mlp_packed = jnp.concatenate(
        [g.astype(jnp.bfloat16) for g in (gate_grad, up_grad, down_grad_t, out_weight_grad_t)],
        axis=1,
    )
    head_grad = jnp.dot(attn_grad_all, w_out, preferred_element_type=jnp.float32).astype(
        jnp.bfloat16
    )
    head_float = head_grad.astype(jnp.float32).reshape(group_rows, kv_heads, share, HEAD_SIZE)
    scaled_grad = (head_float / row_totals[..., None]).astype(jnp.bfloat16)
    delta = jnp.sum(head_float * heads_out, axis=-1) / row_totals

    grad_t = jnp.transpose(scaled_grad, (1, 2, 0, 3))
    delta_t = jnp.broadcast_to(
        jnp.transpose(delta, (1, 2, 0))[..., None], (kv_heads, share, group_rows, 128)
    )
    mlp_packed, grad_t, delta_t = lax.optimization_barrier((mlp_packed, grad_t, delta_t))
    mlp_shards = split_columns(
        lax.psum_scatter(mlp_packed, "fsdp", scatter_dimension=0, tiled=True),
        [g.shape[1] for g in (gate_grad, up_grad, down_grad_t, out_weight_grad_t)],
    )
    mlp_shards = [part.astype(jnp.float32) for part in mlp_shards]
    dq_raw, dk_far, dv_far = attention_backward(
        query_t, grad_t, delta_t, query_start, moved[0], moved[1],
        jnp.zeros(query_t.shape, jnp.float32), piece, quarter, 1,
    )
    unseen = (piece == 1) & (jnp.arange(group_rows) >= quarter)
    far_grads = jnp.where(unseen[None, None, :, None], 0.0, jnp.stack([dk_far, dv_far]))
    returned = swapped(far_grads.astype(jnp.bfloat16), "fsdp", 0)
    dq_raw, dk_own, dv_own = attention_backward(
        query_t, grad_t, delta_t, query_start, own_keys, own_values,
        dq_raw, piece, quarter, 0,
    )
    mlp_shards, dq_raw = lax.optimization_barrier((mlp_shards, dq_raw))
    grad_keys_total = jnp.transpose(dk_own + returned[0].astype(jnp.float32), (1, 0, 2))
    grad_values_total = jnp.transpose(dv_own + returned[1].astype(jnp.float32), (1, 0, 2))
    query_grads = jnp.transpose(dq_raw, (2, 0, 1, 3)) * scale
    query_grads = query_grads.reshape(group_rows, q_heads, HEAD_SIZE)
    unused, pull_query = jax.vjp(
        lambda projected, gain: prepare_inputs(projected, gain, group_offset, q_heads),
        query_projected,
        gain_q,
    )
    query_proj_grad, q_gain_part = pull_query(query_grads)
    unused, pull_key = jax.vjp(
        lambda projected, gain: prepare_inputs(projected, gain, group_offset, kv_heads),
        key_projected,
        gain_k,
    )
    key_proj_grad, k_gain_part = pull_key(grad_keys_total)
    query_low = query_proj_grad.astype(jnp.bfloat16)
    key_low = key_proj_grad.astype(jnp.bfloat16)
    value_low = grad_values_total.reshape(group_rows, kv_heads * HEAD_SIZE).astype(jnp.bfloat16)
    query_weight_grad = contract_rows(first_all, query_low)
    key_weight_grad = contract_rows(first_all, key_low)
    value_weight_grad = contract_rows(first_all, value_low)

    def first_term(start, count):
        return (
            contract_last(query_low, w_query)
            + contract_last(key_low, w_key)
            + contract_last(value_low, w_value)
        )

    first_back = token_sum(first_term, rows)
    unused, pull_first = jax.vjp(rms_scale, x_float, gain_first)
    norm_first_grad, input_gain_part = pull_first(first_back)
    input_grad = (residual_grad + norm_first_grad).astype(jnp.bfloat16)
    query_shard, key_shard, value_shard = halving_scatter(
        (query_weight_grad, key_weight_grad, value_weight_grad)
    )
    gain_totals = all_sum(
        jnp.concatenate([input_gain_part, q_gain_part, k_gain_part, post_gain_part])
    )
    member_f = lax.axis_index("fsdp")
    sizes = (input_gain.shape[0], q_gain.shape[0], k_gain.shape[0], post_gain.shape[0])
    gain_shards = []
    at = 0
    for own in sizes:
        whole = own * fs
        gain_shards.append(lax.dynamic_slice_in_dim(gain_totals, at + member_f * own, own, 0))
        at += whole
    input_gain_shard, q_gain_shard, k_gain_shard, post_gain_shard = gain_shards
    gate_shard, up_shard, down_shard_t, out_shard_t = mlp_shards
    return (
        output,
        input_grad,
        query_shard,
        key_shard,
        value_shard,
        jnp.transpose(out_shard_t),
        gate_shard,
        up_shard,
        jnp.transpose(down_shard_t),
        input_gain_shard,
        q_gain_shard,
        k_gain_shard,
        post_gain_shard,
    )


def solution(mesh):
    return layer_program(mesh)


def layer_program(mesh):
    placed = (
        P(("fsdp", "tensor"), None),
        P(("fsdp", "tensor"), None),
        P(),
        P("fsdp", "tensor"),
        P("fsdp", "tensor"),
        P("fsdp", "tensor"),
        P("tensor", "fsdp"),
        P("fsdp", "tensor"),
        P("fsdp", "tensor"),
        P("tensor", "fsdp"),
        P("fsdp"),
        P("fsdp"),
        P("fsdp"),
        P("fsdp"),
    )
    return jax.shard_map(
        shards,
        mesh=mesh,
        in_specs=placed,
        out_specs=(
            P(("fsdp", "tensor"), None),
            P(("fsdp", "tensor"), None),
            P("fsdp", "tensor"),
            P("fsdp", "tensor"),
            P("fsdp", "tensor"),
            P("tensor", "fsdp"),
            P("fsdp", "tensor"),
            P("fsdp", "tensor"),
            P("tensor", "fsdp"),
            P("fsdp"),
            P("fsdp"),
            P("fsdp"),
            P("fsdp"),
        ),
        check_vma=False,
    )
```

```python
import functools

import numpy as np
import jax
import jax.numpy as jnp
from jax import lax
from jax.experimental import pallas as pl
from jax.experimental.pallas import tpu as pltpu
from jax.sharding import PartitionSpec as P


HEAD_SIZE = 128
TRANS_B = (((1,), (1,)), ((), ()))
TRANS_A = (((0,), (0,)), ((), ()))


def _own_place(p, quarter, r):
    return (p * quarter + r) if r < quarter else ((3 - p) * quarter + r - quarter)


def _far_place(p, quarter, r):
    return ((1 - p) * quarter + r) if r < quarter else ((2 + p) * quarter + r - quarter)


def _pair_tables(p, quarter, block, by_key, source):
    rows = 2 * quarter
    count = rows // block
    kmap = {}
    for src, fn in ((0, _own_place), (1, _far_place)):
        for j in range(count):
            kmap[fn(p, quarter, j * block) // block] = (src, j)
    pairs = []
    for j in range(count):
        qpb = _own_place(p, quarter, j * block) // block
        for kpb in range(qpb + 1):
            if kmap[kpb][0] == source:
                pairs.append((j, qpb, kpb))
    if by_key:
        pairs.sort(key=lambda t: (t[2], t[0]))
    group = [t[2] if by_key else t[0] for t in pairs]
    size = len(pairs)
    first = [1 if n == 0 or group[n - 1] != group[n] else 0 for n in range(size)]
    last = [1 if n == size - 1 or group[n + 1] != group[n] else 0 for n in range(size)]
    return np.array(
        [
            [t[0] for t in pairs],
            [t[1] for t in pairs],
            [t[2] for t in pairs],
            [kmap[t[2]][0] for t in pairs],
            [kmap[t[2]][1] for t in pairs],
            first,
            last,
        ],
        np.int32,
    )


def pair_tables(piece, quarter, block, by_key, source):
    t0 = _pair_tables(0, quarter, block, by_key, source)
    t1 = _pair_tables(1, quarter, block, by_key, source)
    assert t0.shape == t1.shape
    return jnp.where(piece == 0, jnp.asarray(t0), jnp.asarray(t1))


def _mask(qpb, kpb, qs, block):
    qp = qpb * block + lax.broadcasted_iota(jnp.int32, (block, block), 0)
    kp = kpb * block + lax.broadcasted_iota(jnp.int32, (block, block), 1)
    start = jnp.tile(qs, (1, block // 128))
    return (kp >= start) & (kp <= qp)


def _fwd_kernel(tab_ref, q_ref, qs_ref, k_ref, v_ref, a_in_ref, l_in_ref, a_ref, l_ref, acc_ref, sum_ref, *, scale, block):
    n = pl.program_id(1)
    share = q_ref.shape[1]

    @pl.when(tab_ref[5, n] == 1)
    def _():
        acc_ref[...] = a_in_ref[0].reshape(share * block, HEAD_SIZE)
        sum_ref[...] = l_in_ref[0][:, :, :1]

    q = q_ref[0].reshape(share * block, HEAD_SIZE)
    k = k_ref[0]
    v = v_ref[0]
    s = lax.dot_general(q, k, TRANS_B, preferred_element_type=jnp.float32) * scale
    allowed = _mask(tab_ref[1, n], tab_ref[2, n], qs_ref[...], block)
    e = jnp.where(allowed[None], jnp.exp(s.reshape(share, block, block)), 0.0)
    sum_ref[...] += jnp.sum(e, axis=-1, keepdims=True)
    acc_ref[...] += jnp.dot(
        e.reshape(share * block, block).astype(jnp.bfloat16), v, preferred_element_type=jnp.float32
    )

    @pl.when(tab_ref[6, n] == 1)
    def _():
        a_ref[0] = acc_ref[...].reshape(share, block, HEAD_SIZE)
        l_ref[0] = jnp.broadcast_to(sum_ref[...], (share, block, 128))


def attention_forward(q, qs, keys, values, a_in, l_in, piece, quarter, source, block=512):
    kvh, share, _, _ = q.shape
    tab = pair_tables(piece, quarter, block, False, source)
    npairs = tab.shape[1]
    scale = HEAD_SIZE ** (-0.5)
    row_spec = pl.BlockSpec((1, share, block, HEAD_SIZE), lambda h, n, t: (h, 0, t[0, n], 0))
    lane_spec = pl.BlockSpec((1, share, block, 128), lambda h, n, t: (h, 0, t[0, n], 0))
    key_spec = pl.BlockSpec((1, block, HEAD_SIZE), lambda h, n, t: (h, t[4, n], 0))
    grid_spec = pltpu.PrefetchScalarGridSpec(
        num_scalar_prefetch=1,
        grid=(kvh, npairs),
        in_specs=[
            row_spec,
            pl.BlockSpec((block, 128), lambda h, n, t: (t[0, n], 0)),
            key_spec,
            key_spec,
            row_spec,
            lane_spec,
        ],
        out_specs=[row_spec, lane_spec],
        scratch_shapes=[
            pltpu.VMEM((share * block, HEAD_SIZE), jnp.float32),
            pltpu.VMEM((share, block, 1), jnp.float32),
        ],
    )
    flops = 4 * kvh * npairs * share * block * block * HEAD_SIZE
    return pl.pallas_call(
        functools.partial(_fwd_kernel, scale=scale, block=block),
        grid_spec=grid_spec,
        out_shape=[
            jax.ShapeDtypeStruct(a_in.shape, jnp.float32),
            jax.ShapeDtypeStruct(l_in.shape, jnp.float32),
        ],
        input_output_aliases={5: 0, 6: 1},
        compiler_params=pltpu.CompilerParams(
            dimension_semantics=("arbitrary", "arbitrary"), vmem_limit_bytes=48 * 1024 * 1024
        ),
        cost_estimate=pl.CostEstimate(
            flops=flops,
            transcendentals=kvh * npairs * share * block * block,
            bytes_accessed=kvh * npairs * (8 * block * HEAD_SIZE * 2),
        ),
        name="attn_fwd",
    )(tab, q, qs, keys, values, a_in, l_in)


def _bwd_kernel(tab_ref, q_ref, h_ref, dl_ref, qs_ref, k_ref, v_ref, dq_in_ref, dq_ref, dk_ref, dv_ref, dk_acc, dv_acc, *, scale, block):
    n = pl.program_id(1)
    share = q_ref.shape[1]

    @pl.when(n == 0)
    def _():
        dq_ref[...] = dq_in_ref[...]

    @pl.when(tab_ref[5, n] == 1)
    def _():
        dk_acc[...] = jnp.zeros(dk_acc.shape, dk_acc.dtype)
        dv_acc[...] = jnp.zeros(dv_acc.shape, dv_acc.dtype)

    q = q_ref[0].reshape(share * block, HEAD_SIZE)
    hh = h_ref[0].reshape(share * block, HEAD_SIZE)
    k = k_ref[0]
    v = v_ref[0]
    s = lax.dot_general(q, k, TRANS_B, preferred_element_type=jnp.float32) * scale
    allowed = _mask(tab_ref[1, n], tab_ref[2, n], qs_ref[...], block)
    e = jnp.where(allowed[None], jnp.exp(s.reshape(share, block, block)), 0.0)
    dp = lax.dot_general(hh, v, TRANS_B, preferred_element_type=jnp.float32).reshape(share, block, block)
    delta = jnp.tile(dl_ref[0], (1, 1, block // 128))
    ds = (e * (dp - delta)).reshape(share * block, block).astype(jnp.bfloat16)
    rows = pl.ds(pl.multiple_of(tab_ref[0, n] * block, block), block)
    dq_ref[0, :, rows, :] += jnp.dot(ds, k, preferred_element_type=jnp.float32).reshape(share, block, HEAD_SIZE)
    dk_acc[...] += lax.dot_general(ds, q, TRANS_A, preferred_element_type=jnp.float32)
    dv_acc[...] += lax.dot_general(
        e.reshape(share * block, block).astype(jnp.bfloat16), hh, TRANS_A, preferred_element_type=jnp.float32
    )

    @pl.when(tab_ref[6, n] == 1)
    def _():
        dk_ref[0] = dk_acc[...] * scale
        dv_ref[0] = dv_acc[...]


def attention_backward(q, hgrad, delta, qs, keys, values, dq_in, piece, quarter, source, block=512):
    kvh, share, rows, _ = q.shape
    tab = pair_tables(piece, quarter, block, True, source)
    npairs = tab.shape[1]
    scale = HEAD_SIZE ** (-0.5)
    row_spec = pl.BlockSpec((1, share, block, HEAD_SIZE), lambda h, n, t: (h, 0, t[0, n], 0))
    key_spec = pl.BlockSpec((1, block, HEAD_SIZE), lambda h, n, t: (h, t[4, n], 0))
    full_spec = pl.BlockSpec((1, share, rows, HEAD_SIZE), lambda h, n, t: (h, 0, 0, 0))
    grid_spec = pltpu.PrefetchScalarGridSpec(
        num_scalar_prefetch=1,
        grid=(kvh, npairs),
        in_specs=[
            row_spec,
            row_spec,
            pl.BlockSpec((1, share, block, 128), lambda h, n, t: (h, 0, t[0, n], 0)),
            pl.BlockSpec((block, 128), lambda h, n, t: (t[0, n], 0)),
            key_spec,
            key_spec,
            full_spec,
        ],
        out_specs=[full_spec, key_spec, key_spec],
        scratch_shapes=[
            pltpu.VMEM((block, HEAD_SIZE), jnp.float32),
            pltpu.VMEM((block, HEAD_SIZE), jnp.float32),
        ],
    )
    flops = 10 * kvh * npairs * share * block * block * HEAD_SIZE
    return pl.pallas_call(
        functools.partial(_bwd_kernel, scale=scale, block=block),
        grid_spec=grid_spec,
        out_shape=[
            jax.ShapeDtypeStruct(dq_in.shape, jnp.float32),
            jax.ShapeDtypeStruct(keys.shape, jnp.float32),
            jax.ShapeDtypeStruct(values.shape, jnp.float32),
        ],
        input_output_aliases={7: 0},
        compiler_params=pltpu.CompilerParams(
            dimension_semantics=("arbitrary", "arbitrary"), vmem_limit_bytes=56 * 1024 * 1024
        ),
        cost_estimate=pl.CostEstimate(
            flops=flops,
            transcendentals=kvh * npairs * share * block * block,
            bytes_accessed=kvh * npairs * (10 * block * HEAD_SIZE * 2),
        ),
        name="attn_bwd",
    )(tab, q, hgrad, delta, qs, keys, values, dq_in)


PIECES = 2


EPSILON = 1e-06
THETA = 1000000.0


def swapped(shard, axis, distance):
    return lax.ppermute(shard, axis, [(i, i ^ 1 << distance) for i in range(lax.axis_size(axis))])


def rms_scale(values, gain):
    inverse = lax.rsqrt(jnp.mean(values * values, axis=-1, keepdims=True) + EPSILON)
    return values * inverse * gain


def rotary(values, start_offset):
    half = values.shape[-1] // 2
    frequency = THETA ** (-(jnp.arange(half, dtype=jnp.float32) * 2.0 / values.shape[-1]))
    angle = start_offset.astype(jnp.float32)[:, None] * frequency[None, :]
    cosine = jnp.cos(angle)
    sine = jnp.sin(angle)
    cos_full = jnp.concatenate([cosine, cosine], axis=-1)[:, None, :]
    sin_signed = jnp.concatenate([-sine, sine], axis=-1)[:, None, :]
    return values * cos_full + jnp.roll(values, half, axis=-1) * sin_signed


def prepare_inputs(projected, gain, start_offset, head_groups):
    shaped = projected.reshape(projected.shape[0], head_groups, -1)
    return rotary(rms_scale(shaped, gain), start_offset)


def piece_places(which, group_rows):
    quarter = group_rows // 2
    local = jnp.arange(group_rows, dtype=jnp.int32)
    chosen = jnp.where(local < quarter, which, 3 - which)
    return chosen * quarter + local % quarter


def contract_rows(left, right):
    return lax.dot_general(
        left, right, (((0,), (0,)), ((), ())), preferred_element_type=jnp.float32
    )


def contract_last(left, right):
    return lax.dot_general(
        left, right, (((1,), (1,)), ((), ())), preferred_element_type=jnp.float32
    )


def split_columns(full, widths):
    parts = []
    at = 0
    for width in widths:
        parts.append(full[:, at : at + width])
        at += width
    return parts


def halving_scatter(grads):
    widths = [g.shape[1] for g in grads]
    packed = jnp.concatenate(grads, axis=1)
    count = lax.axis_size("fsdp")
    me = lax.axis_index("fsdp")
    bits = count.bit_length() - 1
    rows_f = packed.shape[0] // count
    order = [int(format(b, f"0{bits}b")[::-1], 2) for b in range(count)]
    buf = jnp.concatenate([packed[b * rows_f : (b + 1) * rows_f] for b in order], axis=0)
    for bit in range(bits):
        half = buf.shape[0] // 2
        mine = (me >> bit) & 1
        keep = lax.dynamic_slice_in_dim(buf, mine * half, half, 0)
        send = lax.dynamic_slice_in_dim(buf, (1 - mine) * half, half, 0)
        got = lax.ppermute(
            send.astype(jnp.bfloat16), "fsdp", [(i, i ^ (1 << bit)) for i in range(count)]
        )
        buf = keep + got.astype(jnp.float32)
    return split_columns(buf, widths)


def fsdp_gather(values):
    count = lax.axis_size("fsdp")
    me = lax.axis_index("fsdp")
    distance = 1
    while distance < count:
        got = lax.ppermute(values, "fsdp", [(i, i ^ distance) for i in range(count)])
        low = (me & distance) == 0
        values = jnp.concatenate(
            [jnp.where(low, values, got), jnp.where(low, got, values)]
        )
        distance *= 2
    return values


def all_sum(values):
    for axis in ("tensor", "fsdp"):
        distance = 1
        while distance < lax.axis_size(axis):
            values = values + lax.ppermute(
                values, axis, [(i, i ^ distance) for i in range(lax.axis_size(axis))]
            )
            distance *= 2
    return values


def exchange(values, distance):
    count = lax.axis_size("tensor")
    return lax.ppermute(values, "tensor", [(i, i ^ distance) for i in range(count)])


def token_gather(values):
    rows = values.shape[0]
    me = lax.axis_index("tensor")
    across = exchange(values, 2)
    pair = jnp.stack([values, across])
    beside = exchange(pair, 1)
    full = jnp.zeros((4 * rows,) + values.shape[1:], values.dtype)
    for part, place in ((values, me), (across, me ^ 2), (beside[0], me ^ 1), (beside[1], me ^ 3)):
        full = lax.dynamic_update_slice_in_dim(full, part, place * rows, 0)
    return full


def token_sum(term, rows):
    partial = term(jnp.int32(0), rows * lax.axis_size("tensor"))
    me = lax.axis_index("tensor")

    def block(place):
        return lax.dynamic_slice_in_dim(partial, place * rows, rows, 0)

    sent = jnp.stack([block(me ^ 1), block(me ^ 3)]).astype(jnp.bfloat16)
    got = exchange(sent, 1).astype(jnp.float32)
    mine = block(me) + got[0]
    other = (block(me ^ 2) + got[1]).astype(jnp.bfloat16)
    return mine + exchange(other, 2).astype(jnp.float32)


def shards(
    hidden,
    out_grad,
    lengths,
    q_weight,
    key_matrix,
    value_matrix,
    o_weight,
    gate_weight,
    up_weight,
    down_weight,
    input_gain,
    q_gain,
    k_gain,
    post_gain,
):
    split = lax.axis_size("tensor")
    rows = hidden.shape[0]
    group_rows = rows * split
    q_heads = q_weight.shape[1] // HEAD_SIZE
    kv_heads = key_matrix.shape[1] // HEAD_SIZE
    share = q_heads // kv_heads
    scale = HEAD_SIZE ** (-0.5)
    member = lax.axis_index("fsdp")
    slot = member // PIECES
    piece = member % PIECES
    lengths_row = lax.dynamic_index_in_dim(lengths, slot, 0, keepdims=False)
    ends = jnp.cumsum(lengths_row)
    group_place = piece_places(piece, group_rows)
    passed = group_place[:, None] >= ends[None, :]
    group_start = jnp.sum(jnp.where(passed, lengths_row[None, :], 0), axis=1)
    group_offset = group_place - group_start
    local_valid = lax.dynamic_slice_in_dim(
        group_place < ends[-1], lax.axis_index("tensor") * rows, rows, 0
    )
    fs = lax.axis_size("fsdp")
    gain_sizes = (input_gain.shape[0], q_gain.shape[0], k_gain.shape[0], post_gain.shape[0])
    gains_all = fsdp_gather(
        jnp.concatenate([input_gain, q_gain, k_gain, post_gain]).astype(jnp.bfloat16)
    ).reshape(fs, sum(gain_sizes))
    gain_in, gain_query, gain_keys, gain_post = [
        part.reshape(-1) for part in split_columns(gains_all, gain_sizes)
    ]
    attn_full = lax.all_gather(
        jnp.concatenate(
            [
                q_weight.astype(jnp.bfloat16),
                key_matrix.astype(jnp.bfloat16),
                value_matrix.astype(jnp.bfloat16),
            ],
            axis=1,
        ),
        "fsdp",
        axis=0,
        tiled=True,
    )
    widths = (q_weight.shape[1], key_matrix.shape[1], value_matrix.shape[1])
    w_query, w_key, w_value = split_columns(attn_full, widths)
    x_float = hidden.astype(jnp.float32)
    gain_first = gain_in.astype(jnp.float32)
    first_all = token_gather(rms_scale(x_float, gain_first).astype(jnp.bfloat16))
    cotangent = out_grad.astype(jnp.float32) * local_valid[:, None].astype(jnp.float32)
    mlp_grad_all = token_gather(cotangent.astype(jnp.bfloat16))
    first_all, mlp_grad_all = lax.optimization_barrier((first_all, mlp_grad_all))
    query_projected = jnp.dot(first_all, w_query, preferred_element_type=jnp.float32)
    key_projected = jnp.dot(first_all, w_key, preferred_element_type=jnp.float32)
    value_rows = (
        jnp.dot(first_all, w_value, preferred_element_type=jnp.float32)
        .astype(jnp.bfloat16)
        .reshape(group_rows, kv_heads, HEAD_SIZE)
    )
    gain_q = gain_query.astype(jnp.float32)
    gain_k = gain_keys.astype(jnp.float32)
    query_rope = (
        prepare_inputs(query_projected, gain_q, group_offset, q_heads)
        .astype(jnp.bfloat16)
        .reshape(group_rows, kv_heads, share, HEAD_SIZE)
    )
    key_rope = prepare_inputs(key_projected, gain_k, group_offset, kv_heads).astype(jnp.bfloat16)
    quarter = group_rows // 2
    query_start = jnp.broadcast_to(group_start[:, None], (group_rows, 128))
    query_t = jnp.transpose(query_rope, (1, 2, 0, 3))
    own_keys = jnp.transpose(key_rope, (1, 0, 2))
    own_values = jnp.transpose(value_rows, (1, 0, 2))
    moved = swapped(jnp.stack([own_keys, own_values]), "fsdp", 0)
    sums = jnp.zeros(query_t.shape, jnp.float32)
    totals = jnp.zeros(query_t.shape[:3] + (128,), jnp.float32)
    sums, totals = attention_forward(
        query_t, query_start, own_keys, own_values, sums, totals, piece, quarter, 0
    )
    sums, totals_t = attention_forward(
        query_t, query_start, moved[0], moved[1], sums, totals, piece, quarter, 1
    )
    heads_t = sums / totals_t[..., :1]
    heads_out = jnp.transpose(heads_t, (2, 0, 1, 3))
    row_totals = jnp.transpose(totals_t[..., 0], (2, 0, 1))
    out_rows = heads_out.reshape(group_rows, q_heads * HEAD_SIZE).astype(jnp.bfloat16)

    mlp_full = lax.all_gather(
        jnp.concatenate(
            [
                gate_weight.astype(jnp.bfloat16),
                up_weight.astype(jnp.bfloat16),
                jnp.transpose(down_weight).astype(jnp.bfloat16),
                jnp.transpose(o_weight).astype(jnp.bfloat16),
            ],
            axis=1,
        ),
        "fsdp",
        axis=0,
        tiled=True,
    )
    w_gate, w_up, w_down_t, w_out = split_columns(
        mlp_full, (gate_weight.shape[1], up_weight.shape[1], down_weight.shape[0], o_weight.shape[0])
    )

    def out_term(start, count):
        return contract_last(out_rows, w_out)

    after_attn = x_float + token_sum(out_term, rows)
    gain_second = gain_post.astype(jnp.float32)
    second_all = token_gather(rms_scale(after_attn, gain_second).astype(jnp.bfloat16))
    gate_out = jnp.dot(second_all, w_gate, preferred_element_type=jnp.float32)
    up_out = jnp.dot(second_all, w_up, preferred_element_type=jnp.float32)
    activated = (jax.nn.silu(gate_out) * up_out).astype(jnp.bfloat16)

    down_partial = contract_last(activated, w_down_t)
    grad_act = jnp.dot(mlp_grad_all, w_down_t, preferred_element_type=jnp.float32)
    unused, pull_gate = jax.vjp(
        lambda gate_in, up_in: jax.nn.silu(gate_in) * up_in, gate_out, up_out
    )
    grad_gate, grad_up = pull_gate(grad_act)
    grad_gate = grad_gate.astype(jnp.bfloat16)
    grad_up = grad_up.astype(jnp.bfloat16)
    down_grad_t = contract_rows(mlp_grad_all, activated)
    gate_grad = contract_rows(second_all, grad_gate)
    up_grad = contract_rows(second_all, grad_up)

    def second_term(start, count):
        return contract_last(grad_gate, w_gate) + contract_last(grad_up, w_up)

    second_back = token_sum(second_term, rows)
    unused, pull_second = jax.vjp(rms_scale, after_attn, gain_second)
    norm_second_grad, post_gain_part = pull_second(second_back)
    residual_grad = cotangent + norm_second_grad
    attn_grad_all = token_gather(residual_grad.astype(jnp.bfloat16))
    down_partial, attn_grad_all = lax.optimization_barrier((down_partial, attn_grad_all))
    down_rows = token_sum(lambda start, count: down_partial, rows)
    out_weight_grad_t = contract_rows(attn_grad_all, out_rows)
    mlp_packed = jnp.concatenate(
        [g.astype(jnp.bfloat16) for g in (gate_grad, up_grad, down_grad_t, out_weight_grad_t)],
        axis=1,
    )
    head_grad = jnp.dot(attn_grad_all, w_out, preferred_element_type=jnp.float32).astype(
        jnp.bfloat16
    )
    head_float = head_grad.astype(jnp.float32).reshape(group_rows, kv_heads, share, HEAD_SIZE)
    scaled_grad = (head_float / row_totals[..., None]).astype(jnp.bfloat16)
    delta = jnp.sum(head_float * heads_out, axis=-1) / row_totals

    grad_t = jnp.transpose(scaled_grad, (1, 2, 0, 3))
    delta_t = jnp.broadcast_to(
        jnp.transpose(delta, (1, 2, 0))[..., None], (kv_heads, share, group_rows, 128)
    )
    mlp_packed, grad_t, delta_t = lax.optimization_barrier((mlp_packed, grad_t, delta_t))
    mlp_shards = split_columns(
        lax.psum_scatter(mlp_packed, "fsdp", scatter_dimension=0, tiled=True),
        [g.shape[1] for g in (gate_grad, up_grad, down_grad_t, out_weight_grad_t)],
    )
    mlp_shards = [part.astype(jnp.float32) for part in mlp_shards]
    dq_raw, dk_far, dv_far = attention_backward(
        query_t, grad_t, delta_t, query_start, moved[0], moved[1],
        jnp.zeros(query_t.shape, jnp.float32), piece, quarter, 1,
    )
    unseen = (piece == 1) & (jnp.arange(group_rows) >= quarter)
    far_grads = jnp.where(unseen[None, None, :, None], 0.0, jnp.stack([dk_far, dv_far]))
    returned = swapped(far_grads.astype(jnp.bfloat16), "fsdp", 0)
    down_rows, dq_raw = lax.optimization_barrier((down_rows, dq_raw))
    output = (after_attn + down_rows).astype(jnp.bfloat16)
    dq_raw, dk_own, dv_own = attention_backward(
        query_t, grad_t, delta_t, query_start, own_keys, own_values,
        dq_raw, piece, quarter, 0,
    )
    mlp_shards, dq_raw = lax.optimization_barrier((mlp_shards, dq_raw))
    grad_keys_total = jnp.transpose(dk_own + returned[0].astype(jnp.float32), (1, 0, 2))
    grad_values_total = jnp.transpose(dv_own + returned[1].astype(jnp.float32), (1, 0, 2))
    query_grads = jnp.transpose(dq_raw, (2, 0, 1, 3)) * scale
    query_grads = query_grads.reshape(group_rows, q_heads, HEAD_SIZE)
    unused, pull_query = jax.vjp(
        lambda projected, gain: prepare_inputs(projected, gain, group_offset, q_heads),
        query_projected,
        gain_q,
    )
    query_proj_grad, q_gain_part = pull_query(query_grads)
    unused, pull_key = jax.vjp(
        lambda projected, gain: prepare_inputs(projected, gain, group_offset, kv_heads),
        key_projected,
        gain_k,
    )
    key_proj_grad, k_gain_part = pull_key(grad_keys_total)
    query_low = query_proj_grad.astype(jnp.bfloat16)
    key_low = key_proj_grad.astype(jnp.bfloat16)
    value_low = grad_values_total.reshape(group_rows, kv_heads * HEAD_SIZE).astype(jnp.bfloat16)
    query_weight_grad = contract_rows(first_all, query_low)
    key_weight_grad = contract_rows(first_all, key_low)
    value_weight_grad = contract_rows(first_all, value_low)

    def first_term(start, count):
        return (
            contract_last(query_low, w_query)
            + contract_last(key_low, w_key)
            + contract_last(value_low, w_value)
        )

    first_back = token_sum(first_term, rows)
    unused, pull_first = jax.vjp(rms_scale, x_float, gain_first)
    norm_first_grad, input_gain_part = pull_first(first_back)
    input_grad = (residual_grad + norm_first_grad).astype(jnp.bfloat16)
    query_shard, key_shard, value_shard = halving_scatter(
        (query_weight_grad, key_weight_grad, value_weight_grad)
    )
    gain_totals = all_sum(
        jnp.concatenate([input_gain_part, q_gain_part, k_gain_part, post_gain_part])
    )
    member_f = lax.axis_index("fsdp")
    sizes = (input_gain.shape[0], q_gain.shape[0], k_gain.shape[0], post_gain.shape[0])
    gain_shards = []
    at = 0
    for own in sizes:
        whole = own * fs
        gain_shards.append(lax.dynamic_slice_in_dim(gain_totals, at + member_f * own, own, 0))
        at += whole
    input_gain_shard, q_gain_shard, k_gain_shard, post_gain_shard = gain_shards
    gate_shard, up_shard, down_shard_t, out_shard_t = mlp_shards
    return (
        output,
        input_grad,
        query_shard,
        key_shard,
        value_shard,
        jnp.transpose(out_shard_t),
        gate_shard,
        up_shard,
        jnp.transpose(down_shard_t),
        input_gain_shard,
        q_gain_shard,
        k_gain_shard,
        post_gain_shard,
    )


def solution(mesh):
    return layer_program(mesh)


def layer_program(mesh):
    placed = (
        P(("fsdp", "tensor"), None),
        P(("fsdp", "tensor"), None),
        P(),
        P("fsdp", "tensor"),
        P("fsdp", "tensor"),
        P("fsdp", "tensor"),
        P("tensor", "fsdp"),
        P("fsdp", "tensor"),
        P("fsdp", "tensor"),
        P("tensor", "fsdp"),
        P("fsdp"),
        P("fsdp"),
        P("fsdp"),
        P("fsdp"),
    )
    return jax.shard_map(
        shards,
        mesh=mesh,
        in_specs=placed,
        out_specs=(
            P(("fsdp", "tensor"), None),
            P(("fsdp", "tensor"), None),
            P("fsdp", "tensor"),
            P("fsdp", "tensor"),
            P("fsdp", "tensor"),
            P("tensor", "fsdp"),
            P("fsdp", "tensor"),
            P("fsdp", "tensor"),
            P("tensor", "fsdp"),
            P("fsdp"),
            P("fsdp"),
            P("fsdp"),
            P("fsdp"),
        ),
        check_vma=False,
    )
```

```python
import functools

import numpy as np
import jax
import jax.numpy as jnp
from jax import lax
from jax.experimental import pallas as pl
from jax.experimental.pallas import tpu as pltpu
from jax.sharding import PartitionSpec as P


HEAD_SIZE = 128
TRANS_B = (((1,), (1,)), ((), ()))
TRANS_A = (((0,), (0,)), ((), ()))


def _own_place(p, quarter, r):
    return (p * quarter + r) if r < quarter else ((3 - p) * quarter + r - quarter)


def _far_place(p, quarter, r):
    return ((1 - p) * quarter + r) if r < quarter else ((2 + p) * quarter + r - quarter)


def _pair_tables(p, quarter, block, by_key, source):
    rows = 2 * quarter
    count = rows // block
    kmap = {}
    for src, fn in ((0, _own_place), (1, _far_place)):
        for j in range(count):
            kmap[fn(p, quarter, j * block) // block] = (src, j)
    pairs = []
    for j in range(count):
        qpb = _own_place(p, quarter, j * block) // block
        for kpb in range(qpb + 1):
            if kmap[kpb][0] == source:
                pairs.append((j, qpb, kpb))
    if by_key:
        pairs.sort(key=lambda t: (t[2], t[0]))
    group = [t[2] if by_key else t[0] for t in pairs]
    size = len(pairs)
    first = [1 if n == 0 or group[n - 1] != group[n] else 0 for n in range(size)]
    last = [1 if n == size - 1 or group[n + 1] != group[n] else 0 for n in range(size)]
    return np.array(
        [
            [t[0] for t in pairs],
            [t[1] for t in pairs],
            [t[2] for t in pairs],
            [kmap[t[2]][0] for t in pairs],
            [kmap[t[2]][1] for t in pairs],
            first,
            last,
        ],
        np.int32,
    )


def pair_tables(piece, quarter, block, by_key, source):
    t0 = _pair_tables(0, quarter, block, by_key, source)
    t1 = _pair_tables(1, quarter, block, by_key, source)
    assert t0.shape == t1.shape
    return jnp.where(piece == 0, jnp.asarray(t0), jnp.asarray(t1))


def _mask(qpb, kpb, qs, block):
    qp = qpb * block + lax.broadcasted_iota(jnp.int32, (block, block), 0)
    kp = kpb * block + lax.broadcasted_iota(jnp.int32, (block, block), 1)
    start = jnp.tile(qs, (1, block // 128))
    return (kp >= start) & (kp <= qp)


def _fwd_kernel(tab_ref, q_ref, qs_ref, k_ref, v_ref, a_in_ref, l_in_ref, a_ref, l_ref, acc_ref, sum_ref, *, scale, block):
    n = pl.program_id(1)
    share = q_ref.shape[1]

    @pl.when(tab_ref[5, n] == 1)
    def _():
        acc_ref[...] = a_in_ref[0].reshape(share * block, HEAD_SIZE)
        sum_ref[...] = l_in_ref[0][:, :, :1]

    q = q_ref[0].reshape(share * block, HEAD_SIZE)
    k = k_ref[0]
    v = v_ref[0]
    s = lax.dot_general(q, k, TRANS_B, preferred_element_type=jnp.float32) * scale
    allowed = _mask(tab_ref[1, n], tab_ref[2, n], qs_ref[...], block)
    e = jnp.where(allowed[None], jnp.exp(s.reshape(share, block, block)), 0.0)
    sum_ref[...] += jnp.sum(e, axis=-1, keepdims=True)
    acc_ref[...] += jnp.dot(
        e.reshape(share * block, block).astype(jnp.bfloat16), v, preferred_element_type=jnp.float32
    )

    @pl.when(tab_ref[6, n] == 1)
    def _():
        a_ref[0] = acc_ref[...].reshape(share, block, HEAD_SIZE)
        l_ref[0] = jnp.broadcast_to(sum_ref[...], (share, block, 128))


def attention_forward(q, qs, keys, values, a_in, l_in, piece, quarter, source, block=512):
    kvh, share, _, _ = q.shape
    tab = pair_tables(piece, quarter, block, False, source)
    npairs = tab.shape[1]
    scale = HEAD_SIZE ** (-0.5)
    row_spec = pl.BlockSpec((1, share, block, HEAD_SIZE), lambda h, n, t: (h, 0, t[0, n], 0))
    lane_spec = pl.BlockSpec((1, share, block, 128), lambda h, n, t: (h, 0, t[0, n], 0))
    key_spec = pl.BlockSpec((1, block, HEAD_SIZE), lambda h, n, t: (h, t[4, n], 0))
    grid_spec = pltpu.PrefetchScalarGridSpec(
        num_scalar_prefetch=1,
        grid=(kvh, npairs),
        in_specs=[
            row_spec,
            pl.BlockSpec((block, 128), lambda h, n, t: (t[0, n], 0)),
            key_spec,
            key_spec,
            row_spec,
            lane_spec,
        ],
        out_specs=[row_spec, lane_spec],
        scratch_shapes=[
            pltpu.VMEM((share * block, HEAD_SIZE), jnp.float32),
            pltpu.VMEM((share, block, 1), jnp.float32),
        ],
    )
    flops = 4 * kvh * npairs * share * block * block * HEAD_SIZE
    return pl.pallas_call(
        functools.partial(_fwd_kernel, scale=scale, block=block),
        grid_spec=grid_spec,
        out_shape=[
            jax.ShapeDtypeStruct(a_in.shape, jnp.float32),
            jax.ShapeDtypeStruct(l_in.shape, jnp.float32),
        ],
        input_output_aliases={5: 0, 6: 1},
        compiler_params=pltpu.CompilerParams(
            dimension_semantics=("arbitrary", "arbitrary"), vmem_limit_bytes=48 * 1024 * 1024
        ),
        cost_estimate=pl.CostEstimate(
            flops=flops,
            transcendentals=kvh * npairs * share * block * block,
            bytes_accessed=kvh * npairs * (8 * block * HEAD_SIZE * 2),
        ),
        name="attn_fwd",
    )(tab, q, qs, keys, values, a_in, l_in)


def _bwd_kernel(tab_ref, q_ref, h_ref, dl_ref, qs_ref, k_ref, v_ref, dq_in_ref, dq_ref, dk_ref, dv_ref, dk_acc, dv_acc, *, scale, block):
    n = pl.program_id(1)
    share = q_ref.shape[1]

    @pl.when(n == 0)
    def _():
        dq_ref[...] = dq_in_ref[...]

    @pl.when(tab_ref[5, n] == 1)
    def _():
        dk_acc[...] = jnp.zeros(dk_acc.shape, dk_acc.dtype)
        dv_acc[...] = jnp.zeros(dv_acc.shape, dv_acc.dtype)

    q = q_ref[0].reshape(share * block, HEAD_SIZE)
    hh = h_ref[0].reshape(share * block, HEAD_SIZE)
    k = k_ref[0]
    v = v_ref[0]
    s = lax.dot_general(q, k, TRANS_B, preferred_element_type=jnp.float32) * scale
    allowed = _mask(tab_ref[1, n], tab_ref[2, n], qs_ref[...], block)
    e = jnp.where(allowed[None], jnp.exp(s.reshape(share, block, block)), 0.0)
    dp = lax.dot_general(hh, v, TRANS_B, preferred_element_type=jnp.float32).reshape(share, block, block)
    delta = jnp.tile(dl_ref[0], (1, 1, block // 128))
    ds = (e * (dp - delta)).reshape(share * block, block).astype(jnp.bfloat16)
    rows = pl.ds(pl.multiple_of(tab_ref[0, n] * block, block), block)
    dq_ref[0, :, rows, :] += jnp.dot(ds, k, preferred_element_type=jnp.float32).reshape(share, block, HEAD_SIZE)
    dk_acc[...] += lax.dot_general(ds, q, TRANS_A, preferred_element_type=jnp.float32)
    dv_acc[...] += lax.dot_general(
        e.reshape(share * block, block).astype(jnp.bfloat16), hh, TRANS_A, preferred_element_type=jnp.float32
    )

    @pl.when(tab_ref[6, n] == 1)
    def _():
        dk_ref[0] = dk_acc[...] * scale
        dv_ref[0] = dv_acc[...]


def attention_backward(q, hgrad, delta, qs, keys, values, dq_in, piece, quarter, source, block=512):
    kvh, share, rows, _ = q.shape
    tab = pair_tables(piece, quarter, block, True, source)
    npairs = tab.shape[1]
    scale = HEAD_SIZE ** (-0.5)
    row_spec = pl.BlockSpec((1, share, block, HEAD_SIZE), lambda h, n, t: (h, 0, t[0, n], 0))
    key_spec = pl.BlockSpec((1, block, HEAD_SIZE), lambda h, n, t: (h, t[4, n], 0))
    full_spec = pl.BlockSpec((1, share, rows, HEAD_SIZE), lambda h, n, t: (h, 0, 0, 0))
    grid_spec = pltpu.PrefetchScalarGridSpec(
        num_scalar_prefetch=1,
        grid=(kvh, npairs),
        in_specs=[
            row_spec,
            row_spec,
            pl.BlockSpec((1, share, block, 128), lambda h, n, t: (h, 0, t[0, n], 0)),
            pl.BlockSpec((block, 128), lambda h, n, t: (t[0, n], 0)),
            key_spec,
            key_spec,
            full_spec,
        ],
        out_specs=[full_spec, key_spec, key_spec],
        scratch_shapes=[
            pltpu.VMEM((block, HEAD_SIZE), jnp.float32),
            pltpu.VMEM((block, HEAD_SIZE), jnp.float32),
        ],
    )
    flops = 10 * kvh * npairs * share * block * block * HEAD_SIZE
    return pl.pallas_call(
        functools.partial(_bwd_kernel, scale=scale, block=block),
        grid_spec=grid_spec,
        out_shape=[
            jax.ShapeDtypeStruct(dq_in.shape, jnp.float32),
            jax.ShapeDtypeStruct(keys.shape, jnp.float32),
            jax.ShapeDtypeStruct(values.shape, jnp.float32),
        ],
        input_output_aliases={7: 0},
        compiler_params=pltpu.CompilerParams(
            dimension_semantics=("arbitrary", "arbitrary"), vmem_limit_bytes=56 * 1024 * 1024
        ),
        cost_estimate=pl.CostEstimate(
            flops=flops,
            transcendentals=kvh * npairs * share * block * block,
            bytes_accessed=kvh * npairs * (10 * block * HEAD_SIZE * 2),
        ),
        name="attn_bwd",
    )(tab, q, hgrad, delta, qs, keys, values, dq_in)


PIECES = 2


EPSILON = 1e-06
THETA = 1000000.0


def swapped(shard, axis, distance):
    return lax.ppermute(shard, axis, [(i, i ^ 1 << distance) for i in range(lax.axis_size(axis))])


def rms_scale(values, gain):
    inverse = lax.rsqrt(jnp.mean(values * values, axis=-1, keepdims=True) + EPSILON)
    return values * inverse * gain


def rotary(values, start_offset):
    half = values.shape[-1] // 2
    frequency = THETA ** (-(jnp.arange(half, dtype=jnp.float32) * 2.0 / values.shape[-1]))
    angle = start_offset.astype(jnp.float32)[:, None] * frequency[None, :]
    cosine = jnp.cos(angle)[:, None, :]
    sine = jnp.sin(angle)[:, None, :]
    first = values[..., :half]
    second = values[..., half:]
    return jnp.concatenate(
        [first * cosine - second * sine, second * cosine + first * sine], axis=-1
    )


def prepare_inputs(projected, gain, start_offset, head_groups):
    shaped = projected.reshape(projected.shape[0], head_groups, -1)
    return rotary(rms_scale(shaped, gain), start_offset)


def piece_places(which, group_rows):
    quarter = group_rows // 2
    local = jnp.arange(group_rows, dtype=jnp.int32)
    chosen = jnp.where(local < quarter, which, 3 - which)
    return chosen * quarter + local % quarter


def contract_rows(left, right):
    return lax.dot_general(
        left, right, (((0,), (0,)), ((), ())), preferred_element_type=jnp.float32
    )


def contract_last(left, right):
    return lax.dot_general(
        left, right, (((1,), (1,)), ((), ())), preferred_element_type=jnp.float32
    )


def split_columns(full, widths):
    parts = []
    at = 0
    for width in widths:
        parts.append(full[:, at : at + width])
        at += width
    return parts


def halving_scatter(grads):
    widths = [g.shape[1] for g in grads]
    packed = jnp.concatenate(grads, axis=1)
    count = lax.axis_size("fsdp")
    me = lax.axis_index("fsdp")
    bits = count.bit_length() - 1
    rows_f = packed.shape[0] // count
    order = [int(format(b, f"0{bits}b")[::-1], 2) for b in range(count)]
    buf = jnp.concatenate([packed[b * rows_f : (b + 1) * rows_f] for b in order], axis=0)
    for bit in range(bits):
        half = buf.shape[0] // 2
        mine = (me >> bit) & 1
        keep = lax.dynamic_slice_in_dim(buf, mine * half, half, 0)
        send = lax.dynamic_slice_in_dim(buf, (1 - mine) * half, half, 0)
        got = lax.ppermute(
            send.astype(jnp.bfloat16), "fsdp", [(i, i ^ (1 << bit)) for i in range(count)]
        )
        buf = keep + got.astype(jnp.float32)
    return split_columns(buf, widths)


def fsdp_gather(values):
    count = lax.axis_size("fsdp")
    me = lax.axis_index("fsdp")
    distance = 1
    while distance < count:
        got = lax.ppermute(values, "fsdp", [(i, i ^ distance) for i in range(count)])
        low = (me & distance) == 0
        values = jnp.concatenate(
            [jnp.where(low, values, got), jnp.where(low, got, values)]
        )
        distance *= 2
    return values


def all_sum(values):
    for axis in ("tensor", "fsdp"):
        distance = 1
        while distance < lax.axis_size(axis):
            values = values + lax.ppermute(
                values, axis, [(i, i ^ distance) for i in range(lax.axis_size(axis))]
            )
            distance *= 2
    return values


def exchange(values, distance):
    count = lax.axis_size("tensor")
    return lax.ppermute(values, "tensor", [(i, i ^ distance) for i in range(count)])


def token_gather(values):
    rows = values.shape[0]
    me = lax.axis_index("tensor")
    across = exchange(values, 2)
    pair = jnp.stack([values, across])
    beside = exchange(pair, 1)
    full = jnp.zeros((4 * rows,) + values.shape[1:], values.dtype)
    for part, place in ((values, me), (across, me ^ 2), (beside[0], me ^ 1), (beside[1], me ^ 3)):
        full = lax.dynamic_update_slice_in_dim(full, part, place * rows, 0)
    return full


def token_sum(term, rows):
    partial = term(jnp.int32(0), rows * lax.axis_size("tensor"))
    me = lax.axis_index("tensor")

    def block(place):
        return lax.dynamic_slice_in_dim(partial, place * rows, rows, 0)

    sent = jnp.stack([block(me ^ 1), block(me ^ 3)]).astype(jnp.bfloat16)
    got = exchange(sent, 1).astype(jnp.float32)
    mine = block(me) + got[0]
    other = (block(me ^ 2) + got[1]).astype(jnp.bfloat16)
    return mine + exchange(other, 2).astype(jnp.float32)


def shards(
    hidden,
    out_grad,
    lengths,
    q_weight,
    key_matrix,
    value_matrix,
    o_weight,
    gate_weight,
    up_weight,
    down_weight,
    input_gain,
    q_gain,
    k_gain,
    post_gain,
):
    split = lax.axis_size("tensor")
    rows = hidden.shape[0]
    group_rows = rows * split
    q_heads = q_weight.shape[1] // HEAD_SIZE
    kv_heads = key_matrix.shape[1] // HEAD_SIZE
    share = q_heads // kv_heads
    scale = HEAD_SIZE ** (-0.5)
    member = lax.axis_index("fsdp")
    slot = member // PIECES
    piece = member % PIECES
    lengths_row = lax.dynamic_index_in_dim(lengths, slot, 0, keepdims=False)
    ends = jnp.cumsum(lengths_row)
    group_place = piece_places(piece, group_rows)
    passed = group_place[:, None] >= ends[None, :]
    group_start = jnp.sum(jnp.where(passed, lengths_row[None, :], 0), axis=1)
    group_offset = group_place - group_start
    local_valid = lax.dynamic_slice_in_dim(
        group_place < ends[-1], lax.axis_index("tensor") * rows, rows, 0
    )
    fs = lax.axis_size("fsdp")
    gain_sizes = (input_gain.shape[0], q_gain.shape[0], k_gain.shape[0], post_gain.shape[0])
    gains_all = fsdp_gather(
        jnp.concatenate([input_gain, q_gain, k_gain, post_gain]).astype(jnp.bfloat16)
    ).reshape(fs, sum(gain_sizes))
    gain_in, gain_query, gain_keys, gain_post = [
        part.reshape(-1) for part in split_columns(gains_all, gain_sizes)
    ]
    attn_full = lax.all_gather(
        jnp.concatenate(
            [
                q_weight.astype(jnp.bfloat16),
                key_matrix.astype(jnp.bfloat16),
                value_matrix.astype(jnp.bfloat16),
            ],
            axis=1,
        ),
        "fsdp",
        axis=0,
        tiled=True,
    )
    widths = (q_weight.shape[1], key_matrix.shape[1], value_matrix.shape[1])
    w_query, w_key, w_value = split_columns(attn_full, widths)
    x_float = hidden.astype(jnp.float32)
    gain_first = gain_in.astype(jnp.float32)
    first_all = token_gather(rms_scale(x_float, gain_first).astype(jnp.bfloat16))
    cotangent = out_grad.astype(jnp.float32) * local_valid[:, None].astype(jnp.float32)
    mlp_grad_all = token_gather(cotangent.astype(jnp.bfloat16))
    first_all, mlp_grad_all = lax.optimization_barrier((first_all, mlp_grad_all))
    query_projected = jnp.dot(first_all, w_query, preferred_element_type=jnp.float32)
    key_projected = jnp.dot(first_all, w_key, preferred_element_type=jnp.float32)
    value_rows = (
        jnp.dot(first_all, w_value, preferred_element_type=jnp.float32)
        .astype(jnp.bfloat16)
        .reshape(group_rows, kv_heads, HEAD_SIZE)
    )
    gain_q = gain_query.astype(jnp.float32)
    gain_k = gain_keys.astype(jnp.float32)
    query_rope = (
        prepare_inputs(query_projected, gain_q, group_offset, q_heads)
        .astype(jnp.bfloat16)
        .reshape(group_rows, kv_heads, share, HEAD_SIZE)
    )
    key_rope = prepare_inputs(key_projected, gain_k, group_offset, kv_heads).astype(jnp.bfloat16)
    quarter = group_rows // 2
    query_start = jnp.broadcast_to(group_start[:, None], (group_rows, 128))
    query_t = jnp.transpose(query_rope, (1, 2, 0, 3))
    own_keys = jnp.transpose(key_rope, (1, 0, 2))
    own_values = jnp.transpose(value_rows, (1, 0, 2))
    moved = swapped(jnp.stack([own_keys, own_values]), "fsdp", 0)
    sums = jnp.zeros(query_t.shape, jnp.float32)
    totals = jnp.zeros(query_t.shape[:3] + (128,), jnp.float32)
    sums, totals = attention_forward(
        query_t, query_start, own_keys, own_values, sums, totals, piece, quarter, 0
    )
    sums, totals_t = attention_forward(
        query_t, query_start, moved[0], moved[1], sums, totals, piece, quarter, 1
    )
    heads_t = sums / totals_t[..., :1]
    heads_out = jnp.transpose(heads_t, (2, 0, 1, 3))
    row_totals = jnp.transpose(totals_t[..., 0], (2, 0, 1))
    out_rows = heads_out.reshape(group_rows, q_heads * HEAD_SIZE).astype(jnp.bfloat16)

    mlp_full = lax.all_gather(
        jnp.concatenate(
            [
                gate_weight.astype(jnp.bfloat16),
                up_weight.astype(jnp.bfloat16),
                jnp.transpose(down_weight).astype(jnp.bfloat16),
                jnp.transpose(o_weight).astype(jnp.bfloat16),
            ],
            axis=1,
        ),
        "fsdp",
        axis=0,
        tiled=True,
    )
    w_gate, w_up, w_down_t, w_out = split_columns(
        mlp_full, (gate_weight.shape[1], up_weight.shape[1], down_weight.shape[0], o_weight.shape[0])
    )

    def out_term(start, count):
        return contract_last(out_rows, w_out)

    after_attn = x_float + token_sum(out_term, rows)
    gain_second = gain_post.astype(jnp.float32)
    second_all = token_gather(rms_scale(after_attn, gain_second).astype(jnp.bfloat16))
    gate_out = jnp.dot(second_all, w_gate, preferred_element_type=jnp.float32)
    up_out = jnp.dot(second_all, w_up, preferred_element_type=jnp.float32)
    activated = (jax.nn.silu(gate_out) * up_out).astype(jnp.bfloat16)

    grad_act = jnp.dot(mlp_grad_all, w_down_t, preferred_element_type=jnp.float32)
    unused, pull_gate = jax.vjp(
        lambda gate_in, up_in: jax.nn.silu(gate_in) * up_in, gate_out, up_out
    )
    grad_gate, grad_up = pull_gate(grad_act)
    grad_gate = grad_gate.astype(jnp.bfloat16)
    grad_up = grad_up.astype(jnp.bfloat16)
    down_grad_t = contract_rows(mlp_grad_all, activated)
    gate_grad = contract_rows(second_all, grad_gate)
    up_grad = contract_rows(second_all, grad_up)

    def second_term(start, count):
        return contract_last(grad_gate, w_gate) + contract_last(grad_up, w_up)

    second_back = token_sum(second_term, rows)
    unused, pull_second = jax.vjp(rms_scale, after_attn, gain_second)
    norm_second_grad, post_gain_part = pull_second(second_back)
    residual_grad = cotangent + norm_second_grad
    attn_grad_all = token_gather(residual_grad.astype(jnp.bfloat16))
    activated_late, attn_grad_all = lax.optimization_barrier((activated, attn_grad_all))
    down_rows = token_sum(lambda start, count: contract_last(activated_late, w_down_t), rows)
    out_weight_grad_t = contract_rows(attn_grad_all, out_rows)
    mlp_packed = jnp.concatenate(
        [g.astype(jnp.bfloat16) for g in (gate_grad, up_grad, down_grad_t, out_weight_grad_t)],
        axis=1,
    )
    head_grad = jnp.dot(attn_grad_all, w_out, preferred_element_type=jnp.float32).astype(
        jnp.bfloat16
    )
    head_float = head_grad.astype(jnp.float32).reshape(group_rows, kv_heads, share, HEAD_SIZE)
    scaled_grad = (head_float / row_totals[..., None]).astype(jnp.bfloat16)
    delta = jnp.sum(head_float * heads_out, axis=-1) / row_totals

    grad_t = jnp.transpose(scaled_grad, (1, 2, 0, 3))
    delta_t = jnp.broadcast_to(
        jnp.transpose(delta, (1, 2, 0))[..., None], (kv_heads, share, group_rows, 128)
    )
    mlp_packed, grad_t, delta_t = lax.optimization_barrier((mlp_packed, grad_t, delta_t))
    mlp_shards = split_columns(
        lax.psum_scatter(mlp_packed, "fsdp", scatter_dimension=0, tiled=True),
        [g.shape[1] for g in (gate_grad, up_grad, down_grad_t, out_weight_grad_t)],
    )
    mlp_shards = [part.astype(jnp.float32) for part in mlp_shards]
    dq_raw, dk_far, dv_far = attention_backward(
        query_t, grad_t, delta_t, query_start, moved[0], moved[1],
        jnp.zeros(query_t.shape, jnp.float32), piece, quarter, 1,
    )
    unseen = (piece == 1) & (jnp.arange(group_rows) >= quarter)
    far_grads = jnp.where(unseen[None, None, :, None], 0.0, jnp.stack([dk_far, dv_far]))
    returned = swapped(far_grads.astype(jnp.bfloat16), "fsdp", 0)
    down_rows, dq_raw = lax.optimization_barrier((down_rows, dq_raw))
    output = (after_attn + down_rows).astype(jnp.bfloat16)
    dq_raw, dk_own, dv_own = attention_backward(
        query_t, grad_t, delta_t, query_start, own_keys, own_values,
        dq_raw, piece, quarter, 0,
    )
    mlp_shards, dq_raw = lax.optimization_barrier((mlp_shards, dq_raw))
    grad_keys_total = jnp.transpose(dk_own + returned[0].astype(jnp.float32), (1, 0, 2))
    grad_values_total = jnp.transpose(dv_own + returned[1].astype(jnp.float32), (1, 0, 2))
    query_grads = jnp.transpose(dq_raw, (2, 0, 1, 3)) * scale
    query_grads = query_grads.reshape(group_rows, q_heads, HEAD_SIZE)
    unused, pull_query = jax.vjp(
        lambda projected, gain: prepare_inputs(projected, gain, group_offset, q_heads),
        query_projected,
        gain_q,
    )
    query_proj_grad, q_gain_part = pull_query(query_grads)
    unused, pull_key = jax.vjp(
        lambda projected, gain: prepare_inputs(projected, gain, group_offset, kv_heads),
        key_projected,
        gain_k,
    )
    key_proj_grad, k_gain_part = pull_key(grad_keys_total)
    query_low = query_proj_grad.astype(jnp.bfloat16)
    key_low = key_proj_grad.astype(jnp.bfloat16)
    value_low = grad_values_total.reshape(group_rows, kv_heads * HEAD_SIZE).astype(jnp.bfloat16)
    query_weight_grad = contract_rows(first_all, query_low)
    key_weight_grad = contract_rows(first_all, key_low)
    value_weight_grad = contract_rows(first_all, value_low)

    def first_term(start, count):
        return (
            contract_last(query_low, w_query)
            + contract_last(key_low, w_key)
            + contract_last(value_low, w_value)
        )

    first_back = token_sum(first_term, rows)
    unused, pull_first = jax.vjp(rms_scale, x_float, gain_first)
    norm_first_grad, input_gain_part = pull_first(first_back)
    input_grad = (residual_grad + norm_first_grad).astype(jnp.bfloat16)
    (query_shard,) = halving_scatter((query_weight_grad,))
    key_shard, value_shard = halving_scatter((key_weight_grad, value_weight_grad))
    gain_totals = all_sum(
        jnp.concatenate([input_gain_part, q_gain_part, k_gain_part, post_gain_part])
    )
    member_f = lax.axis_index("fsdp")
    sizes = (input_gain.shape[0], q_gain.shape[0], k_gain.shape[0], post_gain.shape[0])
    gain_shards = []
    at = 0
    for own in sizes:
        whole = own * fs
        gain_shards.append(lax.dynamic_slice_in_dim(gain_totals, at + member_f * own, own, 0))
        at += whole
    input_gain_shard, q_gain_shard, k_gain_shard, post_gain_shard = gain_shards
    gate_shard, up_shard, down_shard_t, out_shard_t = mlp_shards
    return (
        output,
        input_grad,
        query_shard,
        key_shard,
        value_shard,
        jnp.transpose(out_shard_t),
        gate_shard,
        up_shard,
        jnp.transpose(down_shard_t),
        input_gain_shard,
        q_gain_shard,
        k_gain_shard,
        post_gain_shard,
    )


def solution(mesh):
    return layer_program(mesh)


def layer_program(mesh):
    placed = (
        P(("fsdp", "tensor"), None),
        P(("fsdp", "tensor"), None),
        P(),
        P("fsdp", "tensor"),
        P("fsdp", "tensor"),
        P("fsdp", "tensor"),
        P("tensor", "fsdp"),
        P("fsdp", "tensor"),
        P("fsdp", "tensor"),
        P("tensor", "fsdp"),
        P("fsdp"),
        P("fsdp"),
        P("fsdp"),
        P("fsdp"),
    )
    return jax.shard_map(
        shards,
        mesh=mesh,
        in_specs=placed,
        out_specs=(
            P(("fsdp", "tensor"), None),
            P(("fsdp", "tensor"), None),
            P("fsdp", "tensor"),
            P("fsdp", "tensor"),
            P("fsdp", "tensor"),
            P("tensor", "fsdp"),
            P("fsdp", "tensor"),
            P("fsdp", "tensor"),
            P("tensor", "fsdp"),
            P("fsdp"),
            P("fsdp"),
            P("fsdp"),
            P("fsdp"),
        ),
        check_vma=False,
    )
```

```python
import functools

import numpy as np
import jax
import jax.numpy as jnp
from jax import lax
from jax.experimental import pallas as pl
from jax.experimental.pallas import tpu as pltpu
from jax.sharding import PartitionSpec as P


HEAD_SIZE = 128
TRANS_B = (((1,), (1,)), ((), ()))
TRANS_A = (((0,), (0,)), ((), ()))


def _own_place(p, quarter, r):
    return (p * quarter + r) if r < quarter else ((3 - p) * quarter + r - quarter)


def _far_place(p, quarter, r):
    return ((1 - p) * quarter + r) if r < quarter else ((2 + p) * quarter + r - quarter)


def _pair_tables(p, quarter, block, by_key, source):
    rows = 2 * quarter
    count = rows // block
    kmap = {}
    for src, fn in ((0, _own_place), (1, _far_place)):
        for j in range(count):
            kmap[fn(p, quarter, j * block) // block] = (src, j)
    pairs = []
    for j in range(count):
        qpb = _own_place(p, quarter, j * block) // block
        for kpb in range(qpb + 1):
            if kmap[kpb][0] == source:
                pairs.append((j, qpb, kpb))
    if by_key:
        pairs.sort(key=lambda t: (t[2], t[0]))
    group = [t[2] if by_key else t[0] for t in pairs]
    size = len(pairs)
    first = [1 if n == 0 or group[n - 1] != group[n] else 0 for n in range(size)]
    last = [1 if n == size - 1 or group[n + 1] != group[n] else 0 for n in range(size)]
    return np.array(
        [
            [t[0] for t in pairs],
            [t[1] for t in pairs],
            [t[2] for t in pairs],
            [kmap[t[2]][0] for t in pairs],
            [kmap[t[2]][1] for t in pairs],
            first,
            last,
        ],
        np.int32,
    )


def pair_tables(piece, quarter, block, by_key, source):
    t0 = _pair_tables(0, quarter, block, by_key, source)
    t1 = _pair_tables(1, quarter, block, by_key, source)
    assert t0.shape == t1.shape
    return jnp.where(piece == 0, jnp.asarray(t0), jnp.asarray(t1))


def _mask(qpb, kpb, qs, block):
    qp = qpb * block + lax.broadcasted_iota(jnp.int32, (block, block), 0)
    kp = kpb * block + lax.broadcasted_iota(jnp.int32, (block, block), 1)
    start = jnp.tile(qs, (1, block // 128))
    return (kp >= start) & (kp <= qp)


def _fwd_kernel(tab_ref, q_ref, qs_ref, k_ref, v_ref, a_in_ref, l_in_ref, a_ref, l_ref, acc_ref, sum_ref, *, scale, block):
    n = pl.program_id(1)
    share = q_ref.shape[1]

    @pl.when(tab_ref[5, n] == 1)
    def _():
        acc_ref[...] = a_in_ref[0].reshape(share * block, HEAD_SIZE)
        sum_ref[...] = l_in_ref[0][:, :, :1]

    q = q_ref[0].reshape(share * block, HEAD_SIZE)
    k = k_ref[0]
    v = v_ref[0]
    s = lax.dot_general(q, k, TRANS_B, preferred_element_type=jnp.float32) * scale
    allowed = _mask(tab_ref[1, n], tab_ref[2, n], qs_ref[...], block)
    e = jnp.where(allowed[None], jnp.exp(s.reshape(share, block, block)), 0.0)
    sum_ref[...] += jnp.sum(e, axis=-1, keepdims=True)
    acc_ref[...] += jnp.dot(
        e.reshape(share * block, block).astype(jnp.bfloat16), v, preferred_element_type=jnp.float32
    )

    @pl.when(tab_ref[6, n] == 1)
    def _():
        a_ref[0] = acc_ref[...].reshape(share, block, HEAD_SIZE)
        l_ref[0] = jnp.broadcast_to(sum_ref[...], (share, block, 128))


def attention_forward(q, qs, keys, values, a_in, l_in, piece, quarter, source, block=512):
    kvh, share, _, _ = q.shape
    tab = pair_tables(piece, quarter, block, False, source)
    npairs = tab.shape[1]
    scale = HEAD_SIZE ** (-0.5)
    row_spec = pl.BlockSpec((1, share, block, HEAD_SIZE), lambda h, n, t: (h, 0, t[0, n], 0))
    lane_spec = pl.BlockSpec((1, share, block, 128), lambda h, n, t: (h, 0, t[0, n], 0))
    key_spec = pl.BlockSpec((1, block, HEAD_SIZE), lambda h, n, t: (h, t[4, n], 0))
    grid_spec = pltpu.PrefetchScalarGridSpec(
        num_scalar_prefetch=1,
        grid=(kvh, npairs),
        in_specs=[
            row_spec,
            pl.BlockSpec((block, 128), lambda h, n, t: (t[0, n], 0)),
            key_spec,
            key_spec,
            row_spec,
            lane_spec,
        ],
        out_specs=[row_spec, lane_spec],
        scratch_shapes=[
            pltpu.VMEM((share * block, HEAD_SIZE), jnp.float32),
            pltpu.VMEM((share, block, 1), jnp.float32),
        ],
    )
    flops = 4 * kvh * npairs * share * block * block * HEAD_SIZE
    return pl.pallas_call(
        functools.partial(_fwd_kernel, scale=scale, block=block),
        grid_spec=grid_spec,
        out_shape=[
            jax.ShapeDtypeStruct(a_in.shape, jnp.float32),
            jax.ShapeDtypeStruct(l_in.shape, jnp.float32),
        ],
        input_output_aliases={5: 0, 6: 1},
        compiler_params=pltpu.CompilerParams(
            dimension_semantics=("arbitrary", "arbitrary"), vmem_limit_bytes=48 * 1024 * 1024
        ),
        cost_estimate=pl.CostEstimate(
            flops=flops,
            transcendentals=kvh * npairs * share * block * block,
            bytes_accessed=kvh * npairs * (8 * block * HEAD_SIZE * 2),
        ),
        name="attn_fwd",
    )(tab, q, qs, keys, values, a_in, l_in)


def _bwd_kernel(tab_ref, q_ref, h_ref, dl_ref, qs_ref, k_ref, v_ref, dq_in_ref, dq_ref, dk_ref, dv_ref, dk_acc, dv_acc, *, scale, block):
    n = pl.program_id(1)
    share = q_ref.shape[1]

    @pl.when(n == 0)
    def _():
        dq_ref[...] = dq_in_ref[...]

    @pl.when(tab_ref[5, n] == 1)
    def _():
        dk_acc[...] = jnp.zeros(dk_acc.shape, dk_acc.dtype)
        dv_acc[...] = jnp.zeros(dv_acc.shape, dv_acc.dtype)

    q = q_ref[0].reshape(share * block, HEAD_SIZE)
    hh = h_ref[0].reshape(share * block, HEAD_SIZE)
    k = k_ref[0]
    v = v_ref[0]
    s = lax.dot_general(q, k, TRANS_B, preferred_element_type=jnp.float32) * scale
    allowed = _mask(tab_ref[1, n], tab_ref[2, n], qs_ref[...], block)
    e = jnp.where(allowed[None], jnp.exp(s.reshape(share, block, block)), 0.0)
    dp = lax.dot_general(hh, v, TRANS_B, preferred_element_type=jnp.float32).reshape(share, block, block)
    delta = jnp.tile(dl_ref[0], (1, 1, block // 128))
    ds = (e * (dp - delta)).reshape(share * block, block).astype(jnp.bfloat16)
    rows = pl.ds(pl.multiple_of(tab_ref[0, n] * block, block), block)
    dq_ref[0, :, rows, :] += jnp.dot(ds, k, preferred_element_type=jnp.float32).reshape(share, block, HEAD_SIZE)
    dk_acc[...] += lax.dot_general(ds, q, TRANS_A, preferred_element_type=jnp.float32)
    dv_acc[...] += lax.dot_general(
        e.reshape(share * block, block).astype(jnp.bfloat16), hh, TRANS_A, preferred_element_type=jnp.float32
    )

    @pl.when(tab_ref[6, n] == 1)
    def _():
        dk_ref[0] = dk_acc[...] * scale
        dv_ref[0] = dv_acc[...]


def attention_backward(q, hgrad, delta, qs, keys, values, dq_in, piece, quarter, source, block=512):
    kvh, share, rows, _ = q.shape
    tab = pair_tables(piece, quarter, block, True, source)
    npairs = tab.shape[1]
    scale = HEAD_SIZE ** (-0.5)
    row_spec = pl.BlockSpec((1, share, block, HEAD_SIZE), lambda h, n, t: (h, 0, t[0, n], 0))
    key_spec = pl.BlockSpec((1, block, HEAD_SIZE), lambda h, n, t: (h, t[4, n], 0))
    full_spec = pl.BlockSpec((1, share, rows, HEAD_SIZE), lambda h, n, t: (h, 0, 0, 0))
    grid_spec = pltpu.PrefetchScalarGridSpec(
        num_scalar_prefetch=1,
        grid=(kvh, npairs),
        in_specs=[
            row_spec,
            row_spec,
            pl.BlockSpec((1, share, block, 128), lambda h, n, t: (h, 0, t[0, n], 0)),
            pl.BlockSpec((block, 128), lambda h, n, t: (t[0, n], 0)),
            key_spec,
            key_spec,
            full_spec,
        ],
        out_specs=[full_spec, key_spec, key_spec],
        scratch_shapes=[
            pltpu.VMEM((block, HEAD_SIZE), jnp.float32),
            pltpu.VMEM((block, HEAD_SIZE), jnp.float32),
        ],
    )
    flops = 10 * kvh * npairs * share * block * block * HEAD_SIZE
    return pl.pallas_call(
        functools.partial(_bwd_kernel, scale=scale, block=block),
        grid_spec=grid_spec,
        out_shape=[
            jax.ShapeDtypeStruct(dq_in.shape, jnp.float32),
            jax.ShapeDtypeStruct(keys.shape, jnp.float32),
            jax.ShapeDtypeStruct(values.shape, jnp.float32),
        ],
        input_output_aliases={7: 0},
        compiler_params=pltpu.CompilerParams(
            dimension_semantics=("arbitrary", "arbitrary"), vmem_limit_bytes=56 * 1024 * 1024
        ),
        cost_estimate=pl.CostEstimate(
            flops=flops,
            transcendentals=kvh * npairs * share * block * block,
            bytes_accessed=kvh * npairs * (10 * block * HEAD_SIZE * 2),
        ),
        name="attn_bwd",
    )(tab, q, hgrad, delta, qs, keys, values, dq_in)


PIECES = 2


EPSILON = 1e-06
THETA = 1000000.0


def swapped(shard, axis, distance):
    return lax.ppermute(shard, axis, [(i, i ^ 1 << distance) for i in range(lax.axis_size(axis))])


def rms_scale(values, gain):
    inverse = lax.rsqrt(jnp.mean(values * values, axis=-1, keepdims=True) + EPSILON)
    return values * inverse * gain


def rotary(values, start_offset):
    half = values.shape[-1] // 2
    frequency = THETA ** (-(jnp.arange(half, dtype=jnp.float32) * 2.0 / values.shape[-1]))
    angle = start_offset.astype(jnp.float32)[:, None] * frequency[None, :]
    cosine = jnp.cos(angle)[:, None, :]
    sine = jnp.sin(angle)[:, None, :]
    first = values[..., :half]
    second = values[..., half:]
    return jnp.concatenate(
        [first * cosine - second * sine, second * cosine + first * sine], axis=-1
    )


def prepare_inputs(projected, gain, start_offset, head_groups):
    shaped = projected.reshape(projected.shape[0], head_groups, -1)
    return rotary(rms_scale(shaped, gain), start_offset)


def piece_places(which, group_rows):
    quarter = group_rows // 2
    local = jnp.arange(group_rows, dtype=jnp.int32)
    chosen = jnp.where(local < quarter, which, 3 - which)
    return chosen * quarter + local % quarter


def contract_rows(left, right):
    return lax.dot_general(
        left, right, (((0,), (0,)), ((), ())), preferred_element_type=jnp.float32
    )


def contract_last(left, right):
    return lax.dot_general(
        left, right, (((1,), (1,)), ((), ())), preferred_element_type=jnp.float32
    )


def split_columns(full, widths):
    parts = []
    at = 0
    for width in widths:
        parts.append(full[:, at : at + width])
        at += width
    return parts


def halving_scatter(grads):
    widths = [g.shape[1] for g in grads]
    packed = jnp.concatenate(grads, axis=1)
    count = lax.axis_size("fsdp")
    me = lax.axis_index("fsdp")
    bits = count.bit_length() - 1
    rows_f = packed.shape[0] // count
    order = [int(format(b, f"0{bits}b")[::-1], 2) for b in range(count)]
    buf = jnp.concatenate([packed[b * rows_f : (b + 1) * rows_f] for b in order], axis=0)
    for bit in range(bits):
        half = buf.shape[0] // 2
        mine = (me >> bit) & 1
        keep = lax.dynamic_slice_in_dim(buf, mine * half, half, 0)
        send = lax.dynamic_slice_in_dim(buf, (1 - mine) * half, half, 0)
        got = lax.ppermute(
            send.astype(jnp.bfloat16), "fsdp", [(i, i ^ (1 << bit)) for i in range(count)]
        )
        buf = keep + got.astype(jnp.float32)
    return split_columns(buf, widths)


def doubling_gather(values):
    count = lax.axis_size("fsdp")
    me = lax.axis_index("fsdp")
    rows_f = values.shape[0]
    full = jnp.zeros((count,) + values.shape, values.dtype)
    full = lax.dynamic_update_slice_in_dim(full, values[None], me, 0)
    bit = count // 2
    while bit >= 1:
        view = full.reshape((count // (2 * bit), 2 * bit) + values.shape)
        held = lax.dynamic_index_in_dim(view, me % (2 * bit), 1, keepdims=True)
        got = lax.ppermute(held, "fsdp", [(i, i ^ bit) for i in range(count)])
        view = lax.dynamic_update_slice_in_dim(view, got, (me ^ bit) % (2 * bit), 1)
        full = view.reshape(full.shape)
        bit //= 2
    return full.reshape((count * rows_f,) + values.shape[1:])


def fsdp_gather(values):
    count = lax.axis_size("fsdp")
    me = lax.axis_index("fsdp")
    distance = 1
    while distance < count:
        got = lax.ppermute(values, "fsdp", [(i, i ^ distance) for i in range(count)])
        low = (me & distance) == 0
        values = jnp.concatenate(
            [jnp.where(low, values, got), jnp.where(low, got, values)]
        )
        distance *= 2
    return values


def all_sum(values):
    for axis in ("tensor", "fsdp"):
        distance = 1
        while distance < lax.axis_size(axis):
            values = values + lax.ppermute(
                values, axis, [(i, i ^ distance) for i in range(lax.axis_size(axis))]
            )
            distance *= 2
    return values


def exchange(values, distance):
    count = lax.axis_size("tensor")
    return lax.ppermute(values, "tensor", [(i, i ^ distance) for i in range(count)])


def token_gather(values):
    rows = values.shape[0]
    me = lax.axis_index("tensor")
    across = exchange(values, 2)
    pair = jnp.stack([values, across])
    beside = exchange(pair, 1)
    full = jnp.zeros((4 * rows,) + values.shape[1:], values.dtype)
    for part, place in ((values, me), (across, me ^ 2), (beside[0], me ^ 1), (beside[1], me ^ 3)):
        full = lax.dynamic_update_slice_in_dim(full, part, place * rows, 0)
    return full


def token_sum(term, rows):
    partial = term(jnp.int32(0), rows * lax.axis_size("tensor"))
    me = lax.axis_index("tensor")

    def block(place):
        return lax.dynamic_slice_in_dim(partial, place * rows, rows, 0)

    sent = jnp.stack([block(me ^ 1), block(me ^ 3)]).astype(jnp.bfloat16)
    got = exchange(sent, 1).astype(jnp.float32)
    mine = block(me) + got[0]
    other = (block(me ^ 2) + got[1]).astype(jnp.bfloat16)
    return mine + exchange(other, 2).astype(jnp.float32)


def shards(
    hidden,
    out_grad,
    lengths,
    q_weight,
    key_matrix,
    value_matrix,
    o_weight,
    gate_weight,
    up_weight,
    down_weight,
    input_gain,
    q_gain,
    k_gain,
    post_gain,
):
    split = lax.axis_size("tensor")
    rows = hidden.shape[0]
    group_rows = rows * split
    q_heads = q_weight.shape[1] // HEAD_SIZE
    kv_heads = key_matrix.shape[1] // HEAD_SIZE
    share = q_heads // kv_heads
    scale = HEAD_SIZE ** (-0.5)
    member = lax.axis_index("fsdp")
    slot = member // PIECES
    piece = member % PIECES
    lengths_row = lax.dynamic_index_in_dim(lengths, slot, 0, keepdims=False)
    ends = jnp.cumsum(lengths_row)
    group_place = piece_places(piece, group_rows)
    passed = group_place[:, None] >= ends[None, :]
    group_start = jnp.sum(jnp.where(passed, lengths_row[None, :], 0), axis=1)
    group_offset = group_place - group_start
    local_valid = lax.dynamic_slice_in_dim(
        group_place < ends[-1], lax.axis_index("tensor") * rows, rows, 0
    )
    fs = lax.axis_size("fsdp")
    gain_sizes = (input_gain.shape[0], q_gain.shape[0], k_gain.shape[0], post_gain.shape[0])
    gains_all = fsdp_gather(
        jnp.concatenate([input_gain, q_gain, k_gain, post_gain]).astype(jnp.bfloat16)
    ).reshape(fs, sum(gain_sizes))
    gain_in, gain_query, gain_keys, gain_post = [
        part.reshape(-1) for part in split_columns(gains_all, gain_sizes)
    ]
    attn_full = doubling_gather(
        jnp.concatenate(
            [
                q_weight.astype(jnp.bfloat16),
                key_matrix.astype(jnp.bfloat16),
                value_matrix.astype(jnp.bfloat16),
            ],
            axis=1,
        )
    )
    widths = (q_weight.shape[1], key_matrix.shape[1], value_matrix.shape[1])
    w_query, w_key, w_value = split_columns(attn_full, widths)
    x_float = hidden.astype(jnp.float32)
    gain_first = gain_in.astype(jnp.float32)
    first_all = token_gather(rms_scale(x_float, gain_first).astype(jnp.bfloat16))
    cotangent = out_grad.astype(jnp.float32) * local_valid[:, None].astype(jnp.float32)
    mlp_grad_all = token_gather(cotangent.astype(jnp.bfloat16))
    first_all, mlp_grad_all = lax.optimization_barrier((first_all, mlp_grad_all))
    query_projected = jnp.dot(first_all, w_query, preferred_element_type=jnp.float32)
    key_projected = jnp.dot(first_all, w_key, preferred_element_type=jnp.float32)
    value_rows = (
        jnp.dot(first_all, w_value, preferred_element_type=jnp.float32)
        .astype(jnp.bfloat16)
        .reshape(group_rows, kv_heads, HEAD_SIZE)
    )
    gain_q = gain_query.astype(jnp.float32)
    gain_k = gain_keys.astype(jnp.float32)
    query_rope = (
        prepare_inputs(query_projected, gain_q, group_offset, q_heads)
        .astype(jnp.bfloat16)
        .reshape(group_rows, kv_heads, share, HEAD_SIZE)
    )
    key_rope = prepare_inputs(key_projected, gain_k, group_offset, kv_heads).astype(jnp.bfloat16)
    quarter = group_rows // 2
    query_start = jnp.broadcast_to(group_start[:, None], (group_rows, 128))
    query_t = jnp.transpose(query_rope, (1, 2, 0, 3))
    own_keys = jnp.transpose(key_rope, (1, 0, 2))
    own_values = jnp.transpose(value_rows, (1, 0, 2))
    moved = swapped(jnp.stack([own_keys, own_values]), "fsdp", 0)
    sums = jnp.zeros(query_t.shape, jnp.float32)
    totals = jnp.zeros(query_t.shape[:3] + (128,), jnp.float32)
    sums, totals = attention_forward(
        query_t, query_start, own_keys, own_values, sums, totals, piece, quarter, 0
    )
    sums, totals_t = attention_forward(
        query_t, query_start, moved[0], moved[1], sums, totals, piece, quarter, 1
    )
    heads_t = sums / totals_t[..., :1]
    heads_out = jnp.transpose(heads_t, (2, 0, 1, 3))
    row_totals = jnp.transpose(totals_t[..., 0], (2, 0, 1))
    out_rows = heads_out.reshape(group_rows, q_heads * HEAD_SIZE).astype(jnp.bfloat16)

    mlp_full = lax.all_gather(
        jnp.concatenate(
            [
                gate_weight.astype(jnp.bfloat16),
                up_weight.astype(jnp.bfloat16),
                jnp.transpose(down_weight).astype(jnp.bfloat16),
                jnp.transpose(o_weight).astype(jnp.bfloat16),
            ],
            axis=1,
        ),
        "fsdp",
        axis=0,
        tiled=True,
    )
    w_gate, w_up, w_down_t, w_out = split_columns(
        mlp_full, (gate_weight.shape[1], up_weight.shape[1], down_weight.shape[0], o_weight.shape[0])
    )

    def out_term(start, count):
        return contract_last(out_rows, w_out)

    after_attn = x_float + token_sum(out_term, rows)
    gain_second = gain_post.astype(jnp.float32)
    second_all = token_gather(rms_scale(after_attn, gain_second).astype(jnp.bfloat16))
    gate_out = jnp.dot(second_all, w_gate, preferred_element_type=jnp.float32)
    up_out = jnp.dot(second_all, w_up, preferred_element_type=jnp.float32)
    activated = (jax.nn.silu(gate_out) * up_out).astype(jnp.bfloat16)

    grad_act = jnp.dot(mlp_grad_all, w_down_t, preferred_element_type=jnp.float32)
    unused, pull_gate = jax.vjp(
        lambda gate_in, up_in: jax.nn.silu(gate_in) * up_in, gate_out, up_out
    )
    grad_gate, grad_up = pull_gate(grad_act)
    grad_gate = grad_gate.astype(jnp.bfloat16)
    grad_up = grad_up.astype(jnp.bfloat16)
    down_grad_t = contract_rows(mlp_grad_all, activated)
    gate_grad = contract_rows(second_all, grad_gate)
    up_grad = contract_rows(second_all, grad_up)

    def second_term(start, count):
        return contract_last(grad_gate, w_gate) + contract_last(grad_up, w_up)

    second_back = token_sum(second_term, rows)
    unused, pull_second = jax.vjp(rms_scale, after_attn, gain_second)
    norm_second_grad, post_gain_part = pull_second(second_back)
    residual_grad = cotangent + norm_second_grad
    attn_grad_all = token_gather(residual_grad.astype(jnp.bfloat16))
    activated_late, attn_grad_all = lax.optimization_barrier((activated, attn_grad_all))
    down_rows = token_sum(lambda start, count: contract_last(activated_late, w_down_t), rows)
    out_weight_grad_t = contract_rows(attn_grad_all, out_rows)
    mlp_packed = jnp.concatenate(
        [g.astype(jnp.bfloat16) for g in (gate_grad, up_grad, down_grad_t, out_weight_grad_t)],
        axis=1,
    )
    head_grad = jnp.dot(attn_grad_all, w_out, preferred_element_type=jnp.float32).astype(
        jnp.bfloat16
    )
    head_float = head_grad.astype(jnp.float32).reshape(group_rows, kv_heads, share, HEAD_SIZE)
    scaled_grad = (head_float / row_totals[..., None]).astype(jnp.bfloat16)
    delta = jnp.sum(head_float * heads_out, axis=-1) / row_totals

    grad_t = jnp.transpose(scaled_grad, (1, 2, 0, 3))
    delta_t = jnp.broadcast_to(
        jnp.transpose(delta, (1, 2, 0))[..., None], (kv_heads, share, group_rows, 128)
    )
    mlp_packed, grad_t, delta_t = lax.optimization_barrier((mlp_packed, grad_t, delta_t))
    mlp_shards = split_columns(
        lax.psum_scatter(mlp_packed, "fsdp", scatter_dimension=0, tiled=True),
        [g.shape[1] for g in (gate_grad, up_grad, down_grad_t, out_weight_grad_t)],
    )
    mlp_shards = [part.astype(jnp.float32) for part in mlp_shards]
    dq_raw, dk_far, dv_far = attention_backward(
        query_t, grad_t, delta_t, query_start, moved[0], moved[1],
        jnp.zeros(query_t.shape, jnp.float32), piece, quarter, 1,
    )
    unseen = (piece == 1) & (jnp.arange(group_rows) >= quarter)
    far_grads = jnp.where(unseen[None, None, :, None], 0.0, jnp.stack([dk_far, dv_far]))
    returned = swapped(far_grads.astype(jnp.bfloat16), "fsdp", 0)
    down_rows, dq_raw = lax.optimization_barrier((down_rows, dq_raw))
    output = (after_attn + down_rows).astype(jnp.bfloat16)
    dq_raw, dk_own, dv_own = attention_backward(
        query_t, grad_t, delta_t, query_start, own_keys, own_values,
        dq_raw, piece, quarter, 0,
    )
    mlp_shards, dq_raw = lax.optimization_barrier((mlp_shards, dq_raw))
    grad_keys_total = jnp.transpose(dk_own + returned[0].astype(jnp.float32), (1, 0, 2))
    grad_values_total = jnp.transpose(dv_own + returned[1].astype(jnp.float32), (1, 0, 2))
    query_grads = jnp.transpose(dq_raw, (2, 0, 1, 3)) * scale
    query_grads = query_grads.reshape(group_rows, q_heads, HEAD_SIZE)
    unused, pull_query = jax.vjp(
        lambda projected, gain: prepare_inputs(projected, gain, group_offset, q_heads),
        query_projected,
        gain_q,
    )
    query_proj_grad, q_gain_part = pull_query(query_grads)
    unused, pull_key = jax.vjp(
        lambda projected, gain: prepare_inputs(projected, gain, group_offset, kv_heads),
        key_projected,
        gain_k,
    )
    key_proj_grad, k_gain_part = pull_key(grad_keys_total)
    query_low = query_proj_grad.astype(jnp.bfloat16)
    key_low = key_proj_grad.astype(jnp.bfloat16)
    value_low = grad_values_total.reshape(group_rows, kv_heads * HEAD_SIZE).astype(jnp.bfloat16)
    query_weight_grad = contract_rows(first_all, query_low)
    key_weight_grad = contract_rows(first_all, key_low)
    value_weight_grad = contract_rows(first_all, value_low)

    def first_term(start, count):
        return (
            contract_last(query_low, w_query)
            + contract_last(key_low, w_key)
            + contract_last(value_low, w_value)
        )

    first_back = token_sum(first_term, rows)
    unused, pull_first = jax.vjp(rms_scale, x_float, gain_first)
    norm_first_grad, input_gain_part = pull_first(first_back)
    input_grad = (residual_grad + norm_first_grad).astype(jnp.bfloat16)
    (query_shard,) = halving_scatter((query_weight_grad,))
    key_shard, value_shard = halving_scatter((key_weight_grad, value_weight_grad))
    gain_totals = all_sum(
        jnp.concatenate([input_gain_part, q_gain_part, k_gain_part, post_gain_part])
    )
    member_f = lax.axis_index("fsdp")
    sizes = (input_gain.shape[0], q_gain.shape[0], k_gain.shape[0], post_gain.shape[0])
    gain_shards = []
    at = 0
    for own in sizes:
        whole = own * fs
        gain_shards.append(lax.dynamic_slice_in_dim(gain_totals, at + member_f * own, own, 0))
        at += whole
    input_gain_shard, q_gain_shard, k_gain_shard, post_gain_shard = gain_shards
    gate_shard, up_shard, down_shard_t, out_shard_t = mlp_shards
    return (
        output,
        input_grad,
        query_shard,
        key_shard,
        value_shard,
        jnp.transpose(out_shard_t),
        gate_shard,
        up_shard,
        jnp.transpose(down_shard_t),
        input_gain_shard,
        q_gain_shard,
        k_gain_shard,
        post_gain_shard,
    )


def solution(mesh):
    return layer_program(mesh)


def layer_program(mesh):
    placed = (
        P(("fsdp", "tensor"), None),
        P(("fsdp", "tensor"), None),
        P(),
        P("fsdp", "tensor"),
        P("fsdp", "tensor"),
        P("fsdp", "tensor"),
        P("tensor", "fsdp"),
        P("fsdp", "tensor"),
        P("fsdp", "tensor"),
        P("tensor", "fsdp"),
        P("fsdp"),
        P("fsdp"),
        P("fsdp"),
        P("fsdp"),
    )
    return jax.shard_map(
        shards,
        mesh=mesh,
        in_specs=placed,
        out_specs=(
            P(("fsdp", "tensor"), None),
            P(("fsdp", "tensor"), None),
            P("fsdp", "tensor"),
            P("fsdp", "tensor"),
            P("fsdp", "tensor"),
            P("tensor", "fsdp"),
            P("fsdp", "tensor"),
            P("fsdp", "tensor"),
            P("tensor", "fsdp"),
            P("fsdp"),
            P("fsdp"),
            P("fsdp"),
            P("fsdp"),
        ),
        check_vma=False,
    )
```

```python
import functools

import numpy as np
import jax
import jax.numpy as jnp
from jax import lax
from jax.experimental import pallas as pl
from jax.experimental.pallas import tpu as pltpu
from jax.sharding import PartitionSpec as P


HEAD_SIZE = 128
TRANS_B = (((1,), (1,)), ((), ()))
TRANS_A = (((0,), (0,)), ((), ()))


def _own_place(p, quarter, r):
    return (p * quarter + r) if r < quarter else ((3 - p) * quarter + r - quarter)


def _far_place(p, quarter, r):
    return ((1 - p) * quarter + r) if r < quarter else ((2 + p) * quarter + r - quarter)


def _pair_tables(p, quarter, block, by_key, source):
    rows = 2 * quarter
    count = rows // block
    kmap = {}
    for src, fn in ((0, _own_place), (1, _far_place)):
        for j in range(count):
            kmap[fn(p, quarter, j * block) // block] = (src, j)
    pairs = []
    for j in range(count):
        qpb = _own_place(p, quarter, j * block) // block
        for kpb in range(qpb + 1):
            if kmap[kpb][0] == source:
                pairs.append((j, qpb, kpb))
    if by_key:
        pairs.sort(key=lambda t: (t[2], t[0]))
    group = [t[2] if by_key else t[0] for t in pairs]
    size = len(pairs)
    first = [1 if n == 0 or group[n - 1] != group[n] else 0 for n in range(size)]
    last = [1 if n == size - 1 or group[n + 1] != group[n] else 0 for n in range(size)]
    return np.array(
        [
            [t[0] for t in pairs],
            [t[1] for t in pairs],
            [t[2] for t in pairs],
            [kmap[t[2]][0] for t in pairs],
            [kmap[t[2]][1] for t in pairs],
            first,
            last,
        ],
        np.int32,
    )


def pair_tables(piece, quarter, block, by_key, source):
    t0 = _pair_tables(0, quarter, block, by_key, source)
    t1 = _pair_tables(1, quarter, block, by_key, source)
    assert t0.shape == t1.shape
    return jnp.where(piece == 0, jnp.asarray(t0), jnp.asarray(t1))


def _mask(qpb, kpb, qs, block):
    qp = qpb * block + lax.broadcasted_iota(jnp.int32, (block, block), 0)
    kp = kpb * block + lax.broadcasted_iota(jnp.int32, (block, block), 1)
    start = jnp.tile(qs, (1, block // 128))
    return (kp >= start) & (kp <= qp)


def _fwd_kernel(tab_ref, q_ref, qs_ref, k_ref, v_ref, a_in_ref, l_in_ref, a_ref, l_ref, acc_ref, sum_ref, *, scale, block):
    n = pl.program_id(1)
    share = q_ref.shape[1]

    @pl.when(tab_ref[5, n] == 1)
    def _():
        acc_ref[...] = a_in_ref[0].reshape(share * block, HEAD_SIZE)
        sum_ref[...] = l_in_ref[0][:, :, :1]

    q = q_ref[0].reshape(share * block, HEAD_SIZE)
    k = k_ref[0]
    v = v_ref[0]
    s = lax.dot_general(q, k, TRANS_B, preferred_element_type=jnp.float32) * scale
    allowed = _mask(tab_ref[1, n], tab_ref[2, n], qs_ref[...], block)
    e = jnp.where(allowed[None], jnp.exp(s.reshape(share, block, block)), 0.0)
    sum_ref[...] += jnp.sum(e, axis=-1, keepdims=True)
    acc_ref[...] += jnp.dot(
        e.reshape(share * block, block).astype(jnp.bfloat16), v, preferred_element_type=jnp.float32
    )

    @pl.when(tab_ref[6, n] == 1)
    def _():
        a_ref[0] = acc_ref[...].reshape(share, block, HEAD_SIZE)
        l_ref[0] = jnp.broadcast_to(sum_ref[...], (share, block, 128))


def attention_forward(q, qs, keys, values, a_in, l_in, piece, quarter, source, block=512):
    kvh, share, _, _ = q.shape
    tab = pair_tables(piece, quarter, block, False, source)
    npairs = tab.shape[1]
    scale = HEAD_SIZE ** (-0.5)
    row_spec = pl.BlockSpec((1, share, block, HEAD_SIZE), lambda h, n, t: (h, 0, t[0, n], 0))
    lane_spec = pl.BlockSpec((1, share, block, 128), lambda h, n, t: (h, 0, t[0, n], 0))
    key_spec = pl.BlockSpec((1, block, HEAD_SIZE), lambda h, n, t: (h, t[4, n], 0))
    grid_spec = pltpu.PrefetchScalarGridSpec(
        num_scalar_prefetch=1,
        grid=(kvh, npairs),
        in_specs=[
            row_spec,
            pl.BlockSpec((block, 128), lambda h, n, t: (t[0, n], 0)),
            key_spec,
            key_spec,
            row_spec,
            lane_spec,
        ],
        out_specs=[row_spec, lane_spec],
        scratch_shapes=[
            pltpu.VMEM((share * block, HEAD_SIZE), jnp.float32),
            pltpu.VMEM((share, block, 1), jnp.float32),
        ],
    )
    flops = 4 * kvh * npairs * share * block * block * HEAD_SIZE
    return pl.pallas_call(
        functools.partial(_fwd_kernel, scale=scale, block=block),
        grid_spec=grid_spec,
        out_shape=[
            jax.ShapeDtypeStruct(a_in.shape, jnp.float32),
            jax.ShapeDtypeStruct(l_in.shape, jnp.float32),
        ],
        input_output_aliases={5: 0, 6: 1},
        compiler_params=pltpu.CompilerParams(
            dimension_semantics=("arbitrary", "arbitrary"), vmem_limit_bytes=48 * 1024 * 1024
        ),
        cost_estimate=pl.CostEstimate(
            flops=flops,
            transcendentals=kvh * npairs * share * block * block,
            bytes_accessed=kvh * npairs * (8 * block * HEAD_SIZE * 2),
        ),
        name="attn_fwd",
    )(tab, q, qs, keys, values, a_in, l_in)


def _bwd_kernel(tab_ref, q_ref, h_ref, dl_ref, qs_ref, k_ref, v_ref, dq_in_ref, dq_ref, dk_ref, dv_ref, dk_acc, dv_acc, *, scale, block):
    n = pl.program_id(1)
    share = q_ref.shape[1]

    @pl.when(n == 0)
    def _():
        dq_ref[...] = dq_in_ref[...]

    @pl.when(tab_ref[5, n] == 1)
    def _():
        dk_acc[...] = jnp.zeros(dk_acc.shape, dk_acc.dtype)
        dv_acc[...] = jnp.zeros(dv_acc.shape, dv_acc.dtype)

    q = q_ref[0].reshape(share * block, HEAD_SIZE)
    hh = h_ref[0].reshape(share * block, HEAD_SIZE)
    k = k_ref[0]
    v = v_ref[0]
    s = lax.dot_general(q, k, TRANS_B, preferred_element_type=jnp.float32) * scale
    allowed = _mask(tab_ref[1, n], tab_ref[2, n], qs_ref[...], block)
    e = jnp.where(allowed[None], jnp.exp(s.reshape(share, block, block)), 0.0)
    dp = lax.dot_general(hh, v, TRANS_B, preferred_element_type=jnp.float32).reshape(share, block, block)
    delta = jnp.tile(dl_ref[0], (1, 1, block // 128))
    ds = (e * (dp - delta)).reshape(share * block, block).astype(jnp.bfloat16)
    rows = pl.ds(pl.multiple_of(tab_ref[0, n] * block, block), block)
    dq_ref[0, :, rows, :] += jnp.dot(ds, k, preferred_element_type=jnp.float32).reshape(share, block, HEAD_SIZE)
    dk_acc[...] += lax.dot_general(ds, q, TRANS_A, preferred_element_type=jnp.float32)
    dv_acc[...] += lax.dot_general(
        e.reshape(share * block, block).astype(jnp.bfloat16), hh, TRANS_A, preferred_element_type=jnp.float32
    )

    @pl.when(tab_ref[6, n] == 1)
    def _():
        dk_ref[0] = dk_acc[...] * scale
        dv_ref[0] = dv_acc[...]


def attention_backward(q, hgrad, delta, qs, keys, values, dq_in, piece, quarter, source, block=512):
    kvh, share, rows, _ = q.shape
    tab = pair_tables(piece, quarter, block, True, source)
    npairs = tab.shape[1]
    scale = HEAD_SIZE ** (-0.5)
    row_spec = pl.BlockSpec((1, share, block, HEAD_SIZE), lambda h, n, t: (h, 0, t[0, n], 0))
    key_spec = pl.BlockSpec((1, block, HEAD_SIZE), lambda h, n, t: (h, t[4, n], 0))
    full_spec = pl.BlockSpec((1, share, rows, HEAD_SIZE), lambda h, n, t: (h, 0, 0, 0))
    grid_spec = pltpu.PrefetchScalarGridSpec(
        num_scalar_prefetch=1,
        grid=(kvh, npairs),
        in_specs=[
            row_spec,
            row_spec,
            pl.BlockSpec((1, share, block, 128), lambda h, n, t: (h, 0, t[0, n], 0)),
            pl.BlockSpec((block, 128), lambda h, n, t: (t[0, n], 0)),
            key_spec,
            key_spec,
            full_spec,
        ],
        out_specs=[full_spec, key_spec, key_spec],
        scratch_shapes=[
            pltpu.VMEM((block, HEAD_SIZE), jnp.float32),
            pltpu.VMEM((block, HEAD_SIZE), jnp.float32),
        ],
    )
    flops = 10 * kvh * npairs * share * block * block * HEAD_SIZE
    return pl.pallas_call(
        functools.partial(_bwd_kernel, scale=scale, block=block),
        grid_spec=grid_spec,
        out_shape=[
            jax.ShapeDtypeStruct(dq_in.shape, jnp.float32),
            jax.ShapeDtypeStruct(keys.shape, jnp.float32),
            jax.ShapeDtypeStruct(values.shape, jnp.float32),
        ],
        input_output_aliases={7: 0},
        compiler_params=pltpu.CompilerParams(
            dimension_semantics=("arbitrary", "arbitrary"), vmem_limit_bytes=56 * 1024 * 1024
        ),
        cost_estimate=pl.CostEstimate(
            flops=flops,
            transcendentals=kvh * npairs * share * block * block,
            bytes_accessed=kvh * npairs * (10 * block * HEAD_SIZE * 2),
        ),
        name="attn_bwd",
    )(tab, q, hgrad, delta, qs, keys, values, dq_in)


PIECES = 2


EPSILON = 1e-06
THETA = 1000000.0


def swapped(shard, axis, distance):
    return lax.ppermute(shard, axis, [(i, i ^ 1 << distance) for i in range(lax.axis_size(axis))])


def rms_scale(values, gain):
    inverse = lax.rsqrt(jnp.mean(values * values, axis=-1, keepdims=True) + EPSILON)
    return values * inverse * gain


def rotary(values, start_offset):
    half = values.shape[-1] // 2
    frequency = THETA ** (-(jnp.arange(half, dtype=jnp.float32) * 2.0 / values.shape[-1]))
    angle = start_offset.astype(jnp.float32)[:, None] * frequency[None, :]
    cosine = jnp.cos(angle)[:, None, :]
    sine = jnp.sin(angle)[:, None, :]
    first = values[..., :half]
    second = values[..., half:]
    return jnp.concatenate(
        [first * cosine - second * sine, second * cosine + first * sine], axis=-1
    )


def prepare_inputs(projected, gain, start_offset, head_groups):
    shaped = projected.reshape(projected.shape[0], head_groups, -1)
    return rotary(rms_scale(shaped, gain), start_offset)


def piece_places(which, group_rows):
    quarter = group_rows // 2
    local = jnp.arange(group_rows, dtype=jnp.int32)
    chosen = jnp.where(local < quarter, which, 3 - which)
    return chosen * quarter + local % quarter


def contract_rows(left, right):
    return lax.dot_general(
        left, right, (((0,), (0,)), ((), ())), preferred_element_type=jnp.float32
    )


def contract_last(left, right):
    return lax.dot_general(
        left, right, (((1,), (1,)), ((), ())), preferred_element_type=jnp.float32
    )


def split_columns(full, widths):
    parts = []
    at = 0
    for width in widths:
        parts.append(full[:, at : at + width])
        at += width
    return parts


def halving_scatter(grads):
    widths = [g.shape[1] for g in grads]
    packed = jnp.concatenate(grads, axis=1)
    count = lax.axis_size("fsdp")
    me = lax.axis_index("fsdp")
    bits = count.bit_length() - 1
    rows_f = packed.shape[0] // count
    order = [int(format(b, f"0{bits}b")[::-1], 2) for b in range(count)]
    buf = jnp.concatenate([packed[b * rows_f : (b + 1) * rows_f] for b in order], axis=0)
    for bit in range(bits):
        half = buf.shape[0] // 2
        mine = (me >> bit) & 1
        keep = lax.dynamic_slice_in_dim(buf, mine * half, half, 0)
        send = lax.dynamic_slice_in_dim(buf, (1 - mine) * half, half, 0)
        got = lax.ppermute(
            send.astype(jnp.bfloat16), "fsdp", [(i, i ^ (1 << bit)) for i in range(count)]
        )
        buf = keep + got.astype(jnp.float32)
    return split_columns(buf, widths)


def fsdp_gather(values):
    count = lax.axis_size("fsdp")
    me = lax.axis_index("fsdp")
    distance = 1
    while distance < count:
        got = lax.ppermute(values, "fsdp", [(i, i ^ distance) for i in range(count)])
        low = (me & distance) == 0
        values = jnp.concatenate(
            [jnp.where(low, values, got), jnp.where(low, got, values)]
        )
        distance *= 2
    return values


def all_sum(values):
    for axis in ("tensor", "fsdp"):
        distance = 1
        while distance < lax.axis_size(axis):
            values = values + lax.ppermute(
                values, axis, [(i, i ^ distance) for i in range(lax.axis_size(axis))]
            )
            distance *= 2
    return values


def exchange(values, distance):
    count = lax.axis_size("tensor")
    return lax.ppermute(values, "tensor", [(i, i ^ distance) for i in range(count)])


def token_gather(values):
    rows = values.shape[0]
    me = lax.axis_index("tensor")
    across = exchange(values, 2)
    pair = jnp.stack([values, across])
    beside = exchange(pair, 1)
    full = jnp.zeros((4 * rows,) + values.shape[1:], values.dtype)
    for part, place in ((values, me), (across, me ^ 2), (beside[0], me ^ 1), (beside[1], me ^ 3)):
        full = lax.dynamic_update_slice_in_dim(full, part, place * rows, 0)
    return full


def token_sum(term, rows):
    partial = term(jnp.int32(0), rows * lax.axis_size("tensor"))
    me = lax.axis_index("tensor")

    def block(place):
        return lax.dynamic_slice_in_dim(partial, place * rows, rows, 0)

    sent = jnp.stack([block(me ^ 1), block(me ^ 3)]).astype(jnp.bfloat16)
    got = exchange(sent, 1).astype(jnp.float32)
    mine = block(me) + got[0]
    other = (block(me ^ 2) + got[1]).astype(jnp.bfloat16)
    return mine + exchange(other, 2).astype(jnp.float32)


def shards(
    hidden,
    out_grad,
    lengths,
    q_weight,
    key_matrix,
    value_matrix,
    o_weight,
    gate_weight,
    up_weight,
    down_weight,
    input_gain,
    q_gain,
    k_gain,
    post_gain,
):
    split = lax.axis_size("tensor")
    rows = hidden.shape[0]
    group_rows = rows * split
    q_heads = q_weight.shape[1] // HEAD_SIZE
    kv_heads = key_matrix.shape[1] // HEAD_SIZE
    share = q_heads // kv_heads
    scale = HEAD_SIZE ** (-0.5)
    member = lax.axis_index("fsdp")
    slot = member // PIECES
    piece = member % PIECES
    lengths_row = lax.dynamic_index_in_dim(lengths, slot, 0, keepdims=False)
    ends = jnp.cumsum(lengths_row)
    group_place = piece_places(piece, group_rows)
    passed = group_place[:, None] >= ends[None, :]
    group_start = jnp.sum(jnp.where(passed, lengths_row[None, :], 0), axis=1)
    group_offset = group_place - group_start
    local_valid = lax.dynamic_slice_in_dim(
        group_place < ends[-1], lax.axis_index("tensor") * rows, rows, 0
    )
    fs = lax.axis_size("fsdp")
    gain_sizes = (input_gain.shape[0], q_gain.shape[0], k_gain.shape[0], post_gain.shape[0])
    gains_all = fsdp_gather(
        jnp.concatenate([input_gain, q_gain, k_gain, post_gain]).astype(jnp.bfloat16)
    ).reshape(fs, sum(gain_sizes))
    gain_in, gain_query, gain_keys, gain_post = [
        part.reshape(-1) for part in split_columns(gains_all, gain_sizes)
    ]
    attn_full = lax.all_gather(
        jnp.concatenate(
            [
                q_weight.astype(jnp.bfloat16),
                key_matrix.astype(jnp.bfloat16),
                value_matrix.astype(jnp.bfloat16),
            ],
            axis=1,
        ),
        "fsdp",
        axis=0,
        tiled=True,
    )
    widths = (q_weight.shape[1], key_matrix.shape[1], value_matrix.shape[1])
    w_query, w_key, w_value = split_columns(attn_full, widths)
    x_float = hidden.astype(jnp.float32)
    gain_first = gain_in.astype(jnp.float32)
    first_all = token_gather(rms_scale(x_float, gain_first).astype(jnp.bfloat16))
    cotangent = out_grad.astype(jnp.float32) * local_valid[:, None].astype(jnp.float32)
    mlp_grad_all = token_gather(cotangent.astype(jnp.bfloat16))
    first_all, mlp_grad_all = lax.optimization_barrier((first_all, mlp_grad_all))
    query_projected = jnp.dot(first_all, w_query, preferred_element_type=jnp.float32)
    key_projected = jnp.dot(first_all, w_key, preferred_element_type=jnp.float32)
    value_rows = (
        jnp.dot(first_all, w_value, preferred_element_type=jnp.float32)
        .astype(jnp.bfloat16)
        .reshape(group_rows, kv_heads, HEAD_SIZE)
    )
    gain_q = gain_query.astype(jnp.float32)
    gain_k = gain_keys.astype(jnp.float32)
    query_rope = (
        prepare_inputs(query_projected, gain_q, group_offset, q_heads)
        .astype(jnp.bfloat16)
        .reshape(group_rows, kv_heads, share, HEAD_SIZE)
    )
    key_rope = prepare_inputs(key_projected, gain_k, group_offset, kv_heads).astype(jnp.bfloat16)
    quarter = group_rows // 2
    query_start = jnp.broadcast_to(group_start[:, None], (group_rows, 128))
    query_t = jnp.transpose(query_rope, (1, 2, 0, 3))
    own_keys = jnp.transpose(key_rope, (1, 0, 2))
    own_values = jnp.transpose(value_rows, (1, 0, 2))
    moved = swapped(jnp.stack([own_keys, own_values]), "fsdp", 0)
    sums = jnp.zeros(query_t.shape, jnp.float32)
    totals = jnp.zeros(query_t.shape[:3] + (128,), jnp.float32)
    sums, totals = attention_forward(
        query_t, query_start, own_keys, own_values, sums, totals, piece, quarter, 0
    )
    sums, totals_t = attention_forward(
        query_t, query_start, moved[0], moved[1], sums, totals, piece, quarter, 1
    )
    heads_t = sums / totals_t[..., :1]
    heads_out = jnp.transpose(heads_t, (2, 0, 1, 3))
    row_totals = jnp.transpose(totals_t[..., 0], (2, 0, 1))
    out_rows = heads_out.reshape(group_rows, q_heads * HEAD_SIZE).astype(jnp.bfloat16)

    mlp_full = lax.all_gather(
        jnp.concatenate(
            [
                gate_weight.astype(jnp.bfloat16),
                up_weight.astype(jnp.bfloat16),
                jnp.transpose(down_weight).astype(jnp.bfloat16),
                jnp.transpose(o_weight).astype(jnp.bfloat16),
            ],
            axis=1,
        ),
        "fsdp",
        axis=0,
        tiled=True,
    )
    w_gate, w_up, w_down_t, w_out = split_columns(
        mlp_full, (gate_weight.shape[1], up_weight.shape[1], down_weight.shape[0], o_weight.shape[0])
    )
    out_partial = contract_last(out_rows, w_out)
    late_grad_all, out_partial = lax.optimization_barrier((mlp_grad_all, out_partial))
    grad_act = jnp.dot(late_grad_all, w_down_t, preferred_element_type=jnp.float32)
    after_attn = x_float + token_sum(lambda start, count: out_partial, rows)
    grad_act, after_attn = lax.optimization_barrier((grad_act, after_attn))
    gain_second = gain_post.astype(jnp.float32)
    second_all = token_gather(rms_scale(after_attn, gain_second).astype(jnp.bfloat16))
    gate_out = jnp.dot(second_all, w_gate, preferred_element_type=jnp.float32)
    up_out = jnp.dot(second_all, w_up, preferred_element_type=jnp.float32)
    activated = (jax.nn.silu(gate_out) * up_out).astype(jnp.bfloat16)

    unused, pull_gate = jax.vjp(
        lambda gate_in, up_in: jax.nn.silu(gate_in) * up_in, gate_out, up_out
    )
    grad_gate, grad_up = pull_gate(grad_act)
    grad_gate = grad_gate.astype(jnp.bfloat16)
    grad_up = grad_up.astype(jnp.bfloat16)
    second_partial = contract_last(grad_gate, w_gate) + contract_last(grad_up, w_up)
    grad_inputs, second_partial = lax.optimization_barrier(
        ((mlp_grad_all, activated, second_all, grad_gate, grad_up), second_partial)
    )
    late_c, late_act, late_second, late_gate, late_up = grad_inputs
    down_grad_t = contract_rows(late_c, late_act)
    gate_grad = contract_rows(late_second, late_gate)
    up_grad = contract_rows(late_second, late_up)
    second_back = token_sum(lambda start, count: second_partial, rows)
    unused, pull_second = jax.vjp(rms_scale, after_attn, gain_second)
    norm_second_grad, post_gain_part = pull_second(second_back)
    residual_grad = cotangent + norm_second_grad
    weight_grads, residual_grad = lax.optimization_barrier(
        ((gate_grad, up_grad, down_grad_t), residual_grad)
    )
    gate_grad, up_grad, down_grad_t = weight_grads
    attn_grad_all = token_gather(residual_grad.astype(jnp.bfloat16))
    activated_late, attn_grad_all = lax.optimization_barrier((activated, attn_grad_all))
    down_rows = token_sum(lambda start, count: contract_last(activated_late, w_down_t), rows)
    out_weight_grad_t = contract_rows(attn_grad_all, out_rows)
    mlp_packed = jnp.concatenate(
        [g.astype(jnp.bfloat16) for g in (gate_grad, up_grad, down_grad_t, out_weight_grad_t)],
        axis=1,
    )
    head_grad = jnp.dot(attn_grad_all, w_out, preferred_element_type=jnp.float32).astype(
        jnp.bfloat16
    )
    head_float = head_grad.astype(jnp.float32).reshape(group_rows, kv_heads, share, HEAD_SIZE)
    scaled_grad = (head_float / row_totals[..., None]).astype(jnp.bfloat16)
    delta = jnp.sum(head_float * heads_out, axis=-1) / row_totals

    grad_t = jnp.transpose(scaled_grad, (1, 2, 0, 3))
    delta_t = jnp.broadcast_to(
        jnp.transpose(delta, (1, 2, 0))[..., None], (kv_heads, share, group_rows, 128)
    )
    mlp_packed, grad_t, delta_t = lax.optimization_barrier((mlp_packed, grad_t, delta_t))
    mlp_shards = split_columns(
        lax.psum_scatter(mlp_packed, "fsdp", scatter_dimension=0, tiled=True),
        [g.shape[1] for g in (gate_grad, up_grad, down_grad_t, out_weight_grad_t)],
    )
    mlp_shards = [part.astype(jnp.float32) for part in mlp_shards]
    dq_raw, dk_far, dv_far = attention_backward(
        query_t, grad_t, delta_t, query_start, moved[0], moved[1],
        jnp.zeros(query_t.shape, jnp.float32), piece, quarter, 1,
    )
    unseen = (piece == 1) & (jnp.arange(group_rows) >= quarter)
    far_grads = jnp.where(unseen[None, None, :, None], 0.0, jnp.stack([dk_far, dv_far]))
    returned = swapped(far_grads.astype(jnp.bfloat16), "fsdp", 0)
    down_rows, dq_raw = lax.optimization_barrier((down_rows, dq_raw))
    output = (after_attn + down_rows).astype(jnp.bfloat16)
    dq_raw, dk_own, dv_own = attention_backward(
        query_t, grad_t, delta_t, query_start, own_keys, own_values,
        dq_raw, piece, quarter, 0,
    )
    mlp_shards, dq_raw = lax.optimization_barrier((mlp_shards, dq_raw))
    grad_keys_total = jnp.transpose(dk_own + returned[0].astype(jnp.float32), (1, 0, 2))
    grad_values_total = jnp.transpose(dv_own + returned[1].astype(jnp.float32), (1, 0, 2))
    query_grads = jnp.transpose(dq_raw, (2, 0, 1, 3)) * scale
    query_grads = query_grads.reshape(group_rows, q_heads, HEAD_SIZE)
    unused, pull_query = jax.vjp(
        lambda projected, gain: prepare_inputs(projected, gain, group_offset, q_heads),
        query_projected,
        gain_q,
    )
    query_proj_grad, q_gain_part = pull_query(query_grads)
    unused, pull_key = jax.vjp(
        lambda projected, gain: prepare_inputs(projected, gain, group_offset, kv_heads),
        key_projected,
        gain_k,
    )
    key_proj_grad, k_gain_part = pull_key(grad_keys_total)
    query_low = query_proj_grad.astype(jnp.bfloat16)
    key_low = key_proj_grad.astype(jnp.bfloat16)
    value_low = grad_values_total.reshape(group_rows, kv_heads * HEAD_SIZE).astype(jnp.bfloat16)
    query_weight_grad = contract_rows(first_all, query_low)
    key_weight_grad = contract_rows(first_all, key_low)
    value_weight_grad = contract_rows(first_all, value_low)

    def first_term(start, count):
        return (
            contract_last(query_low, w_query)
            + contract_last(key_low, w_key)
            + contract_last(value_low, w_value)
        )

    first_back = token_sum(first_term, rows)
    unused, pull_first = jax.vjp(rms_scale, x_float, gain_first)
    norm_first_grad, input_gain_part = pull_first(first_back)
    input_grad = (residual_grad + norm_first_grad).astype(jnp.bfloat16)
    (query_shard,) = halving_scatter((query_weight_grad,))
    key_shard, value_shard = halving_scatter((key_weight_grad, value_weight_grad))
    gain_totals = all_sum(
        jnp.concatenate([input_gain_part, q_gain_part, k_gain_part, post_gain_part])
    )
    member_f = lax.axis_index("fsdp")
    sizes = (input_gain.shape[0], q_gain.shape[0], k_gain.shape[0], post_gain.shape[0])
    gain_shards = []
    at = 0
    for own in sizes:
        whole = own * fs
        gain_shards.append(lax.dynamic_slice_in_dim(gain_totals, at + member_f * own, own, 0))
        at += whole
    input_gain_shard, q_gain_shard, k_gain_shard, post_gain_shard = gain_shards
    gate_shard, up_shard, down_shard_t, out_shard_t = mlp_shards
    return (
        output,
        input_grad,
        query_shard,
        key_shard,
        value_shard,
        jnp.transpose(out_shard_t),
        gate_shard,
        up_shard,
        jnp.transpose(down_shard_t),
        input_gain_shard,
        q_gain_shard,
        k_gain_shard,
        post_gain_shard,
    )


def solution(mesh):
    return layer_program(mesh)


def layer_program(mesh):
    placed = (
        P(("fsdp", "tensor"), None),
        P(("fsdp", "tensor"), None),
        P(),
        P("fsdp", "tensor"),
        P("fsdp", "tensor"),
        P("fsdp", "tensor"),
        P("tensor", "fsdp"),
        P("fsdp", "tensor"),
        P("fsdp", "tensor"),
        P("tensor", "fsdp"),
        P("fsdp"),
        P("fsdp"),
        P("fsdp"),
        P("fsdp"),
    )
    return jax.shard_map(
        shards,
        mesh=mesh,
        in_specs=placed,
        out_specs=(
            P(("fsdp", "tensor"), None),
            P(("fsdp", "tensor"), None),
            P("fsdp", "tensor"),
            P("fsdp", "tensor"),
            P("fsdp", "tensor"),
            P("tensor", "fsdp"),
            P("fsdp", "tensor"),
            P("fsdp", "tensor"),
            P("tensor", "fsdp"),
            P("fsdp"),
            P("fsdp"),
            P("fsdp"),
            P("fsdp"),
        ),
        check_vma=False,
    )
```

```python
import functools

import numpy as np
import jax
import jax.numpy as jnp
from jax import lax
from jax.experimental import pallas as pl
from jax.experimental.pallas import tpu as pltpu
from jax.sharding import PartitionSpec as P


HEAD_SIZE = 128
TRANS_B = (((1,), (1,)), ((), ()))
TRANS_A = (((0,), (0,)), ((), ()))


def _own_place(p, quarter, r):
    return (p * quarter + r) if r < quarter else ((3 - p) * quarter + r - quarter)


def _far_place(p, quarter, r):
    return ((1 - p) * quarter + r) if r < quarter else ((2 + p) * quarter + r - quarter)


def _pair_tables(p, quarter, block, by_key, source):
    rows = 2 * quarter
    count = rows // block
    kmap = {}
    for src, fn in ((0, _own_place), (1, _far_place)):
        for j in range(count):
            kmap[fn(p, quarter, j * block) // block] = (src, j)
    pairs = []
    for j in range(count):
        qpb = _own_place(p, quarter, j * block) // block
        for kpb in range(qpb + 1):
            if kmap[kpb][0] == source:
                pairs.append((j, qpb, kpb))
    if by_key:
        pairs.sort(key=lambda t: (t[2], t[0]))
    group = [t[2] if by_key else t[0] for t in pairs]
    size = len(pairs)
    first = [1 if n == 0 or group[n - 1] != group[n] else 0 for n in range(size)]
    last = [1 if n == size - 1 or group[n + 1] != group[n] else 0 for n in range(size)]
    return np.array(
        [
            [t[0] for t in pairs],
            [t[1] for t in pairs],
            [t[2] for t in pairs],
            [kmap[t[2]][0] for t in pairs],
            [kmap[t[2]][1] for t in pairs],
            first,
            last,
        ],
        np.int32,
    )


def pair_tables(piece, quarter, block, by_key, source):
    t0 = _pair_tables(0, quarter, block, by_key, source)
    t1 = _pair_tables(1, quarter, block, by_key, source)
    assert t0.shape == t1.shape
    return jnp.where(piece == 0, jnp.asarray(t0), jnp.asarray(t1))


def _mask(qpb, kpb, qs, block):
    qp = qpb * block + lax.broadcasted_iota(jnp.int32, (block, block), 0)
    kp = kpb * block + lax.broadcasted_iota(jnp.int32, (block, block), 1)
    start = jnp.tile(qs, (1, block // 128))
    return (kp >= start) & (kp <= qp)


def _fwd_kernel(tab_ref, q_ref, qs_ref, k_ref, v_ref, a_in_ref, l_in_ref, a_ref, l_ref, acc_ref, sum_ref, *, scale, block):
    n = pl.program_id(1)
    share = q_ref.shape[1]

    @pl.when(tab_ref[5, n] == 1)
    def _():
        acc_ref[...] = a_in_ref[0].reshape(share * block, HEAD_SIZE)
        sum_ref[...] = l_in_ref[0][:, :, :1]

    q = q_ref[0].reshape(share * block, HEAD_SIZE)
    k = k_ref[0]
    v = v_ref[0]
    s = lax.dot_general(q, k, TRANS_B, preferred_element_type=jnp.float32) * scale
    allowed = _mask(tab_ref[1, n], tab_ref[2, n], qs_ref[...], block)
    e = jnp.where(allowed[None], jnp.exp(s.reshape(share, block, block)), 0.0)
    sum_ref[...] += jnp.sum(e, axis=-1, keepdims=True)
    acc_ref[...] += jnp.dot(
        e.reshape(share * block, block).astype(jnp.bfloat16), v, preferred_element_type=jnp.float32
    )

    @pl.when(tab_ref[6, n] == 1)
    def _():
        a_ref[0] = acc_ref[...].reshape(share, block, HEAD_SIZE)
        l_ref[0] = jnp.broadcast_to(sum_ref[...], (share, block, 128))


def attention_forward(q, qs, keys, values, a_in, l_in, piece, quarter, source, block=512):
    kvh, share, _, _ = q.shape
    tab = pair_tables(piece, quarter, block, False, source)
    npairs = tab.shape[1]
    scale = HEAD_SIZE ** (-0.5)
    row_spec = pl.BlockSpec((1, share, block, HEAD_SIZE), lambda h, n, t: (h, 0, t[0, n], 0))
    lane_spec = pl.BlockSpec((1, share, block, 128), lambda h, n, t: (h, 0, t[0, n], 0))
    key_spec = pl.BlockSpec((1, block, HEAD_SIZE), lambda h, n, t: (h, t[4, n], 0))
    grid_spec = pltpu.PrefetchScalarGridSpec(
        num_scalar_prefetch=1,
        grid=(kvh, npairs),
        in_specs=[
            row_spec,
            pl.BlockSpec((block, 128), lambda h, n, t: (t[0, n], 0)),
            key_spec,
            key_spec,
            row_spec,
            lane_spec,
        ],
        out_specs=[row_spec, lane_spec],
        scratch_shapes=[
            pltpu.VMEM((share * block, HEAD_SIZE), jnp.float32),
            pltpu.VMEM((share, block, 1), jnp.float32),
        ],
    )
    flops = 4 * kvh * npairs * share * block * block * HEAD_SIZE
    return pl.pallas_call(
        functools.partial(_fwd_kernel, scale=scale, block=block),
        grid_spec=grid_spec,
        out_shape=[
            jax.ShapeDtypeStruct(a_in.shape, jnp.float32),
            jax.ShapeDtypeStruct(l_in.shape, jnp.float32),
        ],
        input_output_aliases={5: 0, 6: 1},
        compiler_params=pltpu.CompilerParams(
            dimension_semantics=("arbitrary", "arbitrary"), vmem_limit_bytes=48 * 1024 * 1024
        ),
        cost_estimate=pl.CostEstimate(
            flops=flops,
            transcendentals=kvh * npairs * share * block * block,
            bytes_accessed=kvh * npairs * (8 * block * HEAD_SIZE * 2),
        ),
        name="attn_fwd",
    )(tab, q, qs, keys, values, a_in, l_in)


def _bwd_kernel(tab_ref, q_ref, h_ref, dl_ref, qs_ref, k_ref, v_ref, dq_in_ref, dq_ref, dk_ref, dv_ref, dk_acc, dv_acc, *, scale, block):
    n = pl.program_id(1)
    share = q_ref.shape[1]

    @pl.when(n == 0)
    def _():
        dq_ref[...] = dq_in_ref[...]

    @pl.when(tab_ref[5, n] == 1)
    def _():
        dk_acc[...] = jnp.zeros(dk_acc.shape, dk_acc.dtype)
        dv_acc[...] = jnp.zeros(dv_acc.shape, dv_acc.dtype)

    q = q_ref[0].reshape(share * block, HEAD_SIZE)
    hh = h_ref[0].reshape(share * block, HEAD_SIZE)
    k = k_ref[0]
    v = v_ref[0]
    s = lax.dot_general(q, k, TRANS_B, preferred_element_type=jnp.float32) * scale
    allowed = _mask(tab_ref[1, n], tab_ref[2, n], qs_ref[...], block)
    e = jnp.where(allowed[None], jnp.exp(s.reshape(share, block, block)), 0.0)
    dp = lax.dot_general(hh, v, TRANS_B, preferred_element_type=jnp.float32).reshape(share, block, block)
    delta = jnp.tile(dl_ref[0], (1, 1, block // 128))
    ds = (e * (dp - delta)).reshape(share * block, block).astype(jnp.bfloat16)
    rows = pl.ds(pl.multiple_of(tab_ref[0, n] * block, block), block)
    dq_ref[0, :, rows, :] += jnp.dot(ds, k, preferred_element_type=jnp.float32).reshape(share, block, HEAD_SIZE)
    dk_acc[...] += lax.dot_general(ds, q, TRANS_A, preferred_element_type=jnp.float32)
    dv_acc[...] += lax.dot_general(
        e.reshape(share * block, block).astype(jnp.bfloat16), hh, TRANS_A, preferred_element_type=jnp.float32
    )

    @pl.when(tab_ref[6, n] == 1)
    def _():
        dk_ref[0] = dk_acc[...] * scale
        dv_ref[0] = dv_acc[...]


def attention_backward(q, hgrad, delta, qs, keys, values, dq_in, piece, quarter, source, block=512):
    kvh, share, rows, _ = q.shape
    tab = pair_tables(piece, quarter, block, True, source)
    npairs = tab.shape[1]
    scale = HEAD_SIZE ** (-0.5)
    row_spec = pl.BlockSpec((1, share, block, HEAD_SIZE), lambda h, n, t: (h, 0, t[0, n], 0))
    key_spec = pl.BlockSpec((1, block, HEAD_SIZE), lambda h, n, t: (h, t[4, n], 0))
    full_spec = pl.BlockSpec((1, share, rows, HEAD_SIZE), lambda h, n, t: (h, 0, 0, 0))
    grid_spec = pltpu.PrefetchScalarGridSpec(
        num_scalar_prefetch=1,
        grid=(kvh, npairs),
        in_specs=[
            row_spec,
            row_spec,
            pl.BlockSpec((1, share, block, 128), lambda h, n, t: (h, 0, t[0, n], 0)),
            pl.BlockSpec((block, 128), lambda h, n, t: (t[0, n], 0)),
            key_spec,
            key_spec,
            full_spec,
        ],
        out_specs=[full_spec, key_spec, key_spec],
        scratch_shapes=[
            pltpu.VMEM((block, HEAD_SIZE), jnp.float32),
            pltpu.VMEM((block, HEAD_SIZE), jnp.float32),
        ],
    )
    flops = 10 * kvh * npairs * share * block * block * HEAD_SIZE
    return pl.pallas_call(
        functools.partial(_bwd_kernel, scale=scale, block=block),
        grid_spec=grid_spec,
        out_shape=[
            jax.ShapeDtypeStruct(dq_in.shape, jnp.float32),
            jax.ShapeDtypeStruct(keys.shape, jnp.float32),
            jax.ShapeDtypeStruct(values.shape, jnp.float32),
        ],
        input_output_aliases={7: 0},
        compiler_params=pltpu.CompilerParams(
            dimension_semantics=("arbitrary", "arbitrary"), vmem_limit_bytes=56 * 1024 * 1024
        ),
        cost_estimate=pl.CostEstimate(
            flops=flops,
            transcendentals=kvh * npairs * share * block * block,
            bytes_accessed=kvh * npairs * (10 * block * HEAD_SIZE * 2),
        ),
        name="attn_bwd",
    )(tab, q, hgrad, delta, qs, keys, values, dq_in)


PIECES = 2


EPSILON = 1e-06
THETA = 1000000.0


def swapped(shard, axis, distance):
    return lax.ppermute(shard, axis, [(i, i ^ 1 << distance) for i in range(lax.axis_size(axis))])


def rms_scale(values, gain):
    inverse = lax.rsqrt(jnp.mean(values * values, axis=-1, keepdims=True) + EPSILON)
    return values * inverse * gain


def rotary(values, start_offset):
    half = values.shape[-1] // 2
    frequency = THETA ** (-(jnp.arange(half, dtype=jnp.float32) * 2.0 / values.shape[-1]))
    angle = start_offset.astype(jnp.float32)[:, None] * frequency[None, :]
    cosine = jnp.cos(angle)[:, None, :]
    sine = jnp.sin(angle)[:, None, :]
    first = values[..., :half]
    second = values[..., half:]
    return jnp.concatenate(
        [first * cosine - second * sine, second * cosine + first * sine], axis=-1
    )


def prepare_inputs(projected, gain, start_offset, head_groups):
    shaped = projected.reshape(projected.shape[0], head_groups, -1)
    return rotary(rms_scale(shaped, gain), start_offset)


def piece_places(which, group_rows):
    quarter = group_rows // 2
    local = jnp.arange(group_rows, dtype=jnp.int32)
    chosen = jnp.where(local < quarter, which, 3 - which)
    return chosen * quarter + local % quarter


def contract_rows(left, right):
    return lax.dot_general(
        left, right, (((0,), (0,)), ((), ())), preferred_element_type=jnp.float32
    )


def contract_last(left, right):
    return lax.dot_general(
        left, right, (((1,), (1,)), ((), ())), preferred_element_type=jnp.float32
    )


def split_columns(full, widths):
    parts = []
    at = 0
    for width in widths:
        parts.append(full[:, at : at + width])
        at += width
    return parts


def halving_scatter(grads):
    widths = [g.shape[1] for g in grads]
    packed = jnp.concatenate(grads, axis=1)
    count = lax.axis_size("fsdp")
    me = lax.axis_index("fsdp")
    bits = count.bit_length() - 1
    rows_f = packed.shape[0] // count
    order = [int(format(b, f"0{bits}b")[::-1], 2) for b in range(count)]
    buf = jnp.concatenate([packed[b * rows_f : (b + 1) * rows_f] for b in order], axis=0)
    for bit in range(bits):
        half = buf.shape[0] // 2
        mine = (me >> bit) & 1
        keep = lax.dynamic_slice_in_dim(buf, mine * half, half, 0)
        send = lax.dynamic_slice_in_dim(buf, (1 - mine) * half, half, 0)
        got = lax.ppermute(
            send.astype(jnp.bfloat16), "fsdp", [(i, i ^ (1 << bit)) for i in range(count)]
        )
        buf = keep + got.astype(jnp.float32)
    return split_columns(buf, widths)


def fsdp_gather(values):
    count = lax.axis_size("fsdp")
    me = lax.axis_index("fsdp")
    distance = 1
    while distance < count:
        got = lax.ppermute(values, "fsdp", [(i, i ^ distance) for i in range(count)])
        low = (me & distance) == 0
        values = jnp.concatenate(
            [jnp.where(low, values, got), jnp.where(low, got, values)]
        )
        distance *= 2
    return values


def all_sum(values):
    for axis in ("tensor", "fsdp"):
        distance = 1
        while distance < lax.axis_size(axis):
            values = values + lax.ppermute(
                values, axis, [(i, i ^ distance) for i in range(lax.axis_size(axis))]
            )
            distance *= 2
    return values


def exchange(values, distance):
    count = lax.axis_size("tensor")
    return lax.ppermute(values, "tensor", [(i, i ^ distance) for i in range(count)])


def token_gather(values):
    rows = values.shape[0]
    me = lax.axis_index("tensor")
    across = exchange(values, 2)
    pair = jnp.stack([values, across])
    beside = exchange(pair, 1)
    full = jnp.zeros((4 * rows,) + values.shape[1:], values.dtype)
    for part, place in ((values, me), (across, me ^ 2), (beside[0], me ^ 1), (beside[1], me ^ 3)):
        full = lax.dynamic_update_slice_in_dim(full, part, place * rows, 0)
    return full


def token_sum(term, rows):
    partial = term(jnp.int32(0), rows * lax.axis_size("tensor"))
    me = lax.axis_index("tensor")

    def block(place):
        return lax.dynamic_slice_in_dim(partial, place * rows, rows, 0)

    sent = jnp.stack([block(me ^ 1), block(me ^ 3)]).astype(jnp.bfloat16)
    got = exchange(sent, 1).astype(jnp.float32)
    mine = block(me) + got[0]
    other = (block(me ^ 2) + got[1]).astype(jnp.bfloat16)
    return mine + exchange(other, 2).astype(jnp.float32)


def shards(
    hidden,
    out_grad,
    lengths,
    q_weight,
    key_matrix,
    value_matrix,
    o_weight,
    gate_weight,
    up_weight,
    down_weight,
    input_gain,
    q_gain,
    k_gain,
    post_gain,
):
    split = lax.axis_size("tensor")
    rows = hidden.shape[0]
    group_rows = rows * split
    q_heads = q_weight.shape[1] // HEAD_SIZE
    kv_heads = key_matrix.shape[1] // HEAD_SIZE
    share = q_heads // kv_heads
    scale = HEAD_SIZE ** (-0.5)
    member = lax.axis_index("fsdp")
    slot = member // PIECES
    piece = member % PIECES
    lengths_row = lax.dynamic_index_in_dim(lengths, slot, 0, keepdims=False)
    ends = jnp.cumsum(lengths_row)
    group_place = piece_places(piece, group_rows)
    passed = group_place[:, None] >= ends[None, :]
    group_start = jnp.sum(jnp.where(passed, lengths_row[None, :], 0), axis=1)
    group_offset = group_place - group_start
    local_valid = lax.dynamic_slice_in_dim(
        group_place < ends[-1], lax.axis_index("tensor") * rows, rows, 0
    )
    fs = lax.axis_size("fsdp")
    gain_sizes = (input_gain.shape[0], q_gain.shape[0], k_gain.shape[0], post_gain.shape[0])
    gains_all = fsdp_gather(
        jnp.concatenate([input_gain, q_gain, k_gain, post_gain]).astype(jnp.bfloat16)
    ).reshape(fs, sum(gain_sizes))
    gain_in, gain_query, gain_keys, gain_post = [
        part.reshape(-1) for part in split_columns(gains_all, gain_sizes)
    ]
    kv_full = lax.all_gather(
        jnp.concatenate(
            [key_matrix.astype(jnp.bfloat16), value_matrix.astype(jnp.bfloat16)], axis=1
        ),
        "fsdp",
        axis=0,
        tiled=True,
    )
    w_key, w_value = split_columns(kv_full, (key_matrix.shape[1], value_matrix.shape[1]))
    qo_full = lax.all_gather(
        jnp.concatenate(
            [q_weight.astype(jnp.bfloat16), jnp.transpose(o_weight).astype(jnp.bfloat16)],
            axis=1,
        ),
        "fsdp",
        axis=0,
        tiled=True,
    )
    w_query, w_out = split_columns(qo_full, (q_weight.shape[1], o_weight.shape[0]))
    x_float = hidden.astype(jnp.float32)
    gain_first = gain_in.astype(jnp.float32)
    first_all = token_gather(rms_scale(x_float, gain_first).astype(jnp.bfloat16))
    cotangent = out_grad.astype(jnp.float32) * local_valid[:, None].astype(jnp.float32)
    mlp_grad_all = token_gather(cotangent.astype(jnp.bfloat16))
    first_all, mlp_grad_all = lax.optimization_barrier((first_all, mlp_grad_all))
    query_projected = jnp.dot(first_all, w_query, preferred_element_type=jnp.float32)
    key_projected = jnp.dot(first_all, w_key, preferred_element_type=jnp.float32)
    value_rows = (
        jnp.dot(first_all, w_value, preferred_element_type=jnp.float32)
        .astype(jnp.bfloat16)
        .reshape(group_rows, kv_heads, HEAD_SIZE)
    )
    gain_q = gain_query.astype(jnp.float32)
    gain_k = gain_keys.astype(jnp.float32)
    query_rope = (
        prepare_inputs(query_projected, gain_q, group_offset, q_heads)
        .astype(jnp.bfloat16)
        .reshape(group_rows, kv_heads, share, HEAD_SIZE)
    )
    key_rope = prepare_inputs(key_projected, gain_k, group_offset, kv_heads).astype(jnp.bfloat16)
    quarter = group_rows // 2
    query_start = jnp.broadcast_to(group_start[:, None], (group_rows, 128))
    query_t = jnp.transpose(query_rope, (1, 2, 0, 3))
    own_keys = jnp.transpose(key_rope, (1, 0, 2))
    own_values = jnp.transpose(value_rows, (1, 0, 2))
    moved = swapped(jnp.stack([own_keys, own_values]), "fsdp", 0)
    sums = jnp.zeros(query_t.shape, jnp.float32)
    totals = jnp.zeros(query_t.shape[:3] + (128,), jnp.float32)
    sums, totals = attention_forward(
        query_t, query_start, own_keys, own_values, sums, totals, piece, quarter, 0
    )
    sums, totals_t = attention_forward(
        query_t, query_start, moved[0], moved[1], sums, totals, piece, quarter, 1
    )
    heads_t = sums / totals_t[..., :1]
    heads_out = jnp.transpose(heads_t, (2, 0, 1, 3))
    row_totals = jnp.transpose(totals_t[..., 0], (2, 0, 1))
    out_rows = heads_out.reshape(group_rows, q_heads * HEAD_SIZE).astype(jnp.bfloat16)

    mlp_full = lax.all_gather(
        jnp.concatenate(
            [
                gate_weight.astype(jnp.bfloat16),
                up_weight.astype(jnp.bfloat16),
                jnp.transpose(down_weight).astype(jnp.bfloat16),
            ],
            axis=1,
        ),
        "fsdp",
        axis=0,
        tiled=True,
    )
    w_gate, w_up, w_down_t = split_columns(
        mlp_full, (gate_weight.shape[1], up_weight.shape[1], down_weight.shape[0])
    )
    out_partial = contract_last(out_rows, w_out)
    late_grad_all, out_partial = lax.optimization_barrier((mlp_grad_all, out_partial))
    grad_act = jnp.dot(late_grad_all, w_down_t, preferred_element_type=jnp.float32)
    after_attn = x_float + token_sum(lambda start, count: out_partial, rows)
    grad_act, after_attn = lax.optimization_barrier((grad_act, after_attn))
    gain_second = gain_post.astype(jnp.float32)
    second_all = token_gather(rms_scale(after_attn, gain_second).astype(jnp.bfloat16))
    gate_out = jnp.dot(second_all, w_gate, preferred_element_type=jnp.float32)
    up_out = jnp.dot(second_all, w_up, preferred_element_type=jnp.float32)
    activated = (jax.nn.silu(gate_out) * up_out).astype(jnp.bfloat16)

    unused, pull_gate = jax.vjp(
        lambda gate_in, up_in: jax.nn.silu(gate_in) * up_in, gate_out, up_out
    )
    grad_gate, grad_up = pull_gate(grad_act)
    grad_gate = grad_gate.astype(jnp.bfloat16)
    grad_up = grad_up.astype(jnp.bfloat16)
    second_partial = contract_last(grad_gate, w_gate) + contract_last(grad_up, w_up)
    grad_inputs, second_partial = lax.optimization_barrier(
        ((mlp_grad_all, activated, second_all, grad_gate, grad_up), second_partial)
    )
    late_c, late_act, late_second, late_gate, late_up = grad_inputs
    down_grad_t = contract_rows(late_c, late_act)
    gate_grad = contract_rows(late_second, late_gate)
    up_grad = contract_rows(late_second, late_up)
    second_back = token_sum(lambda start, count: second_partial, rows)
    unused, pull_second = jax.vjp(rms_scale, after_attn, gain_second)
    norm_second_grad, post_gain_part = pull_second(second_back)
    residual_grad = cotangent + norm_second_grad
    weight_grads, residual_grad = lax.optimization_barrier(
        ((gate_grad, up_grad, down_grad_t), residual_grad)
    )
    gate_grad, up_grad, down_grad_t = weight_grads
    attn_grad_all = token_gather(residual_grad.astype(jnp.bfloat16))
    activated_late, attn_grad_all = lax.optimization_barrier((activated, attn_grad_all))
    down_rows = token_sum(lambda start, count: contract_last(activated_late, w_down_t), rows)
    out_weight_grad_t = contract_rows(attn_grad_all, out_rows)
    mlp_packed = jnp.concatenate(
        [g.astype(jnp.bfloat16) for g in (gate_grad, up_grad, down_grad_t, out_weight_grad_t)],
        axis=1,
    )
    head_grad = jnp.dot(attn_grad_all, w_out, preferred_element_type=jnp.float32).astype(
        jnp.bfloat16
    )
    head_float = head_grad.astype(jnp.float32).reshape(group_rows, kv_heads, share, HEAD_SIZE)
    scaled_grad = (head_float / row_totals[..., None]).astype(jnp.bfloat16)
    delta = jnp.sum(head_float * heads_out, axis=-1) / row_totals

    grad_t = jnp.transpose(scaled_grad, (1, 2, 0, 3))
    delta_t = jnp.broadcast_to(
        jnp.transpose(delta, (1, 2, 0))[..., None], (kv_heads, share, group_rows, 128)
    )
    mlp_packed, grad_t, delta_t = lax.optimization_barrier((mlp_packed, grad_t, delta_t))
    mlp_shards = split_columns(
        lax.psum_scatter(mlp_packed, "fsdp", scatter_dimension=0, tiled=True),
        [g.shape[1] for g in (gate_grad, up_grad, down_grad_t, out_weight_grad_t)],
    )
    mlp_shards = [part.astype(jnp.float32) for part in mlp_shards]
    dq_raw, dk_far, dv_far = attention_backward(
        query_t, grad_t, delta_t, query_start, moved[0], moved[1],
        jnp.zeros(query_t.shape, jnp.float32), piece, quarter, 1,
    )
    unseen = (piece == 1) & (jnp.arange(group_rows) >= quarter)
    far_grads = jnp.where(unseen[None, None, :, None], 0.0, jnp.stack([dk_far, dv_far]))
    returned = swapped(far_grads.astype(jnp.bfloat16), "fsdp", 0)
    down_rows, dq_raw = lax.optimization_barrier((down_rows, dq_raw))
    output = (after_attn + down_rows).astype(jnp.bfloat16)
    dq_raw, dk_own, dv_own = attention_backward(
        query_t, grad_t, delta_t, query_start, own_keys, own_values,
        dq_raw, piece, quarter, 0,
    )
    mlp_shards, dq_raw = lax.optimization_barrier((mlp_shards, dq_raw))
    grad_keys_total = jnp.transpose(dk_own + returned[0].astype(jnp.float32), (1, 0, 2))
    grad_values_total = jnp.transpose(dv_own + returned[1].astype(jnp.float32), (1, 0, 2))
    query_grads = jnp.transpose(dq_raw, (2, 0, 1, 3)) * scale
    query_grads = query_grads.reshape(group_rows, q_heads, HEAD_SIZE)
    unused, pull_query = jax.vjp(
        lambda projected, gain: prepare_inputs(projected, gain, group_offset, q_heads),
        query_projected,
        gain_q,
    )
    query_proj_grad, q_gain_part = pull_query(query_grads)
    unused, pull_key = jax.vjp(
        lambda projected, gain: prepare_inputs(projected, gain, group_offset, kv_heads),
        key_projected,
        gain_k,
    )
    key_proj_grad, k_gain_part = pull_key(grad_keys_total)
    query_low = query_proj_grad.astype(jnp.bfloat16)
    key_low = key_proj_grad.astype(jnp.bfloat16)
    value_low = grad_values_total.reshape(group_rows, kv_heads * HEAD_SIZE).astype(jnp.bfloat16)
    query_weight_grad = contract_rows(first_all, query_low)
    key_weight_grad = contract_rows(first_all, key_low)
    value_weight_grad = contract_rows(first_all, value_low)

    def first_term(start, count):
        return (
            contract_last(query_low, w_query)
            + contract_last(key_low, w_key)
            + contract_last(value_low, w_value)
        )

    first_back = token_sum(first_term, rows)
    unused, pull_first = jax.vjp(rms_scale, x_float, gain_first)
    norm_first_grad, input_gain_part = pull_first(first_back)
    input_grad = (residual_grad + norm_first_grad).astype(jnp.bfloat16)
    (query_shard,) = halving_scatter((query_weight_grad,))
    key_shard, value_shard = halving_scatter((key_weight_grad, value_weight_grad))
    gain_totals = all_sum(
        jnp.concatenate([input_gain_part, q_gain_part, k_gain_part, post_gain_part])
    )
    member_f = lax.axis_index("fsdp")
    sizes = (input_gain.shape[0], q_gain.shape[0], k_gain.shape[0], post_gain.shape[0])
    gain_shards = []
    at = 0
    for own in sizes:
        whole = own * fs
        gain_shards.append(lax.dynamic_slice_in_dim(gain_totals, at + member_f * own, own, 0))
        at += whole
    input_gain_shard, q_gain_shard, k_gain_shard, post_gain_shard = gain_shards
    gate_shard, up_shard, down_shard_t, out_shard_t = mlp_shards
    return (
        output,
        input_grad,
        query_shard,
        key_shard,
        value_shard,
        jnp.transpose(out_shard_t),
        gate_shard,
        up_shard,
        jnp.transpose(down_shard_t),
        input_gain_shard,
        q_gain_shard,
        k_gain_shard,
        post_gain_shard,
    )


def solution(mesh):
    return layer_program(mesh)


def layer_program(mesh):
    placed = (
        P(("fsdp", "tensor"), None),
        P(("fsdp", "tensor"), None),
        P(),
        P("fsdp", "tensor"),
        P("fsdp", "tensor"),
        P("fsdp", "tensor"),
        P("tensor", "fsdp"),
        P("fsdp", "tensor"),
        P("fsdp", "tensor"),
        P("tensor", "fsdp"),
        P("fsdp"),
        P("fsdp"),
        P("fsdp"),
        P("fsdp"),
    )
    return jax.shard_map(
        shards,
        mesh=mesh,
        in_specs=placed,
        out_specs=(
            P(("fsdp", "tensor"), None),
            P(("fsdp", "tensor"), None),
            P("fsdp", "tensor"),
            P("fsdp", "tensor"),
            P("fsdp", "tensor"),
            P("tensor", "fsdp"),
            P("fsdp", "tensor"),
            P("fsdp", "tensor"),
            P("tensor", "fsdp"),
            P("fsdp"),
            P("fsdp"),
            P("fsdp"),
            P("fsdp"),
        ),
        check_vma=False,
    )
```

```python
import functools

import numpy as np
import jax
import jax.numpy as jnp
from jax import lax
from jax.experimental import pallas as pl
from jax.experimental.pallas import tpu as pltpu
from jax.sharding import PartitionSpec as P


HEAD_SIZE = 128
TRANS_B = (((1,), (1,)), ((), ()))
TRANS_A = (((0,), (0,)), ((), ()))


def _own_place(p, quarter, r):
    return (p * quarter + r) if r < quarter else ((3 - p) * quarter + r - quarter)


def _far_place(p, quarter, r):
    return ((1 - p) * quarter + r) if r < quarter else ((2 + p) * quarter + r - quarter)


def _pair_tables(p, quarter, block, by_key, source):
    rows = 2 * quarter
    count = rows // block
    kmap = {}
    for src, fn in ((0, _own_place), (1, _far_place)):
        for j in range(count):
            kmap[fn(p, quarter, j * block) // block] = (src, j)
    pairs = []
    for j in range(count):
        qpb = _own_place(p, quarter, j * block) // block
        for kpb in range(qpb + 1):
            if kmap[kpb][0] == source:
                pairs.append((j, qpb, kpb))
    if by_key:
        pairs.sort(key=lambda t: (t[2], t[0]))
    group = [t[2] if by_key else t[0] for t in pairs]
    size = len(pairs)
    first = [1 if n == 0 or group[n - 1] != group[n] else 0 for n in range(size)]
    last = [1 if n == size - 1 or group[n + 1] != group[n] else 0 for n in range(size)]
    return np.array(
        [
            [t[0] for t in pairs],
            [t[1] for t in pairs],
            [t[2] for t in pairs],
            [kmap[t[2]][0] for t in pairs],
            [kmap[t[2]][1] for t in pairs],
            first,
            last,
        ],
        np.int32,
    )


def pair_tables(piece, quarter, block, by_key, source):
    t0 = _pair_tables(0, quarter, block, by_key, source)
    t1 = _pair_tables(1, quarter, block, by_key, source)
    assert t0.shape == t1.shape
    return jnp.where(piece == 0, jnp.asarray(t0), jnp.asarray(t1))


def _mask(qpb, kpb, qs, block):
    qp = qpb * block + lax.broadcasted_iota(jnp.int32, (block, block), 0)
    kp = kpb * block + lax.broadcasted_iota(jnp.int32, (block, block), 1)
    start = jnp.tile(qs, (1, block // 128))
    return (kp >= start) & (kp <= qp)


def _fwd_kernel(tab_ref, q_ref, qs_ref, k_ref, v_ref, a_in_ref, l_in_ref, a_ref, l_ref, acc_ref, sum_ref, *, scale, block):
    n = pl.program_id(1)
    share = q_ref.shape[1]

    @pl.when(tab_ref[5, n] == 1)
    def _():
        acc_ref[...] = a_in_ref[0].reshape(share * block, HEAD_SIZE)
        sum_ref[...] = l_in_ref[0][:, :, :1]

    q = q_ref[0].reshape(share * block, HEAD_SIZE)
    k = k_ref[0]
    v = v_ref[0]
    s = lax.dot_general(q, k, TRANS_B, preferred_element_type=jnp.float32) * scale
    allowed = _mask(tab_ref[1, n], tab_ref[2, n], qs_ref[...], block)
    e = jnp.where(allowed[None], jnp.exp(s.reshape(share, block, block)), 0.0)
    sum_ref[...] += jnp.sum(e, axis=-1, keepdims=True)
    acc_ref[...] += jnp.dot(
        e.reshape(share * block, block).astype(jnp.bfloat16), v, preferred_element_type=jnp.float32
    )

    @pl.when(tab_ref[6, n] == 1)
    def _():
        a_ref[0] = acc_ref[...].reshape(share, block, HEAD_SIZE)
        l_ref[0] = jnp.broadcast_to(sum_ref[...], (share, block, 128))


def attention_forward(q, qs, keys, values, a_in, l_in, piece, quarter, source, block=512):
    kvh, share, _, _ = q.shape
    tab = pair_tables(piece, quarter, block, False, source)
    npairs = tab.shape[1]
    scale = HEAD_SIZE ** (-0.5)
    row_spec = pl.BlockSpec((1, share, block, HEAD_SIZE), lambda h, n, t: (h, 0, t[0, n], 0))
    lane_spec = pl.BlockSpec((1, share, block, 128), lambda h, n, t: (h, 0, t[0, n], 0))
    key_spec = pl.BlockSpec((1, block, HEAD_SIZE), lambda h, n, t: (h, t[4, n], 0))
    grid_spec = pltpu.PrefetchScalarGridSpec(
        num_scalar_prefetch=1,
        grid=(kvh, npairs),
        in_specs=[
            row_spec,
            pl.BlockSpec((block, 128), lambda h, n, t: (t[0, n], 0)),
            key_spec,
            key_spec,
            row_spec,
            lane_spec,
        ],
        out_specs=[row_spec, lane_spec],
        scratch_shapes=[
            pltpu.VMEM((share * block, HEAD_SIZE), jnp.float32),
            pltpu.VMEM((share, block, 1), jnp.float32),
        ],
    )
    flops = 4 * kvh * npairs * share * block * block * HEAD_SIZE
    return pl.pallas_call(
        functools.partial(_fwd_kernel, scale=scale, block=block),
        grid_spec=grid_spec,
        out_shape=[
            jax.ShapeDtypeStruct(a_in.shape, jnp.float32),
            jax.ShapeDtypeStruct(l_in.shape, jnp.float32),
        ],
        input_output_aliases={5: 0, 6: 1},
        compiler_params=pltpu.CompilerParams(
            dimension_semantics=("arbitrary", "arbitrary"), vmem_limit_bytes=48 * 1024 * 1024
        ),
        cost_estimate=pl.CostEstimate(
            flops=flops,
            transcendentals=kvh * npairs * share * block * block,
            bytes_accessed=kvh * npairs * (8 * block * HEAD_SIZE * 2),
        ),
        name="attn_fwd",
    )(tab, q, qs, keys, values, a_in, l_in)


def _bwd_kernel(tab_ref, q_ref, h_ref, dl_ref, qs_ref, k_ref, v_ref, dq_in_ref, dq_ref, dk_ref, dv_ref, dk_acc, dv_acc, *, scale, block):
    n = pl.program_id(1)
    share = q_ref.shape[1]

    @pl.when(n == 0)
    def _():
        dq_ref[...] = dq_in_ref[...]

    @pl.when(tab_ref[5, n] == 1)
    def _():
        dk_acc[...] = jnp.zeros(dk_acc.shape, dk_acc.dtype)
        dv_acc[...] = jnp.zeros(dv_acc.shape, dv_acc.dtype)

    q = q_ref[0].reshape(share * block, HEAD_SIZE)
    hh = h_ref[0].reshape(share * block, HEAD_SIZE)
    k = k_ref[0]
    v = v_ref[0]
    s = lax.dot_general(q, k, TRANS_B, preferred_element_type=jnp.float32) * scale
    allowed = _mask(tab_ref[1, n], tab_ref[2, n], qs_ref[...], block)
    e = jnp.where(allowed[None], jnp.exp(s.reshape(share, block, block)), 0.0)
    dp = lax.dot_general(hh, v, TRANS_B, preferred_element_type=jnp.float32).reshape(share, block, block)
    delta = jnp.tile(dl_ref[0], (1, 1, block // 128))
    ds = (e * (dp - delta)).reshape(share * block, block).astype(jnp.bfloat16)
    rows = pl.ds(pl.multiple_of(tab_ref[0, n] * block, block), block)
    dq_ref[0, :, rows, :] += jnp.dot(ds, k, preferred_element_type=jnp.float32).reshape(share, block, HEAD_SIZE)
    dk_acc[...] += lax.dot_general(ds, q, TRANS_A, preferred_element_type=jnp.float32)
    dv_acc[...] += lax.dot_general(
        e.reshape(share * block, block).astype(jnp.bfloat16), hh, TRANS_A, preferred_element_type=jnp.float32
    )

    @pl.when(tab_ref[6, n] == 1)
    def _():
        dk_ref[0] = dk_acc[...] * scale
        dv_ref[0] = dv_acc[...]


def attention_backward(q, hgrad, delta, qs, keys, values, dq_in, piece, quarter, source, block=512):
    kvh, share, rows, _ = q.shape
    tab = pair_tables(piece, quarter, block, True, source)
    npairs = tab.shape[1]
    scale = HEAD_SIZE ** (-0.5)
    row_spec = pl.BlockSpec((1, share, block, HEAD_SIZE), lambda h, n, t: (h, 0, t[0, n], 0))
    key_spec = pl.BlockSpec((1, block, HEAD_SIZE), lambda h, n, t: (h, t[4, n], 0))
    full_spec = pl.BlockSpec((1, share, rows, HEAD_SIZE), lambda h, n, t: (h, 0, 0, 0))
    grid_spec = pltpu.PrefetchScalarGridSpec(
        num_scalar_prefetch=1,
        grid=(kvh, npairs),
        in_specs=[
            row_spec,
            row_spec,
            pl.BlockSpec((1, share, block, 128), lambda h, n, t: (h, 0, t[0, n], 0)),
            pl.BlockSpec((block, 128), lambda h, n, t: (t[0, n], 0)),
            key_spec,
            key_spec,
            full_spec,
        ],
        out_specs=[full_spec, key_spec, key_spec],
        scratch_shapes=[
            pltpu.VMEM((block, HEAD_SIZE), jnp.float32),
            pltpu.VMEM((block, HEAD_SIZE), jnp.float32),
        ],
    )
    flops = 10 * kvh * npairs * share * block * block * HEAD_SIZE
    return pl.pallas_call(
        functools.partial(_bwd_kernel, scale=scale, block=block),
        grid_spec=grid_spec,
        out_shape=[
            jax.ShapeDtypeStruct(dq_in.shape, jnp.float32),
            jax.ShapeDtypeStruct(keys.shape, jnp.float32),
            jax.ShapeDtypeStruct(values.shape, jnp.float32),
        ],
        input_output_aliases={7: 0},
        compiler_params=pltpu.CompilerParams(
            dimension_semantics=("arbitrary", "arbitrary"), vmem_limit_bytes=56 * 1024 * 1024
        ),
        cost_estimate=pl.CostEstimate(
            flops=flops,
            transcendentals=kvh * npairs * share * block * block,
            bytes_accessed=kvh * npairs * (10 * block * HEAD_SIZE * 2),
        ),
        name="attn_bwd",
    )(tab, q, hgrad, delta, qs, keys, values, dq_in)


PIECES = 2


EPSILON = 1e-06
THETA = 1000000.0


def swapped(shard, axis, distance):
    return lax.ppermute(shard, axis, [(i, i ^ 1 << distance) for i in range(lax.axis_size(axis))])


def rms_scale(values, gain):
    inverse = lax.rsqrt(jnp.mean(values * values, axis=-1, keepdims=True) + EPSILON)
    return values * inverse * gain


def rotary(values, start_offset):
    half = values.shape[-1] // 2
    frequency = THETA ** (-(jnp.arange(half, dtype=jnp.float32) * 2.0 / values.shape[-1]))
    angle = start_offset.astype(jnp.float32)[:, None] * frequency[None, :]
    cosine = jnp.cos(angle)[:, None, :]
    sine = jnp.sin(angle)[:, None, :]
    first = values[..., :half]
    second = values[..., half:]
    return jnp.concatenate(
        [first * cosine - second * sine, second * cosine + first * sine], axis=-1
    )


def prepare_inputs(projected, gain, start_offset, head_groups):
    shaped = projected.reshape(projected.shape[0], head_groups, -1)
    return rotary(rms_scale(shaped, gain), start_offset)


def piece_places(which, group_rows):
    quarter = group_rows // 2
    local = jnp.arange(group_rows, dtype=jnp.int32)
    chosen = jnp.where(local < quarter, which, 3 - which)
    return chosen * quarter + local % quarter


def contract_rows(left, right):
    return lax.dot_general(
        left, right, (((0,), (0,)), ((), ())), preferred_element_type=jnp.float32
    )


def contract_last(left, right):
    return lax.dot_general(
        left, right, (((1,), (1,)), ((), ())), preferred_element_type=jnp.float32
    )


def split_columns(full, widths):
    parts = []
    at = 0
    for width in widths:
        parts.append(full[:, at : at + width])
        at += width
    return parts


def halving_scatter(grads):
    widths = [g.shape[1] for g in grads]
    packed = jnp.concatenate(grads, axis=1)
    count = lax.axis_size("fsdp")
    me = lax.axis_index("fsdp")
    bits = count.bit_length() - 1
    rows_f = packed.shape[0] // count
    order = [int(format(b, f"0{bits}b")[::-1], 2) for b in range(count)]
    buf = jnp.concatenate([packed[b * rows_f : (b + 1) * rows_f] for b in order], axis=0)
    for bit in range(bits):
        half = buf.shape[0] // 2
        mine = (me >> bit) & 1
        keep = lax.dynamic_slice_in_dim(buf, mine * half, half, 0)
        send = lax.dynamic_slice_in_dim(buf, (1 - mine) * half, half, 0)
        got = lax.ppermute(
            send.astype(jnp.bfloat16), "fsdp", [(i, i ^ (1 << bit)) for i in range(count)]
        )
        buf = keep + got.astype(jnp.float32)
    return split_columns(buf, widths)


def fsdp_gather(values):
    count = lax.axis_size("fsdp")
    me = lax.axis_index("fsdp")
    distance = 1
    while distance < count:
        got = lax.ppermute(values, "fsdp", [(i, i ^ distance) for i in range(count)])
        low = (me & distance) == 0
        values = jnp.concatenate(
            [jnp.where(low, values, got), jnp.where(low, got, values)]
        )
        distance *= 2
    return values


def all_sum(values):
    for axis in ("tensor", "fsdp"):
        distance = 1
        while distance < lax.axis_size(axis):
            values = values + lax.ppermute(
                values, axis, [(i, i ^ distance) for i in range(lax.axis_size(axis))]
            )
            distance *= 2
    return values


def exchange(values, distance):
    count = lax.axis_size("tensor")
    return lax.ppermute(values, "tensor", [(i, i ^ distance) for i in range(count)])


def token_gather(values):
    rows = values.shape[0]
    me = lax.axis_index("tensor")
    across = exchange(values, 2)
    pair = jnp.stack([values, across])
    beside = exchange(pair, 1)
    full = jnp.zeros((4 * rows,) + values.shape[1:], values.dtype)
    for part, place in ((values, me), (across, me ^ 2), (beside[0], me ^ 1), (beside[1], me ^ 3)):
        full = lax.dynamic_update_slice_in_dim(full, part, place * rows, 0)
    return full


def token_sum(term, rows):
    partial = term(jnp.int32(0), rows * lax.axis_size("tensor"))
    me = lax.axis_index("tensor")

    def block(place):
        return lax.dynamic_slice_in_dim(partial, place * rows, rows, 0)

    sent = jnp.stack([block(me ^ 1), block(me ^ 3)]).astype(jnp.bfloat16)
    got = exchange(sent, 1).astype(jnp.float32)
    mine = block(me) + got[0]
    other = (block(me ^ 2) + got[1]).astype(jnp.bfloat16)
    return mine + exchange(other, 2).astype(jnp.float32)


def shards(
    hidden,
    out_grad,
    lengths,
    q_weight,
    key_matrix,
    value_matrix,
    o_weight,
    gate_weight,
    up_weight,
    down_weight,
    input_gain,
    q_gain,
    k_gain,
    post_gain,
):
    split = lax.axis_size("tensor")
    rows = hidden.shape[0]
    group_rows = rows * split
    q_heads = q_weight.shape[1] // HEAD_SIZE
    kv_heads = key_matrix.shape[1] // HEAD_SIZE
    share = q_heads // kv_heads
    scale = HEAD_SIZE ** (-0.5)
    member = lax.axis_index("fsdp")
    slot = member // PIECES
    piece = member % PIECES
    lengths_row = lax.dynamic_index_in_dim(lengths, slot, 0, keepdims=False)
    ends = jnp.cumsum(lengths_row)
    group_place = piece_places(piece, group_rows)
    passed = group_place[:, None] >= ends[None, :]
    group_start = jnp.sum(jnp.where(passed, lengths_row[None, :], 0), axis=1)
    group_offset = group_place - group_start
    local_valid = lax.dynamic_slice_in_dim(
        group_place < ends[-1], lax.axis_index("tensor") * rows, rows, 0
    )
    fs = lax.axis_size("fsdp")
    gain_sizes = (input_gain.shape[0], q_gain.shape[0], k_gain.shape[0], post_gain.shape[0])
    gains_all = fsdp_gather(
        jnp.concatenate([input_gain, q_gain, k_gain, post_gain]).astype(jnp.bfloat16)
    ).reshape(fs, sum(gain_sizes))
    gain_in, gain_query, gain_keys, gain_post = [
        part.reshape(-1) for part in split_columns(gains_all, gain_sizes)
    ]
    kv_full = lax.all_gather(
        jnp.concatenate(
            [key_matrix.astype(jnp.bfloat16), value_matrix.astype(jnp.bfloat16)], axis=1
        ),
        "fsdp",
        axis=0,
        tiled=True,
    )
    w_key, w_value = split_columns(kv_full, (key_matrix.shape[1], value_matrix.shape[1]))
    qo_full = lax.all_gather(
        jnp.concatenate(
            [q_weight.astype(jnp.bfloat16), jnp.transpose(o_weight).astype(jnp.bfloat16)],
            axis=1,
        ),
        "fsdp",
        axis=0,
        tiled=True,
    )
    w_query, w_out = split_columns(qo_full, (q_weight.shape[1], o_weight.shape[0]))
    x_float = hidden.astype(jnp.float32)
    gain_first = gain_in.astype(jnp.float32)
    first_all = token_gather(rms_scale(x_float, gain_first).astype(jnp.bfloat16))
    cotangent = out_grad.astype(jnp.float32) * local_valid[:, None].astype(jnp.float32)
    cotangent_low, first_all = lax.optimization_barrier((cotangent.astype(jnp.bfloat16), first_all))
    mlp_grad_all = token_gather(cotangent_low)
    query_projected = jnp.dot(first_all, w_query, preferred_element_type=jnp.float32)
    key_projected = jnp.dot(first_all, w_key, preferred_element_type=jnp.float32)
    value_rows = (
        jnp.dot(first_all, w_value, preferred_element_type=jnp.float32)
        .astype(jnp.bfloat16)
        .reshape(group_rows, kv_heads, HEAD_SIZE)
    )
    gain_q = gain_query.astype(jnp.float32)
    gain_k = gain_keys.astype(jnp.float32)
    query_rope = (
        prepare_inputs(query_projected, gain_q, group_offset, q_heads)
        .astype(jnp.bfloat16)
        .reshape(group_rows, kv_heads, share, HEAD_SIZE)
    )
    key_rope = prepare_inputs(key_projected, gain_k, group_offset, kv_heads).astype(jnp.bfloat16)
    quarter = group_rows // 2
    query_start = jnp.broadcast_to(group_start[:, None], (group_rows, 128))
    query_t = jnp.transpose(query_rope, (1, 2, 0, 3))
    own_keys = jnp.transpose(key_rope, (1, 0, 2))
    own_values = jnp.transpose(value_rows, (1, 0, 2))
    moved = swapped(jnp.stack([own_keys, own_values]), "fsdp", 0)
    sums = jnp.zeros(query_t.shape, jnp.float32)
    totals = jnp.zeros(query_t.shape[:3] + (128,), jnp.float32)
    sums, totals = attention_forward(
        query_t, query_start, own_keys, own_values, sums, totals, piece, quarter, 0
    )
    sums, totals_t = attention_forward(
        query_t, query_start, moved[0], moved[1], sums, totals, piece, quarter, 1
    )
    mlp_grad_all, sums, totals_t = lax.optimization_barrier((mlp_grad_all, sums, totals_t))
    heads_t = sums / totals_t[..., :1]
    heads_out = jnp.transpose(heads_t, (2, 0, 1, 3))
    row_totals = jnp.transpose(totals_t[..., 0], (2, 0, 1))
    out_rows = heads_out.reshape(group_rows, q_heads * HEAD_SIZE).astype(jnp.bfloat16)

    mlp_full = lax.all_gather(
        jnp.concatenate(
            [
                gate_weight.astype(jnp.bfloat16),
                up_weight.astype(jnp.bfloat16),
                jnp.transpose(down_weight).astype(jnp.bfloat16),
            ],
            axis=1,
        ),
        "fsdp",
        axis=0,
        tiled=True,
    )
    w_gate, w_up, w_down_t = split_columns(
        mlp_full, (gate_weight.shape[1], up_weight.shape[1], down_weight.shape[0])
    )
    out_partial = contract_last(out_rows, w_out)
    late_grad_all, out_partial = lax.optimization_barrier((mlp_grad_all, out_partial))
    grad_act = jnp.dot(late_grad_all, w_down_t, preferred_element_type=jnp.float32)
    after_attn = x_float + token_sum(lambda start, count: out_partial, rows)
    grad_act, after_attn = lax.optimization_barrier((grad_act, after_attn))
    gain_second = gain_post.astype(jnp.float32)
    second_all = token_gather(rms_scale(after_attn, gain_second).astype(jnp.bfloat16))
    gate_out = jnp.dot(second_all, w_gate, preferred_element_type=jnp.float32)
    up_out = jnp.dot(second_all, w_up, preferred_element_type=jnp.float32)
    activated = (jax.nn.silu(gate_out) * up_out).astype(jnp.bfloat16)

    unused, pull_gate = jax.vjp(
        lambda gate_in, up_in: jax.nn.silu(gate_in) * up_in, gate_out, up_out
    )
    grad_gate, grad_up = pull_gate(grad_act)
    grad_gate = grad_gate.astype(jnp.bfloat16)
    grad_up = grad_up.astype(jnp.bfloat16)
    second_partial = contract_last(grad_gate, w_gate) + contract_last(grad_up, w_up)
    grad_inputs, second_partial = lax.optimization_barrier(
        ((mlp_grad_all, activated, second_all, grad_gate, grad_up), second_partial)
    )
    late_c, late_act, late_second, late_gate, late_up = grad_inputs
    down_grad_t = contract_rows(late_c, late_act)
    gate_grad = contract_rows(late_second, late_gate)
    up_grad = contract_rows(late_second, late_up)
    second_back = token_sum(lambda start, count: second_partial, rows)
    unused, pull_second = jax.vjp(rms_scale, after_attn, gain_second)
    norm_second_grad, post_gain_part = pull_second(second_back)
    residual_grad = cotangent + norm_second_grad
    weight_grads, residual_grad = lax.optimization_barrier(
        ((gate_grad, up_grad, down_grad_t), residual_grad)
    )
    gate_grad, up_grad, down_grad_t = weight_grads
    attn_grad_all = token_gather(residual_grad.astype(jnp.bfloat16))
    activated_late, attn_grad_all = lax.optimization_barrier((activated, attn_grad_all))
    down_rows = token_sum(lambda start, count: contract_last(activated_late, w_down_t), rows)
    out_weight_grad_t = contract_rows(attn_grad_all, out_rows)
    mlp_packed = jnp.concatenate(
        [g.astype(jnp.bfloat16) for g in (gate_grad, up_grad, down_grad_t, out_weight_grad_t)],
        axis=1,
    )
    head_grad = jnp.dot(attn_grad_all, w_out, preferred_element_type=jnp.float32).astype(
        jnp.bfloat16
    )
    head_float = head_grad.astype(jnp.float32).reshape(group_rows, kv_heads, share, HEAD_SIZE)
    scaled_grad = (head_float / row_totals[..., None]).astype(jnp.bfloat16)
    delta = jnp.sum(head_float * heads_out, axis=-1) / row_totals

    grad_t = jnp.transpose(scaled_grad, (1, 2, 0, 3))
    delta_t = jnp.broadcast_to(
        jnp.transpose(delta, (1, 2, 0))[..., None], (kv_heads, share, group_rows, 128)
    )
    mlp_packed, grad_t, delta_t = lax.optimization_barrier((mlp_packed, grad_t, delta_t))
    mlp_shards = split_columns(
        lax.psum_scatter(mlp_packed, "fsdp", scatter_dimension=0, tiled=True),
        [g.shape[1] for g in (gate_grad, up_grad, down_grad_t, out_weight_grad_t)],
    )
    mlp_shards = [part.astype(jnp.float32) for part in mlp_shards]
    dq_raw, dk_far, dv_far = attention_backward(
        query_t, grad_t, delta_t, query_start, moved[0], moved[1],
        jnp.zeros(query_t.shape, jnp.float32), piece, quarter, 1,
    )
    unseen = (piece == 1) & (jnp.arange(group_rows) >= quarter)
    far_grads = jnp.where(unseen[None, None, :, None], 0.0, jnp.stack([dk_far, dv_far]))
    returned = swapped(far_grads.astype(jnp.bfloat16), "fsdp", 0)
    down_rows, dq_raw = lax.optimization_barrier((down_rows, dq_raw))
    output = (after_attn + down_rows).astype(jnp.bfloat16)
    dq_raw, dk_own, dv_own = attention_backward(
        query_t, grad_t, delta_t, query_start, own_keys, own_values,
        dq_raw, piece, quarter, 0,
    )
    mlp_shards, dq_raw = lax.optimization_barrier((mlp_shards, dq_raw))
    grad_keys_total = jnp.transpose(dk_own + returned[0].astype(jnp.float32), (1, 0, 2))
    grad_values_total = jnp.transpose(dv_own + returned[1].astype(jnp.float32), (1, 0, 2))
    query_grads = jnp.transpose(dq_raw, (2, 0, 1, 3)) * scale
    query_grads = query_grads.reshape(group_rows, q_heads, HEAD_SIZE)
    unused, pull_query = jax.vjp(
        lambda projected, gain: prepare_inputs(projected, gain, group_offset, q_heads),
        query_projected,
        gain_q,
    )
    query_proj_grad, q_gain_part = pull_query(query_grads)
    unused, pull_key = jax.vjp(
        lambda projected, gain: prepare_inputs(projected, gain, group_offset, kv_heads),
        key_projected,
        gain_k,
    )
    key_proj_grad, k_gain_part = pull_key(grad_keys_total)
    query_low = query_proj_grad.astype(jnp.bfloat16)
    key_low = key_proj_grad.astype(jnp.bfloat16)
    value_low = grad_values_total.reshape(group_rows, kv_heads * HEAD_SIZE).astype(jnp.bfloat16)
    query_weight_grad = contract_rows(first_all, query_low)
    key_weight_grad = contract_rows(first_all, key_low)
    value_weight_grad = contract_rows(first_all, value_low)

    def first_term(start, count):
        return (
            contract_last(query_low, w_query)
            + contract_last(key_low, w_key)
            + contract_last(value_low, w_value)
        )

    first_back = token_sum(first_term, rows)
    unused, pull_first = jax.vjp(rms_scale, x_float, gain_first)
    norm_first_grad, input_gain_part = pull_first(first_back)
    input_grad = (residual_grad + norm_first_grad).astype(jnp.bfloat16)
    (query_shard,) = halving_scatter((query_weight_grad,))
    key_shard, value_shard = halving_scatter((key_weight_grad, value_weight_grad))
    gain_totals = all_sum(
        jnp.concatenate([input_gain_part, q_gain_part, k_gain_part, post_gain_part])
    )
    member_f = lax.axis_index("fsdp")
    sizes = (input_gain.shape[0], q_gain.shape[0], k_gain.shape[0], post_gain.shape[0])
    gain_shards = []
    at = 0
    for own in sizes:
        whole = own * fs
        gain_shards.append(lax.dynamic_slice_in_dim(gain_totals, at + member_f * own, own, 0))
        at += whole
    input_gain_shard, q_gain_shard, k_gain_shard, post_gain_shard = gain_shards
    gate_shard, up_shard, down_shard_t, out_shard_t = mlp_shards
    return (
        output,
        input_grad,
        query_shard,
        key_shard,
        value_shard,
        jnp.transpose(out_shard_t),
        gate_shard,
        up_shard,
        jnp.transpose(down_shard_t),
        input_gain_shard,
        q_gain_shard,
        k_gain_shard,
        post_gain_shard,
    )


def solution(mesh):
    return layer_program(mesh)


def layer_program(mesh):
    placed = (
        P(("fsdp", "tensor"), None),
        P(("fsdp", "tensor"), None),
        P(),
        P("fsdp", "tensor"),
        P("fsdp", "tensor"),
        P("fsdp", "tensor"),
        P("tensor", "fsdp"),
        P("fsdp", "tensor"),
        P("fsdp", "tensor"),
        P("tensor", "fsdp"),
        P("fsdp"),
        P("fsdp"),
        P("fsdp"),
        P("fsdp"),
    )
    return jax.shard_map(
        shards,
        mesh=mesh,
        in_specs=placed,
        out_specs=(
            P(("fsdp", "tensor"), None),
            P(("fsdp", "tensor"), None),
            P("fsdp", "tensor"),
            P("fsdp", "tensor"),
            P("fsdp", "tensor"),
            P("tensor", "fsdp"),
            P("fsdp", "tensor"),
            P("fsdp", "tensor"),
            P("tensor", "fsdp"),
            P("fsdp"),
            P("fsdp"),
            P("fsdp"),
            P("fsdp"),
        ),
        check_vma=False,
    )
```

```python
import functools

import numpy as np
import jax
import jax.numpy as jnp
from jax import lax
from jax.experimental import pallas as pl
from jax.experimental.pallas import tpu as pltpu
from jax.sharding import PartitionSpec as P


HEAD_SIZE = 128
TRANS_B = (((1,), (1,)), ((), ()))
TRANS_A = (((0,), (0,)), ((), ()))


def _own_place(p, quarter, r):
    return (p * quarter + r) if r < quarter else ((3 - p) * quarter + r - quarter)


def _far_place(p, quarter, r):
    return ((1 - p) * quarter + r) if r < quarter else ((2 + p) * quarter + r - quarter)


def _pair_tables(p, quarter, block, by_key, source):
    rows = 2 * quarter
    count = rows // block
    kmap = {}
    for src, fn in ((0, _own_place), (1, _far_place)):
        for j in range(count):
            kmap[fn(p, quarter, j * block) // block] = (src, j)
    pairs = []
    for j in range(count):
        qpb = _own_place(p, quarter, j * block) // block
        for kpb in range(qpb + 1):
            if kmap[kpb][0] == source:
                pairs.append((j, qpb, kpb))
    if by_key:
        pairs.sort(key=lambda t: (t[2], t[0]))
    group = [t[2] if by_key else t[0] for t in pairs]
    size = len(pairs)
    first = [1 if n == 0 or group[n - 1] != group[n] else 0 for n in range(size)]
    last = [1 if n == size - 1 or group[n + 1] != group[n] else 0 for n in range(size)]
    return np.array(
        [
            [t[0] for t in pairs],
            [t[1] for t in pairs],
            [t[2] for t in pairs],
            [kmap[t[2]][0] for t in pairs],
            [kmap[t[2]][1] for t in pairs],
            first,
            last,
        ],
        np.int32,
    )


def pair_tables(piece, quarter, block, by_key, source):
    t0 = _pair_tables(0, quarter, block, by_key, source)
    t1 = _pair_tables(1, quarter, block, by_key, source)
    assert t0.shape == t1.shape
    return jnp.where(piece == 0, jnp.asarray(t0), jnp.asarray(t1))


def _mask(qpb, kpb, qs, block):
    qp = qpb * block + lax.broadcasted_iota(jnp.int32, (block, block), 0)
    kp = kpb * block + lax.broadcasted_iota(jnp.int32, (block, block), 1)
    start = jnp.tile(qs, (1, block // 128))
    return (kp >= start) & (kp <= qp)


def _fwd_kernel(tab_ref, q_ref, qs_ref, k_ref, v_ref, a_in_ref, l_in_ref, a_ref, l_ref, acc_ref, sum_ref, *, scale, block):
    n = pl.program_id(1)
    share = q_ref.shape[1]

    @pl.when(tab_ref[5, n] == 1)
    def _():
        acc_ref[...] = a_in_ref[0].reshape(share * block, HEAD_SIZE)
        sum_ref[...] = l_in_ref[0][:, :, :1]

    q = q_ref[0].reshape(share * block, HEAD_SIZE)
    k = k_ref[0]
    v = v_ref[0]
    s = lax.dot_general(q, k, TRANS_B, preferred_element_type=jnp.float32) * scale
    allowed = _mask(tab_ref[1, n], tab_ref[2, n], qs_ref[...], block)
    e = jnp.where(allowed[None], jnp.exp(s.reshape(share, block, block)), 0.0)
    sum_ref[...] += jnp.sum(e, axis=-1, keepdims=True)
    acc_ref[...] += jnp.dot(
        e.reshape(share * block, block).astype(jnp.bfloat16), v, preferred_element_type=jnp.float32
    )

    @pl.when(tab_ref[6, n] == 1)
    def _():
        a_ref[0] = acc_ref[...].reshape(share, block, HEAD_SIZE)
        l_ref[0] = jnp.broadcast_to(sum_ref[...], (share, block, 128))


def attention_forward(q, qs, keys, values, a_in, l_in, piece, quarter, source, block=512):
    kvh, share, _, _ = q.shape
    tab = pair_tables(piece, quarter, block, False, source)
    npairs = tab.shape[1]
    scale = HEAD_SIZE ** (-0.5)
    row_spec = pl.BlockSpec((1, share, block, HEAD_SIZE), lambda h, n, t: (h, 0, t[0, n], 0))
    lane_spec = pl.BlockSpec((1, share, block, 128), lambda h, n, t: (h, 0, t[0, n], 0))
    key_spec = pl.BlockSpec((1, block, HEAD_SIZE), lambda h, n, t: (h, t[4, n], 0))
    grid_spec = pltpu.PrefetchScalarGridSpec(
        num_scalar_prefetch=1,
        grid=(kvh, npairs),
        in_specs=[
            row_spec,
            pl.BlockSpec((block, 128), lambda h, n, t: (t[0, n], 0)),
            key_spec,
            key_spec,
            row_spec,
            lane_spec,
        ],
        out_specs=[row_spec, lane_spec],
        scratch_shapes=[
            pltpu.VMEM((share * block, HEAD_SIZE), jnp.float32),
            pltpu.VMEM((share, block, 1), jnp.float32),
        ],
    )
    flops = 4 * kvh * npairs * share * block * block * HEAD_SIZE
    return pl.pallas_call(
        functools.partial(_fwd_kernel, scale=scale, block=block),
        grid_spec=grid_spec,
        out_shape=[
            jax.ShapeDtypeStruct(a_in.shape, jnp.float32),
            jax.ShapeDtypeStruct(l_in.shape, jnp.float32),
        ],
        input_output_aliases={5: 0, 6: 1},
        compiler_params=pltpu.CompilerParams(
            dimension_semantics=("arbitrary", "arbitrary"), vmem_limit_bytes=48 * 1024 * 1024
        ),
        cost_estimate=pl.CostEstimate(
            flops=flops,
            transcendentals=kvh * npairs * share * block * block,
            bytes_accessed=kvh * npairs * (8 * block * HEAD_SIZE * 2),
        ),
        name="attn_fwd",
    )(tab, q, qs, keys, values, a_in, l_in)


def _bwd_kernel(tab_ref, q_ref, h_ref, dl_ref, qs_ref, k_ref, v_ref, dq_in_ref, dq_ref, dk_ref, dv_ref, dk_acc, dv_acc, *, scale, block):
    n = pl.program_id(1)
    share = q_ref.shape[1]

    @pl.when(n == 0)
    def _():
        dq_ref[...] = dq_in_ref[...]

    @pl.when(tab_ref[5, n] == 1)
    def _():
        dk_acc[...] = jnp.zeros(dk_acc.shape, dk_acc.dtype)
        dv_acc[...] = jnp.zeros(dv_acc.shape, dv_acc.dtype)

    q = q_ref[0].reshape(share * block, HEAD_SIZE)
    hh = h_ref[0].reshape(share * block, HEAD_SIZE)
    k = k_ref[0]
    v = v_ref[0]
    s = lax.dot_general(q, k, TRANS_B, preferred_element_type=jnp.float32) * scale
    allowed = _mask(tab_ref[1, n], tab_ref[2, n], qs_ref[...], block)
    e = jnp.where(allowed[None], jnp.exp(s.reshape(share, block, block)), 0.0)
    dp = lax.dot_general(hh, v, TRANS_B, preferred_element_type=jnp.float32).reshape(share, block, block)
    delta = jnp.tile(dl_ref[0], (1, 1, block // 128))
    ds = (e * (dp - delta)).reshape(share * block, block).astype(jnp.bfloat16)
    rows = pl.ds(pl.multiple_of(tab_ref[0, n] * block, block), block)
    dq_ref[0, :, rows, :] += jnp.dot(ds, k, preferred_element_type=jnp.float32).reshape(share, block, HEAD_SIZE)
    dk_acc[...] += lax.dot_general(ds, q, TRANS_A, preferred_element_type=jnp.float32)
    dv_acc[...] += lax.dot_general(
        e.reshape(share * block, block).astype(jnp.bfloat16), hh, TRANS_A, preferred_element_type=jnp.float32
    )

    @pl.when(tab_ref[6, n] == 1)
    def _():
        dk_ref[0] = dk_acc[...] * scale
        dv_ref[0] = dv_acc[...]


def attention_backward(q, hgrad, delta, qs, keys, values, dq_in, piece, quarter, source, block=512):
    kvh, share, rows, _ = q.shape
    tab = pair_tables(piece, quarter, block, True, source)
    npairs = tab.shape[1]
    scale = HEAD_SIZE ** (-0.5)
    row_spec = pl.BlockSpec((1, share, block, HEAD_SIZE), lambda h, n, t: (h, 0, t[0, n], 0))
    key_spec = pl.BlockSpec((1, block, HEAD_SIZE), lambda h, n, t: (h, t[4, n], 0))
    full_spec = pl.BlockSpec((1, share, rows, HEAD_SIZE), lambda h, n, t: (h, 0, 0, 0))
    grid_spec = pltpu.PrefetchScalarGridSpec(
        num_scalar_prefetch=1,
        grid=(kvh, npairs),
        in_specs=[
            row_spec,
            row_spec,
            pl.BlockSpec((1, share, block, 128), lambda h, n, t: (h, 0, t[0, n], 0)),
            pl.BlockSpec((block, 128), lambda h, n, t: (t[0, n], 0)),
            key_spec,
            key_spec,
            full_spec,
        ],
        out_specs=[full_spec, key_spec, key_spec],
        scratch_shapes=[
            pltpu.VMEM((block, HEAD_SIZE), jnp.float32),
            pltpu.VMEM((block, HEAD_SIZE), jnp.float32),
        ],
    )
    flops = 10 * kvh * npairs * share * block * block * HEAD_SIZE
    return pl.pallas_call(
        functools.partial(_bwd_kernel, scale=scale, block=block),
        grid_spec=grid_spec,
        out_shape=[
            jax.ShapeDtypeStruct(dq_in.shape, jnp.float32),
            jax.ShapeDtypeStruct(keys.shape, jnp.float32),
            jax.ShapeDtypeStruct(values.shape, jnp.float32),
        ],
        input_output_aliases={7: 0},
        compiler_params=pltpu.CompilerParams(
            dimension_semantics=("arbitrary", "arbitrary"), vmem_limit_bytes=56 * 1024 * 1024
        ),
        cost_estimate=pl.CostEstimate(
            flops=flops,
            transcendentals=kvh * npairs * share * block * block,
            bytes_accessed=kvh * npairs * (10 * block * HEAD_SIZE * 2),
        ),
        name="attn_bwd",
    )(tab, q, hgrad, delta, qs, keys, values, dq_in)


PIECES = 2


EPSILON = 1e-06
THETA = 1000000.0


def swapped(shard, axis, distance):
    return lax.ppermute(shard, axis, [(i, i ^ 1 << distance) for i in range(lax.axis_size(axis))])


def rms_scale(values, gain):
    inverse = lax.rsqrt(jnp.mean(values * values, axis=-1, keepdims=True) + EPSILON)
    return values * inverse * gain


def rotary(values, start_offset):
    half = values.shape[-1] // 2
    frequency = THETA ** (-(jnp.arange(half, dtype=jnp.float32) * 2.0 / values.shape[-1]))
    angle = start_offset.astype(jnp.float32)[:, None] * frequency[None, :]
    cosine = jnp.cos(angle)[:, None, :]
    sine = jnp.sin(angle)[:, None, :]
    first = values[..., :half]
    second = values[..., half:]
    return jnp.concatenate(
        [first * cosine - second * sine, second * cosine + first * sine], axis=-1
    )


def prepare_inputs(projected, gain, start_offset, head_groups):
    shaped = projected.reshape(projected.shape[0], head_groups, -1)
    return rotary(rms_scale(shaped, gain), start_offset)


def piece_places(which, group_rows):
    quarter = group_rows // 2
    local = jnp.arange(group_rows, dtype=jnp.int32)
    chosen = jnp.where(local < quarter, which, 3 - which)
    return chosen * quarter + local % quarter


def contract_rows(left, right):
    return lax.dot_general(
        left, right, (((0,), (0,)), ((), ())), preferred_element_type=jnp.float32
    )


def contract_last(left, right):
    return lax.dot_general(
        left, right, (((1,), (1,)), ((), ())), preferred_element_type=jnp.float32
    )


def split_columns(full, widths):
    parts = []
    at = 0
    for width in widths:
        parts.append(full[:, at : at + width])
        at += width
    return parts


def halving_scatter(grads):
    widths = [g.shape[1] for g in grads]
    packed = jnp.concatenate(grads, axis=1)
    count = lax.axis_size("fsdp")
    me = lax.axis_index("fsdp")
    bits = count.bit_length() - 1
    rows_f = packed.shape[0] // count
    order = [int(format(b, f"0{bits}b")[::-1], 2) for b in range(count)]
    buf = jnp.concatenate([packed[b * rows_f : (b + 1) * rows_f] for b in order], axis=0)
    for bit in range(bits):
        half = buf.shape[0] // 2
        mine = (me >> bit) & 1
        keep = lax.dynamic_slice_in_dim(buf, mine * half, half, 0)
        send = lax.dynamic_slice_in_dim(buf, (1 - mine) * half, half, 0)
        got = lax.ppermute(
            send.astype(jnp.bfloat16), "fsdp", [(i, i ^ (1 << bit)) for i in range(count)]
        )
        buf = keep + got.astype(jnp.float32)
    return split_columns(buf, widths)


def fsdp_gather(values):
    count = lax.axis_size("fsdp")
    me = lax.axis_index("fsdp")
    distance = 1
    while distance < count:
        got = lax.ppermute(values, "fsdp", [(i, i ^ distance) for i in range(count)])
        low = (me & distance) == 0
        values = jnp.concatenate(
            [jnp.where(low, values, got), jnp.where(low, got, values)]
        )
        distance *= 2
    return values


def all_sum(values):
    for axis in ("tensor", "fsdp"):
        distance = 1
        while distance < lax.axis_size(axis):
            values = values + lax.ppermute(
                values, axis, [(i, i ^ distance) for i in range(lax.axis_size(axis))]
            )
            distance *= 2
    return values


def exchange(values, distance):
    count = lax.axis_size("tensor")
    return lax.ppermute(values, "tensor", [(i, i ^ distance) for i in range(count)])


def token_gather(values):
    rows = values.shape[0]
    me = lax.axis_index("tensor")
    across = exchange(values, 2)
    pair = jnp.stack([values, across])
    beside = exchange(pair, 1)
    full = jnp.zeros((4 * rows,) + values.shape[1:], values.dtype)
    for part, place in ((values, me), (across, me ^ 2), (beside[0], me ^ 1), (beside[1], me ^ 3)):
        full = lax.dynamic_update_slice_in_dim(full, part, place * rows, 0)
    return full


def token_sum(term, rows):
    partial = term(jnp.int32(0), rows * lax.axis_size("tensor"))
    me = lax.axis_index("tensor")

    def block(place):
        return lax.dynamic_slice_in_dim(partial, place * rows, rows, 0)

    sent = jnp.stack([block(me ^ 1), block(me ^ 3)]).astype(jnp.bfloat16)
    got = exchange(sent, 1).astype(jnp.float32)
    mine = block(me) + got[0]
    other = (block(me ^ 2) + got[1]).astype(jnp.bfloat16)
    return mine + exchange(other, 2).astype(jnp.float32)


def shards(
    hidden,
    out_grad,
    lengths,
    q_weight,
    key_matrix,
    value_matrix,
    o_weight,
    gate_weight,
    up_weight,
    down_weight,
    input_gain,
    q_gain,
    k_gain,
    post_gain,
):
    split = lax.axis_size("tensor")
    rows = hidden.shape[0]
    group_rows = rows * split
    q_heads = q_weight.shape[1] // HEAD_SIZE
    kv_heads = key_matrix.shape[1] // HEAD_SIZE
    share = q_heads // kv_heads
    scale = HEAD_SIZE ** (-0.5)
    member = lax.axis_index("fsdp")
    slot = member // PIECES
    piece = member % PIECES
    lengths_row = lax.dynamic_index_in_dim(lengths, slot, 0, keepdims=False)
    ends = jnp.cumsum(lengths_row)
    group_place = piece_places(piece, group_rows)
    passed = group_place[:, None] >= ends[None, :]
    group_start = jnp.sum(jnp.where(passed, lengths_row[None, :], 0), axis=1)
    group_offset = group_place - group_start
    local_valid = lax.dynamic_slice_in_dim(
        group_place < ends[-1], lax.axis_index("tensor") * rows, rows, 0
    )
    fs = lax.axis_size("fsdp")
    gain_sizes = (input_gain.shape[0], q_gain.shape[0], k_gain.shape[0], post_gain.shape[0])
    gains_all = fsdp_gather(
        jnp.concatenate([input_gain, q_gain, k_gain, post_gain]).astype(jnp.bfloat16)
    ).reshape(fs, sum(gain_sizes))
    gain_in, gain_query, gain_keys, gain_post = [
        part.reshape(-1) for part in split_columns(gains_all, gain_sizes)
    ]
    kv_full = lax.all_gather(
        jnp.concatenate(
            [key_matrix.astype(jnp.bfloat16), value_matrix.astype(jnp.bfloat16)], axis=1
        ),
        "fsdp",
        axis=0,
        tiled=True,
    )
    w_key, w_value = split_columns(kv_full, (key_matrix.shape[1], value_matrix.shape[1]))
    w_query = lax.all_gather(q_weight.astype(jnp.bfloat16), "fsdp", axis=0, tiled=True)
    x_float = hidden.astype(jnp.float32)
    gain_first = gain_in.astype(jnp.float32)
    first_all = token_gather(rms_scale(x_float, gain_first).astype(jnp.bfloat16))
    cotangent = out_grad.astype(jnp.float32) * local_valid[:, None].astype(jnp.float32)
    cotangent_low, first_all = lax.optimization_barrier((cotangent.astype(jnp.bfloat16), first_all))
    mlp_grad_all = token_gather(cotangent_low)
    query_projected = jnp.dot(first_all, w_query, preferred_element_type=jnp.float32)
    key_projected = jnp.dot(first_all, w_key, preferred_element_type=jnp.float32)
    value_rows = (
        jnp.dot(first_all, w_value, preferred_element_type=jnp.float32)
        .astype(jnp.bfloat16)
        .reshape(group_rows, kv_heads, HEAD_SIZE)
    )
    gain_q = gain_query.astype(jnp.float32)
    gain_k = gain_keys.astype(jnp.float32)
    query_rope = (
        prepare_inputs(query_projected, gain_q, group_offset, q_heads)
        .astype(jnp.bfloat16)
        .reshape(group_rows, kv_heads, share, HEAD_SIZE)
    )
    key_rope = prepare_inputs(key_projected, gain_k, group_offset, kv_heads).astype(jnp.bfloat16)
    quarter = group_rows // 2
    query_start = jnp.broadcast_to(group_start[:, None], (group_rows, 128))
    query_t = jnp.transpose(query_rope, (1, 2, 0, 3))
    own_keys = jnp.transpose(key_rope, (1, 0, 2))
    own_values = jnp.transpose(value_rows, (1, 0, 2))
    moved = swapped(jnp.stack([own_keys, own_values]), "fsdp", 0)
    sums = jnp.zeros(query_t.shape, jnp.float32)
    totals = jnp.zeros(query_t.shape[:3] + (128,), jnp.float32)
    sums, totals = attention_forward(
        query_t, query_start, own_keys, own_values, sums, totals, piece, quarter, 0
    )
    sums, totals_t = attention_forward(
        query_t, query_start, moved[0], moved[1], sums, totals, piece, quarter, 1
    )
    mlp_grad_all, sums, totals_t = lax.optimization_barrier((mlp_grad_all, sums, totals_t))
    heads_t = sums / totals_t[..., :1]
    heads_out = jnp.transpose(heads_t, (2, 0, 1, 3))
    row_totals = jnp.transpose(totals_t[..., 0], (2, 0, 1))
    out_rows = heads_out.reshape(group_rows, q_heads * HEAD_SIZE).astype(jnp.bfloat16)

    mlp_full = lax.all_gather(
        jnp.concatenate(
            [
                gate_weight.astype(jnp.bfloat16),
                up_weight.astype(jnp.bfloat16),
                jnp.transpose(down_weight).astype(jnp.bfloat16),
                jnp.transpose(o_weight).astype(jnp.bfloat16),
            ],
            axis=1,
        ),
        "fsdp",
        axis=0,
        tiled=True,
    )
    w_gate, w_up, w_down_t, w_out = split_columns(
        mlp_full, (gate_weight.shape[1], up_weight.shape[1], down_weight.shape[0], o_weight.shape[0])
    )
    out_partial = contract_last(out_rows, w_out)
    late_grad_all, out_partial = lax.optimization_barrier((mlp_grad_all, out_partial))
    grad_act = jnp.dot(late_grad_all, w_down_t, preferred_element_type=jnp.float32)
    after_attn = x_float + token_sum(lambda start, count: out_partial, rows)
    grad_act, after_attn = lax.optimization_barrier((grad_act, after_attn))
    gain_second = gain_post.astype(jnp.float32)
    second_all = token_gather(rms_scale(after_attn, gain_second).astype(jnp.bfloat16))
    gate_out = jnp.dot(second_all, w_gate, preferred_element_type=jnp.float32)
    up_out = jnp.dot(second_all, w_up, preferred_element_type=jnp.float32)
    activated = (jax.nn.silu(gate_out) * up_out).astype(jnp.bfloat16)

    unused, pull_gate = jax.vjp(
        lambda gate_in, up_in: jax.nn.silu(gate_in) * up_in, gate_out, up_out
    )
    grad_gate, grad_up = pull_gate(grad_act)
    grad_gate = grad_gate.astype(jnp.bfloat16)
    grad_up = grad_up.astype(jnp.bfloat16)
    second_partial = contract_last(grad_gate, w_gate) + contract_last(grad_up, w_up)
    grad_inputs, second_partial = lax.optimization_barrier(
        ((mlp_grad_all, activated, second_all, grad_gate, grad_up), second_partial)
    )
    late_c, late_act, late_second, late_gate, late_up = grad_inputs
    down_grad_t = contract_rows(late_c, late_act)
    gate_grad = contract_rows(late_second, late_gate)
    up_grad = contract_rows(late_second, late_up)
    second_back = token_sum(lambda start, count: second_partial, rows)
    unused, pull_second = jax.vjp(rms_scale, after_attn, gain_second)
    norm_second_grad, post_gain_part = pull_second(second_back)
    residual_grad = cotangent + norm_second_grad
    weight_grads, residual_grad = lax.optimization_barrier(
        ((gate_grad, up_grad, down_grad_t), residual_grad)
    )
    gate_grad, up_grad, down_grad_t = weight_grads
    attn_grad_all = token_gather(residual_grad.astype(jnp.bfloat16))
    activated_late, attn_grad_all = lax.optimization_barrier((activated, attn_grad_all))
    down_rows = token_sum(lambda start, count: contract_last(activated_late, w_down_t), rows)
    out_weight_grad_t = contract_rows(attn_grad_all, out_rows)
    mlp_packed = jnp.concatenate(
        [g.astype(jnp.bfloat16) for g in (gate_grad, up_grad, down_grad_t, out_weight_grad_t)],
        axis=1,
    )
    head_grad = jnp.dot(attn_grad_all, w_out, preferred_element_type=jnp.float32).astype(
        jnp.bfloat16
    )
    head_float = head_grad.astype(jnp.float32).reshape(group_rows, kv_heads, share, HEAD_SIZE)
    scaled_grad = (head_float / row_totals[..., None]).astype(jnp.bfloat16)
    delta = jnp.sum(head_float * heads_out, axis=-1) / row_totals

    grad_t = jnp.transpose(scaled_grad, (1, 2, 0, 3))
    delta_t = jnp.broadcast_to(
        jnp.transpose(delta, (1, 2, 0))[..., None], (kv_heads, share, group_rows, 128)
    )
    mlp_packed, grad_t, delta_t = lax.optimization_barrier((mlp_packed, grad_t, delta_t))
    mlp_shards = split_columns(
        lax.psum_scatter(mlp_packed, "fsdp", scatter_dimension=0, tiled=True),
        [g.shape[1] for g in (gate_grad, up_grad, down_grad_t, out_weight_grad_t)],
    )
    mlp_shards = [part.astype(jnp.float32) for part in mlp_shards]
    dq_raw, dk_far, dv_far = attention_backward(
        query_t, grad_t, delta_t, query_start, moved[0], moved[1],
        jnp.zeros(query_t.shape, jnp.float32), piece, quarter, 1,
    )
    unseen = (piece == 1) & (jnp.arange(group_rows) >= quarter)
    far_grads = jnp.where(unseen[None, None, :, None], 0.0, jnp.stack([dk_far, dv_far]))
    returned = swapped(far_grads.astype(jnp.bfloat16), "fsdp", 0)
    down_rows, dq_raw = lax.optimization_barrier((down_rows, dq_raw))
    output = (after_attn + down_rows).astype(jnp.bfloat16)
    dq_raw, dk_own, dv_own = attention_backward(
        query_t, grad_t, delta_t, query_start, own_keys, own_values,
        dq_raw, piece, quarter, 0,
    )
    mlp_shards, dq_raw = lax.optimization_barrier((mlp_shards, dq_raw))
    grad_keys_total = jnp.transpose(dk_own + returned[0].astype(jnp.float32), (1, 0, 2))
    grad_values_total = jnp.transpose(dv_own + returned[1].astype(jnp.float32), (1, 0, 2))
    query_grads = jnp.transpose(dq_raw, (2, 0, 1, 3)) * scale
    query_grads = query_grads.reshape(group_rows, q_heads, HEAD_SIZE)
    unused, pull_query = jax.vjp(
        lambda projected, gain: prepare_inputs(projected, gain, group_offset, q_heads),
        query_projected,
        gain_q,
    )
    query_proj_grad, q_gain_part = pull_query(query_grads)
    unused, pull_key = jax.vjp(
        lambda projected, gain: prepare_inputs(projected, gain, group_offset, kv_heads),
        key_projected,
        gain_k,
    )
    key_proj_grad, k_gain_part = pull_key(grad_keys_total)
    query_low = query_proj_grad.astype(jnp.bfloat16)
    key_low = key_proj_grad.astype(jnp.bfloat16)
    value_low = grad_values_total.reshape(group_rows, kv_heads * HEAD_SIZE).astype(jnp.bfloat16)
    query_weight_grad = contract_rows(first_all, query_low)
    key_weight_grad = contract_rows(first_all, key_low)
    value_weight_grad = contract_rows(first_all, value_low)

    def first_term(start, count):
        return (
            contract_last(query_low, w_query)
            + contract_last(key_low, w_key)
            + contract_last(value_low, w_value)
        )

    first_back = token_sum(first_term, rows)
    unused, pull_first = jax.vjp(rms_scale, x_float, gain_first)
    norm_first_grad, input_gain_part = pull_first(first_back)
    input_grad = (residual_grad + norm_first_grad).astype(jnp.bfloat16)
    (query_shard,) = halving_scatter((query_weight_grad,))
    key_shard, value_shard = halving_scatter((key_weight_grad, value_weight_grad))
    gain_totals = all_sum(
        jnp.concatenate([input_gain_part, q_gain_part, k_gain_part, post_gain_part])
    )
    member_f = lax.axis_index("fsdp")
    sizes = (input_gain.shape[0], q_gain.shape[0], k_gain.shape[0], post_gain.shape[0])
    gain_shards = []
    at = 0
    for own in sizes:
        whole = own * fs
        gain_shards.append(lax.dynamic_slice_in_dim(gain_totals, at + member_f * own, own, 0))
        at += whole
    input_gain_shard, q_gain_shard, k_gain_shard, post_gain_shard = gain_shards
    gate_shard, up_shard, down_shard_t, out_shard_t = mlp_shards
    return (
        output,
        input_grad,
        query_shard,
        key_shard,
        value_shard,
        jnp.transpose(out_shard_t),
        gate_shard,
        up_shard,
        jnp.transpose(down_shard_t),
        input_gain_shard,
        q_gain_shard,
        k_gain_shard,
        post_gain_shard,
    )


def solution(mesh):
    return layer_program(mesh)


def layer_program(mesh):
    placed = (
        P(("fsdp", "tensor"), None),
        P(("fsdp", "tensor"), None),
        P(),
        P("fsdp", "tensor"),
        P("fsdp", "tensor"),
        P("fsdp", "tensor"),
        P("tensor", "fsdp"),
        P("fsdp", "tensor"),
        P("fsdp", "tensor"),
        P("tensor", "fsdp"),
        P("fsdp"),
        P("fsdp"),
        P("fsdp"),
        P("fsdp"),
    )
    return jax.shard_map(
        shards,
        mesh=mesh,
        in_specs=placed,
        out_specs=(
            P(("fsdp", "tensor"), None),
            P(("fsdp", "tensor"), None),
            P("fsdp", "tensor"),
            P("fsdp", "tensor"),
            P("fsdp", "tensor"),
            P("tensor", "fsdp"),
            P("fsdp", "tensor"),
            P("fsdp", "tensor"),
            P("tensor", "fsdp"),
            P("fsdp"),
            P("fsdp"),
            P("fsdp"),
            P("fsdp"),
        ),
        check_vma=False,
    )
```

```python
import functools

import numpy as np
import jax
import jax.numpy as jnp
from jax import lax
from jax.experimental import pallas as pl
from jax.experimental.pallas import tpu as pltpu
from jax.sharding import PartitionSpec as P


HEAD_SIZE = 128
TRANS_B = (((1,), (1,)), ((), ()))
TRANS_A = (((0,), (0,)), ((), ()))


def _own_place(p, quarter, r):
    return (p * quarter + r) if r < quarter else ((3 - p) * quarter + r - quarter)


def _far_place(p, quarter, r):
    return ((1 - p) * quarter + r) if r < quarter else ((2 + p) * quarter + r - quarter)


def _pair_tables(p, quarter, block, by_key, source):
    rows = 2 * quarter
    count = rows // block
    kmap = {}
    for src, fn in ((0, _own_place), (1, _far_place)):
        for j in range(count):
            kmap[fn(p, quarter, j * block) // block] = (src, j)
    pairs = []
    for j in range(count):
        qpb = _own_place(p, quarter, j * block) // block
        for kpb in range(qpb + 1):
            if kmap[kpb][0] == source:
                pairs.append((j, qpb, kpb))
    if by_key:
        pairs.sort(key=lambda t: (t[2], t[0]))
    group = [t[2] if by_key else t[0] for t in pairs]
    size = len(pairs)
    first = [1 if n == 0 or group[n - 1] != group[n] else 0 for n in range(size)]
    last = [1 if n == size - 1 or group[n + 1] != group[n] else 0 for n in range(size)]
    return np.array(
        [
            [t[0] for t in pairs],
            [t[1] for t in pairs],
            [t[2] for t in pairs],
            [kmap[t[2]][0] for t in pairs],
            [kmap[t[2]][1] for t in pairs],
            first,
            last,
        ],
        np.int32,
    )


def pair_tables(piece, quarter, block, by_key, source):
    t0 = _pair_tables(0, quarter, block, by_key, source)
    t1 = _pair_tables(1, quarter, block, by_key, source)
    assert t0.shape == t1.shape
    return jnp.where(piece == 0, jnp.asarray(t0), jnp.asarray(t1))


def _mask(qpb, kpb, qs, block):
    qp = qpb * block + lax.broadcasted_iota(jnp.int32, (block, block), 0)
    kp = kpb * block + lax.broadcasted_iota(jnp.int32, (block, block), 1)
    start = jnp.tile(qs, (1, block // 128))
    return (kp >= start) & (kp <= qp)


def _fwd_kernel(tab_ref, q_ref, qs_ref, k_ref, v_ref, a_in_ref, l_in_ref, a_ref, l_ref, acc_ref, sum_ref, *, scale, block):
    n = pl.program_id(1)
    share = q_ref.shape[1]

    @pl.when(tab_ref[5, n] == 1)
    def _():
        acc_ref[...] = a_in_ref[0].reshape(share * block, HEAD_SIZE)
        sum_ref[...] = l_in_ref[0][:, :, :1]

    q = q_ref[0].reshape(share * block, HEAD_SIZE)
    k = k_ref[0]
    v = v_ref[0]
    s = lax.dot_general(q, k, TRANS_B, preferred_element_type=jnp.float32) * scale
    allowed = _mask(tab_ref[1, n], tab_ref[2, n], qs_ref[...], block)
    e = jnp.where(allowed[None], jnp.exp(s.reshape(share, block, block)), 0.0)
    sum_ref[...] += jnp.sum(e, axis=-1, keepdims=True)
    acc_ref[...] += jnp.dot(
        e.reshape(share * block, block).astype(jnp.bfloat16), v, preferred_element_type=jnp.float32
    )

    @pl.when(tab_ref[6, n] == 1)
    def _():
        a_ref[0] = acc_ref[...].reshape(share, block, HEAD_SIZE)
        l_ref[0] = jnp.broadcast_to(sum_ref[...], (share, block, 128))


def attention_forward(q, qs, keys, values, a_in, l_in, piece, quarter, source, block=512):
    kvh, share, _, _ = q.shape
    tab = pair_tables(piece, quarter, block, False, source)
    npairs = tab.shape[1]
    scale = HEAD_SIZE ** (-0.5)
    row_spec = pl.BlockSpec((1, share, block, HEAD_SIZE), lambda h, n, t: (h, 0, t[0, n], 0))
    lane_spec = pl.BlockSpec((1, share, block, 128), lambda h, n, t: (h, 0, t[0, n], 0))
    key_spec = pl.BlockSpec((1, block, HEAD_SIZE), lambda h, n, t: (h, t[4, n], 0))
    grid_spec = pltpu.PrefetchScalarGridSpec(
        num_scalar_prefetch=1,
        grid=(kvh, npairs),
        in_specs=[
            row_spec,
            pl.BlockSpec((block, 128), lambda h, n, t: (t[0, n], 0)),
            key_spec,
            key_spec,
            row_spec,
            lane_spec,
        ],
        out_specs=[row_spec, lane_spec],
        scratch_shapes=[
            pltpu.VMEM((share * block, HEAD_SIZE), jnp.float32),
            pltpu.VMEM((share, block, 1), jnp.float32),
        ],
    )
    flops = 4 * kvh * npairs * share * block * block * HEAD_SIZE
    return pl.pallas_call(
        functools.partial(_fwd_kernel, scale=scale, block=block),
        grid_spec=grid_spec,
        out_shape=[
            jax.ShapeDtypeStruct(a_in.shape, jnp.float32),
            jax.ShapeDtypeStruct(l_in.shape, jnp.float32),
        ],
        input_output_aliases={5: 0, 6: 1},
        compiler_params=pltpu.CompilerParams(
            dimension_semantics=("arbitrary", "arbitrary"), vmem_limit_bytes=48 * 1024 * 1024
        ),
        cost_estimate=pl.CostEstimate(
            flops=flops,
            transcendentals=kvh * npairs * share * block * block,
            bytes_accessed=kvh * npairs * (8 * block * HEAD_SIZE * 2),
        ),
        name="attn_fwd",
    )(tab, q, qs, keys, values, a_in, l_in)


def _bwd_kernel(tab_ref, q_ref, h_ref, dl_ref, qs_ref, k_ref, v_ref, dq_in_ref, dq_ref, dk_ref, dv_ref, dk_acc, dv_acc, *, scale, block):
    n = pl.program_id(1)
    share = q_ref.shape[1]

    @pl.when(n == 0)
    def _():
        dq_ref[...] = dq_in_ref[...]

    @pl.when(tab_ref[5, n] == 1)
    def _():
        dk_acc[...] = jnp.zeros(dk_acc.shape, dk_acc.dtype)
        dv_acc[...] = jnp.zeros(dv_acc.shape, dv_acc.dtype)

    q = q_ref[0].reshape(share * block, HEAD_SIZE)
    hh = h_ref[0].reshape(share * block, HEAD_SIZE)
    k = k_ref[0]
    v = v_ref[0]
    s = lax.dot_general(q, k, TRANS_B, preferred_element_type=jnp.float32) * scale
    allowed = _mask(tab_ref[1, n], tab_ref[2, n], qs_ref[...], block)
    e = jnp.where(allowed[None], jnp.exp(s.reshape(share, block, block)), 0.0)
    dp = lax.dot_general(hh, v, TRANS_B, preferred_element_type=jnp.float32).reshape(share, block, block)
    delta = jnp.tile(dl_ref[0], (1, 1, block // 128))
    ds = (e * (dp - delta)).reshape(share * block, block).astype(jnp.bfloat16)
    rows = pl.ds(pl.multiple_of(tab_ref[0, n] * block, block), block)
    dq_ref[0, :, rows, :] += jnp.dot(ds, k, preferred_element_type=jnp.float32).reshape(share, block, HEAD_SIZE)
    dk_acc[...] += lax.dot_general(ds, q, TRANS_A, preferred_element_type=jnp.float32)
    dv_acc[...] += lax.dot_general(
        e.reshape(share * block, block).astype(jnp.bfloat16), hh, TRANS_A, preferred_element_type=jnp.float32
    )

    @pl.when(tab_ref[6, n] == 1)
    def _():
        dk_ref[0] = dk_acc[...] * scale
        dv_ref[0] = dv_acc[...]


def attention_backward(q, hgrad, delta, qs, keys, values, dq_in, piece, quarter, source, block=512):
    kvh, share, rows, _ = q.shape
    tab = pair_tables(piece, quarter, block, True, source)
    npairs = tab.shape[1]
    scale = HEAD_SIZE ** (-0.5)
    row_spec = pl.BlockSpec((1, share, block, HEAD_SIZE), lambda h, n, t: (h, 0, t[0, n], 0))
    key_spec = pl.BlockSpec((1, block, HEAD_SIZE), lambda h, n, t: (h, t[4, n], 0))
    full_spec = pl.BlockSpec((1, share, rows, HEAD_SIZE), lambda h, n, t: (h, 0, 0, 0))
    grid_spec = pltpu.PrefetchScalarGridSpec(
        num_scalar_prefetch=1,
        grid=(kvh, npairs),
        in_specs=[
            row_spec,
            row_spec,
            pl.BlockSpec((1, share, block, 128), lambda h, n, t: (h, 0, t[0, n], 0)),
            pl.BlockSpec((block, 128), lambda h, n, t: (t[0, n], 0)),
            key_spec,
            key_spec,
            full_spec,
        ],
        out_specs=[full_spec, key_spec, key_spec],
        scratch_shapes=[
            pltpu.VMEM((block, HEAD_SIZE), jnp.float32),
            pltpu.VMEM((block, HEAD_SIZE), jnp.float32),
        ],
    )
    flops = 10 * kvh * npairs * share * block * block * HEAD_SIZE
    return pl.pallas_call(
        functools.partial(_bwd_kernel, scale=scale, block=block),
        grid_spec=grid_spec,
        out_shape=[
            jax.ShapeDtypeStruct(dq_in.shape, jnp.float32),
            jax.ShapeDtypeStruct(keys.shape, jnp.float32),
            jax.ShapeDtypeStruct(values.shape, jnp.float32),
        ],
        input_output_aliases={7: 0},
        compiler_params=pltpu.CompilerParams(
            dimension_semantics=("arbitrary", "arbitrary"), vmem_limit_bytes=56 * 1024 * 1024
        ),
        cost_estimate=pl.CostEstimate(
            flops=flops,
            transcendentals=kvh * npairs * share * block * block,
            bytes_accessed=kvh * npairs * (10 * block * HEAD_SIZE * 2),
        ),
        name="attn_bwd",
    )(tab, q, hgrad, delta, qs, keys, values, dq_in)


PIECES = 2


EPSILON = 1e-06
THETA = 1000000.0


def swapped(shard, axis, distance):
    return lax.ppermute(shard, axis, [(i, i ^ 1 << distance) for i in range(lax.axis_size(axis))])


def rms_scale(values, gain):
    inverse = lax.rsqrt(jnp.mean(values * values, axis=-1, keepdims=True) + EPSILON)
    return values * inverse * gain


def rotary(values, start_offset):
    half = values.shape[-1] // 2
    frequency = THETA ** (-(jnp.arange(half, dtype=jnp.float32) * 2.0 / values.shape[-1]))
    angle = start_offset.astype(jnp.float32)[:, None] * frequency[None, :]
    cosine = jnp.cos(angle)[:, None, :]
    sine = jnp.sin(angle)[:, None, :]
    first = values[..., :half]
    second = values[..., half:]
    return jnp.concatenate(
        [first * cosine - second * sine, second * cosine + first * sine], axis=-1
    )


def prepare_inputs(projected, gain, start_offset, head_groups):
    shaped = projected.reshape(projected.shape[0], head_groups, -1)
    return rotary(rms_scale(shaped, gain), start_offset)


def piece_places(which, group_rows):
    quarter = group_rows // 2
    local = jnp.arange(group_rows, dtype=jnp.int32)
    chosen = jnp.where(local < quarter, which, 3 - which)
    return chosen * quarter + local % quarter


def contract_rows(left, right):
    return lax.dot_general(
        left, right, (((0,), (0,)), ((), ())), preferred_element_type=jnp.float32
    )


def contract_last(left, right):
    return lax.dot_general(
        left, right, (((1,), (1,)), ((), ())), preferred_element_type=jnp.float32
    )


def split_columns(full, widths):
    parts = []
    at = 0
    for width in widths:
        parts.append(full[:, at : at + width])
        at += width
    return parts


def halving_scatter(grads):
    widths = [g.shape[1] for g in grads]
    packed = jnp.concatenate(grads, axis=1)
    count = lax.axis_size("fsdp")
    me = lax.axis_index("fsdp")
    bits = count.bit_length() - 1
    rows_f = packed.shape[0] // count
    order = [int(format(b, f"0{bits}b")[::-1], 2) for b in range(count)]
    buf = jnp.concatenate([packed[b * rows_f : (b + 1) * rows_f] for b in order], axis=0)
    for bit in range(bits):
        half = buf.shape[0] // 2
        mine = (me >> bit) & 1
        keep = lax.dynamic_slice_in_dim(buf, mine * half, half, 0)
        send = lax.dynamic_slice_in_dim(buf, (1 - mine) * half, half, 0)
        got = lax.ppermute(
            send.astype(jnp.bfloat16), "fsdp", [(i, i ^ (1 << bit)) for i in range(count)]
        )
        buf = keep + got.astype(jnp.float32)
    return split_columns(buf, widths)


def fsdp_gather(values):
    count = lax.axis_size("fsdp")
    me = lax.axis_index("fsdp")
    distance = 1
    while distance < count:
        got = lax.ppermute(values, "fsdp", [(i, i ^ distance) for i in range(count)])
        low = (me & distance) == 0
        values = jnp.concatenate(
            [jnp.where(low, values, got), jnp.where(low, got, values)]
        )
        distance *= 2
    return values


def all_sum(values):
    for axis in ("tensor", "fsdp"):
        distance = 1
        while distance < lax.axis_size(axis):
            values = values + lax.ppermute(
                values, axis, [(i, i ^ distance) for i in range(lax.axis_size(axis))]
            )
            distance *= 2
    return values


def exchange(values, distance):
    count = lax.axis_size("tensor")
    return lax.ppermute(values, "tensor", [(i, i ^ distance) for i in range(count)])


def token_gather(values):
    return finish_gather(values, exchange(values, 2))


def finish_gather(values, across):
    rows = values.shape[0]
    me = lax.axis_index("tensor")
    pair = jnp.stack([values, across])
    beside = exchange(pair, 1)
    full = jnp.zeros((4 * rows,) + values.shape[1:], values.dtype)
    for part, place in ((values, me), (across, me ^ 2), (beside[0], me ^ 1), (beside[1], me ^ 3)):
        full = lax.dynamic_update_slice_in_dim(full, part, place * rows, 0)
    return full


def token_sum(term, rows):
    partial = term(jnp.int32(0), rows * lax.axis_size("tensor"))
    me = lax.axis_index("tensor")

    def block(place):
        return lax.dynamic_slice_in_dim(partial, place * rows, rows, 0)

    sent = jnp.stack([block(me ^ 1), block(me ^ 3)]).astype(jnp.bfloat16)
    got = exchange(sent, 1).astype(jnp.float32)
    mine = block(me) + got[0]
    other = (block(me ^ 2) + got[1]).astype(jnp.bfloat16)
    return mine + exchange(other, 2).astype(jnp.float32)


def shards(
    hidden,
    out_grad,
    lengths,
    q_weight,
    key_matrix,
    value_matrix,
    o_weight,
    gate_weight,
    up_weight,
    down_weight,
    input_gain,
    q_gain,
    k_gain,
    post_gain,
):
    split = lax.axis_size("tensor")
    rows = hidden.shape[0]
    group_rows = rows * split
    q_heads = q_weight.shape[1] // HEAD_SIZE
    kv_heads = key_matrix.shape[1] // HEAD_SIZE
    share = q_heads // kv_heads
    scale = HEAD_SIZE ** (-0.5)
    member = lax.axis_index("fsdp")
    slot = member // PIECES
    piece = member % PIECES
    lengths_row = lax.dynamic_index_in_dim(lengths, slot, 0, keepdims=False)
    ends = jnp.cumsum(lengths_row)
    group_place = piece_places(piece, group_rows)
    passed = group_place[:, None] >= ends[None, :]
    group_start = jnp.sum(jnp.where(passed, lengths_row[None, :], 0), axis=1)
    group_offset = group_place - group_start
    local_valid = lax.dynamic_slice_in_dim(
        group_place < ends[-1], lax.axis_index("tensor") * rows, rows, 0
    )
    fs = lax.axis_size("fsdp")
    gain_sizes = (input_gain.shape[0], q_gain.shape[0], k_gain.shape[0], post_gain.shape[0])
    gains_all = fsdp_gather(
        jnp.concatenate([input_gain, q_gain, k_gain, post_gain]).astype(jnp.bfloat16)
    ).reshape(fs, sum(gain_sizes))
    gain_in, gain_query, gain_keys, gain_post = [
        part.reshape(-1) for part in split_columns(gains_all, gain_sizes)
    ]
    kv_full = lax.all_gather(
        jnp.concatenate(
            [key_matrix.astype(jnp.bfloat16), value_matrix.astype(jnp.bfloat16)], axis=1
        ),
        "fsdp",
        axis=0,
        tiled=True,
    )
    w_key, w_value = split_columns(kv_full, (key_matrix.shape[1], value_matrix.shape[1]))
    w_query = lax.all_gather(q_weight.astype(jnp.bfloat16), "fsdp", axis=0, tiled=True)
    x_float = hidden.astype(jnp.float32)
    gain_first = gain_in.astype(jnp.float32)
    first_all = token_gather(rms_scale(x_float, gain_first).astype(jnp.bfloat16))
    cotangent = out_grad.astype(jnp.float32) * local_valid[:, None].astype(jnp.float32)
    cotangent_low, first_all = lax.optimization_barrier((cotangent.astype(jnp.bfloat16), first_all))
    cotangent_across = exchange(cotangent_low, 2)
    query_projected = jnp.dot(first_all, w_query, preferred_element_type=jnp.float32)
    key_projected = jnp.dot(first_all, w_key, preferred_element_type=jnp.float32)
    value_rows = (
        jnp.dot(first_all, w_value, preferred_element_type=jnp.float32)
        .astype(jnp.bfloat16)
        .reshape(group_rows, kv_heads, HEAD_SIZE)
    )
    gain_q = gain_query.astype(jnp.float32)
    gain_k = gain_keys.astype(jnp.float32)
    query_rope = (
        prepare_inputs(query_projected, gain_q, group_offset, q_heads)
        .astype(jnp.bfloat16)
        .reshape(group_rows, kv_heads, share, HEAD_SIZE)
    )
    key_rope = prepare_inputs(key_projected, gain_k, group_offset, kv_heads).astype(jnp.bfloat16)
    quarter = group_rows // 2
    query_start = jnp.broadcast_to(group_start[:, None], (group_rows, 128))
    query_t = jnp.transpose(query_rope, (1, 2, 0, 3))
    own_keys = jnp.transpose(key_rope, (1, 0, 2))
    own_values = jnp.transpose(value_rows, (1, 0, 2))
    moved = swapped(jnp.stack([own_keys, own_values]), "fsdp", 0)
    sums = jnp.zeros(query_t.shape, jnp.float32)
    totals = jnp.zeros(query_t.shape[:3] + (128,), jnp.float32)
    sums, totals = attention_forward(
        query_t, query_start, own_keys, own_values, sums, totals, piece, quarter, 0
    )
    cotangent_across, sums, totals = lax.optimization_barrier((cotangent_across, sums, totals))
    mlp_grad_all = finish_gather(cotangent_low, cotangent_across)
    sums, totals_t = attention_forward(
        query_t, query_start, moved[0], moved[1], sums, totals, piece, quarter, 1
    )
    mlp_grad_all, sums, totals_t = lax.optimization_barrier((mlp_grad_all, sums, totals_t))
    heads_t = sums / totals_t[..., :1]
    heads_out = jnp.transpose(heads_t, (2, 0, 1, 3))
    row_totals = jnp.transpose(totals_t[..., 0], (2, 0, 1))
    out_rows = heads_out.reshape(group_rows, q_heads * HEAD_SIZE).astype(jnp.bfloat16)

    mlp_full = lax.all_gather(
        jnp.concatenate(
            [
                gate_weight.astype(jnp.bfloat16),
                up_weight.astype(jnp.bfloat16),
                jnp.transpose(down_weight).astype(jnp.bfloat16),
                jnp.transpose(o_weight).astype(jnp.bfloat16),
            ],
            axis=1,
        ),
        "fsdp",
        axis=0,
        tiled=True,
    )
    w_gate, w_up, w_down_t, w_out = split_columns(
        mlp_full, (gate_weight.shape[1], up_weight.shape[1], down_weight.shape[0], o_weight.shape[0])
    )
    out_partial = contract_last(out_rows, w_out)
    late_grad_all, out_partial = lax.optimization_barrier((mlp_grad_all, out_partial))
    grad_act = jnp.dot(late_grad_all, w_down_t, preferred_element_type=jnp.float32)
    after_attn = x_float + token_sum(lambda start, count: out_partial, rows)
    grad_act, after_attn = lax.optimization_barrier((grad_act, after_attn))
    gain_second = gain_post.astype(jnp.float32)
    second_all = token_gather(rms_scale(after_attn, gain_second).astype(jnp.bfloat16))
    gate_out = jnp.dot(second_all, w_gate, preferred_element_type=jnp.float32)
    up_out = jnp.dot(second_all, w_up, preferred_element_type=jnp.float32)
    activated = (jax.nn.silu(gate_out) * up_out).astype(jnp.bfloat16)

    unused, pull_gate = jax.vjp(
        lambda gate_in, up_in: jax.nn.silu(gate_in) * up_in, gate_out, up_out
    )
    grad_gate, grad_up = pull_gate(grad_act)
    grad_gate = grad_gate.astype(jnp.bfloat16)
    grad_up = grad_up.astype(jnp.bfloat16)
    second_partial = contract_last(grad_gate, w_gate) + contract_last(grad_up, w_up)
    grad_inputs, second_partial = lax.optimization_barrier(
        ((mlp_grad_all, activated, second_all, grad_gate, grad_up), second_partial)
    )
    late_c, late_act, late_second, late_gate, late_up = grad_inputs
    down_grad_t = contract_rows(late_c, late_act)
    gate_grad = contract_rows(late_second, late_gate)
    up_grad = contract_rows(late_second, late_up)
    second_back = token_sum(lambda start, count: second_partial, rows)
    unused, pull_second = jax.vjp(rms_scale, after_attn, gain_second)
    norm_second_grad, post_gain_part = pull_second(second_back)
    residual_grad = cotangent + norm_second_grad
    weight_grads, residual_grad = lax.optimization_barrier(
        ((gate_grad, up_grad, down_grad_t), residual_grad)
    )
    gate_grad, up_grad, down_grad_t = weight_grads
    attn_grad_all = token_gather(residual_grad.astype(jnp.bfloat16))
    activated_late, attn_grad_all = lax.optimization_barrier((activated, attn_grad_all))
    down_rows = token_sum(lambda start, count: contract_last(activated_late, w_down_t), rows)
    out_weight_grad_t = contract_rows(attn_grad_all, out_rows)
    mlp_packed = jnp.concatenate(
        [g.astype(jnp.bfloat16) for g in (gate_grad, up_grad, down_grad_t, out_weight_grad_t)],
        axis=1,
    )
    head_grad = jnp.dot(attn_grad_all, w_out, preferred_element_type=jnp.float32).astype(
        jnp.bfloat16
    )
    head_float = head_grad.astype(jnp.float32).reshape(group_rows, kv_heads, share, HEAD_SIZE)
    scaled_grad = (head_float / row_totals[..., None]).astype(jnp.bfloat16)
    delta = jnp.sum(head_float * heads_out, axis=-1) / row_totals

    grad_t = jnp.transpose(scaled_grad, (1, 2, 0, 3))
    delta_t = jnp.broadcast_to(
        jnp.transpose(delta, (1, 2, 0))[..., None], (kv_heads, share, group_rows, 128)
    )
    mlp_packed, grad_t, delta_t = lax.optimization_barrier((mlp_packed, grad_t, delta_t))
    mlp_shards = split_columns(
        lax.psum_scatter(mlp_packed, "fsdp", scatter_dimension=0, tiled=True),
        [g.shape[1] for g in (gate_grad, up_grad, down_grad_t, out_weight_grad_t)],
    )
    mlp_shards = [part.astype(jnp.float32) for part in mlp_shards]
    dq_raw, dk_far, dv_far = attention_backward(
        query_t, grad_t, delta_t, query_start, moved[0], moved[1],
        jnp.zeros(query_t.shape, jnp.float32), piece, quarter, 1,
    )
    unseen = (piece == 1) & (jnp.arange(group_rows) >= quarter)
    far_grads = jnp.where(unseen[None, None, :, None], 0.0, jnp.stack([dk_far, dv_far]))
    returned = swapped(far_grads.astype(jnp.bfloat16), "fsdp", 0)
    down_rows, dq_raw = lax.optimization_barrier((down_rows, dq_raw))
    output = (after_attn + down_rows).astype(jnp.bfloat16)
    dq_raw, dk_own, dv_own = attention_backward(
        query_t, grad_t, delta_t, query_start, own_keys, own_values,
        dq_raw, piece, quarter, 0,
    )
    mlp_shards, dq_raw = lax.optimization_barrier((mlp_shards, dq_raw))
    grad_keys_total = jnp.transpose(dk_own + returned[0].astype(jnp.float32), (1, 0, 2))
    grad_values_total = jnp.transpose(dv_own + returned[1].astype(jnp.float32), (1, 0, 2))
    query_grads = jnp.transpose(dq_raw, (2, 0, 1, 3)) * scale
    query_grads = query_grads.reshape(group_rows, q_heads, HEAD_SIZE)
    unused, pull_query = jax.vjp(
        lambda projected, gain: prepare_inputs(projected, gain, group_offset, q_heads),
        query_projected,
        gain_q,
    )
    query_proj_grad, q_gain_part = pull_query(query_grads)
    unused, pull_key = jax.vjp(
        lambda projected, gain: prepare_inputs(projected, gain, group_offset, kv_heads),
        key_projected,
        gain_k,
    )
    key_proj_grad, k_gain_part = pull_key(grad_keys_total)
    query_low = query_proj_grad.astype(jnp.bfloat16)
    key_low = key_proj_grad.astype(jnp.bfloat16)
    value_low = grad_values_total.reshape(group_rows, kv_heads * HEAD_SIZE).astype(jnp.bfloat16)
    query_weight_grad = contract_rows(first_all, query_low)
    key_weight_grad = contract_rows(first_all, key_low)
    value_weight_grad = contract_rows(first_all, value_low)

    def first_term(start, count):
        return (
            contract_last(query_low, w_query)
            + contract_last(key_low, w_key)
            + contract_last(value_low, w_value)
        )

    first_back = token_sum(first_term, rows)
    unused, pull_first = jax.vjp(rms_scale, x_float, gain_first)
    norm_first_grad, input_gain_part = pull_first(first_back)
    input_grad = (residual_grad + norm_first_grad).astype(jnp.bfloat16)
    (query_shard,) = halving_scatter((query_weight_grad,))
    key_shard, value_shard = halving_scatter((key_weight_grad, value_weight_grad))
    gain_totals = all_sum(
        jnp.concatenate([input_gain_part, q_gain_part, k_gain_part, post_gain_part])
    )
    member_f = lax.axis_index("fsdp")
    sizes = (input_gain.shape[0], q_gain.shape[0], k_gain.shape[0], post_gain.shape[0])
    gain_shards = []
    at = 0
    for own in sizes:
        whole = own * fs
        gain_shards.append(lax.dynamic_slice_in_dim(gain_totals, at + member_f * own, own, 0))
        at += whole
    input_gain_shard, q_gain_shard, k_gain_shard, post_gain_shard = gain_shards
    gate_shard, up_shard, down_shard_t, out_shard_t = mlp_shards
    return (
        output,
        input_grad,
        query_shard,
        key_shard,
        value_shard,
        jnp.transpose(out_shard_t),
        gate_shard,
        up_shard,
        jnp.transpose(down_shard_t),
        input_gain_shard,
        q_gain_shard,
        k_gain_shard,
        post_gain_shard,
    )


def solution(mesh):
    return layer_program(mesh)


def layer_program(mesh):
    placed = (
        P(("fsdp", "tensor"), None),
        P(("fsdp", "tensor"), None),
        P(),
        P("fsdp", "tensor"),
        P("fsdp", "tensor"),
        P("fsdp", "tensor"),
        P("tensor", "fsdp"),
        P("fsdp", "tensor"),
        P("fsdp", "tensor"),
        P("tensor", "fsdp"),
        P("fsdp"),
        P("fsdp"),
        P("fsdp"),
        P("fsdp"),
    )
    return jax.shard_map(
        shards,
        mesh=mesh,
        in_specs=placed,
        out_specs=(
            P(("fsdp", "tensor"), None),
            P(("fsdp", "tensor"), None),
            P("fsdp", "tensor"),
            P("fsdp", "tensor"),
            P("fsdp", "tensor"),
            P("tensor", "fsdp"),
            P("fsdp", "tensor"),
            P("fsdp", "tensor"),
            P("tensor", "fsdp"),
            P("fsdp"),
            P("fsdp"),
            P("fsdp"),
            P("fsdp"),
        ),
        check_vma=False,
    )
```

```python
import functools

import numpy as np
import jax
import jax.numpy as jnp
from jax import lax
from jax.experimental import pallas as pl
from jax.experimental.pallas import tpu as pltpu
from jax.sharding import PartitionSpec as P


HEAD_SIZE = 128
TRANS_B = (((1,), (1,)), ((), ()))
TRANS_A = (((0,), (0,)), ((), ()))


def _own_place(p, quarter, r):
    return (p * quarter + r) if r < quarter else ((3 - p) * quarter + r - quarter)


def _far_place(p, quarter, r):
    return ((1 - p) * quarter + r) if r < quarter else ((2 + p) * quarter + r - quarter)


def _pair_tables(p, quarter, block, by_key, source):
    rows = 2 * quarter
    count = rows // block
    kmap = {}
    for src, fn in ((0, _own_place), (1, _far_place)):
        for j in range(count):
            kmap[fn(p, quarter, j * block) // block] = (src, j)
    pairs = []
    for j in range(count):
        qpb = _own_place(p, quarter, j * block) // block
        for kpb in range(qpb + 1):
            if kmap[kpb][0] == source:
                pairs.append((j, qpb, kpb))
    if by_key:
        pairs.sort(key=lambda t: (t[2], t[0]))
    group = [t[2] if by_key else t[0] for t in pairs]
    size = len(pairs)
    first = [1 if n == 0 or group[n - 1] != group[n] else 0 for n in range(size)]
    last = [1 if n == size - 1 or group[n + 1] != group[n] else 0 for n in range(size)]
    return np.array(
        [
            [t[0] for t in pairs],
            [t[1] for t in pairs],
            [t[2] for t in pairs],
            [kmap[t[2]][0] for t in pairs],
            [kmap[t[2]][1] for t in pairs],
            first,
            last,
        ],
        np.int32,
    )


def pair_tables(piece, quarter, block, by_key, source):
    t0 = _pair_tables(0, quarter, block, by_key, source)
    t1 = _pair_tables(1, quarter, block, by_key, source)
    assert t0.shape == t1.shape
    return jnp.where(piece == 0, jnp.asarray(t0), jnp.asarray(t1))


def _mask(qpb, kpb, qs, block):
    qp = qpb * block + lax.broadcasted_iota(jnp.int32, (block, block), 0)
    kp = kpb * block + lax.broadcasted_iota(jnp.int32, (block, block), 1)
    start = jnp.tile(qs, (1, block // 128))
    return (kp >= start) & (kp <= qp)


def _fwd_kernel(tab_ref, q_ref, qs_ref, k_ref, v_ref, a_in_ref, l_in_ref, a_ref, l_ref, acc_ref, sum_ref, *, scale, block):
    n = pl.program_id(1)
    share = q_ref.shape[1]

    @pl.when(tab_ref[5, n] == 1)
    def _():
        acc_ref[...] = a_in_ref[0].reshape(share * block, HEAD_SIZE)
        sum_ref[...] = l_in_ref[0][:, :, :1]

    q = q_ref[0].reshape(share * block, HEAD_SIZE)
    k = k_ref[0]
    v = v_ref[0]
    s = lax.dot_general(q, k, TRANS_B, preferred_element_type=jnp.float32) * scale
    allowed = _mask(tab_ref[1, n], tab_ref[2, n], qs_ref[...], block)
    e = jnp.where(allowed[None], jnp.exp(s.reshape(share, block, block)), 0.0)
    sum_ref[...] += jnp.sum(e, axis=-1, keepdims=True)
    acc_ref[...] += jnp.dot(
        e.reshape(share * block, block).astype(jnp.bfloat16), v, preferred_element_type=jnp.float32
    )

    @pl.when(tab_ref[6, n] == 1)
    def _():
        a_ref[0] = acc_ref[...].reshape(share, block, HEAD_SIZE)
        l_ref[0] = jnp.broadcast_to(sum_ref[...], (share, block, 128))


def attention_forward(q, qs, keys, values, a_in, l_in, piece, quarter, source, block=512):
    kvh, share, _, _ = q.shape
    tab = pair_tables(piece, quarter, block, False, source)
    npairs = tab.shape[1]
    scale = HEAD_SIZE ** (-0.5)
    row_spec = pl.BlockSpec((1, share, block, HEAD_SIZE), lambda h, n, t: (h, 0, t[0, n], 0))
    lane_spec = pl.BlockSpec((1, share, block, 128), lambda h, n, t: (h, 0, t[0, n], 0))
    key_spec = pl.BlockSpec((1, block, HEAD_SIZE), lambda h, n, t: (h, t[4, n], 0))
    grid_spec = pltpu.PrefetchScalarGridSpec(
        num_scalar_prefetch=1,
        grid=(kvh, npairs),
        in_specs=[
            row_spec,
            pl.BlockSpec((block, 128), lambda h, n, t: (t[0, n], 0)),
            key_spec,
            key_spec,
            row_spec,
            lane_spec,
        ],
        out_specs=[row_spec, lane_spec],
        scratch_shapes=[
            pltpu.VMEM((share * block, HEAD_SIZE), jnp.float32),
            pltpu.VMEM((share, block, 1), jnp.float32),
        ],
    )
    flops = 4 * kvh * npairs * share * block * block * HEAD_SIZE
    return pl.pallas_call(
        functools.partial(_fwd_kernel, scale=scale, block=block),
        grid_spec=grid_spec,
        out_shape=[
            jax.ShapeDtypeStruct(a_in.shape, jnp.float32),
            jax.ShapeDtypeStruct(l_in.shape, jnp.float32),
        ],
        input_output_aliases={5: 0, 6: 1},
        compiler_params=pltpu.CompilerParams(
            dimension_semantics=("arbitrary", "arbitrary"), vmem_limit_bytes=48 * 1024 * 1024
        ),
        cost_estimate=pl.CostEstimate(
            flops=flops,
            transcendentals=kvh * npairs * share * block * block,
            bytes_accessed=kvh * npairs * (8 * block * HEAD_SIZE * 2),
        ),
        name="attn_fwd",
    )(tab, q, qs, keys, values, a_in, l_in)


def _bwd_kernel(tab_ref, q_ref, h_ref, dl_ref, qs_ref, k_ref, v_ref, dq_in_ref, dq_ref, dk_ref, dv_ref, dk_acc, dv_acc, *, scale, block):
    n = pl.program_id(1)
    share = q_ref.shape[1]

    @pl.when(n == 0)
    def _():
        dq_ref[...] = dq_in_ref[...]

    @pl.when(tab_ref[5, n] == 1)
    def _():
        dk_acc[...] = jnp.zeros(dk_acc.shape, dk_acc.dtype)
        dv_acc[...] = jnp.zeros(dv_acc.shape, dv_acc.dtype)

    q = q_ref[0].reshape(share * block, HEAD_SIZE)
    hh = h_ref[0].reshape(share * block, HEAD_SIZE)
    k = k_ref[0]
    v = v_ref[0]
    s = lax.dot_general(q, k, TRANS_B, preferred_element_type=jnp.float32) * scale
    allowed = _mask(tab_ref[1, n], tab_ref[2, n], qs_ref[...], block)
    e = jnp.where(allowed[None], jnp.exp(s.reshape(share, block, block)), 0.0)
    dp = lax.dot_general(hh, v, TRANS_B, preferred_element_type=jnp.float32).reshape(share, block, block)
    delta = jnp.tile(dl_ref[0], (1, 1, block // 128))
    ds = (e * (dp - delta)).reshape(share * block, block).astype(jnp.bfloat16)
    rows = pl.ds(pl.multiple_of(tab_ref[0, n] * block, block), block)
    dq_ref[0, :, rows, :] += jnp.dot(ds, k, preferred_element_type=jnp.float32).reshape(share, block, HEAD_SIZE)
    dk_acc[...] += lax.dot_general(ds, q, TRANS_A, preferred_element_type=jnp.float32)
    dv_acc[...] += lax.dot_general(
        e.reshape(share * block, block).astype(jnp.bfloat16), hh, TRANS_A, preferred_element_type=jnp.float32
    )

    @pl.when(tab_ref[6, n] == 1)
    def _():
        dk_ref[0] = dk_acc[...] * scale
        dv_ref[0] = dv_acc[...]


def attention_backward(q, hgrad, delta, qs, keys, values, dq_in, piece, quarter, source, block=512):
    kvh, share, rows, _ = q.shape
    tab = pair_tables(piece, quarter, block, True, source)
    npairs = tab.shape[1]
    scale = HEAD_SIZE ** (-0.5)
    row_spec = pl.BlockSpec((1, share, block, HEAD_SIZE), lambda h, n, t: (h, 0, t[0, n], 0))
    key_spec = pl.BlockSpec((1, block, HEAD_SIZE), lambda h, n, t: (h, t[4, n], 0))
    full_spec = pl.BlockSpec((1, share, rows, HEAD_SIZE), lambda h, n, t: (h, 0, 0, 0))
    grid_spec = pltpu.PrefetchScalarGridSpec(
        num_scalar_prefetch=1,
        grid=(kvh, npairs),
        in_specs=[
            row_spec,
            row_spec,
            pl.BlockSpec((1, share, block, 128), lambda h, n, t: (h, 0, t[0, n], 0)),
            pl.BlockSpec((block, 128), lambda h, n, t: (t[0, n], 0)),
            key_spec,
            key_spec,
            full_spec,
        ],
        out_specs=[full_spec, key_spec, key_spec],
        scratch_shapes=[
            pltpu.VMEM((block, HEAD_SIZE), jnp.float32),
            pltpu.VMEM((block, HEAD_SIZE), jnp.float32),
        ],
    )
    flops = 10 * kvh * npairs * share * block * block * HEAD_SIZE
    return pl.pallas_call(
        functools.partial(_bwd_kernel, scale=scale, block=block),
        grid_spec=grid_spec,
        out_shape=[
            jax.ShapeDtypeStruct(dq_in.shape, jnp.float32),
            jax.ShapeDtypeStruct(keys.shape, jnp.float32),
            jax.ShapeDtypeStruct(values.shape, jnp.float32),
        ],
        input_output_aliases={7: 0},
        compiler_params=pltpu.CompilerParams(
            dimension_semantics=("arbitrary", "arbitrary"), vmem_limit_bytes=56 * 1024 * 1024
        ),
        cost_estimate=pl.CostEstimate(
            flops=flops,
            transcendentals=kvh * npairs * share * block * block,
            bytes_accessed=kvh * npairs * (10 * block * HEAD_SIZE * 2),
        ),
        name="attn_bwd",
    )(tab, q, hgrad, delta, qs, keys, values, dq_in)


PIECES = 2


EPSILON = 1e-06
THETA = 1000000.0


def swapped(shard, axis, distance):
    return lax.ppermute(shard, axis, [(i, i ^ 1 << distance) for i in range(lax.axis_size(axis))])


def rms_scale(values, gain):
    inverse = lax.rsqrt(jnp.mean(values * values, axis=-1, keepdims=True) + EPSILON)
    return values * inverse * gain


def rotary(values, start_offset):
    half = values.shape[-1] // 2
    frequency = THETA ** (-(jnp.arange(half, dtype=jnp.float32) * 2.0 / values.shape[-1]))
    angle = start_offset.astype(jnp.float32)[:, None] * frequency[None, :]
    cosine = jnp.cos(angle)[:, None, :]
    sine = jnp.sin(angle)[:, None, :]
    first = values[..., :half]
    second = values[..., half:]
    return jnp.concatenate(
        [first * cosine - second * sine, second * cosine + first * sine], axis=-1
    )


def prepare_inputs(projected, gain, start_offset, head_groups):
    shaped = projected.reshape(projected.shape[0], head_groups, -1)
    return rotary(rms_scale(shaped, gain), start_offset)


def piece_places(which, group_rows):
    quarter = group_rows // 2
    local = jnp.arange(group_rows, dtype=jnp.int32)
    chosen = jnp.where(local < quarter, which, 3 - which)
    return chosen * quarter + local % quarter


def contract_rows(left, right):
    return lax.dot_general(
        left, right, (((0,), (0,)), ((), ())), preferred_element_type=jnp.float32
    )


def contract_last(left, right):
    return lax.dot_general(
        left, right, (((1,), (1,)), ((), ())), preferred_element_type=jnp.float32
    )


def split_columns(full, widths):
    parts = []
    at = 0
    for width in widths:
        parts.append(full[:, at : at + width])
        at += width
    return parts


def halving_scatter(grads):
    widths = [g.shape[1] for g in grads]
    packed = jnp.concatenate(grads, axis=1)
    count = lax.axis_size("fsdp")
    me = lax.axis_index("fsdp")
    bits = count.bit_length() - 1
    rows_f = packed.shape[0] // count
    order = [int(format(b, f"0{bits}b")[::-1], 2) for b in range(count)]
    buf = jnp.concatenate([packed[b * rows_f : (b + 1) * rows_f] for b in order], axis=0)
    for bit in range(bits):
        half = buf.shape[0] // 2
        mine = (me >> bit) & 1
        keep = lax.dynamic_slice_in_dim(buf, mine * half, half, 0)
        send = lax.dynamic_slice_in_dim(buf, (1 - mine) * half, half, 0)
        got = lax.ppermute(
            send.astype(jnp.bfloat16), "fsdp", [(i, i ^ (1 << bit)) for i in range(count)]
        )
        buf = keep + got.astype(jnp.float32)
    return split_columns(buf, widths)


def fsdp_gather(values):
    count = lax.axis_size("fsdp")
    me = lax.axis_index("fsdp")
    distance = 1
    while distance < count:
        got = lax.ppermute(values, "fsdp", [(i, i ^ distance) for i in range(count)])
        low = (me & distance) == 0
        values = jnp.concatenate(
            [jnp.where(low, values, got), jnp.where(low, got, values)]
        )
        distance *= 2
    return values


def all_sum(values):
    for axis in ("tensor", "fsdp"):
        distance = 1
        while distance < lax.axis_size(axis):
            values = values + lax.ppermute(
                values, axis, [(i, i ^ distance) for i in range(lax.axis_size(axis))]
            )
            distance *= 2
    return values


def exchange(values, distance):
    count = lax.axis_size("tensor")
    return lax.ppermute(values, "tensor", [(i, i ^ distance) for i in range(count)])


def token_gather(values):
    return finish_gather(values, exchange(values, 2))


def finish_gather(values, across):
    rows = values.shape[0]
    me = lax.axis_index("tensor")
    pair = jnp.stack([values, across])
    beside = exchange(pair, 1)
    full = jnp.zeros((4 * rows,) + values.shape[1:], values.dtype)
    for part, place in ((values, me), (across, me ^ 2), (beside[0], me ^ 1), (beside[1], me ^ 3)):
        full = lax.dynamic_update_slice_in_dim(full, part, place * rows, 0)
    return full


def token_sum(term, rows):
    partial = term(jnp.int32(0), rows * lax.axis_size("tensor"))
    me = lax.axis_index("tensor")

    def block(place):
        return lax.dynamic_slice_in_dim(partial, place * rows, rows, 0)

    sent = jnp.stack([block(me ^ 1), block(me ^ 3)]).astype(jnp.bfloat16)
    got = exchange(sent, 1).astype(jnp.float32)
    mine = block(me) + got[0]
    other = (block(me ^ 2) + got[1]).astype(jnp.bfloat16)
    return mine + exchange(other, 2).astype(jnp.float32)


def shards(
    hidden,
    out_grad,
    lengths,
    q_weight,
    key_matrix,
    value_matrix,
    o_weight,
    gate_weight,
    up_weight,
    down_weight,
    input_gain,
    q_gain,
    k_gain,
    post_gain,
):
    split = lax.axis_size("tensor")
    rows = hidden.shape[0]
    group_rows = rows * split
    q_heads = q_weight.shape[1] // HEAD_SIZE
    kv_heads = key_matrix.shape[1] // HEAD_SIZE
    share = q_heads // kv_heads
    scale = HEAD_SIZE ** (-0.5)
    member = lax.axis_index("fsdp")
    slot = member // PIECES
    piece = member % PIECES
    lengths_row = lax.dynamic_index_in_dim(lengths, slot, 0, keepdims=False)
    ends = jnp.cumsum(lengths_row)
    group_place = piece_places(piece, group_rows)
    passed = group_place[:, None] >= ends[None, :]
    group_start = jnp.sum(jnp.where(passed, lengths_row[None, :], 0), axis=1)
    group_offset = group_place - group_start
    local_valid = lax.dynamic_slice_in_dim(
        group_place < ends[-1], lax.axis_index("tensor") * rows, rows, 0
    )
    fs = lax.axis_size("fsdp")
    gain_sizes = (input_gain.shape[0], q_gain.shape[0], k_gain.shape[0], post_gain.shape[0])
    gains_all = fsdp_gather(
        jnp.concatenate([input_gain, q_gain, k_gain, post_gain]).astype(jnp.bfloat16)
    ).reshape(fs, sum(gain_sizes))
    gain_in, gain_query, gain_keys, gain_post = [
        part.reshape(-1) for part in split_columns(gains_all, gain_sizes)
    ]
    kv_full = lax.all_gather(
        jnp.concatenate(
            [key_matrix.astype(jnp.bfloat16), value_matrix.astype(jnp.bfloat16)], axis=1
        ),
        "fsdp",
        axis=0,
        tiled=True,
    )
    w_key, w_value = split_columns(kv_full, (key_matrix.shape[1], value_matrix.shape[1]))
    w_query = lax.all_gather(q_weight.astype(jnp.bfloat16), "fsdp", axis=0, tiled=True)
    w_out = lax.all_gather(
        jnp.transpose(o_weight).astype(jnp.bfloat16), "fsdp", axis=0, tiled=True
    )
    x_float = hidden.astype(jnp.float32)
    gain_first = gain_in.astype(jnp.float32)
    first_all = token_gather(rms_scale(x_float, gain_first).astype(jnp.bfloat16))
    cotangent = out_grad.astype(jnp.float32) * local_valid[:, None].astype(jnp.float32)
    cotangent_low, first_all = lax.optimization_barrier((cotangent.astype(jnp.bfloat16), first_all))
    cotangent_across = exchange(cotangent_low, 2)
    query_projected = jnp.dot(first_all, w_query, preferred_element_type=jnp.float32)
    key_projected = jnp.dot(first_all, w_key, preferred_element_type=jnp.float32)
    value_rows = (
        jnp.dot(first_all, w_value, preferred_element_type=jnp.float32)
        .astype(jnp.bfloat16)
        .reshape(group_rows, kv_heads, HEAD_SIZE)
    )
    gain_q = gain_query.astype(jnp.float32)
    gain_k = gain_keys.astype(jnp.float32)
    query_rope = (
        prepare_inputs(query_projected, gain_q, group_offset, q_heads)
        .astype(jnp.bfloat16)
        .reshape(group_rows, kv_heads, share, HEAD_SIZE)
    )
    key_rope = prepare_inputs(key_projected, gain_k, group_offset, kv_heads).astype(jnp.bfloat16)
    quarter = group_rows // 2
    query_start = jnp.broadcast_to(group_start[:, None], (group_rows, 128))
    query_t = jnp.transpose(query_rope, (1, 2, 0, 3))
    own_keys = jnp.transpose(key_rope, (1, 0, 2))
    own_values = jnp.transpose(value_rows, (1, 0, 2))
    moved = swapped(jnp.stack([own_keys, own_values]), "fsdp", 0)
    sums = jnp.zeros(query_t.shape, jnp.float32)
    totals = jnp.zeros(query_t.shape[:3] + (128,), jnp.float32)
    sums, totals = attention_forward(
        query_t, query_start, own_keys, own_values, sums, totals, piece, quarter, 0
    )
    cotangent_across, sums, totals = lax.optimization_barrier((cotangent_across, sums, totals))
    mlp_grad_all = finish_gather(cotangent_low, cotangent_across)
    sums, totals_t = attention_forward(
        query_t, query_start, moved[0], moved[1], sums, totals, piece, quarter, 1
    )
    mlp_grad_all, sums, totals_t = lax.optimization_barrier((mlp_grad_all, sums, totals_t))
    heads_t = sums / totals_t[..., :1]
    heads_out = jnp.transpose(heads_t, (2, 0, 1, 3))
    row_totals = jnp.transpose(totals_t[..., 0], (2, 0, 1))
    out_rows = heads_out.reshape(group_rows, q_heads * HEAD_SIZE).astype(jnp.bfloat16)

    mlp_full = lax.all_gather(
        jnp.concatenate(
            [
                gate_weight.astype(jnp.bfloat16),
                up_weight.astype(jnp.bfloat16),
                jnp.transpose(down_weight).astype(jnp.bfloat16),
            ],
            axis=1,
        ),
        "fsdp",
        axis=0,
        tiled=True,
    )
    w_gate, w_up, w_down_t = split_columns(
        mlp_full, (gate_weight.shape[1], up_weight.shape[1], down_weight.shape[0])
    )
    out_partial = contract_last(out_rows, w_out)
    late_grad_all, out_partial = lax.optimization_barrier((mlp_grad_all, out_partial))
    grad_act = jnp.dot(late_grad_all, w_down_t, preferred_element_type=jnp.float32)
    after_attn = x_float + token_sum(lambda start, count: out_partial, rows)
    grad_act, after_attn = lax.optimization_barrier((grad_act, after_attn))
    gain_second = gain_post.astype(jnp.float32)
    second_all = token_gather(rms_scale(after_attn, gain_second).astype(jnp.bfloat16))
    gate_out = jnp.dot(second_all, w_gate, preferred_element_type=jnp.float32)
    up_out = jnp.dot(second_all, w_up, preferred_element_type=jnp.float32)
    activated = (jax.nn.silu(gate_out) * up_out).astype(jnp.bfloat16)

    unused, pull_gate = jax.vjp(
        lambda gate_in, up_in: jax.nn.silu(gate_in) * up_in, gate_out, up_out
    )
    grad_gate, grad_up = pull_gate(grad_act)
    grad_gate = grad_gate.astype(jnp.bfloat16)
    grad_up = grad_up.astype(jnp.bfloat16)
    second_partial = contract_last(grad_gate, w_gate) + contract_last(grad_up, w_up)
    grad_inputs, second_partial = lax.optimization_barrier(
        ((mlp_grad_all, activated, second_all, grad_gate, grad_up), second_partial)
    )
    late_c, late_act, late_second, late_gate, late_up = grad_inputs
    down_grad_t = contract_rows(late_c, late_act)
    gate_grad = contract_rows(late_second, late_gate)
    up_grad = contract_rows(late_second, late_up)
    second_back = token_sum(lambda start, count: second_partial, rows)
    unused, pull_second = jax.vjp(rms_scale, after_attn, gain_second)
    norm_second_grad, post_gain_part = pull_second(second_back)
    residual_grad = cotangent + norm_second_grad
    weight_grads, residual_grad = lax.optimization_barrier(
        ((gate_grad, up_grad, down_grad_t), residual_grad)
    )
    gate_grad, up_grad, down_grad_t = weight_grads
    attn_grad_all = token_gather(residual_grad.astype(jnp.bfloat16))
    activated_late, attn_grad_all = lax.optimization_barrier((activated, attn_grad_all))
    down_rows = token_sum(lambda start, count: contract_last(activated_late, w_down_t), rows)
    out_weight_grad_t = contract_rows(attn_grad_all, out_rows)
    mlp_packed = jnp.concatenate(
        [g.astype(jnp.bfloat16) for g in (gate_grad, up_grad, down_grad_t, out_weight_grad_t)],
        axis=1,
    )
    head_grad = jnp.dot(attn_grad_all, w_out, preferred_element_type=jnp.float32).astype(
        jnp.bfloat16
    )
    head_float = head_grad.astype(jnp.float32).reshape(group_rows, kv_heads, share, HEAD_SIZE)
    scaled_grad = (head_float / row_totals[..., None]).astype(jnp.bfloat16)
    delta = jnp.sum(head_float * heads_out, axis=-1) / row_totals

    grad_t = jnp.transpose(scaled_grad, (1, 2, 0, 3))
    delta_t = jnp.broadcast_to(
        jnp.transpose(delta, (1, 2, 0))[..., None], (kv_heads, share, group_rows, 128)
    )
    mlp_packed, grad_t, delta_t = lax.optimization_barrier((mlp_packed, grad_t, delta_t))
    mlp_shards = split_columns(
        lax.psum_scatter(mlp_packed, "fsdp", scatter_dimension=0, tiled=True),
        [g.shape[1] for g in (gate_grad, up_grad, down_grad_t, out_weight_grad_t)],
    )
    mlp_shards = [part.astype(jnp.float32) for part in mlp_shards]
    dq_raw, dk_far, dv_far = attention_backward(
        query_t, grad_t, delta_t, query_start, moved[0], moved[1],
        jnp.zeros(query_t.shape, jnp.float32), piece, quarter, 1,
    )
    unseen = (piece == 1) & (jnp.arange(group_rows) >= quarter)
    far_grads = jnp.where(unseen[None, None, :, None], 0.0, jnp.stack([dk_far, dv_far]))
    returned = swapped(far_grads.astype(jnp.bfloat16), "fsdp", 0)
    down_rows, dq_raw = lax.optimization_barrier((down_rows, dq_raw))
    output = (after_attn + down_rows).astype(jnp.bfloat16)
    dq_raw, dk_own, dv_own = attention_backward(
        query_t, grad_t, delta_t, query_start, own_keys, own_values,
        dq_raw, piece, quarter, 0,
    )
    mlp_shards, dq_raw = lax.optimization_barrier((mlp_shards, dq_raw))
    grad_keys_total = jnp.transpose(dk_own + returned[0].astype(jnp.float32), (1, 0, 2))
    grad_values_total = jnp.transpose(dv_own + returned[1].astype(jnp.float32), (1, 0, 2))
    query_grads = jnp.transpose(dq_raw, (2, 0, 1, 3)) * scale
    query_grads = query_grads.reshape(group_rows, q_heads, HEAD_SIZE)
    unused, pull_query = jax.vjp(
        lambda projected, gain: prepare_inputs(projected, gain, group_offset, q_heads),
        query_projected,
        gain_q,
    )
    query_proj_grad, q_gain_part = pull_query(query_grads)
    unused, pull_key = jax.vjp(
        lambda projected, gain: prepare_inputs(projected, gain, group_offset, kv_heads),
        key_projected,
        gain_k,
    )
    key_proj_grad, k_gain_part = pull_key(grad_keys_total)
    query_low = query_proj_grad.astype(jnp.bfloat16)
    key_low = key_proj_grad.astype(jnp.bfloat16)
    value_low = grad_values_total.reshape(group_rows, kv_heads * HEAD_SIZE).astype(jnp.bfloat16)
    query_weight_grad = contract_rows(first_all, query_low)
    key_weight_grad = contract_rows(first_all, key_low)
    value_weight_grad = contract_rows(first_all, value_low)

    def first_term(start, count):
        return (
            contract_last(query_low, w_query)
            + contract_last(key_low, w_key)
            + contract_last(value_low, w_value)
        )

    first_back = token_sum(first_term, rows)
    unused, pull_first = jax.vjp(rms_scale, x_float, gain_first)
    norm_first_grad, input_gain_part = pull_first(first_back)
    input_grad = (residual_grad + norm_first_grad).astype(jnp.bfloat16)
    (query_shard,) = halving_scatter((query_weight_grad,))
    key_shard, value_shard = halving_scatter((key_weight_grad, value_weight_grad))
    gain_totals = all_sum(
        jnp.concatenate([input_gain_part, q_gain_part, k_gain_part, post_gain_part])
    )
    member_f = lax.axis_index("fsdp")
    sizes = (input_gain.shape[0], q_gain.shape[0], k_gain.shape[0], post_gain.shape[0])
    gain_shards = []
    at = 0
    for own in sizes:
        whole = own * fs
        gain_shards.append(lax.dynamic_slice_in_dim(gain_totals, at + member_f * own, own, 0))
        at += whole
    input_gain_shard, q_gain_shard, k_gain_shard, post_gain_shard = gain_shards
    gate_shard, up_shard, down_shard_t, out_shard_t = mlp_shards
    return (
        output,
        input_grad,
        query_shard,
        key_shard,
        value_shard,
        jnp.transpose(out_shard_t),
        gate_shard,
        up_shard,
        jnp.transpose(down_shard_t),
        input_gain_shard,
        q_gain_shard,
        k_gain_shard,
        post_gain_shard,
    )


def solution(mesh):
    return layer_program(mesh)


def layer_program(mesh):
    placed = (
        P(("fsdp", "tensor"), None),
        P(("fsdp", "tensor"), None),
        P(),
        P("fsdp", "tensor"),
        P("fsdp", "tensor"),
        P("fsdp", "tensor"),
        P("tensor", "fsdp"),
        P("fsdp", "tensor"),
        P("fsdp", "tensor"),
        P("tensor", "fsdp"),
        P("fsdp"),
        P("fsdp"),
        P("fsdp"),
        P("fsdp"),
    )
    return jax.shard_map(
        shards,
        mesh=mesh,
        in_specs=placed,
        out_specs=(
            P(("fsdp", "tensor"), None),
            P(("fsdp", "tensor"), None),
            P("fsdp", "tensor"),
            P("fsdp", "tensor"),
            P("fsdp", "tensor"),
            P("tensor", "fsdp"),
            P("fsdp", "tensor"),
            P("fsdp", "tensor"),
            P("tensor", "fsdp"),
            P("fsdp"),
            P("fsdp"),
            P("fsdp"),
            P("fsdp"),
        ),
        check_vma=False,
    )
```

```python
import functools

import numpy as np
import jax
import jax.numpy as jnp
from jax import lax
from jax.experimental import pallas as pl
from jax.experimental.pallas import tpu as pltpu
from jax.sharding import PartitionSpec as P


HEAD_SIZE = 128
TRANS_B = (((1,), (1,)), ((), ()))
TRANS_A = (((0,), (0,)), ((), ()))


def _own_place(p, quarter, r):
    return (p * quarter + r) if r < quarter else ((3 - p) * quarter + r - quarter)


def _far_place(p, quarter, r):
    return ((1 - p) * quarter + r) if r < quarter else ((2 + p) * quarter + r - quarter)


def _pair_tables(p, quarter, block, by_key, source):
    rows = 2 * quarter
    count = rows // block
    kmap = {}
    for src, fn in ((0, _own_place), (1, _far_place)):
        for j in range(count):
            kmap[fn(p, quarter, j * block) // block] = (src, j)
    pairs = []
    for j in range(count):
        qpb = _own_place(p, quarter, j * block) // block
        for kpb in range(qpb + 1):
            if kmap[kpb][0] == source:
                pairs.append((j, qpb, kpb))
    if by_key:
        pairs.sort(key=lambda t: (t[2], t[0]))
    group = [t[2] if by_key else t[0] for t in pairs]
    size = len(pairs)
    first = [1 if n == 0 or group[n - 1] != group[n] else 0 for n in range(size)]
    last = [1 if n == size - 1 or group[n + 1] != group[n] else 0 for n in range(size)]
    return np.array(
        [
            [t[0] for t in pairs],
            [t[1] for t in pairs],
            [t[2] for t in pairs],
            [kmap[t[2]][0] for t in pairs],
            [kmap[t[2]][1] for t in pairs],
            first,
            last,
        ],
        np.int32,
    )


def pair_tables(piece, quarter, block, by_key, source):
    t0 = _pair_tables(0, quarter, block, by_key, source)
    t1 = _pair_tables(1, quarter, block, by_key, source)
    assert t0.shape == t1.shape
    return jnp.where(piece == 0, jnp.asarray(t0), jnp.asarray(t1))


def _mask(qpb, kpb, qs, block):
    qp = qpb * block + lax.broadcasted_iota(jnp.int32, (block, block), 0)
    kp = kpb * block + lax.broadcasted_iota(jnp.int32, (block, block), 1)
    start = jnp.tile(qs, (1, block // 128))
    return (kp >= start) & (kp <= qp)


def _fwd_kernel(tab_ref, q_ref, qs_ref, k_ref, v_ref, a_in_ref, l_in_ref, a_ref, l_ref, acc_ref, sum_ref, *, scale, block):
    n = pl.program_id(1)
    share = q_ref.shape[1]

    @pl.when(tab_ref[5, n] == 1)
    def _():
        acc_ref[...] = a_in_ref[0].reshape(share * block, HEAD_SIZE)
        sum_ref[...] = l_in_ref[0][:, :, :1]

    q = q_ref[0].reshape(share * block, HEAD_SIZE)
    k = k_ref[0]
    v = v_ref[0]
    s = lax.dot_general(q, k, TRANS_B, preferred_element_type=jnp.float32) * scale
    allowed = _mask(tab_ref[1, n], tab_ref[2, n], qs_ref[...], block)
    e = jnp.where(allowed[None], jnp.exp(s.reshape(share, block, block)), 0.0)
    sum_ref[...] += jnp.sum(e, axis=-1, keepdims=True)
    acc_ref[...] += jnp.dot(
        e.reshape(share * block, block).astype(jnp.bfloat16), v, preferred_element_type=jnp.float32
    )

    @pl.when(tab_ref[6, n] == 1)
    def _():
        a_ref[0] = acc_ref[...].reshape(share, block, HEAD_SIZE)
        l_ref[0] = jnp.broadcast_to(sum_ref[...], (share, block, 128))


def attention_forward(q, qs, keys, values, a_in, l_in, piece, quarter, source, block=512):
    kvh, share, _, _ = q.shape
    tab = pair_tables(piece, quarter, block, False, source)
    npairs = tab.shape[1]
    scale = HEAD_SIZE ** (-0.5)
    row_spec = pl.BlockSpec((1, share, block, HEAD_SIZE), lambda h, n, t: (h, 0, t[0, n], 0))
    lane_spec = pl.BlockSpec((1, share, block, 128), lambda h, n, t: (h, 0, t[0, n], 0))
    key_spec = pl.BlockSpec((1, block, HEAD_SIZE), lambda h, n, t: (h, t[4, n], 0))
    grid_spec = pltpu.PrefetchScalarGridSpec(
        num_scalar_prefetch=1,
        grid=(kvh, npairs),
        in_specs=[
            row_spec,
            pl.BlockSpec((block, 128), lambda h, n, t: (t[0, n], 0)),
            key_spec,
            key_spec,
            row_spec,
            lane_spec,
        ],
        out_specs=[row_spec, lane_spec],
        scratch_shapes=[
            pltpu.VMEM((share * block, HEAD_SIZE), jnp.float32),
            pltpu.VMEM((share, block, 1), jnp.float32),
        ],
    )
    flops = 4 * kvh * npairs * share * block * block * HEAD_SIZE
    return pl.pallas_call(
        functools.partial(_fwd_kernel, scale=scale, block=block),
        grid_spec=grid_spec,
        out_shape=[
            jax.ShapeDtypeStruct(a_in.shape, jnp.float32),
            jax.ShapeDtypeStruct(l_in.shape, jnp.float32),
        ],
        input_output_aliases={5: 0, 6: 1},
        compiler_params=pltpu.CompilerParams(
            dimension_semantics=("arbitrary", "arbitrary"), vmem_limit_bytes=48 * 1024 * 1024
        ),
        cost_estimate=pl.CostEstimate(
            flops=flops,
            transcendentals=kvh * npairs * share * block * block,
            bytes_accessed=kvh * npairs * (8 * block * HEAD_SIZE * 2),
        ),
        name="attn_fwd",
    )(tab, q, qs, keys, values, a_in, l_in)


def _bwd_kernel(tab_ref, q_ref, h_ref, dl_ref, qs_ref, k_ref, v_ref, dq_in_ref, dq_ref, dk_ref, dv_ref, dk_acc, dv_acc, *, scale, block):
    n = pl.program_id(1)
    share = q_ref.shape[1]

    @pl.when(n == 0)
    def _():
        dq_ref[...] = dq_in_ref[...]

    @pl.when(tab_ref[5, n] == 1)
    def _():
        dk_acc[...] = jnp.zeros(dk_acc.shape, dk_acc.dtype)
        dv_acc[...] = jnp.zeros(dv_acc.shape, dv_acc.dtype)

    q = q_ref[0].reshape(share * block, HEAD_SIZE)
    hh = h_ref[0].reshape(share * block, HEAD_SIZE)
    k = k_ref[0]
    v = v_ref[0]
    s = lax.dot_general(q, k, TRANS_B, preferred_element_type=jnp.float32) * scale
    allowed = _mask(tab_ref[1, n], tab_ref[2, n], qs_ref[...], block)
    e = jnp.where(allowed[None], jnp.exp(s.reshape(share, block, block)), 0.0)
    dp = lax.dot_general(hh, v, TRANS_B, preferred_element_type=jnp.float32).reshape(share, block, block)
    delta = jnp.tile(dl_ref[0], (1, 1, block // 128))
    ds = (e * (dp - delta)).reshape(share * block, block).astype(jnp.bfloat16)
    rows = pl.ds(pl.multiple_of(tab_ref[0, n] * block, block), block)
    dq_ref[0, :, rows, :] += jnp.dot(ds, k, preferred_element_type=jnp.float32).reshape(share, block, HEAD_SIZE)
    dk_acc[...] += lax.dot_general(ds, q, TRANS_A, preferred_element_type=jnp.float32)
    dv_acc[...] += lax.dot_general(
        e.reshape(share * block, block).astype(jnp.bfloat16), hh, TRANS_A, preferred_element_type=jnp.float32
    )

    @pl.when(tab_ref[6, n] == 1)
    def _():
        dk_ref[0] = dk_acc[...] * scale
        dv_ref[0] = dv_acc[...]


def attention_backward(q, hgrad, delta, qs, keys, values, dq_in, piece, quarter, source, block=512):
    kvh, share, rows, _ = q.shape
    tab = pair_tables(piece, quarter, block, True, source)
    npairs = tab.shape[1]
    scale = HEAD_SIZE ** (-0.5)
    row_spec = pl.BlockSpec((1, share, block, HEAD_SIZE), lambda h, n, t: (h, 0, t[0, n], 0))
    key_spec = pl.BlockSpec((1, block, HEAD_SIZE), lambda h, n, t: (h, t[4, n], 0))
    full_spec = pl.BlockSpec((1, share, rows, HEAD_SIZE), lambda h, n, t: (h, 0, 0, 0))
    grid_spec = pltpu.PrefetchScalarGridSpec(
        num_scalar_prefetch=1,
        grid=(kvh, npairs),
        in_specs=[
            row_spec,
            row_spec,
            pl.BlockSpec((1, share, block, 128), lambda h, n, t: (h, 0, t[0, n], 0)),
            pl.BlockSpec((block, 128), lambda h, n, t: (t[0, n], 0)),
            key_spec,
            key_spec,
            full_spec,
        ],
        out_specs=[full_spec, key_spec, key_spec],
        scratch_shapes=[
            pltpu.VMEM((block, HEAD_SIZE), jnp.float32),
            pltpu.VMEM((block, HEAD_SIZE), jnp.float32),
        ],
    )
    flops = 10 * kvh * npairs * share * block * block * HEAD_SIZE
    return pl.pallas_call(
        functools.partial(_bwd_kernel, scale=scale, block=block),
        grid_spec=grid_spec,
        out_shape=[
            jax.ShapeDtypeStruct(dq_in.shape, jnp.float32),
            jax.ShapeDtypeStruct(keys.shape, jnp.float32),
            jax.ShapeDtypeStruct(values.shape, jnp.float32),
        ],
        input_output_aliases={7: 0},
        compiler_params=pltpu.CompilerParams(
            dimension_semantics=("arbitrary", "arbitrary"), vmem_limit_bytes=56 * 1024 * 1024
        ),
        cost_estimate=pl.CostEstimate(
            flops=flops,
            transcendentals=kvh * npairs * share * block * block,
            bytes_accessed=kvh * npairs * (10 * block * HEAD_SIZE * 2),
        ),
        name="attn_bwd",
    )(tab, q, hgrad, delta, qs, keys, values, dq_in)


PIECES = 2


EPSILON = 1e-06
THETA = 1000000.0


def swapped(shard, axis, distance):
    return lax.ppermute(shard, axis, [(i, i ^ 1 << distance) for i in range(lax.axis_size(axis))])


def rms_scale(values, gain):
    inverse = lax.rsqrt(jnp.mean(values * values, axis=-1, keepdims=True) + EPSILON)
    return values * inverse * gain


def rotary(values, start_offset):
    half = values.shape[-1] // 2
    frequency = THETA ** (-(jnp.arange(half, dtype=jnp.float32) * 2.0 / values.shape[-1]))
    angle = start_offset.astype(jnp.float32)[:, None] * frequency[None, :]
    cosine = jnp.cos(angle)[:, None, :]
    sine = jnp.sin(angle)[:, None, :]
    first = values[..., :half]
    second = values[..., half:]
    return jnp.concatenate(
        [first * cosine - second * sine, second * cosine + first * sine], axis=-1
    )


def prepare_inputs(projected, gain, start_offset, head_groups):
    shaped = projected.reshape(projected.shape[0], head_groups, -1)
    return rotary(rms_scale(shaped, gain), start_offset)


def piece_places(which, group_rows):
    quarter = group_rows // 2
    local = jnp.arange(group_rows, dtype=jnp.int32)
    chosen = jnp.where(local < quarter, which, 3 - which)
    return chosen * quarter + local % quarter


def contract_rows(left, right):
    return lax.dot_general(
        left, right, (((0,), (0,)), ((), ())), preferred_element_type=jnp.float32
    )


def contract_last(left, right):
    return lax.dot_general(
        left, right, (((1,), (1,)), ((), ())), preferred_element_type=jnp.float32
    )


def split_columns(full, widths):
    parts = []
    at = 0
    for width in widths:
        parts.append(full[:, at : at + width])
        at += width
    return parts


def halving_scatter(grads):
    widths = [g.shape[1] for g in grads]
    packed = jnp.concatenate(grads, axis=1)
    count = lax.axis_size("fsdp")
    me = lax.axis_index("fsdp")
    bits = count.bit_length() - 1
    rows_f = packed.shape[0] // count
    order = [int(format(b, f"0{bits}b")[::-1], 2) for b in range(count)]
    buf = jnp.concatenate([packed[b * rows_f : (b + 1) * rows_f] for b in order], axis=0)
    for bit in range(bits):
        half = buf.shape[0] // 2
        mine = (me >> bit) & 1
        keep = lax.dynamic_slice_in_dim(buf, mine * half, half, 0)
        send = lax.dynamic_slice_in_dim(buf, (1 - mine) * half, half, 0)
        got = lax.ppermute(
            send.astype(jnp.bfloat16), "fsdp", [(i, i ^ (1 << bit)) for i in range(count)]
        )
        buf = keep + got.astype(jnp.float32)
    return split_columns(buf, widths)


def fsdp_gather(values):
    count = lax.axis_size("fsdp")
    me = lax.axis_index("fsdp")
    distance = 1
    while distance < count:
        got = lax.ppermute(values, "fsdp", [(i, i ^ distance) for i in range(count)])
        low = (me & distance) == 0
        values = jnp.concatenate(
            [jnp.where(low, values, got), jnp.where(low, got, values)]
        )
        distance *= 2
    return values


def all_sum(values):
    for axis in ("tensor", "fsdp"):
        distance = 1
        while distance < lax.axis_size(axis):
            values = values + lax.ppermute(
                values, axis, [(i, i ^ distance) for i in range(lax.axis_size(axis))]
            )
            distance *= 2
    return values


def exchange(values, distance):
    count = lax.axis_size("tensor")
    return lax.ppermute(values, "tensor", [(i, i ^ distance) for i in range(count)])


def token_gather(values):
    return finish_gather(values, exchange(values, 2))


def finish_gather(values, across):
    rows = values.shape[0]
    me = lax.axis_index("tensor")
    pair = jnp.stack([values, across])
    beside = exchange(pair, 1)
    full = jnp.zeros((4 * rows,) + values.shape[1:], values.dtype)
    for part, place in ((values, me), (across, me ^ 2), (beside[0], me ^ 1), (beside[1], me ^ 3)):
        full = lax.dynamic_update_slice_in_dim(full, part, place * rows, 0)
    return full


def token_sum(term, rows):
    partial = term(jnp.int32(0), rows * lax.axis_size("tensor"))
    me = lax.axis_index("tensor")

    def block(place):
        return lax.dynamic_slice_in_dim(partial, place * rows, rows, 0)

    sent = jnp.stack([block(me ^ 1), block(me ^ 3)]).astype(jnp.bfloat16)
    got = exchange(sent, 1).astype(jnp.float32)
    mine = block(me) + got[0]
    other = (block(me ^ 2) + got[1]).astype(jnp.bfloat16)
    return mine + exchange(other, 2).astype(jnp.float32)


def shards(
    hidden,
    out_grad,
    lengths,
    q_weight,
    key_matrix,
    value_matrix,
    o_weight,
    gate_weight,
    up_weight,
    down_weight,
    input_gain,
    q_gain,
    k_gain,
    post_gain,
):
    split = lax.axis_size("tensor")
    rows = hidden.shape[0]
    group_rows = rows * split
    q_heads = q_weight.shape[1] // HEAD_SIZE
    kv_heads = key_matrix.shape[1] // HEAD_SIZE
    share = q_heads // kv_heads
    scale = HEAD_SIZE ** (-0.5)
    member = lax.axis_index("fsdp")
    slot = member // PIECES
    piece = member % PIECES
    lengths_row = lax.dynamic_index_in_dim(lengths, slot, 0, keepdims=False)
    ends = jnp.cumsum(lengths_row)
    group_place = piece_places(piece, group_rows)
    passed = group_place[:, None] >= ends[None, :]
    group_start = jnp.sum(jnp.where(passed, lengths_row[None, :], 0), axis=1)
    group_offset = group_place - group_start
    local_valid = lax.dynamic_slice_in_dim(
        group_place < ends[-1], lax.axis_index("tensor") * rows, rows, 0
    )
    fs = lax.axis_size("fsdp")
    gain_sizes = (input_gain.shape[0], q_gain.shape[0], k_gain.shape[0], post_gain.shape[0])
    gains_all = fsdp_gather(
        jnp.concatenate([input_gain, q_gain, k_gain, post_gain]).astype(jnp.bfloat16)
    ).reshape(fs, sum(gain_sizes))
    gain_in, gain_query, gain_keys, gain_post = [
        part.reshape(-1) for part in split_columns(gains_all, gain_sizes)
    ]
    kv_full = lax.all_gather(
        jnp.concatenate(
            [key_matrix.astype(jnp.bfloat16), value_matrix.astype(jnp.bfloat16)], axis=1
        ),
        "fsdp",
        axis=0,
        tiled=True,
    )
    w_key, w_value = split_columns(kv_full, (key_matrix.shape[1], value_matrix.shape[1]))
    w_query = lax.all_gather(q_weight.astype(jnp.bfloat16), "fsdp", axis=0, tiled=True)
    w_out = lax.all_gather(
        jnp.transpose(o_weight).astype(jnp.bfloat16), "fsdp", axis=0, tiled=True
    )
    x_float = hidden.astype(jnp.float32)
    gain_first = gain_in.astype(jnp.float32)
    first_all = token_gather(rms_scale(x_float, gain_first).astype(jnp.bfloat16))
    cotangent = out_grad.astype(jnp.float32) * local_valid[:, None].astype(jnp.float32)
    cotangent_low, first_all = lax.optimization_barrier((cotangent.astype(jnp.bfloat16), first_all))
    cotangent_across = exchange(cotangent_low, 2)
    query_projected = jnp.dot(first_all, w_query, preferred_element_type=jnp.float32)
    key_projected = jnp.dot(first_all, w_key, preferred_element_type=jnp.float32)
    value_rows = (
        jnp.dot(first_all, w_value, preferred_element_type=jnp.float32)
        .astype(jnp.bfloat16)
        .reshape(group_rows, kv_heads, HEAD_SIZE)
    )
    gain_q = gain_query.astype(jnp.float32)
    gain_k = gain_keys.astype(jnp.float32)
    query_rope = (
        prepare_inputs(query_projected, gain_q, group_offset, q_heads)
        .astype(jnp.bfloat16)
        .reshape(group_rows, kv_heads, share, HEAD_SIZE)
    )
    key_rope = prepare_inputs(key_projected, gain_k, group_offset, kv_heads).astype(jnp.bfloat16)
    quarter = group_rows // 2
    query_start = jnp.broadcast_to(group_start[:, None], (group_rows, 128))
    query_t = jnp.transpose(query_rope, (1, 2, 0, 3))
    own_keys = jnp.transpose(key_rope, (1, 0, 2))
    own_values = jnp.transpose(value_rows, (1, 0, 2))
    moved = swapped(jnp.stack([own_keys, own_values]), "fsdp", 0)
    sums = jnp.zeros(query_t.shape, jnp.float32)
    totals = jnp.zeros(query_t.shape[:3] + (128,), jnp.float32)
    sums, totals = attention_forward(
        query_t, query_start, own_keys, own_values, sums, totals, piece, quarter, 0
    )
    cotangent_across, sums, totals = lax.optimization_barrier((cotangent_across, sums, totals))
    mlp_grad_all = finish_gather(cotangent_low, cotangent_across)
    sums, totals_t = attention_forward(
        query_t, query_start, moved[0], moved[1], sums, totals, piece, quarter, 1
    )
    mlp_grad_all, sums, totals_t = lax.optimization_barrier((mlp_grad_all, sums, totals_t))
    heads_t = sums / totals_t[..., :1]
    heads_out = jnp.transpose(heads_t, (2, 0, 1, 3))
    row_totals = jnp.transpose(totals_t[..., 0], (2, 0, 1))
    out_rows = heads_out.reshape(group_rows, q_heads * HEAD_SIZE).astype(jnp.bfloat16)

    mlp_full = lax.all_gather(
        jnp.concatenate(
            [
                gate_weight.astype(jnp.bfloat16),
                up_weight.astype(jnp.bfloat16),
                jnp.transpose(down_weight).astype(jnp.bfloat16),
            ],
            axis=1,
        ),
        "fsdp",
        axis=0,
        tiled=True,
    )
    w_gate, w_up, w_down_t = split_columns(
        mlp_full, (gate_weight.shape[1], up_weight.shape[1], down_weight.shape[0])
    )
    out_partial = contract_last(out_rows, w_out)
    after_attn = x_float + token_sum(lambda start, count: out_partial, rows)
    gain_second = gain_post.astype(jnp.float32)
    second_rows = rms_scale(after_attn, gain_second).astype(jnp.bfloat16)
    late_grad_all, second_rows = lax.optimization_barrier((mlp_grad_all, second_rows))
    grad_act = jnp.dot(late_grad_all, w_down_t, preferred_element_type=jnp.float32)
    second_all = token_gather(second_rows)
    grad_act, second_all = lax.optimization_barrier((grad_act, second_all))
    gate_out = jnp.dot(second_all, w_gate, preferred_element_type=jnp.float32)
    up_out = jnp.dot(second_all, w_up, preferred_element_type=jnp.float32)
    activated = (jax.nn.silu(gate_out) * up_out).astype(jnp.bfloat16)

    unused, pull_gate = jax.vjp(
        lambda gate_in, up_in: jax.nn.silu(gate_in) * up_in, gate_out, up_out
    )
    grad_gate, grad_up = pull_gate(grad_act)
    grad_gate = grad_gate.astype(jnp.bfloat16)
    grad_up = grad_up.astype(jnp.bfloat16)
    second_partial = contract_last(grad_gate, w_gate) + contract_last(grad_up, w_up)
    grad_inputs, second_partial = lax.optimization_barrier(
        ((mlp_grad_all, activated, second_all, grad_gate, grad_up), second_partial)
    )
    late_c, late_act, late_second, late_gate, late_up = grad_inputs
    down_grad_t = contract_rows(late_c, late_act)
    gate_grad = contract_rows(late_second, late_gate)
    up_grad = contract_rows(late_second, late_up)
    second_back = token_sum(lambda start, count: second_partial, rows)
    unused, pull_second = jax.vjp(rms_scale, after_attn, gain_second)
    norm_second_grad, post_gain_part = pull_second(second_back)
    residual_grad = cotangent + norm_second_grad
    weight_grads, residual_grad = lax.optimization_barrier(
        ((gate_grad, up_grad, down_grad_t), residual_grad)
    )
    gate_grad, up_grad, down_grad_t = weight_grads
    attn_grad_all = token_gather(residual_grad.astype(jnp.bfloat16))
    activated_late, attn_grad_all = lax.optimization_barrier((activated, attn_grad_all))
    down_rows = token_sum(lambda start, count: contract_last(activated_late, w_down_t), rows)
    out_weight_grad_t = contract_rows(attn_grad_all, out_rows)
    mlp_packed = jnp.concatenate(
        [g.astype(jnp.bfloat16) for g in (gate_grad, up_grad, down_grad_t, out_weight_grad_t)],
        axis=1,
    )
    head_grad = jnp.dot(attn_grad_all, w_out, preferred_element_type=jnp.float32).astype(
        jnp.bfloat16
    )
    head_float = head_grad.astype(jnp.float32).reshape(group_rows, kv_heads, share, HEAD_SIZE)
    scaled_grad = (head_float / row_totals[..., None]).astype(jnp.bfloat16)
    delta = jnp.sum(head_float * heads_out, axis=-1) / row_totals

    grad_t = jnp.transpose(scaled_grad, (1, 2, 0, 3))
    delta_t = jnp.broadcast_to(
        jnp.transpose(delta, (1, 2, 0))[..., None], (kv_heads, share, group_rows, 128)
    )
    mlp_packed, grad_t, delta_t = lax.optimization_barrier((mlp_packed, grad_t, delta_t))
    mlp_shards = split_columns(
        lax.psum_scatter(mlp_packed, "fsdp", scatter_dimension=0, tiled=True),
        [g.shape[1] for g in (gate_grad, up_grad, down_grad_t, out_weight_grad_t)],
    )
    mlp_shards = [part.astype(jnp.float32) for part in mlp_shards]
    dq_raw, dk_far, dv_far = attention_backward(
        query_t, grad_t, delta_t, query_start, moved[0], moved[1],
        jnp.zeros(query_t.shape, jnp.float32), piece, quarter, 1,
    )
    unseen = (piece == 1) & (jnp.arange(group_rows) >= quarter)
    far_grads = jnp.where(unseen[None, None, :, None], 0.0, jnp.stack([dk_far, dv_far]))
    returned = swapped(far_grads.astype(jnp.bfloat16), "fsdp", 0)
    down_rows, dq_raw = lax.optimization_barrier((down_rows, dq_raw))
    output = (after_attn + down_rows).astype(jnp.bfloat16)
    dq_raw, dk_own, dv_own = attention_backward(
        query_t, grad_t, delta_t, query_start, own_keys, own_values,
        dq_raw, piece, quarter, 0,
    )
    mlp_shards, dq_raw = lax.optimization_barrier((mlp_shards, dq_raw))
    grad_keys_total = jnp.transpose(dk_own + returned[0].astype(jnp.float32), (1, 0, 2))
    grad_values_total = jnp.transpose(dv_own + returned[1].astype(jnp.float32), (1, 0, 2))
    query_grads = jnp.transpose(dq_raw, (2, 0, 1, 3)) * scale
    query_grads = query_grads.reshape(group_rows, q_heads, HEAD_SIZE)
    unused, pull_query = jax.vjp(
        lambda projected, gain: prepare_inputs(projected, gain, group_offset, q_heads),
        query_projected,
        gain_q,
    )
    query_proj_grad, q_gain_part = pull_query(query_grads)
    unused, pull_key = jax.vjp(
        lambda projected, gain: prepare_inputs(projected, gain, group_offset, kv_heads),
        key_projected,
        gain_k,
    )
    key_proj_grad, k_gain_part = pull_key(grad_keys_total)
    query_low = query_proj_grad.astype(jnp.bfloat16)
    key_low = key_proj_grad.astype(jnp.bfloat16)
    value_low = grad_values_total.reshape(group_rows, kv_heads * HEAD_SIZE).astype(jnp.bfloat16)
    query_weight_grad = contract_rows(first_all, query_low)
    key_weight_grad = contract_rows(first_all, key_low)
    value_weight_grad = contract_rows(first_all, value_low)

    def first_term(start, count):
        return (
            contract_last(query_low, w_query)
            + contract_last(key_low, w_key)
            + contract_last(value_low, w_value)
        )

    first_back = token_sum(first_term, rows)
    unused, pull_first = jax.vjp(rms_scale, x_float, gain_first)
    norm_first_grad, input_gain_part = pull_first(first_back)
    input_grad = (residual_grad + norm_first_grad).astype(jnp.bfloat16)
    (query_shard,) = halving_scatter((query_weight_grad,))
    key_shard, value_shard = halving_scatter((key_weight_grad, value_weight_grad))
    gain_totals = all_sum(
        jnp.concatenate([input_gain_part, q_gain_part, k_gain_part, post_gain_part])
    )
    member_f = lax.axis_index("fsdp")
    sizes = (input_gain.shape[0], q_gain.shape[0], k_gain.shape[0], post_gain.shape[0])
    gain_shards = []
    at = 0
    for own in sizes:
        whole = own * fs
        gain_shards.append(lax.dynamic_slice_in_dim(gain_totals, at + member_f * own, own, 0))
        at += whole
    input_gain_shard, q_gain_shard, k_gain_shard, post_gain_shard = gain_shards
    gate_shard, up_shard, down_shard_t, out_shard_t = mlp_shards
    return (
        output,
        input_grad,
        query_shard,
        key_shard,
        value_shard,
        jnp.transpose(out_shard_t),
        gate_shard,
        up_shard,
        jnp.transpose(down_shard_t),
        input_gain_shard,
        q_gain_shard,
        k_gain_shard,
        post_gain_shard,
    )


def solution(mesh):
    return layer_program(mesh)


def layer_program(mesh):
    placed = (
        P(("fsdp", "tensor"), None),
        P(("fsdp", "tensor"), None),
        P(),
        P("fsdp", "tensor"),
        P("fsdp", "tensor"),
        P("fsdp", "tensor"),
        P("tensor", "fsdp"),
        P("fsdp", "tensor"),
        P("fsdp", "tensor"),
        P("tensor", "fsdp"),
        P("fsdp"),
        P("fsdp"),
        P("fsdp"),
        P("fsdp"),
    )
    return jax.shard_map(
        shards,
        mesh=mesh,
        in_specs=placed,
        out_specs=(
            P(("fsdp", "tensor"), None),
            P(("fsdp", "tensor"), None),
            P("fsdp", "tensor"),
            P("fsdp", "tensor"),
            P("fsdp", "tensor"),
            P("tensor", "fsdp"),
            P("fsdp", "tensor"),
            P("fsdp", "tensor"),
            P("tensor", "fsdp"),
            P("fsdp"),
            P("fsdp"),
            P("fsdp"),
            P("fsdp"),
        ),
        check_vma=False,
    )
```

```python
import functools

import numpy as np
import jax
import jax.numpy as jnp
from jax import lax
from jax.experimental import pallas as pl
from jax.experimental.pallas import tpu as pltpu
from jax.sharding import PartitionSpec as P


HEAD_SIZE = 128
TRANS_B = (((1,), (1,)), ((), ()))
TRANS_A = (((0,), (0,)), ((), ()))


def _own_place(p, quarter, r):
    return (p * quarter + r) if r < quarter else ((3 - p) * quarter + r - quarter)


def _far_place(p, quarter, r):
    return ((1 - p) * quarter + r) if r < quarter else ((2 + p) * quarter + r - quarter)


def _pair_tables(p, quarter, block, by_key, source):
    rows = 2 * quarter
    count = rows // block
    kmap = {}
    for src, fn in ((0, _own_place), (1, _far_place)):
        for j in range(count):
            kmap[fn(p, quarter, j * block) // block] = (src, j)
    pairs = []
    for j in range(count):
        qpb = _own_place(p, quarter, j * block) // block
        for kpb in range(qpb + 1):
            if kmap[kpb][0] == source:
                pairs.append((j, qpb, kpb))
    if by_key:
        pairs.sort(key=lambda t: (t[2], t[0]))
    group = [t[2] if by_key else t[0] for t in pairs]
    size = len(pairs)
    first = [1 if n == 0 or group[n - 1] != group[n] else 0 for n in range(size)]
    last = [1 if n == size - 1 or group[n + 1] != group[n] else 0 for n in range(size)]
    return np.array(
        [
            [t[0] for t in pairs],
            [t[1] for t in pairs],
            [t[2] for t in pairs],
            [kmap[t[2]][0] for t in pairs],
            [kmap[t[2]][1] for t in pairs],
            first,
            last,
        ],
        np.int32,
    )


def pair_tables(piece, quarter, block, by_key, source):
    t0 = _pair_tables(0, quarter, block, by_key, source)
    t1 = _pair_tables(1, quarter, block, by_key, source)
    assert t0.shape == t1.shape
    return jnp.where(piece == 0, jnp.asarray(t0), jnp.asarray(t1))


def _mask(qpb, kpb, qs, block):
    qp = qpb * block + lax.broadcasted_iota(jnp.int32, (block, block), 0)
    kp = kpb * block + lax.broadcasted_iota(jnp.int32, (block, block), 1)
    start = jnp.tile(qs, (1, block // 128))
    return (kp >= start) & (kp <= qp)


def _fwd_kernel(tab_ref, q_ref, qs_ref, k_ref, v_ref, a_in_ref, l_in_ref, a_ref, l_ref, acc_ref, sum_ref, *, scale, block):
    n = pl.program_id(1)
    share = q_ref.shape[1]

    @pl.when(tab_ref[5, n] == 1)
    def _():
        acc_ref[...] = a_in_ref[0].reshape(share * block, HEAD_SIZE)
        sum_ref[...] = l_in_ref[0][:, :, :1]

    q = q_ref[0].reshape(share * block, HEAD_SIZE)
    k = k_ref[0]
    v = v_ref[0]
    s = lax.dot_general(q, k, TRANS_B, preferred_element_type=jnp.float32) * scale
    allowed = _mask(tab_ref[1, n], tab_ref[2, n], qs_ref[...], block)
    e = jnp.where(allowed[None], jnp.exp(s.reshape(share, block, block)), 0.0)
    sum_ref[...] += jnp.sum(e, axis=-1, keepdims=True)
    acc_ref[...] += jnp.dot(
        e.reshape(share * block, block).astype(jnp.bfloat16), v, preferred_element_type=jnp.float32
    )

    @pl.when(tab_ref[6, n] == 1)
    def _():
        a_ref[0] = acc_ref[...].reshape(share, block, HEAD_SIZE)
        l_ref[0] = jnp.broadcast_to(sum_ref[...], (share, block, 128))


def attention_forward(q, qs, keys, values, a_in, l_in, piece, quarter, source, block=512):
    kvh, share, _, _ = q.shape
    tab = pair_tables(piece, quarter, block, False, source)
    npairs = tab.shape[1]
    scale = HEAD_SIZE ** (-0.5)
    row_spec = pl.BlockSpec((1, share, block, HEAD_SIZE), lambda h, n, t: (h, 0, t[0, n], 0))
    lane_spec = pl.BlockSpec((1, share, block, 128), lambda h, n, t: (h, 0, t[0, n], 0))
    key_spec = pl.BlockSpec((1, block, HEAD_SIZE), lambda h, n, t: (h, t[4, n], 0))
    grid_spec = pltpu.PrefetchScalarGridSpec(
        num_scalar_prefetch=1,
        grid=(kvh, npairs),
        in_specs=[
            row_spec,
            pl.BlockSpec((block, 128), lambda h, n, t: (t[0, n], 0)),
            key_spec,
            key_spec,
            row_spec,
            lane_spec,
        ],
        out_specs=[row_spec, lane_spec],
        scratch_shapes=[
            pltpu.VMEM((share * block, HEAD_SIZE), jnp.float32),
            pltpu.VMEM((share, block, 1), jnp.float32),
        ],
    )
    flops = 4 * kvh * npairs * share * block * block * HEAD_SIZE
    return pl.pallas_call(
        functools.partial(_fwd_kernel, scale=scale, block=block),
        grid_spec=grid_spec,
        out_shape=[
            jax.ShapeDtypeStruct(a_in.shape, jnp.float32),
            jax.ShapeDtypeStruct(l_in.shape, jnp.float32),
        ],
        input_output_aliases={5: 0, 6: 1},
        compiler_params=pltpu.CompilerParams(
            dimension_semantics=("arbitrary", "arbitrary"), vmem_limit_bytes=48 * 1024 * 1024
        ),
        cost_estimate=pl.CostEstimate(
            flops=flops,
            transcendentals=kvh * npairs * share * block * block,
            bytes_accessed=kvh * npairs * (8 * block * HEAD_SIZE * 2),
        ),
        name="attn_fwd",
    )(tab, q, qs, keys, values, a_in, l_in)


def _bwd_kernel(tab_ref, q_ref, h_ref, dl_ref, qs_ref, k_ref, v_ref, dq_in_ref, dq_ref, dk_ref, dv_ref, dk_acc, dv_acc, *, scale, block):
    n = pl.program_id(1)
    share = q_ref.shape[1]

    @pl.when(n == 0)
    def _():
        dq_ref[...] = dq_in_ref[...]

    @pl.when(tab_ref[5, n] == 1)
    def _():
        dk_acc[...] = jnp.zeros(dk_acc.shape, dk_acc.dtype)
        dv_acc[...] = jnp.zeros(dv_acc.shape, dv_acc.dtype)

    q = q_ref[0].reshape(share * block, HEAD_SIZE)
    hh = h_ref[0].reshape(share * block, HEAD_SIZE)
    k = k_ref[0]
    v = v_ref[0]
    s = lax.dot_general(q, k, TRANS_B, preferred_element_type=jnp.float32) * scale
    allowed = _mask(tab_ref[1, n], tab_ref[2, n], qs_ref[...], block)
    e = jnp.where(allowed[None], jnp.exp(s.reshape(share, block, block)), 0.0)
    dp = lax.dot_general(hh, v, TRANS_B, preferred_element_type=jnp.float32).reshape(share, block, block)
    delta = jnp.tile(dl_ref[0], (1, 1, block // 128))
    ds = (e * (dp - delta)).reshape(share * block, block).astype(jnp.bfloat16)
    rows = pl.ds(pl.multiple_of(tab_ref[0, n] * block, block), block)
    dq_ref[0, :, rows, :] += jnp.dot(ds, k, preferred_element_type=jnp.float32).reshape(share, block, HEAD_SIZE)
    dk_acc[...] += lax.dot_general(ds, q, TRANS_A, preferred_element_type=jnp.float32)
    dv_acc[...] += lax.dot_general(
        e.reshape(share * block, block).astype(jnp.bfloat16), hh, TRANS_A, preferred_element_type=jnp.float32
    )

    @pl.when(tab_ref[6, n] == 1)
    def _():
        dk_ref[0] = dk_acc[...] * scale
        dv_ref[0] = dv_acc[...]


def attention_backward(q, hgrad, delta, qs, keys, values, dq_in, piece, quarter, source, block=512):
    kvh, share, rows, _ = q.shape
    tab = pair_tables(piece, quarter, block, True, source)
    npairs = tab.shape[1]
    scale = HEAD_SIZE ** (-0.5)
    row_spec = pl.BlockSpec((1, share, block, HEAD_SIZE), lambda h, n, t: (h, 0, t[0, n], 0))
    key_spec = pl.BlockSpec((1, block, HEAD_SIZE), lambda h, n, t: (h, t[4, n], 0))
    full_spec = pl.BlockSpec((1, share, rows, HEAD_SIZE), lambda h, n, t: (h, 0, 0, 0))
    grid_spec = pltpu.PrefetchScalarGridSpec(
        num_scalar_prefetch=1,
        grid=(kvh, npairs),
        in_specs=[
            row_spec,
            row_spec,
            pl.BlockSpec((1, share, block, 128), lambda h, n, t: (h, 0, t[0, n], 0)),
            pl.BlockSpec((block, 128), lambda h, n, t: (t[0, n], 0)),
            key_spec,
            key_spec,
            full_spec,
        ],
        out_specs=[full_spec, key_spec, key_spec],
        scratch_shapes=[
            pltpu.VMEM((block, HEAD_SIZE), jnp.float32),
            pltpu.VMEM((block, HEAD_SIZE), jnp.float32),
        ],
    )
    flops = 10 * kvh * npairs * share * block * block * HEAD_SIZE
    return pl.pallas_call(
        functools.partial(_bwd_kernel, scale=scale, block=block),
        grid_spec=grid_spec,
        out_shape=[
            jax.ShapeDtypeStruct(dq_in.shape, jnp.float32),
            jax.ShapeDtypeStruct(keys.shape, jnp.float32),
            jax.ShapeDtypeStruct(values.shape, jnp.float32),
        ],
        input_output_aliases={7: 0},
        compiler_params=pltpu.CompilerParams(
            dimension_semantics=("arbitrary", "arbitrary"), vmem_limit_bytes=56 * 1024 * 1024
        ),
        cost_estimate=pl.CostEstimate(
            flops=flops,
            transcendentals=kvh * npairs * share * block * block,
            bytes_accessed=kvh * npairs * (10 * block * HEAD_SIZE * 2),
        ),
        name="attn_bwd",
    )(tab, q, hgrad, delta, qs, keys, values, dq_in)


PIECES = 2


EPSILON = 1e-06
THETA = 1000000.0


def swapped(shard, axis, distance):
    return lax.ppermute(shard, axis, [(i, i ^ 1 << distance) for i in range(lax.axis_size(axis))])


def rms_scale(values, gain):
    inverse = lax.rsqrt(jnp.mean(values * values, axis=-1, keepdims=True) + EPSILON)
    return values * inverse * gain


def rotary(values, start_offset):
    half = values.shape[-1] // 2
    frequency = THETA ** (-(jnp.arange(half, dtype=jnp.float32) * 2.0 / values.shape[-1]))
    angle = start_offset.astype(jnp.float32)[:, None] * frequency[None, :]
    cosine = jnp.cos(angle)[:, None, :]
    sine = jnp.sin(angle)[:, None, :]
    first = values[..., :half]
    second = values[..., half:]
    return jnp.concatenate(
        [first * cosine - second * sine, second * cosine + first * sine], axis=-1
    )


def prepare_inputs(projected, gain, start_offset, head_groups):
    shaped = projected.reshape(projected.shape[0], head_groups, -1)
    return rotary(rms_scale(shaped, gain), start_offset)


def piece_places(which, group_rows):
    quarter = group_rows // 2
    local = jnp.arange(group_rows, dtype=jnp.int32)
    chosen = jnp.where(local < quarter, which, 3 - which)
    return chosen * quarter + local % quarter


def contract_rows(left, right):
    return lax.dot_general(
        left, right, (((0,), (0,)), ((), ())), preferred_element_type=jnp.float32
    )


def contract_last(left, right):
    return lax.dot_general(
        left, right, (((1,), (1,)), ((), ())), preferred_element_type=jnp.float32
    )


def split_columns(full, widths):
    parts = []
    at = 0
    for width in widths:
        parts.append(full[:, at : at + width])
        at += width
    return parts


def halving_scatter(grads):
    widths = [g.shape[1] for g in grads]
    packed = jnp.concatenate(grads, axis=1)
    count = lax.axis_size("fsdp")
    me = lax.axis_index("fsdp")
    bits = count.bit_length() - 1
    rows_f = packed.shape[0] // count
    order = [int(format(b, f"0{bits}b")[::-1], 2) for b in range(count)]
    buf = jnp.concatenate([packed[b * rows_f : (b + 1) * rows_f] for b in order], axis=0)
    for bit in range(bits):
        half = buf.shape[0] // 2
        mine = (me >> bit) & 1
        keep = lax.dynamic_slice_in_dim(buf, mine * half, half, 0)
        send = lax.dynamic_slice_in_dim(buf, (1 - mine) * half, half, 0)
        got = lax.ppermute(
            send.astype(jnp.bfloat16), "fsdp", [(i, i ^ (1 << bit)) for i in range(count)]
        )
        buf = keep + got.astype(jnp.float32)
    return split_columns(buf, widths)


def fsdp_gather(values):
    count = lax.axis_size("fsdp")
    me = lax.axis_index("fsdp")
    distance = 1
    while distance < count:
        got = lax.ppermute(values, "fsdp", [(i, i ^ distance) for i in range(count)])
        low = (me & distance) == 0
        values = jnp.concatenate(
            [jnp.where(low, values, got), jnp.where(low, got, values)]
        )
        distance *= 2
    return values


def all_sum(values):
    for axis in ("tensor", "fsdp"):
        distance = 1
        while distance < lax.axis_size(axis):
            values = values + lax.ppermute(
                values, axis, [(i, i ^ distance) for i in range(lax.axis_size(axis))]
            )
            distance *= 2
    return values


def exchange(values, distance):
    count = lax.axis_size("tensor")
    return lax.ppermute(values, "tensor", [(i, i ^ distance) for i in range(count)])


def token_gather(values):
    return finish_gather(values, exchange(values, 2))


def finish_gather(values, across):
    rows = values.shape[0]
    me = lax.axis_index("tensor")
    pair = jnp.stack([values, across])
    beside = exchange(pair, 1)
    full = jnp.zeros((4 * rows,) + values.shape[1:], values.dtype)
    for part, place in ((values, me), (across, me ^ 2), (beside[0], me ^ 1), (beside[1], me ^ 3)):
        full = lax.dynamic_update_slice_in_dim(full, part, place * rows, 0)
    return full


def token_sum(term, rows):
    partial = term(jnp.int32(0), rows * lax.axis_size("tensor"))
    me = lax.axis_index("tensor")

    def block(place):
        return lax.dynamic_slice_in_dim(partial, place * rows, rows, 0)

    sent = jnp.stack([block(me ^ 1), block(me ^ 3)]).astype(jnp.bfloat16)
    got = exchange(sent, 1).astype(jnp.float32)
    mine = block(me) + got[0]
    other = (block(me ^ 2) + got[1]).astype(jnp.bfloat16)
    return mine + exchange(other, 2).astype(jnp.float32)


def shards(
    hidden,
    out_grad,
    lengths,
    q_weight,
    key_matrix,
    value_matrix,
    o_weight,
    gate_weight,
    up_weight,
    down_weight,
    input_gain,
    q_gain,
    k_gain,
    post_gain,
):
    split = lax.axis_size("tensor")
    rows = hidden.shape[0]
    group_rows = rows * split
    q_heads = q_weight.shape[1] // HEAD_SIZE
    kv_heads = key_matrix.shape[1] // HEAD_SIZE
    share = q_heads // kv_heads
    scale = HEAD_SIZE ** (-0.5)
    member = lax.axis_index("fsdp")
    slot = member // PIECES
    piece = member % PIECES
    lengths_row = lax.dynamic_index_in_dim(lengths, slot, 0, keepdims=False)
    ends = jnp.cumsum(lengths_row)
    group_place = piece_places(piece, group_rows)
    passed = group_place[:, None] >= ends[None, :]
    group_start = jnp.sum(jnp.where(passed, lengths_row[None, :], 0), axis=1)
    group_offset = group_place - group_start
    local_valid = lax.dynamic_slice_in_dim(
        group_place < ends[-1], lax.axis_index("tensor") * rows, rows, 0
    )
    fs = lax.axis_size("fsdp")
    gain_sizes = (input_gain.shape[0], q_gain.shape[0], k_gain.shape[0], post_gain.shape[0])
    gains_all = fsdp_gather(
        jnp.concatenate([input_gain, q_gain, k_gain, post_gain]).astype(jnp.bfloat16)
    ).reshape(fs, sum(gain_sizes))
    gain_in, gain_query, gain_keys, gain_post = [
        part.reshape(-1) for part in split_columns(gains_all, gain_sizes)
    ]
    kv_full = lax.all_gather(
        jnp.concatenate(
            [key_matrix.astype(jnp.bfloat16), value_matrix.astype(jnp.bfloat16)], axis=1
        ),
        "fsdp",
        axis=0,
        tiled=True,
    )
    w_key, w_value = split_columns(kv_full, (key_matrix.shape[1], value_matrix.shape[1]))
    w_query = lax.all_gather(q_weight.astype(jnp.bfloat16), "fsdp", axis=0, tiled=True)
    od_full = lax.all_gather(
        jnp.concatenate(
            [
                jnp.transpose(o_weight).astype(jnp.bfloat16),
                jnp.transpose(down_weight).astype(jnp.bfloat16),
            ],
            axis=1,
        ),
        "fsdp",
        axis=0,
        tiled=True,
    )
    w_out, w_down_t = split_columns(od_full, (o_weight.shape[0], down_weight.shape[0]))
    x_float = hidden.astype(jnp.float32)
    gain_first = gain_in.astype(jnp.float32)
    first_all = token_gather(rms_scale(x_float, gain_first).astype(jnp.bfloat16))
    cotangent = out_grad.astype(jnp.float32) * local_valid[:, None].astype(jnp.float32)
    cotangent_low, first_all = lax.optimization_barrier((cotangent.astype(jnp.bfloat16), first_all))
    cotangent_across = exchange(cotangent_low, 2)
    query_projected = jnp.dot(first_all, w_query, preferred_element_type=jnp.float32)
    key_projected = jnp.dot(first_all, w_key, preferred_element_type=jnp.float32)
    value_rows = (
        jnp.dot(first_all, w_value, preferred_element_type=jnp.float32)
        .astype(jnp.bfloat16)
        .reshape(group_rows, kv_heads, HEAD_SIZE)
    )
    gain_q = gain_query.astype(jnp.float32)
    gain_k = gain_keys.astype(jnp.float32)
    query_rope = (
        prepare_inputs(query_projected, gain_q, group_offset, q_heads)
        .astype(jnp.bfloat16)
        .reshape(group_rows, kv_heads, share, HEAD_SIZE)
    )
    key_rope = prepare_inputs(key_projected, gain_k, group_offset, kv_heads).astype(jnp.bfloat16)
    quarter = group_rows // 2
    query_start = jnp.broadcast_to(group_start[:, None], (group_rows, 128))
    query_t = jnp.transpose(query_rope, (1, 2, 0, 3))
    own_keys = jnp.transpose(key_rope, (1, 0, 2))
    own_values = jnp.transpose(value_rows, (1, 0, 2))
    moved = swapped(jnp.stack([own_keys, own_values]), "fsdp", 0)
    sums = jnp.zeros(query_t.shape, jnp.float32)
    totals = jnp.zeros(query_t.shape[:3] + (128,), jnp.float32)
    sums, totals = attention_forward(
        query_t, query_start, own_keys, own_values, sums, totals, piece, quarter, 0
    )
    cotangent_across, sums, totals = lax.optimization_barrier((cotangent_across, sums, totals))
    mlp_grad_all = finish_gather(cotangent_low, cotangent_across)
    sums, totals_t = attention_forward(
        query_t, query_start, moved[0], moved[1], sums, totals, piece, quarter, 1
    )
    mlp_grad_all, sums, totals_t = lax.optimization_barrier((mlp_grad_all, sums, totals_t))
    heads_t = sums / totals_t[..., :1]
    heads_out = jnp.transpose(heads_t, (2, 0, 1, 3))
    row_totals = jnp.transpose(totals_t[..., 0], (2, 0, 1))
    out_rows = heads_out.reshape(group_rows, q_heads * HEAD_SIZE).astype(jnp.bfloat16)

    mlp_full = lax.all_gather(
        jnp.concatenate(
            [
                gate_weight.astype(jnp.bfloat16),
                up_weight.astype(jnp.bfloat16),
            ],
            axis=1,
        ),
        "fsdp",
        axis=0,
        tiled=True,
    )
    w_gate, w_up = split_columns(mlp_full, (gate_weight.shape[1], up_weight.shape[1]))
    out_partial = contract_last(out_rows, w_out)
    late_grad_all, out_partial = lax.optimization_barrier((mlp_grad_all, out_partial))
    grad_act = jnp.dot(late_grad_all, w_down_t, preferred_element_type=jnp.float32)
    after_attn = x_float + token_sum(lambda start, count: out_partial, rows)
    grad_act, after_attn = lax.optimization_barrier((grad_act, after_attn))
    gain_second = gain_post.astype(jnp.float32)
    second_all = token_gather(rms_scale(after_attn, gain_second).astype(jnp.bfloat16))
    gate_out = jnp.dot(second_all, w_gate, preferred_element_type=jnp.float32)
    up_out = jnp.dot(second_all, w_up, preferred_element_type=jnp.float32)
    activated = (jax.nn.silu(gate_out) * up_out).astype(jnp.bfloat16)

    unused, pull_gate = jax.vjp(
        lambda gate_in, up_in: jax.nn.silu(gate_in) * up_in, gate_out, up_out
    )
    grad_gate, grad_up = pull_gate(grad_act)
    grad_gate = grad_gate.astype(jnp.bfloat16)
    grad_up = grad_up.astype(jnp.bfloat16)
    second_partial = contract_last(grad_gate, w_gate) + contract_last(grad_up, w_up)
    grad_inputs, second_partial = lax.optimization_barrier(
        ((mlp_grad_all, activated, second_all, grad_gate, grad_up), second_partial)
    )
    late_c, late_act, late_second, late_gate, late_up = grad_inputs
    down_grad_t = contract_rows(late_c, late_act)
    gate_grad = contract_rows(late_second, late_gate)
    up_grad = contract_rows(late_second, late_up)
    second_back = token_sum(lambda start, count: second_partial, rows)
    unused, pull_second = jax.vjp(rms_scale, after_attn, gain_second)
    norm_second_grad, post_gain_part = pull_second(second_back)
    residual_grad = cotangent + norm_second_grad
    weight_grads, residual_grad = lax.optimization_barrier(
        ((gate_grad, up_grad, down_grad_t), residual_grad)
    )
    gate_grad, up_grad, down_grad_t = weight_grads
    attn_grad_all = token_gather(residual_grad.astype(jnp.bfloat16))
    activated_late, attn_grad_all = lax.optimization_barrier((activated, attn_grad_all))
    down_rows = token_sum(lambda start, count: contract_last(activated_late, w_down_t), rows)
    out_weight_grad_t = contract_rows(attn_grad_all, out_rows)
    mlp_packed = jnp.concatenate(
        [g.astype(jnp.bfloat16) for g in (gate_grad, up_grad, down_grad_t, out_weight_grad_t)],
        axis=1,
    )
    head_grad = jnp.dot(attn_grad_all, w_out, preferred_element_type=jnp.float32).astype(
        jnp.bfloat16
    )
    head_float = head_grad.astype(jnp.float32).reshape(group_rows, kv_heads, share, HEAD_SIZE)
    scaled_grad = (head_float / row_totals[..., None]).astype(jnp.bfloat16)
    delta = jnp.sum(head_float * heads_out, axis=-1) / row_totals

    grad_t = jnp.transpose(scaled_grad, (1, 2, 0, 3))
    delta_t = jnp.broadcast_to(
        jnp.transpose(delta, (1, 2, 0))[..., None], (kv_heads, share, group_rows, 128)
    )
    mlp_packed, grad_t, delta_t = lax.optimization_barrier((mlp_packed, grad_t, delta_t))
    mlp_shards = split_columns(
        lax.psum_scatter(mlp_packed, "fsdp", scatter_dimension=0, tiled=True),
        [g.shape[1] for g in (gate_grad, up_grad, down_grad_t, out_weight_grad_t)],
    )
    mlp_shards = [part.astype(jnp.float32) for part in mlp_shards]
    dq_raw, dk_far, dv_far = attention_backward(
        query_t, grad_t, delta_t, query_start, moved[0], moved[1],
        jnp.zeros(query_t.shape, jnp.float32), piece, quarter, 1,
    )
    unseen = (piece == 1) & (jnp.arange(group_rows) >= quarter)
    far_grads = jnp.where(unseen[None, None, :, None], 0.0, jnp.stack([dk_far, dv_far]))
    returned = swapped(far_grads.astype(jnp.bfloat16), "fsdp", 0)
    down_rows, dq_raw = lax.optimization_barrier((down_rows, dq_raw))
    output = (after_attn + down_rows).astype(jnp.bfloat16)
    dq_raw, dk_own, dv_own = attention_backward(
        query_t, grad_t, delta_t, query_start, own_keys, own_values,
        dq_raw, piece, quarter, 0,
    )
    mlp_shards, dq_raw = lax.optimization_barrier((mlp_shards, dq_raw))
    grad_keys_total = jnp.transpose(dk_own + returned[0].astype(jnp.float32), (1, 0, 2))
    grad_values_total = jnp.transpose(dv_own + returned[1].astype(jnp.float32), (1, 0, 2))
    query_grads = jnp.transpose(dq_raw, (2, 0, 1, 3)) * scale
    query_grads = query_grads.reshape(group_rows, q_heads, HEAD_SIZE)
    unused, pull_query = jax.vjp(
        lambda projected, gain: prepare_inputs(projected, gain, group_offset, q_heads),
        query_projected,
        gain_q,
    )
    query_proj_grad, q_gain_part = pull_query(query_grads)
    unused, pull_key = jax.vjp(
        lambda projected, gain: prepare_inputs(projected, gain, group_offset, kv_heads),
        key_projected,
        gain_k,
    )
    key_proj_grad, k_gain_part = pull_key(grad_keys_total)
    query_low = query_proj_grad.astype(jnp.bfloat16)
    key_low = key_proj_grad.astype(jnp.bfloat16)
    value_low = grad_values_total.reshape(group_rows, kv_heads * HEAD_SIZE).astype(jnp.bfloat16)
    query_weight_grad = contract_rows(first_all, query_low)
    key_weight_grad = contract_rows(first_all, key_low)
    value_weight_grad = contract_rows(first_all, value_low)

    def first_term(start, count):
        return (
            contract_last(query_low, w_query)
            + contract_last(key_low, w_key)
            + contract_last(value_low, w_value)
        )

    first_back = token_sum(first_term, rows)
    unused, pull_first = jax.vjp(rms_scale, x_float, gain_first)
    norm_first_grad, input_gain_part = pull_first(first_back)
    input_grad = (residual_grad + norm_first_grad).astype(jnp.bfloat16)
    (query_shard,) = halving_scatter((query_weight_grad,))
    key_shard, value_shard = halving_scatter((key_weight_grad, value_weight_grad))
    gain_totals = all_sum(
        jnp.concatenate([input_gain_part, q_gain_part, k_gain_part, post_gain_part])
    )
    member_f = lax.axis_index("fsdp")
    sizes = (input_gain.shape[0], q_gain.shape[0], k_gain.shape[0], post_gain.shape[0])
    gain_shards = []
    at = 0
    for own in sizes:
        whole = own * fs
        gain_shards.append(lax.dynamic_slice_in_dim(gain_totals, at + member_f * own, own, 0))
        at += whole
    input_gain_shard, q_gain_shard, k_gain_shard, post_gain_shard = gain_shards
    gate_shard, up_shard, down_shard_t, out_shard_t = mlp_shards
    return (
        output,
        input_grad,
        query_shard,
        key_shard,
        value_shard,
        jnp.transpose(out_shard_t),
        gate_shard,
        up_shard,
        jnp.transpose(down_shard_t),
        input_gain_shard,
        q_gain_shard,
        k_gain_shard,
        post_gain_shard,
    )


def solution(mesh):
    return layer_program(mesh)


def layer_program(mesh):
    placed = (
        P(("fsdp", "tensor"), None),
        P(("fsdp", "tensor"), None),
        P(),
        P("fsdp", "tensor"),
        P("fsdp", "tensor"),
        P("fsdp", "tensor"),
        P("tensor", "fsdp"),
        P("fsdp", "tensor"),
        P("fsdp", "tensor"),
        P("tensor", "fsdp"),
        P("fsdp"),
        P("fsdp"),
        P("fsdp"),
        P("fsdp"),
    )
    return jax.shard_map(
        shards,
        mesh=mesh,
        in_specs=placed,
        out_specs=(
            P(("fsdp", "tensor"), None),
            P(("fsdp", "tensor"), None),
            P("fsdp", "tensor"),
            P("fsdp", "tensor"),
            P("fsdp", "tensor"),
            P("tensor", "fsdp"),
            P("fsdp", "tensor"),
            P("fsdp", "tensor"),
            P("tensor", "fsdp"),
            P("fsdp"),
            P("fsdp"),
            P("fsdp"),
            P("fsdp"),
        ),
        check_vma=False,
    )
```

```python
import functools

import numpy as np
import jax
import jax.numpy as jnp
from jax import lax
from jax.experimental import pallas as pl
from jax.experimental.pallas import tpu as pltpu
from jax.sharding import PartitionSpec as P


HEAD_SIZE = 128
TRANS_B = (((1,), (1,)), ((), ()))
TRANS_A = (((0,), (0,)), ((), ()))


def _own_place(p, quarter, r):
    return (p * quarter + r) if r < quarter else ((3 - p) * quarter + r - quarter)


def _far_place(p, quarter, r):
    return ((1 - p) * quarter + r) if r < quarter else ((2 + p) * quarter + r - quarter)


def _pair_tables(p, quarter, block, by_key, source):
    rows = 2 * quarter
    count = rows // block
    kmap = {}
    for src, fn in ((0, _own_place), (1, _far_place)):
        for j in range(count):
            kmap[fn(p, quarter, j * block) // block] = (src, j)
    pairs = []
    for j in range(count):
        qpb = _own_place(p, quarter, j * block) // block
        for kpb in range(qpb + 1):
            if kmap[kpb][0] == source:
                pairs.append((j, qpb, kpb))
    if by_key:
        pairs.sort(key=lambda t: (t[2], t[0]))
    group = [t[2] if by_key else t[0] for t in pairs]
    size = len(pairs)
    first = [1 if n == 0 or group[n - 1] != group[n] else 0 for n in range(size)]
    last = [1 if n == size - 1 or group[n + 1] != group[n] else 0 for n in range(size)]
    return np.array(
        [
            [t[0] for t in pairs],
            [t[1] for t in pairs],
            [t[2] for t in pairs],
            [kmap[t[2]][0] for t in pairs],
            [kmap[t[2]][1] for t in pairs],
            first,
            last,
        ],
        np.int32,
    )


def pair_tables(piece, quarter, block, by_key, source):
    t0 = _pair_tables(0, quarter, block, by_key, source)
    t1 = _pair_tables(1, quarter, block, by_key, source)
    assert t0.shape == t1.shape
    return jnp.where(piece == 0, jnp.asarray(t0), jnp.asarray(t1))


def _mask(qpb, kpb, qs, block):
    qp = qpb * block + lax.broadcasted_iota(jnp.int32, (block, block), 0)
    kp = kpb * block + lax.broadcasted_iota(jnp.int32, (block, block), 1)
    start = jnp.tile(qs, (1, block // 128))
    return (kp >= start) & (kp <= qp)


def _block_kind(tab_ref, qb_ref, n, block):
    j = tab_ref[0, n]
    key_first = tab_ref[2, n] * block
    key_last = key_first + block - 1
    full = (key_last < tab_ref[1, n] * block) & (key_first >= qb_ref[1, j])
    empty = key_last < qb_ref[0, j]
    return full, jnp.logical_not(full) & jnp.logical_not(empty)


def _fwd_kernel(tab_ref, qb_ref, q_ref, qs_ref, k_ref, v_ref, a_in_ref, l_in_ref, a_ref, l_ref, acc_ref, sum_ref, *, scale, block):
    n = pl.program_id(1)
    share = q_ref.shape[1]

    @pl.when(tab_ref[5, n] == 1)
    def _():
        acc_ref[...] = a_in_ref[0].reshape(share * block, HEAD_SIZE)
        sum_ref[...] = l_in_ref[0][:, :, :1]

    def step(masked):
        q = q_ref[0].reshape(share * block, HEAD_SIZE)
        k = k_ref[0]
        v = v_ref[0]
        s = lax.dot_general(q, k, TRANS_B, preferred_element_type=jnp.float32) * scale
        e = jnp.exp(s.reshape(share, block, block))
        if masked:
            allowed = _mask(tab_ref[1, n], tab_ref[2, n], qs_ref[...], block)
            e = jnp.where(allowed[None], e, 0.0)
        sum_ref[...] += jnp.sum(e, axis=-1, keepdims=True)
        acc_ref[...] += jnp.dot(
            e.reshape(share * block, block).astype(jnp.bfloat16), v, preferred_element_type=jnp.float32
        )

    full, partial = _block_kind(tab_ref, qb_ref, n, block)
    pl.when(full)(lambda: step(False))
    pl.when(partial)(lambda: step(True))

    @pl.when(tab_ref[6, n] == 1)
    def _():
        a_ref[0] = acc_ref[...].reshape(share, block, HEAD_SIZE)
        l_ref[0] = jnp.broadcast_to(sum_ref[...], (share, block, 128))


def attention_forward(q, qs, qb, keys, values, a_in, l_in, piece, quarter, source, block=512):
    kvh, share, _, _ = q.shape
    tab = pair_tables(piece, quarter, block, False, source)
    npairs = tab.shape[1]
    scale = HEAD_SIZE ** (-0.5)
    row_spec = pl.BlockSpec((1, share, block, HEAD_SIZE), lambda h, n, t, b: (h, 0, t[0, n], 0))
    lane_spec = pl.BlockSpec((1, share, block, 128), lambda h, n, t, b: (h, 0, t[0, n], 0))
    key_spec = pl.BlockSpec((1, block, HEAD_SIZE), lambda h, n, t, b: (h, t[4, n], 0))
    grid_spec = pltpu.PrefetchScalarGridSpec(
        num_scalar_prefetch=2,
        grid=(kvh, npairs),
        in_specs=[
            row_spec,
            pl.BlockSpec((block, 128), lambda h, n, t, b: (t[0, n], 0)),
            key_spec,
            key_spec,
            row_spec,
            lane_spec,
        ],
        out_specs=[row_spec, lane_spec],
        scratch_shapes=[
            pltpu.VMEM((share * block, HEAD_SIZE), jnp.float32),
            pltpu.VMEM((share, block, 1), jnp.float32),
        ],
    )
    flops = 4 * kvh * npairs * share * block * block * HEAD_SIZE
    return pl.pallas_call(
        functools.partial(_fwd_kernel, scale=scale, block=block),
        grid_spec=grid_spec,
        out_shape=[
            jax.ShapeDtypeStruct(a_in.shape, jnp.float32),
            jax.ShapeDtypeStruct(l_in.shape, jnp.float32),
        ],
        input_output_aliases={6: 0, 7: 1},
        compiler_params=pltpu.CompilerParams(
            dimension_semantics=("arbitrary", "arbitrary"), vmem_limit_bytes=48 * 1024 * 1024
        ),
        cost_estimate=pl.CostEstimate(
            flops=flops,
            transcendentals=kvh * npairs * share * block * block,
            bytes_accessed=kvh * npairs * (8 * block * HEAD_SIZE * 2),
        ),
        name="attn_fwd",
    )(tab, qb, q, qs, keys, values, a_in, l_in)


def _bwd_kernel(tab_ref, qb_ref, q_ref, h_ref, dl_ref, qs_ref, k_ref, v_ref, dq_in_ref, dq_ref, dk_ref, dv_ref, dk_acc, dv_acc, *, scale, block):
    n = pl.program_id(1)
    share = q_ref.shape[1]

    @pl.when(n == 0)
    def _():
        dq_ref[...] = dq_in_ref[...]

    @pl.when(tab_ref[5, n] == 1)
    def _():
        dk_acc[...] = jnp.zeros(dk_acc.shape, dk_acc.dtype)
        dv_acc[...] = jnp.zeros(dv_acc.shape, dv_acc.dtype)

    def step(masked):
        q = q_ref[0].reshape(share * block, HEAD_SIZE)
        hh = h_ref[0].reshape(share * block, HEAD_SIZE)
        k = k_ref[0]
        v = v_ref[0]
        s = lax.dot_general(q, k, TRANS_B, preferred_element_type=jnp.float32) * scale
        e = jnp.exp(s.reshape(share, block, block))
        if masked:
            allowed = _mask(tab_ref[1, n], tab_ref[2, n], qs_ref[...], block)
            e = jnp.where(allowed[None], e, 0.0)
        dp = lax.dot_general(hh, v, TRANS_B, preferred_element_type=jnp.float32).reshape(share, block, block)
        delta = jnp.tile(dl_ref[0], (1, 1, block // 128))
        ds = (e * (dp - delta)).reshape(share * block, block).astype(jnp.bfloat16)
        rows = pl.ds(pl.multiple_of(tab_ref[0, n] * block, block), block)
        dq_ref[0, :, rows, :] += jnp.dot(ds, k, preferred_element_type=jnp.float32).reshape(share, block, HEAD_SIZE)
        dk_acc[...] += lax.dot_general(ds, q, TRANS_A, preferred_element_type=jnp.float32)
        dv_acc[...] += lax.dot_general(
            e.reshape(share * block, block).astype(jnp.bfloat16), hh, TRANS_A, preferred_element_type=jnp.float32
        )

    full, partial = _block_kind(tab_ref, qb_ref, n, block)
    pl.when(full)(lambda: step(False))
    pl.when(partial)(lambda: step(True))

    @pl.when(tab_ref[6, n] == 1)
    def _():
        dk_ref[0] = dk_acc[...] * scale
        dv_ref[0] = dv_acc[...]


def attention_backward(q, hgrad, delta, qs, qb, keys, values, dq_in, piece, quarter, source, block=512):
    kvh, share, rows, _ = q.shape
    tab = pair_tables(piece, quarter, block, True, source)
    npairs = tab.shape[1]
    scale = HEAD_SIZE ** (-0.5)
    row_spec = pl.BlockSpec((1, share, block, HEAD_SIZE), lambda h, n, t, b: (h, 0, t[0, n], 0))
    key_spec = pl.BlockSpec((1, block, HEAD_SIZE), lambda h, n, t, b: (h, t[4, n], 0))
    full_spec = pl.BlockSpec((1, share, rows, HEAD_SIZE), lambda h, n, t, b: (h, 0, 0, 0))
    grid_spec = pltpu.PrefetchScalarGridSpec(
        num_scalar_prefetch=2,
        grid=(kvh, npairs),
        in_specs=[
            row_spec,
            row_spec,
            pl.BlockSpec((1, share, block, 128), lambda h, n, t, b: (h, 0, t[0, n], 0)),
            pl.BlockSpec((block, 128), lambda h, n, t, b: (t[0, n], 0)),
            key_spec,
            key_spec,
            full_spec,
        ],
        out_specs=[full_spec, key_spec, key_spec],
        scratch_shapes=[
            pltpu.VMEM((block, HEAD_SIZE), jnp.float32),
            pltpu.VMEM((block, HEAD_SIZE), jnp.float32),
        ],
    )
    flops = 10 * kvh * npairs * share * block * block * HEAD_SIZE
    return pl.pallas_call(
        functools.partial(_bwd_kernel, scale=scale, block=block),
        grid_spec=grid_spec,
        out_shape=[
            jax.ShapeDtypeStruct(dq_in.shape, jnp.float32),
            jax.ShapeDtypeStruct(keys.shape, jnp.float32),
            jax.ShapeDtypeStruct(values.shape, jnp.float32),
        ],
        input_output_aliases={8: 0},
        compiler_params=pltpu.CompilerParams(
            dimension_semantics=("arbitrary", "arbitrary"), vmem_limit_bytes=56 * 1024 * 1024
        ),
        cost_estimate=pl.CostEstimate(
            flops=flops,
            transcendentals=kvh * npairs * share * block * block,
            bytes_accessed=kvh * npairs * (10 * block * HEAD_SIZE * 2),
        ),
        name="attn_bwd",
    )(tab, qb, q, hgrad, delta, qs, keys, values, dq_in)


PIECES = 2


EPSILON = 1e-06
THETA = 1000000.0


def swapped(shard, axis, distance):
    return lax.ppermute(shard, axis, [(i, i ^ 1 << distance) for i in range(lax.axis_size(axis))])


def rms_scale(values, gain):
    inverse = lax.rsqrt(jnp.mean(values * values, axis=-1, keepdims=True) + EPSILON)
    return values * inverse * gain


def rotary(values, start_offset):
    half = values.shape[-1] // 2
    frequency = THETA ** (-(jnp.arange(half, dtype=jnp.float32) * 2.0 / values.shape[-1]))
    angle = start_offset.astype(jnp.float32)[:, None] * frequency[None, :]
    cosine = jnp.cos(angle)[:, None, :]
    sine = jnp.sin(angle)[:, None, :]
    first = values[..., :half]
    second = values[..., half:]
    return jnp.concatenate(
        [first * cosine - second * sine, second * cosine + first * sine], axis=-1
    )


def prepare_inputs(projected, gain, start_offset, head_groups):
    shaped = projected.reshape(projected.shape[0], head_groups, -1)
    return rotary(rms_scale(shaped, gain), start_offset)


def piece_places(which, group_rows):
    quarter = group_rows // 2
    local = jnp.arange(group_rows, dtype=jnp.int32)
    chosen = jnp.where(local < quarter, which, 3 - which)
    return chosen * quarter + local % quarter


def contract_rows(left, right):
    return lax.dot_general(
        left, right, (((0,), (0,)), ((), ())), preferred_element_type=jnp.float32
    )


def contract_last(left, right):
    return lax.dot_general(
        left, right, (((1,), (1,)), ((), ())), preferred_element_type=jnp.float32
    )


def split_columns(full, widths):
    parts = []
    at = 0
    for width in widths:
        parts.append(full[:, at : at + width])
        at += width
    return parts


def halving_scatter(grads):
    widths = [g.shape[1] for g in grads]
    packed = jnp.concatenate(grads, axis=1)
    count = lax.axis_size("fsdp")
    me = lax.axis_index("fsdp")
    bits = count.bit_length() - 1
    rows_f = packed.shape[0] // count
    order = [int(format(b, f"0{bits}b")[::-1], 2) for b in range(count)]
    buf = jnp.concatenate([packed[b * rows_f : (b + 1) * rows_f] for b in order], axis=0)
    for bit in range(bits):
        half = buf.shape[0] // 2
        mine = (me >> bit) & 1
        keep = lax.dynamic_slice_in_dim(buf, mine * half, half, 0)
        send = lax.dynamic_slice_in_dim(buf, (1 - mine) * half, half, 0)
        got = lax.ppermute(
            send.astype(jnp.bfloat16), "fsdp", [(i, i ^ (1 << bit)) for i in range(count)]
        )
        buf = keep + got.astype(jnp.float32)
    return split_columns(buf, widths)


def fsdp_gather(values):
    count = lax.axis_size("fsdp")
    me = lax.axis_index("fsdp")
    distance = 1
    while distance < count:
        got = lax.ppermute(values, "fsdp", [(i, i ^ distance) for i in range(count)])
        low = (me & distance) == 0
        values = jnp.concatenate(
            [jnp.where(low, values, got), jnp.where(low, got, values)]
        )
        distance *= 2
    return values


def all_sum(values):
    for axis in ("tensor", "fsdp"):
        distance = 1
        while distance < lax.axis_size(axis):
            values = values + lax.ppermute(
                values, axis, [(i, i ^ distance) for i in range(lax.axis_size(axis))]
            )
            distance *= 2
    return values


def exchange(values, distance):
    count = lax.axis_size("tensor")
    return lax.ppermute(values, "tensor", [(i, i ^ distance) for i in range(count)])


def token_gather(values):
    return finish_gather(values, exchange(values, 2))


def finish_gather(values, across):
    rows = values.shape[0]
    me = lax.axis_index("tensor")
    pair = jnp.stack([values, across])
    beside = exchange(pair, 1)
    full = jnp.zeros((4 * rows,) + values.shape[1:], values.dtype)
    for part, place in ((values, me), (across, me ^ 2), (beside[0], me ^ 1), (beside[1], me ^ 3)):
        full = lax.dynamic_update_slice_in_dim(full, part, place * rows, 0)
    return full


def token_sum(term, rows):
    partial = term(jnp.int32(0), rows * lax.axis_size("tensor"))
    me = lax.axis_index("tensor")

    def block(place):
        return lax.dynamic_slice_in_dim(partial, place * rows, rows, 0)

    sent = jnp.stack([block(me ^ 1), block(me ^ 3)]).astype(jnp.bfloat16)
    got = exchange(sent, 1).astype(jnp.float32)
    mine = block(me) + got[0]
    other = (block(me ^ 2) + got[1]).astype(jnp.bfloat16)
    return mine + exchange(other, 2).astype(jnp.float32)


def shards(
    hidden,
    out_grad,
    lengths,
    q_weight,
    key_matrix,
    value_matrix,
    o_weight,
    gate_weight,
    up_weight,
    down_weight,
    input_gain,
    q_gain,
    k_gain,
    post_gain,
):
    split = lax.axis_size("tensor")
    rows = hidden.shape[0]
    group_rows = rows * split
    q_heads = q_weight.shape[1] // HEAD_SIZE
    kv_heads = key_matrix.shape[1] // HEAD_SIZE
    share = q_heads // kv_heads
    scale = HEAD_SIZE ** (-0.5)
    member = lax.axis_index("fsdp")
    slot = member // PIECES
    piece = member % PIECES
    lengths_row = lax.dynamic_index_in_dim(lengths, slot, 0, keepdims=False)
    ends = jnp.cumsum(lengths_row)
    group_place = piece_places(piece, group_rows)
    passed = group_place[:, None] >= ends[None, :]
    group_start = jnp.sum(jnp.where(passed, lengths_row[None, :], 0), axis=1)
    group_offset = group_place - group_start
    local_valid = lax.dynamic_slice_in_dim(
        group_place < ends[-1], lax.axis_index("tensor") * rows, rows, 0
    )
    fs = lax.axis_size("fsdp")
    gain_sizes = (input_gain.shape[0], q_gain.shape[0], k_gain.shape[0], post_gain.shape[0])
    gains_all = fsdp_gather(
        jnp.concatenate([input_gain, q_gain, k_gain, post_gain]).astype(jnp.bfloat16)
    ).reshape(fs, sum(gain_sizes))
    gain_in, gain_query, gain_keys, gain_post = [
        part.reshape(-1) for part in split_columns(gains_all, gain_sizes)
    ]
    kv_full = lax.all_gather(
        jnp.concatenate(
            [key_matrix.astype(jnp.bfloat16), value_matrix.astype(jnp.bfloat16)], axis=1
        ),
        "fsdp",
        axis=0,
        tiled=True,
    )
    w_key, w_value = split_columns(kv_full, (key_matrix.shape[1], value_matrix.shape[1]))
    w_query = lax.all_gather(q_weight.astype(jnp.bfloat16), "fsdp", axis=0, tiled=True)
    w_out = lax.all_gather(
        jnp.transpose(o_weight).astype(jnp.bfloat16), "fsdp", axis=0, tiled=True
    )
    x_float = hidden.astype(jnp.float32)
    gain_first = gain_in.astype(jnp.float32)
    first_all = token_gather(rms_scale(x_float, gain_first).astype(jnp.bfloat16))
    cotangent = out_grad.astype(jnp.float32) * local_valid[:, None].astype(jnp.float32)
    cotangent_low, first_all = lax.optimization_barrier((cotangent.astype(jnp.bfloat16), first_all))
    cotangent_across = exchange(cotangent_low, 2)
    query_projected = jnp.dot(first_all, w_query, preferred_element_type=jnp.float32)
    key_projected = jnp.dot(first_all, w_key, preferred_element_type=jnp.float32)
    value_rows = (
        jnp.dot(first_all, w_value, preferred_element_type=jnp.float32)
        .astype(jnp.bfloat16)
        .reshape(group_rows, kv_heads, HEAD_SIZE)
    )
    gain_q = gain_query.astype(jnp.float32)
    gain_k = gain_keys.astype(jnp.float32)
    query_rope = (
        prepare_inputs(query_projected, gain_q, group_offset, q_heads)
        .astype(jnp.bfloat16)
        .reshape(group_rows, kv_heads, share, HEAD_SIZE)
    )
    key_rope = prepare_inputs(key_projected, gain_k, group_offset, kv_heads).astype(jnp.bfloat16)
    quarter = group_rows // 2
    query_start = jnp.broadcast_to(group_start[:, None], (group_rows, 128))
    starts_by_block = group_start.reshape(group_rows // 512, 512)
    query_bounds = jnp.stack([jnp.min(starts_by_block, axis=1), jnp.max(starts_by_block, axis=1)])
    query_t = jnp.transpose(query_rope, (1, 2, 0, 3))
    own_keys = jnp.transpose(key_rope, (1, 0, 2))
    own_values = jnp.transpose(value_rows, (1, 0, 2))
    moved = swapped(jnp.stack([own_keys, own_values]), "fsdp", 0)
    sums = jnp.zeros(query_t.shape, jnp.float32)
    totals = jnp.zeros(query_t.shape[:3] + (128,), jnp.float32)
    sums, totals = attention_forward(
        query_t, query_start, query_bounds, own_keys, own_values, sums, totals, piece, quarter, 0
    )
    cotangent_across, sums, totals = lax.optimization_barrier((cotangent_across, sums, totals))
    mlp_grad_all = finish_gather(cotangent_low, cotangent_across)
    sums, totals_t = attention_forward(
        query_t, query_start, query_bounds, moved[0], moved[1], sums, totals, piece, quarter, 1
    )
    mlp_grad_all, sums, totals_t = lax.optimization_barrier((mlp_grad_all, sums, totals_t))
    heads_t = sums / totals_t[..., :1]
    heads_out = jnp.transpose(heads_t, (2, 0, 1, 3))
    row_totals = jnp.transpose(totals_t[..., 0], (2, 0, 1))
    out_rows = heads_out.reshape(group_rows, q_heads * HEAD_SIZE).astype(jnp.bfloat16)

    mlp_full = lax.all_gather(
        jnp.concatenate(
            [
                gate_weight.astype(jnp.bfloat16),
                up_weight.astype(jnp.bfloat16),
                jnp.transpose(down_weight).astype(jnp.bfloat16),
            ],
            axis=1,
        ),
        "fsdp",
        axis=0,
        tiled=True,
    )
    w_gate, w_up, w_down_t = split_columns(
        mlp_full, (gate_weight.shape[1], up_weight.shape[1], down_weight.shape[0])
    )
    out_partial = contract_last(out_rows, w_out)
    late_grad_all, out_partial = lax.optimization_barrier((mlp_grad_all, out_partial))
    grad_act = jnp.dot(late_grad_all, w_down_t, preferred_element_type=jnp.float32)
    after_attn = x_float + token_sum(lambda start, count: out_partial, rows)
    grad_act, after_attn = lax.optimization_barrier((grad_act, after_attn))
    gain_second = gain_post.astype(jnp.float32)
    second_all = token_gather(rms_scale(after_attn, gain_second).astype(jnp.bfloat16))
    gate_out = jnp.dot(second_all, w_gate, preferred_element_type=jnp.float32)
    up_out = jnp.dot(second_all, w_up, preferred_element_type=jnp.float32)
    activated = (jax.nn.silu(gate_out) * up_out).astype(jnp.bfloat16)

    unused, pull_gate = jax.vjp(
        lambda gate_in, up_in: jax.nn.silu(gate_in) * up_in, gate_out, up_out
    )
    grad_gate, grad_up = pull_gate(grad_act)
    grad_gate = grad_gate.astype(jnp.bfloat16)
    grad_up = grad_up.astype(jnp.bfloat16)
    second_partial = contract_last(grad_gate, w_gate) + contract_last(grad_up, w_up)
    grad_inputs, second_partial = lax.optimization_barrier(
        ((mlp_grad_all, activated, second_all, grad_gate, grad_up), second_partial)
    )
    late_c, late_act, late_second, late_gate, late_up = grad_inputs
    down_grad_t = contract_rows(late_c, late_act)
    gate_grad = contract_rows(late_second, late_gate)
    up_grad = contract_rows(late_second, late_up)
    second_back = token_sum(lambda start, count: second_partial, rows)
    unused, pull_second = jax.vjp(rms_scale, after_attn, gain_second)
    norm_second_grad, post_gain_part = pull_second(second_back)
    residual_grad = cotangent + norm_second_grad
    weight_grads, residual_grad = lax.optimization_barrier(
        ((gate_grad, up_grad, down_grad_t), residual_grad)
    )
    gate_grad, up_grad, down_grad_t = weight_grads
    attn_grad_all = token_gather(residual_grad.astype(jnp.bfloat16))
    activated_late, attn_grad_all = lax.optimization_barrier((activated, attn_grad_all))
    down_rows = token_sum(lambda start, count: contract_last(activated_late, w_down_t), rows)
    out_weight_grad_t = contract_rows(attn_grad_all, out_rows)
    mlp_packed = jnp.concatenate(
        [g.astype(jnp.bfloat16) for g in (gate_grad, up_grad, down_grad_t, out_weight_grad_t)],
        axis=1,
    )
    head_grad = jnp.dot(attn_grad_all, w_out, preferred_element_type=jnp.float32).astype(
        jnp.bfloat16
    )
    head_float = head_grad.astype(jnp.float32).reshape(group_rows, kv_heads, share, HEAD_SIZE)
    scaled_grad = (head_float / row_totals[..., None]).astype(jnp.bfloat16)
    delta = jnp.sum(head_float * heads_out, axis=-1) / row_totals

    grad_t = jnp.transpose(scaled_grad, (1, 2, 0, 3))
    delta_t = jnp.broadcast_to(
        jnp.transpose(delta, (1, 2, 0))[..., None], (kv_heads, share, group_rows, 128)
    )
    mlp_packed, grad_t, delta_t = lax.optimization_barrier((mlp_packed, grad_t, delta_t))
    mlp_shards = split_columns(
        lax.psum_scatter(mlp_packed, "fsdp", scatter_dimension=0, tiled=True),
        [g.shape[1] for g in (gate_grad, up_grad, down_grad_t, out_weight_grad_t)],
    )
    mlp_shards = [part.astype(jnp.float32) for part in mlp_shards]
    dq_raw, dk_far, dv_far = attention_backward(
        query_t, grad_t, delta_t, query_start, query_bounds, moved[0], moved[1],
        jnp.zeros(query_t.shape, jnp.float32), piece, quarter, 1,
    )
    unseen = (piece == 1) & (jnp.arange(group_rows) >= quarter)
    far_grads = jnp.where(unseen[None, None, :, None], 0.0, jnp.stack([dk_far, dv_far]))
    returned = swapped(far_grads.astype(jnp.bfloat16), "fsdp", 0)
    down_rows, dq_raw = lax.optimization_barrier((down_rows, dq_raw))
    output = (after_attn + down_rows).astype(jnp.bfloat16)
    dq_raw, dk_own, dv_own = attention_backward(
        query_t, grad_t, delta_t, query_start, query_bounds, own_keys, own_values,
        dq_raw, piece, quarter, 0,
    )
    mlp_shards, dq_raw = lax.optimization_barrier((mlp_shards, dq_raw))
    grad_keys_total = jnp.transpose(dk_own + returned[0].astype(jnp.float32), (1, 0, 2))
    grad_values_total = jnp.transpose(dv_own + returned[1].astype(jnp.float32), (1, 0, 2))
    query_grads = jnp.transpose(dq_raw, (2, 0, 1, 3)) * scale
    query_grads = query_grads.reshape(group_rows, q_heads, HEAD_SIZE)
    unused, pull_query = jax.vjp(
        lambda projected, gain: prepare_inputs(projected, gain, group_offset, q_heads),
        query_projected,
        gain_q,
    )
    query_proj_grad, q_gain_part = pull_query(query_grads)
    unused, pull_key = jax.vjp(
        lambda projected, gain: prepare_inputs(projected, gain, group_offset, kv_heads),
        key_projected,
        gain_k,
    )
    key_proj_grad, k_gain_part = pull_key(grad_keys_total)
    query_low = query_proj_grad.astype(jnp.bfloat16)
    key_low = key_proj_grad.astype(jnp.bfloat16)
    value_low = grad_values_total.reshape(group_rows, kv_heads * HEAD_SIZE).astype(jnp.bfloat16)
    query_weight_grad = contract_rows(first_all, query_low)
    key_weight_grad = contract_rows(first_all, key_low)
    value_weight_grad = contract_rows(first_all, value_low)

    def first_term(start, count):
        return (
            contract_last(query_low, w_query)
            + contract_last(key_low, w_key)
            + contract_last(value_low, w_value)
        )

    first_back = token_sum(first_term, rows)
    unused, pull_first = jax.vjp(rms_scale, x_float, gain_first)
    norm_first_grad, input_gain_part = pull_first(first_back)
    input_grad = (residual_grad + norm_first_grad).astype(jnp.bfloat16)
    (query_shard,) = halving_scatter((query_weight_grad,))
    key_shard, value_shard = halving_scatter((key_weight_grad, value_weight_grad))
    gain_totals = all_sum(
        jnp.concatenate([input_gain_part, q_gain_part, k_gain_part, post_gain_part])
    )
    member_f = lax.axis_index("fsdp")
    sizes = (input_gain.shape[0], q_gain.shape[0], k_gain.shape[0], post_gain.shape[0])
    gain_shards = []
    at = 0
    for own in sizes:
        whole = own * fs
        gain_shards.append(lax.dynamic_slice_in_dim(gain_totals, at + member_f * own, own, 0))
        at += whole
    input_gain_shard, q_gain_shard, k_gain_shard, post_gain_shard = gain_shards
    gate_shard, up_shard, down_shard_t, out_shard_t = mlp_shards
    return (
        output,
        input_grad,
        query_shard,
        key_shard,
        value_shard,
        jnp.transpose(out_shard_t),
        gate_shard,
        up_shard,
        jnp.transpose(down_shard_t),
        input_gain_shard,
        q_gain_shard,
        k_gain_shard,
        post_gain_shard,
    )


def solution(mesh):
    return layer_program(mesh)


def layer_program(mesh):
    placed = (
        P(("fsdp", "tensor"), None),
        P(("fsdp", "tensor"), None),
        P(),
        P("fsdp", "tensor"),
        P("fsdp", "tensor"),
        P("fsdp", "tensor"),
        P("tensor", "fsdp"),
        P("fsdp", "tensor"),
        P("fsdp", "tensor"),
        P("tensor", "fsdp"),
        P("fsdp"),
        P("fsdp"),
        P("fsdp"),
        P("fsdp"),
    )
    return jax.shard_map(
        shards,
        mesh=mesh,
        in_specs=placed,
        out_specs=(
            P(("fsdp", "tensor"), None),
            P(("fsdp", "tensor"), None),
            P("fsdp", "tensor"),
            P("fsdp", "tensor"),
            P("fsdp", "tensor"),
            P("tensor", "fsdp"),
            P("fsdp", "tensor"),
            P("fsdp", "tensor"),
            P("tensor", "fsdp"),
            P("fsdp"),
            P("fsdp"),
            P("fsdp"),
            P("fsdp"),
        ),
        check_vma=False,
    )
```

```python
import functools

import numpy as np
import jax
import jax.numpy as jnp
from jax import lax
from jax.experimental import pallas as pl
from jax.experimental.pallas import tpu as pltpu
from jax.sharding import PartitionSpec as P


HEAD_SIZE = 128
TRANS_B = (((1,), (1,)), ((), ()))
TRANS_A = (((0,), (0,)), ((), ()))


def _own_place(p, quarter, r):
    return (p * quarter + r) if r < quarter else ((3 - p) * quarter + r - quarter)


def _far_place(p, quarter, r):
    return ((1 - p) * quarter + r) if r < quarter else ((2 + p) * quarter + r - quarter)


def _pair_tables(p, quarter, block, by_key, source):
    rows = 2 * quarter
    count = rows // block
    kmap = {}
    for src, fn in ((0, _own_place), (1, _far_place)):
        for j in range(count):
            kmap[fn(p, quarter, j * block) // block] = (src, j)
    pairs = []
    for j in range(count):
        qpb = _own_place(p, quarter, j * block) // block
        for kpb in range(qpb + 1):
            if kmap[kpb][0] == source:
                pairs.append((j, qpb, kpb))
    if by_key:
        pairs.sort(key=lambda t: (t[2], t[0]))
    group = [t[2] if by_key else t[0] for t in pairs]
    size = len(pairs)
    first = [1 if n == 0 or group[n - 1] != group[n] else 0 for n in range(size)]
    last = [1 if n == size - 1 or group[n + 1] != group[n] else 0 for n in range(size)]
    return np.array(
        [
            [t[0] for t in pairs],
            [t[1] for t in pairs],
            [t[2] for t in pairs],
            [kmap[t[2]][0] for t in pairs],
            [kmap[t[2]][1] for t in pairs],
            first,
            last,
        ],
        np.int32,
    )


def pair_tables(piece, quarter, block, by_key, source):
    t0 = _pair_tables(0, quarter, block, by_key, source)
    t1 = _pair_tables(1, quarter, block, by_key, source)
    assert t0.shape == t1.shape
    return jnp.where(piece == 0, jnp.asarray(t0), jnp.asarray(t1))


def _mask(qpb, kpb, qs, block):
    qp = qpb * block + lax.broadcasted_iota(jnp.int32, (block, block), 0)
    kp = kpb * block + lax.broadcasted_iota(jnp.int32, (block, block), 1)
    start = jnp.tile(qs, (1, block // 128))
    return (kp >= start) & (kp <= qp)


def _block_kind(tab_ref, qb_ref, n, block):
    j = tab_ref[0, n]
    key_first = tab_ref[2, n] * block
    key_last = key_first + block - 1
    full = (key_last < tab_ref[1, n] * block) & (key_first >= qb_ref[1, j])
    empty = key_last < qb_ref[0, j]
    return full, jnp.logical_not(full) & jnp.logical_not(empty)


def _fwd_kernel(tab_ref, qb_ref, q_ref, qs_ref, k_ref, v_ref, a_in_ref, l_in_ref, a_ref, l_ref, acc_ref, sum_ref, *, scale, block):
    n = pl.program_id(1)
    share = q_ref.shape[1]

    @pl.when(tab_ref[5, n] == 1)
    def _():
        acc_ref[...] = a_in_ref[0].reshape(share * block, HEAD_SIZE)
        sum_ref[...] = l_in_ref[0][:, :, :1]

    def step(masked):
        q = q_ref[0].reshape(share * block, HEAD_SIZE)
        k = k_ref[0]
        v = v_ref[0]
        s = lax.dot_general(q, k, TRANS_B, preferred_element_type=jnp.float32) * scale
        e = jnp.exp(s.reshape(share, block, block))
        if masked:
            allowed = _mask(tab_ref[1, n], tab_ref[2, n], qs_ref[...], block)
            e = jnp.where(allowed[None], e, 0.0)
        sum_ref[...] += jnp.sum(e, axis=-1, keepdims=True)
        acc_ref[...] += jnp.dot(
            e.reshape(share * block, block).astype(jnp.bfloat16), v, preferred_element_type=jnp.float32
        )

    full, partial = _block_kind(tab_ref, qb_ref, n, block)
    pl.when(full)(lambda: step(False))
    pl.when(partial)(lambda: step(True))

    @pl.when(tab_ref[6, n] == 1)
    def _():
        a_ref[0] = acc_ref[...].reshape(share, block, HEAD_SIZE)
        l_ref[0] = jnp.broadcast_to(sum_ref[...], (share, block, 128))


def attention_forward(q, qs, qb, keys, values, a_in, l_in, piece, quarter, source, block=512):
    kvh, share, _, _ = q.shape
    tab = pair_tables(piece, quarter, block, False, source)
    npairs = tab.shape[1]
    scale = HEAD_SIZE ** (-0.5)
    row_spec = pl.BlockSpec((1, share, block, HEAD_SIZE), lambda h, n, t, b: (h, 0, t[0, n], 0))
    lane_spec = pl.BlockSpec((1, share, block, 128), lambda h, n, t, b: (h, 0, t[0, n], 0))
    key_spec = pl.BlockSpec((1, block, HEAD_SIZE), lambda h, n, t, b: (h, t[4, n], 0))
    grid_spec = pltpu.PrefetchScalarGridSpec(
        num_scalar_prefetch=2,
        grid=(kvh, npairs),
        in_specs=[
            row_spec,
            pl.BlockSpec((block, 128), lambda h, n, t, b: (t[0, n], 0)),
            key_spec,
            key_spec,
            row_spec,
            lane_spec,
        ],
        out_specs=[row_spec, lane_spec],
        scratch_shapes=[
            pltpu.VMEM((share * block, HEAD_SIZE), jnp.float32),
            pltpu.VMEM((share, block, 1), jnp.float32),
        ],
    )
    flops = 4 * kvh * npairs * share * block * block * HEAD_SIZE
    return pl.pallas_call(
        functools.partial(_fwd_kernel, scale=scale, block=block),
        grid_spec=grid_spec,
        out_shape=[
            jax.ShapeDtypeStruct(a_in.shape, jnp.float32),
            jax.ShapeDtypeStruct(l_in.shape, jnp.float32),
        ],
        input_output_aliases={6: 0, 7: 1},
        compiler_params=pltpu.CompilerParams(
            dimension_semantics=("arbitrary", "arbitrary"), vmem_limit_bytes=48 * 1024 * 1024
        ),
        cost_estimate=pl.CostEstimate(
            flops=flops,
            transcendentals=kvh * npairs * share * block * block,
            bytes_accessed=kvh * npairs * (8 * block * HEAD_SIZE * 2),
        ),
        name="attn_fwd",
    )(tab, qb, q, qs, keys, values, a_in, l_in)


def _bwd_kernel(tab_ref, qb_ref, q_ref, h_ref, dl_ref, qs_ref, k_ref, v_ref, dq_in_ref, dq_ref, dk_ref, dv_ref, dk_acc, dv_acc, *, scale, block):
    n = pl.program_id(1)
    share = q_ref.shape[1]

    @pl.when(n == 0)
    def _():
        dq_ref[...] = dq_in_ref[...]

    @pl.when(tab_ref[5, n] == 1)
    def _():
        dk_acc[...] = jnp.zeros(dk_acc.shape, dk_acc.dtype)
        dv_acc[...] = jnp.zeros(dv_acc.shape, dv_acc.dtype)

    def step(masked):
        q = q_ref[0].reshape(share * block, HEAD_SIZE)
        hh = h_ref[0].reshape(share * block, HEAD_SIZE)
        k = k_ref[0]
        v = v_ref[0]
        s = lax.dot_general(q, k, TRANS_B, preferred_element_type=jnp.float32) * scale
        e = jnp.exp(s.reshape(share, block, block))
        if masked:
            allowed = _mask(tab_ref[1, n], tab_ref[2, n], qs_ref[...], block)
            e = jnp.where(allowed[None], e, 0.0)
        dp = lax.dot_general(hh, v, TRANS_B, preferred_element_type=jnp.float32).reshape(share, block, block)
        delta = jnp.tile(dl_ref[0], (1, 1, block // 128))
        ds = (e * (dp - delta)).reshape(share * block, block).astype(jnp.bfloat16)
        rows = pl.ds(pl.multiple_of(tab_ref[0, n] * block, block), block)
        dq_ref[0, :, rows, :] += jnp.dot(ds, k, preferred_element_type=jnp.float32).reshape(share, block, HEAD_SIZE)
        dk_acc[...] += lax.dot_general(ds, q, TRANS_A, preferred_element_type=jnp.float32)
        dv_acc[...] += lax.dot_general(
            e.reshape(share * block, block).astype(jnp.bfloat16), hh, TRANS_A, preferred_element_type=jnp.float32
        )

    full, partial = _block_kind(tab_ref, qb_ref, n, block)
    pl.when(full)(lambda: step(False))
    pl.when(partial)(lambda: step(True))

    @pl.when(tab_ref[6, n] == 1)
    def _():
        dk_ref[0] = dk_acc[...] * scale
        dv_ref[0] = dv_acc[...]


def attention_backward(q, hgrad, delta, qs, qb, keys, values, dq_in, piece, quarter, source, block=512):
    kvh, share, rows, _ = q.shape
    tab = pair_tables(piece, quarter, block, True, source)
    npairs = tab.shape[1]
    scale = HEAD_SIZE ** (-0.5)
    row_spec = pl.BlockSpec((1, share, block, HEAD_SIZE), lambda h, n, t, b: (h, 0, t[0, n], 0))
    key_spec = pl.BlockSpec((1, block, HEAD_SIZE), lambda h, n, t, b: (h, t[4, n], 0))
    full_spec = pl.BlockSpec((1, share, rows, HEAD_SIZE), lambda h, n, t, b: (h, 0, 0, 0))
    grid_spec = pltpu.PrefetchScalarGridSpec(
        num_scalar_prefetch=2,
        grid=(kvh, npairs),
        in_specs=[
            row_spec,
            row_spec,
            pl.BlockSpec((1, share, block, 128), lambda h, n, t, b: (h, 0, t[0, n], 0)),
            pl.BlockSpec((block, 128), lambda h, n, t, b: (t[0, n], 0)),
            key_spec,
            key_spec,
            full_spec,
        ],
        out_specs=[full_spec, key_spec, key_spec],
        scratch_shapes=[
            pltpu.VMEM((block, HEAD_SIZE), jnp.float32),
            pltpu.VMEM((block, HEAD_SIZE), jnp.float32),
        ],
    )
    flops = 10 * kvh * npairs * share * block * block * HEAD_SIZE
    return pl.pallas_call(
        functools.partial(_bwd_kernel, scale=scale, block=block),
        grid_spec=grid_spec,
        out_shape=[
            jax.ShapeDtypeStruct(dq_in.shape, jnp.float32),
            jax.ShapeDtypeStruct(keys.shape, jnp.float32),
            jax.ShapeDtypeStruct(values.shape, jnp.float32),
        ],
        input_output_aliases={8: 0},
        compiler_params=pltpu.CompilerParams(
            dimension_semantics=("arbitrary", "arbitrary"), vmem_limit_bytes=56 * 1024 * 1024
        ),
        cost_estimate=pl.CostEstimate(
            flops=flops,
            transcendentals=kvh * npairs * share * block * block,
            bytes_accessed=kvh * npairs * (10 * block * HEAD_SIZE * 2),
        ),
        name="attn_bwd",
    )(tab, qb, q, hgrad, delta, qs, keys, values, dq_in)


PIECES = 2


EPSILON = 1e-06
THETA = 1000000.0


def swapped(shard, axis, distance):
    return lax.ppermute(shard, axis, [(i, i ^ 1 << distance) for i in range(lax.axis_size(axis))])


def rms_scale(values, gain):
    inverse = lax.rsqrt(jnp.mean(values * values, axis=-1, keepdims=True) + EPSILON)
    return values * inverse * gain


def rotary(values, start_offset):
    half = values.shape[-1] // 2
    frequency = THETA ** (-(jnp.arange(half, dtype=jnp.float32) * 2.0 / values.shape[-1]))
    angle = start_offset.astype(jnp.float32)[:, None] * frequency[None, :]
    cosine = jnp.cos(angle)[:, None, :]
    sine = jnp.sin(angle)[:, None, :]
    first = values[..., :half]
    second = values[..., half:]
    return jnp.concatenate(
        [first * cosine - second * sine, second * cosine + first * sine], axis=-1
    )


def prepare_inputs(projected, gain, start_offset, head_groups):
    shaped = projected.reshape(projected.shape[0], head_groups, -1)
    return rotary(rms_scale(shaped, gain), start_offset)


def piece_places(which, group_rows):
    quarter = group_rows // 2
    local = jnp.arange(group_rows, dtype=jnp.int32)
    chosen = jnp.where(local < quarter, which, 3 - which)
    return chosen * quarter + local % quarter


def contract_rows(left, right):
    return lax.dot_general(
        left, right, (((0,), (0,)), ((), ())), preferred_element_type=jnp.float32
    )


def contract_last(left, right):
    return lax.dot_general(
        left, right, (((1,), (1,)), ((), ())), preferred_element_type=jnp.float32
    )


def split_columns(full, widths):
    parts = []
    at = 0
    for width in widths:
        parts.append(full[:, at : at + width])
        at += width
    return parts


def halving_scatter(grads):
    widths = [g.shape[1] for g in grads]
    packed = jnp.concatenate(grads, axis=1)
    count = lax.axis_size("fsdp")
    me = lax.axis_index("fsdp")
    bits = count.bit_length() - 1
    rows_f = packed.shape[0] // count
    order = [int(format(b, f"0{bits}b")[::-1], 2) for b in range(count)]
    buf = jnp.concatenate([packed[b * rows_f : (b + 1) * rows_f] for b in order], axis=0)
    for bit in range(bits):
        half = buf.shape[0] // 2
        mine = (me >> bit) & 1
        keep = lax.dynamic_slice_in_dim(buf, mine * half, half, 0)
        send = lax.dynamic_slice_in_dim(buf, (1 - mine) * half, half, 0)
        got = lax.ppermute(
            send.astype(jnp.bfloat16), "fsdp", [(i, i ^ (1 << bit)) for i in range(count)]
        )
        buf = keep + got.astype(jnp.float32)
    return split_columns(buf, widths)


def fsdp_gather(values):
    count = lax.axis_size("fsdp")
    me = lax.axis_index("fsdp")
    distance = 1
    while distance < count:
        got = lax.ppermute(values, "fsdp", [(i, i ^ distance) for i in range(count)])
        low = (me & distance) == 0
        values = jnp.concatenate(
            [jnp.where(low, values, got), jnp.where(low, got, values)]
        )
        distance *= 2
    return values


def all_sum(values):
    for axis in ("tensor", "fsdp"):
        distance = 1
        while distance < lax.axis_size(axis):
            values = values + lax.ppermute(
                values, axis, [(i, i ^ distance) for i in range(lax.axis_size(axis))]
            )
            distance *= 2
    return values


def exchange(values, distance):
    count = lax.axis_size("tensor")
    return lax.ppermute(values, "tensor", [(i, i ^ distance) for i in range(count)])


def token_gather(values):
    return finish_gather(values, exchange(values, 2))


def finish_gather(values, across):
    rows = values.shape[0]
    me = lax.axis_index("tensor")
    pair = jnp.stack([values, across])
    beside = exchange(pair, 1)
    full = jnp.zeros((4 * rows,) + values.shape[1:], values.dtype)
    for part, place in ((values, me), (across, me ^ 2), (beside[0], me ^ 1), (beside[1], me ^ 3)):
        full = lax.dynamic_update_slice_in_dim(full, part, place * rows, 0)
    return full


def token_sum(term, rows):
    partial = term(jnp.int32(0), rows * lax.axis_size("tensor"))
    me = lax.axis_index("tensor")

    def block(place):
        return lax.dynamic_slice_in_dim(partial, place * rows, rows, 0)

    sent = jnp.stack([block(me ^ 1), block(me ^ 3)]).astype(jnp.bfloat16)
    got = exchange(sent, 1).astype(jnp.float32)
    mine = block(me) + got[0]
    other = (block(me ^ 2) + got[1]).astype(jnp.bfloat16)
    return mine + exchange(other, 2).astype(jnp.float32)


def shards(
    hidden,
    out_grad,
    lengths,
    q_weight,
    key_matrix,
    value_matrix,
    o_weight,
    gate_weight,
    up_weight,
    down_weight,
    input_gain,
    q_gain,
    k_gain,
    post_gain,
):
    split = lax.axis_size("tensor")
    rows = hidden.shape[0]
    group_rows = rows * split
    q_heads = q_weight.shape[1] // HEAD_SIZE
    kv_heads = key_matrix.shape[1] // HEAD_SIZE
    share = q_heads // kv_heads
    scale = HEAD_SIZE ** (-0.5)
    member = lax.axis_index("fsdp")
    slot = member // PIECES
    piece = member % PIECES
    lengths_row = lax.dynamic_index_in_dim(lengths, slot, 0, keepdims=False)
    ends = jnp.cumsum(lengths_row)
    group_place = piece_places(piece, group_rows)
    passed = group_place[:, None] >= ends[None, :]
    group_start = jnp.sum(jnp.where(passed, lengths_row[None, :], 0), axis=1)
    group_offset = group_place - group_start
    local_valid = lax.dynamic_slice_in_dim(
        group_place < ends[-1], lax.axis_index("tensor") * rows, rows, 0
    )
    fs = lax.axis_size("fsdp")
    gain_sizes = (input_gain.shape[0], q_gain.shape[0], k_gain.shape[0], post_gain.shape[0])
    gains_all = fsdp_gather(
        jnp.concatenate([input_gain, q_gain, k_gain, post_gain]).astype(jnp.bfloat16)
    ).reshape(fs, sum(gain_sizes))
    gain_in, gain_query, gain_keys, gain_post = [
        part.reshape(-1) for part in split_columns(gains_all, gain_sizes)
    ]
    kv_full = lax.all_gather(
        jnp.concatenate(
            [key_matrix.astype(jnp.bfloat16), value_matrix.astype(jnp.bfloat16)], axis=1
        ),
        "fsdp",
        axis=0,
        tiled=True,
    )
    w_key, w_value = split_columns(kv_full, (key_matrix.shape[1], value_matrix.shape[1]))
    w_query = lax.all_gather(q_weight.astype(jnp.bfloat16), "fsdp", axis=0, tiled=True)
    od_full = lax.all_gather(
        jnp.concatenate(
            [
                jnp.transpose(o_weight).astype(jnp.bfloat16),
                jnp.transpose(down_weight).astype(jnp.bfloat16),
            ],
            axis=1,
        ),
        "fsdp",
        axis=0,
        tiled=True,
    )
    w_out, w_down_t = split_columns(od_full, (o_weight.shape[0], down_weight.shape[0]))
    x_float = hidden.astype(jnp.float32)
    gain_first = gain_in.astype(jnp.float32)
    first_all = token_gather(rms_scale(x_float, gain_first).astype(jnp.bfloat16))
    cotangent = out_grad.astype(jnp.float32) * local_valid[:, None].astype(jnp.float32)
    cotangent_low, first_all = lax.optimization_barrier((cotangent.astype(jnp.bfloat16), first_all))
    cotangent_across = exchange(cotangent_low, 2)
    query_projected = jnp.dot(first_all, w_query, preferred_element_type=jnp.float32)
    key_projected = jnp.dot(first_all, w_key, preferred_element_type=jnp.float32)
    value_rows = (
        jnp.dot(first_all, w_value, preferred_element_type=jnp.float32)
        .astype(jnp.bfloat16)
        .reshape(group_rows, kv_heads, HEAD_SIZE)
    )
    gain_q = gain_query.astype(jnp.float32)
    gain_k = gain_keys.astype(jnp.float32)
    query_rope = (
        prepare_inputs(query_projected, gain_q, group_offset, q_heads)
        .astype(jnp.bfloat16)
        .reshape(group_rows, kv_heads, share, HEAD_SIZE)
    )
    key_rope = prepare_inputs(key_projected, gain_k, group_offset, kv_heads).astype(jnp.bfloat16)
    quarter = group_rows // 2
    query_start = jnp.broadcast_to(group_start[:, None], (group_rows, 128))
    starts_by_block = group_start.reshape(group_rows // 512, 512)
    query_bounds = jnp.stack([jnp.min(starts_by_block, axis=1), jnp.max(starts_by_block, axis=1)])
    query_t = jnp.transpose(query_rope, (1, 2, 0, 3))
    own_keys = jnp.transpose(key_rope, (1, 0, 2))
    own_values = jnp.transpose(value_rows, (1, 0, 2))
    moved = swapped(jnp.stack([own_keys, own_values]), "fsdp", 0)
    sums = jnp.zeros(query_t.shape, jnp.float32)
    totals = jnp.zeros(query_t.shape[:3] + (128,), jnp.float32)
    sums, totals = attention_forward(
        query_t, query_start, query_bounds, own_keys, own_values, sums, totals, piece, quarter, 0
    )
    cotangent_across, sums, totals = lax.optimization_barrier((cotangent_across, sums, totals))
    mlp_grad_all = finish_gather(cotangent_low, cotangent_across)
    sums, totals_t = attention_forward(
        query_t, query_start, query_bounds, moved[0], moved[1], sums, totals, piece, quarter, 1
    )
    mlp_grad_all, sums, totals_t = lax.optimization_barrier((mlp_grad_all, sums, totals_t))
    heads_t = sums / totals_t[..., :1]
    heads_out = jnp.transpose(heads_t, (2, 0, 1, 3))
    row_totals = jnp.transpose(totals_t[..., 0], (2, 0, 1))
    out_rows = heads_out.reshape(group_rows, q_heads * HEAD_SIZE).astype(jnp.bfloat16)

    mlp_full = lax.all_gather(
        jnp.concatenate(
            [
                gate_weight.astype(jnp.bfloat16),
                up_weight.astype(jnp.bfloat16),
            ],
            axis=1,
        ),
        "fsdp",
        axis=0,
        tiled=True,
    )
    w_gate, w_up = split_columns(mlp_full, (gate_weight.shape[1], up_weight.shape[1]))
    out_partial = contract_last(out_rows, w_out)
    late_grad_all, out_partial = lax.optimization_barrier((mlp_grad_all, out_partial))
    grad_act = jnp.dot(late_grad_all, w_down_t, preferred_element_type=jnp.float32)
    after_attn = x_float + token_sum(lambda start, count: out_partial, rows)
    grad_act, after_attn = lax.optimization_barrier((grad_act, after_attn))
    gain_second = gain_post.astype(jnp.float32)
    second_all = token_gather(rms_scale(after_attn, gain_second).astype(jnp.bfloat16))
    gate_out = jnp.dot(second_all, w_gate, preferred_element_type=jnp.float32)
    up_out = jnp.dot(second_all, w_up, preferred_element_type=jnp.float32)
    activated = (jax.nn.silu(gate_out) * up_out).astype(jnp.bfloat16)

    unused, pull_gate = jax.vjp(
        lambda gate_in, up_in: jax.nn.silu(gate_in) * up_in, gate_out, up_out
    )
    grad_gate, grad_up = pull_gate(grad_act)
    grad_gate = grad_gate.astype(jnp.bfloat16)
    grad_up = grad_up.astype(jnp.bfloat16)
    second_partial = contract_last(grad_gate, w_gate) + contract_last(grad_up, w_up)
    grad_inputs, second_partial = lax.optimization_barrier(
        ((mlp_grad_all, activated, second_all, grad_gate, grad_up), second_partial)
    )
    late_c, late_act, late_second, late_gate, late_up = grad_inputs
    down_grad_t = contract_rows(late_c, late_act)
    gate_grad = contract_rows(late_second, late_gate)
    up_grad = contract_rows(late_second, late_up)
    second_back = token_sum(lambda start, count: second_partial, rows)
    unused, pull_second = jax.vjp(rms_scale, after_attn, gain_second)
    norm_second_grad, post_gain_part = pull_second(second_back)
    residual_grad = cotangent + norm_second_grad
    weight_grads, residual_grad = lax.optimization_barrier(
        ((gate_grad, up_grad, down_grad_t), residual_grad)
    )
    gate_grad, up_grad, down_grad_t = weight_grads
    attn_grad_all = token_gather(residual_grad.astype(jnp.bfloat16))
    activated_late, attn_grad_all = lax.optimization_barrier((activated, attn_grad_all))
    down_rows = token_sum(lambda start, count: contract_last(activated_late, w_down_t), rows)
    out_weight_grad_t = contract_rows(attn_grad_all, out_rows)
    mlp_packed = jnp.concatenate(
        [g.astype(jnp.bfloat16) for g in (gate_grad, up_grad, down_grad_t, out_weight_grad_t)],
        axis=1,
    )
    head_grad = jnp.dot(attn_grad_all, w_out, preferred_element_type=jnp.float32).astype(
        jnp.bfloat16
    )
    head_float = head_grad.astype(jnp.float32).reshape(group_rows, kv_heads, share, HEAD_SIZE)
    scaled_grad = (head_float / row_totals[..., None]).astype(jnp.bfloat16)
    delta = jnp.sum(head_float * heads_out, axis=-1) / row_totals

    grad_t = jnp.transpose(scaled_grad, (1, 2, 0, 3))
    delta_t = jnp.broadcast_to(
        jnp.transpose(delta, (1, 2, 0))[..., None], (kv_heads, share, group_rows, 128)
    )
    mlp_packed, grad_t, delta_t = lax.optimization_barrier((mlp_packed, grad_t, delta_t))
    dq_raw, dk_far, dv_far = attention_backward(
        query_t, grad_t, delta_t, query_start, query_bounds, moved[0], moved[1],
        jnp.zeros(query_t.shape, jnp.float32), piece, quarter, 1,
    )
    unseen = (piece == 1) & (jnp.arange(group_rows) >= quarter)
    far_grads = jnp.where(unseen[None, None, :, None], 0.0, jnp.stack([dk_far, dv_far]))
    returned = swapped(far_grads.astype(jnp.bfloat16), "fsdp", 0)
    down_rows, dq_raw = lax.optimization_barrier((down_rows, dq_raw))
    output = (after_attn + down_rows).astype(jnp.bfloat16)
    dq_raw, dk_own, dv_own = attention_backward(
        query_t, grad_t, delta_t, query_start, query_bounds, own_keys, own_values,
        dq_raw, piece, quarter, 0,
    )
    mlp_packed, dq_raw = lax.optimization_barrier((mlp_packed, dq_raw))
    mlp_shards = split_columns(
        lax.psum_scatter(mlp_packed, "fsdp", scatter_dimension=0, tiled=True),
        [g.shape[1] for g in (gate_grad, up_grad, down_grad_t, out_weight_grad_t)],
    )
    mlp_shards = [part.astype(jnp.float32) for part in mlp_shards]
    grad_keys_total = jnp.transpose(dk_own + returned[0].astype(jnp.float32), (1, 0, 2))
    grad_values_total = jnp.transpose(dv_own + returned[1].astype(jnp.float32), (1, 0, 2))
    query_grads = jnp.transpose(dq_raw, (2, 0, 1, 3)) * scale
    query_grads = query_grads.reshape(group_rows, q_heads, HEAD_SIZE)
    unused, pull_query = jax.vjp(
        lambda projected, gain: prepare_inputs(projected, gain, group_offset, q_heads),
        query_projected,
        gain_q,
    )
    query_proj_grad, q_gain_part = pull_query(query_grads)
    unused, pull_key = jax.vjp(
        lambda projected, gain: prepare_inputs(projected, gain, group_offset, kv_heads),
        key_projected,
        gain_k,
    )
    key_proj_grad, k_gain_part = pull_key(grad_keys_total)
    query_low = query_proj_grad.astype(jnp.bfloat16)
    key_low = key_proj_grad.astype(jnp.bfloat16)
    value_low = grad_values_total.reshape(group_rows, kv_heads * HEAD_SIZE).astype(jnp.bfloat16)
    query_weight_grad = contract_rows(first_all, query_low)
    key_weight_grad = contract_rows(first_all, key_low)
    value_weight_grad = contract_rows(first_all, value_low)

    def first_term(start, count):
        return (
            contract_last(query_low, w_query)
            + contract_last(key_low, w_key)
            + contract_last(value_low, w_value)
        )

    first_back = token_sum(first_term, rows)
    unused, pull_first = jax.vjp(rms_scale, x_float, gain_first)
    norm_first_grad, input_gain_part = pull_first(first_back)
    input_grad = (residual_grad + norm_first_grad).astype(jnp.bfloat16)
    (query_shard,) = halving_scatter((query_weight_grad,))
    key_shard, value_shard = halving_scatter((key_weight_grad, value_weight_grad))
    gain_totals = all_sum(
        jnp.concatenate([input_gain_part, q_gain_part, k_gain_part, post_gain_part])
    )
    member_f = lax.axis_index("fsdp")
    sizes = (input_gain.shape[0], q_gain.shape[0], k_gain.shape[0], post_gain.shape[0])
    gain_shards = []
    at = 0
    for own in sizes:
        whole = own * fs
        gain_shards.append(lax.dynamic_slice_in_dim(gain_totals, at + member_f * own, own, 0))
        at += whole
    input_gain_shard, q_gain_shard, k_gain_shard, post_gain_shard = gain_shards
    gate_shard, up_shard, down_shard_t, out_shard_t = mlp_shards
    return (
        output,
        input_grad,
        query_shard,
        key_shard,
        value_shard,
        jnp.transpose(out_shard_t),
        gate_shard,
        up_shard,
        jnp.transpose(down_shard_t),
        input_gain_shard,
        q_gain_shard,
        k_gain_shard,
        post_gain_shard,
    )


def solution(mesh):
    return layer_program(mesh)


def layer_program(mesh):
    placed = (
        P(("fsdp", "tensor"), None),
        P(("fsdp", "tensor"), None),
        P(),
        P("fsdp", "tensor"),
        P("fsdp", "tensor"),
        P("fsdp", "tensor"),
        P("tensor", "fsdp"),
        P("fsdp", "tensor"),
        P("fsdp", "tensor"),
        P("tensor", "fsdp"),
        P("fsdp"),
        P("fsdp"),
        P("fsdp"),
        P("fsdp"),
    )
    return jax.shard_map(
        shards,
        mesh=mesh,
        in_specs=placed,
        out_specs=(
            P(("fsdp", "tensor"), None),
            P(("fsdp", "tensor"), None),
            P("fsdp", "tensor"),
            P("fsdp", "tensor"),
            P("fsdp", "tensor"),
            P("tensor", "fsdp"),
            P("fsdp", "tensor"),
            P("fsdp", "tensor"),
            P("tensor", "fsdp"),
            P("fsdp"),
            P("fsdp"),
            P("fsdp"),
            P("fsdp"),
        ),
        check_vma=False,
    )
```
